32 devices in a mesh: seg: 16 (over z, y, x), lev: 2 (over core).
Axes of the slice: x: 2, y: 2, z: 4, core: 2. Of those that a mesh axis runs over, the one named last changes fastest.
Arguments:
- velocity_pair: float32 [2, 64, 16, 7680], P(None, 'lev', None, 'seg'), may hold values from -4 to 4
- thermal_reading: float32 [64, 16, 7680], P('lev', None, 'seg'), may hold values from 0.7 to 1.3
- layer_depth: float32 [64, 16, 7680], P('lev', None, 'seg'), may hold values from 0.5 to 1.5
- jacobian_terms: float32 [4, 16, 7680], P(None, None, 'seg'), may hold values from 0.25 to 1.5
- rotation_frequency: float32 [16, 7680], P(None, 'seg'), may hold values from -1.5 to 1.5
- integration_mass: float32 [16, 7680], P(None, 'seg'), may hold values from 0.3 to 3
- shared_vertex_label: int32 [16, 7680], P(None, 'seg'), may hold values from 0 to 69119, as said below
- column_owner_slot: int32 [4, 7680], P(None, 'seg'), may hold values from 0 to 30719, as said below
Outputs:
- dyn_state: float32 [4, 64, 16, 7680], P(None, 'lev', None, 'seg')
- phys_state: float32 [4, 64, 30720], P(None, None, ('seg', 'lev'))
- mean_thickness: float32 [30720], P(('seg', 'lev'))
The draws below stay inside these ranges and needn't reach their ends.
Inputs may be any that keep to these rules, and one draw needn't show every extreme that they name: `shared_vertex_label`: element e lies in row e // 120 and column e % 120 of a periodic grid of elements; its point 4 * i + j sits at node row 3 * (e // 120) + a and node column 3 * (e % 120) + b, modulo a node grid of 192 rows by 360 columns, where (a, b) is one of (i, j), (j, 3 - i), (3 - i, 3 - j), (3 - j, i), the same for all points of the element; a node's number is its row times 3 * 120 plus its column. `column_owner_slot`: each value occurs once. A cell with value w goes to position w % 960 of device w // 960 along seg+lev; the 1920 cells of one index of seg send at most 90 cells to one device.
All inputs are finite; a program needn't handle non-finite values.
Results may differ from the reference program's by a relative error of at most 0.0001.
Values sent between devices are 32-bit elements; how exact they have to be, the bound alone decides.
No kernel may reach another device: no remote copies, remote signals or barrier semaphores. Data moves between devices by JAX's collectives and lax.ppermute only.
A program may use at most 128 MiB of HBM per device.

```python
import math
import jax
import jax.numpy as jnp
import numpy as np
from jax import lax

LAYER_NUMBER = 64
COLS = 120
SUBSTEPS = 2
EL_DEV = 480
PATCH_SUM_ALL = 7680
PCOL = 1920
OWN = 960
PAIR = 60
N_SEG = 16
N_LEV = 2
DEVICES = 32


def draw_shared_vertex_label(key, part):
    rotations = jax.random.randint(jax.random.fold_in(key, 7), (PATCH_SUM_ALL,), 0, 4)
    element = jnp.arange(PATCH_SUM_ALL)
    grid_row = element // COLS
    grid_col = element % COLS
    points = jnp.arange(16)
    first_index = points // 4
    second_index = points % 4
    row_offsets = jnp.stack([first_index, second_index, 3 - first_index, 3 - second_index])
    col_offsets = jnp.stack([second_index, 3 - first_index, 3 - second_index, first_index])
    node_rows = 3 * (PATCH_SUM_ALL // COLS)
    node_cols = 3 * COLS
    row_of = (3 * grid_row[None, :] + row_offsets[rotations].T) % node_rows
    col_of = (3 * grid_col[None, :] + col_offsets[rotations].T) % node_cols
    return (row_of * node_cols + col_of).astype(jnp.int32)


def draw_column_owner_slot(key, part):
    chosen = jax.random.permutation(jax.random.fold_in(key, 11), N_SEG)[:6].astype(jnp.int32)
    shifts = jax.random.randint(jax.random.fold_in(key, 12), (3,), 0, N_LEV)
    extra_amounts = jax.random.randint(jax.random.fold_in(key, 13), (2,), 1, PAIR // 2 + 1)
    amounts = jnp.concatenate([jnp.full((1,), PAIR // 2, jnp.int32), extra_amounts.astype(jnp.int32)])
    anchor = N_LEV * chosen[0::2] + shifts
    target = N_LEV * chosen[1::2] + shifts
    position = jnp.arange(PCOL)
    base_group = position // PAIR
    offset = position % PAIR
    in_anchor = base_group[None, :] == anchor[:, None]
    moved = jnp.logical_and(in_anchor, offset[None, :] < amounts[:, None])
    kept_shift = jnp.logical_and(in_anchor, jnp.logical_not(moved))
    any_moved = jnp.any(moved, axis=0)
    new_group = jnp.where(any_moved, jnp.sum(moved * target[:, None], axis=0), base_group)
    rank_value = jnp.where(any_moved, PAIR + offset, offset - jnp.sum(kept_shift * amounts[:, None], axis=0))
    sources = jnp.arange(N_SEG)[:, None]
    owner_index = (sources * N_LEV + new_group[None, :]) % DEVICES
    owner_ids = jnp.arange(DEVICES)
    losses = jnp.sum((((sources * N_LEV + anchor[None, :]) % DEVICES)[:, :, None] == owner_ids) * amounts[None, :, None], axis=1)
    gains = jnp.sum((((sources * N_LEV + target[None, :]) % DEVICES)[:, :, None] == owner_ids) * amounts[None, :, None], axis=1)
    counts = PAIR - losses + gains
    start_slot = jnp.cumsum(counts, axis=0) - counts
    index_value = owner_index * OWN + jnp.take_along_axis(start_slot, owner_index, axis=1) + rank_value[None, :]
    source_keys = jax.random.split(jax.random.fold_in(key, 14), N_SEG)
    orderings = jax.vmap(lambda one_key: jax.random.permutation(one_key, PCOL))(source_keys)
    placed = jnp.zeros((N_SEG, PCOL), jnp.int32).at[sources, orderings].set(index_value.astype(jnp.int32))
    return placed.reshape(N_SEG, 4, EL_DEV).transpose(1, 0, 2).reshape(4, PATCH_SUM_ALL).astype(jnp.int32)


def level_of(key, shape, shards, smallest, top_value):
    def one(dim, shards_of):
        heights = jax.random.uniform(jax.random.fold_in(jax.random.fold_in(key, 6), dim), (shards_of,), jnp.float32, smallest / len(shards), top_value / len(shards))
        return jnp.repeat(jnp.exp(heights), shape[dim] // shards_of).reshape((-1,) + (1,) * (len(shape) - dim - 1))

    level = one(*shards[0])
    for cut in shards[1:]:
        level = level * one(*cut)
    return level


def normal_values(own_key, extent, scale, reach, cuts=(), kind=jnp.bfloat16):
    gain = level_of(own_key, extent, cuts, -0.22, 0.18) if cuts else 1.0
    values = jax.random.normal(own_key, extent, jnp.float32) * scale * gain
    return jnp.minimum(jnp.maximum(values, -reach), reach).astype(kind)


def setup_inputs(seed: int = 0) -> dict:
    key_list = jax.random.split(jax.random.key(seed), 9)
    velocity_pair = normal_values(key_list[0], (2, LAYER_NUMBER, 16, PATCH_SUM_ALL), 1.0, 4.0, ((1, 2), (3, 16)), jnp.float32)
    thermal_reading = jnp.clip(0.7 + 0.59999996 * jax.random.uniform(key_list[1], (LAYER_NUMBER, 16, PATCH_SUM_ALL), jnp.float32) ** level_of(key_list[1], (LAYER_NUMBER, 16, PATCH_SUM_ALL), ((0, 2), (2, 16)), -0.2, 0.2), 0.7, 1.3)
    layer_depth = jnp.clip(0.5 + 1.0 * jax.random.uniform(key_list[2], (LAYER_NUMBER, 16, PATCH_SUM_ALL), jnp.float32) ** level_of(key_list[2], (LAYER_NUMBER, 16, PATCH_SUM_ALL), ((0, 2), (2, 16)), -0.2, 0.2), 0.5, 1.5)
    jacobian_terms = jnp.clip(0.25 + 1.25 * jax.random.uniform(key_list[3], (4, 16, PATCH_SUM_ALL), jnp.float32) ** level_of(key_list[3], (4, 16, PATCH_SUM_ALL), ((2, 16),), -0.2, 0.2), 0.25, 1.5)
    rotation_frequency = jnp.clip(jax.random.uniform(key_list[4], (16, PATCH_SUM_ALL), jnp.float32, -1.5, 1.5) * level_of(key_list[4], (16, PATCH_SUM_ALL), ((1, 16),), -0.4, 0.0), -1.5, 1.5)
    integration_mass = jnp.clip(jnp.exp(math.log(3.0) - 2.3025851 * jax.random.uniform(key_list[5], (16, PATCH_SUM_ALL), jnp.float32) ** level_of(key_list[5], (16, PATCH_SUM_ALL), ((1, 16),), -0.2, 0.2)), 0.3, 3.0)
    shared_vertex_label = draw_shared_vertex_label(jax.random.fold_in(key_list[8], 71), 0)
    column_owner_slot = draw_column_owner_slot(jax.random.fold_in(key_list[8], 71), 0)
    return dict(velocity_pair=velocity_pair, thermal_reading=thermal_reading, layer_depth=layer_depth, jacobian_terms=jacobian_terms, rotation_frequency=rotation_frequency, integration_mass=integration_mass, shared_vertex_label=shared_vertex_label, column_owner_slot=column_owner_slot)


top_pressure = 10.0
time_increment = 0.05

def gll_slopes():
    root_five = np.sqrt(5.0)
    gll_nodes = [-1.0, -1.0 / root_five, 1.0 / root_five, 1.0]
    legendre_values = [-1.0, 1.0 / root_five, -1.0 / root_five, 1.0]
    slopes = np.zeros((4, 4))
    for row_node in range(4):
        for column in range(4):
            if row_node != column:
                slopes[row_node, column] = legendre_values[row_node] / legendre_values[column] / (gll_nodes[row_node] - gll_nodes[column])
    slopes[0, 0] = -3.0
    slopes[3, 3] = 3.0
    return slopes

def initial_axis_derivative(values):
    layout = values.shape
    grouped = values.reshape(layout[:-2] + (4, 4, layout[-1]))
    slopes = jnp.asarray(gll_slopes(), values.dtype)
    derived = jnp.einsum('ak,...kje->...aje', slopes, grouped, precision=lax.Precision.HIGHEST)
    return derived.reshape(layout)

def latter_axis_derivative(values):
    layout = values.shape
    grouped = values.reshape(layout[:-2] + (4, 4, layout[-1]))
    slopes = jnp.asarray(gll_slopes(), values.dtype)
    derived = jnp.einsum('ak,...ike->...iae', slopes, grouped, precision=lax.Precision.HIGHEST)
    return derived.reshape(layout)

def vertical_integral_relation(thermal_reading, layer_depth):
    layer_midpoint_load = top_pressure + jnp.cumsum(layer_depth, axis=0) - 0.5 * layer_depth
    surface_change_rate = thermal_reading * layer_depth / layer_midpoint_load
    return jnp.cumsum(surface_change_rate[::-1], axis=0)[::-1] - 0.5 * surface_change_rate

def tendency_step(prognostic_variables, geopotential, jacobian_terms, rotation_frequency):
    zonal_velocity = prognostic_variables[0]
    meridional_velocity = prognostic_variables[1]
    thermal_reading = prognostic_variables[2]
    layer_depth = prognostic_variables[3]
    energy = geopotential + 0.5 * (zonal_velocity * zonal_velocity + meridional_velocity * meridional_velocity)
    energy_first = initial_axis_derivative(energy)
    energy_second = latter_axis_derivative(energy)
    zonal_slope = jacobian_terms[0] * energy_first + jacobian_terms[1] * energy_second
    meridional_slope = jacobian_terms[2] * energy_first + jacobian_terms[3] * energy_second
    initial_transport = jacobian_terms[0] * zonal_velocity + jacobian_terms[2] * meridional_velocity
    latter_transport = jacobian_terms[1] * zonal_velocity + jacobian_terms[3] * meridional_velocity
    advect_with_motion = initial_transport * initial_axis_derivative(thermal_reading) + latter_transport * latter_axis_derivative(thermal_reading)
    distribute_onto_vertices = initial_axis_derivative(layer_depth * initial_transport) + latter_axis_derivative(layer_depth * latter_transport)
    return jnp.stack([zonal_velocity + time_increment * (rotation_frequency * meridional_velocity - zonal_slope), meridional_velocity - time_increment * (rotation_frequency * zonal_velocity + meridional_slope), thermal_reading - time_increment * advect_with_motion, layer_depth - time_increment * distribute_onto_vertices])

def direct_stiffness(prognostic_variables, integration_mass, shared_vertex_label):
    channels = prognostic_variables.shape[0] * prognostic_variables.shape[1]
    count_nodes = 9 * shared_vertex_label.shape[1]
    flat_ids = shared_vertex_label.reshape(-1)
    weighted = (integration_mass * prognostic_variables).reshape(channels, -1)
    totals = jnp.zeros((channels, count_nodes), jnp.float32).at[:, flat_ids].add(weighted)
    mass_total = jnp.zeros((count_nodes,), jnp.float32).at[flat_ids].add(integration_mass.reshape(-1))
    return (totals[:, flat_ids] / mass_total[flat_ids]).reshape(prognostic_variables.shape)

def to_pg_cells(average, integration_mass):
    leading = average.shape[:-2]
    elements = average.shape[-1]
    quadrants = average.reshape(leading + (2, 2, 2, 2, elements))
    weights = integration_mass.reshape(2, 2, 2, 2, elements)
    summed = lax.optimization_barrier(jnp.sum(quadrants * weights, axis=(-4, -2)))
    cell_area = lax.optimization_barrier(jnp.sum(weights, axis=(-4, -2)))
    return (summed / cell_area).reshape(leading + (4, elements))

def reference(velocity_pair, thermal_reading, layer_depth, jacobian_terms, rotation_frequency, integration_mass, shared_vertex_label, column_owner_slot):
    prognostic_variables = jnp.concatenate([velocity_pair, thermal_reading[None], layer_depth[None]], axis=0)
    running = jnp.zeros_like(prognostic_variables)
    for substep in range(SUBSTEPS):
        geopotential = vertical_integral_relation(prognostic_variables[2], prognostic_variables[3])
        advanced = tendency_step(prognostic_variables, geopotential, jacobian_terms, rotation_frequency)
        prognostic_variables = direct_stiffness(advanced, integration_mass, shared_vertex_label)
        running = running + prognostic_variables
    cell_values = to_pg_cells(running / SUBSTEPS, integration_mass)
    levels = cell_values.shape[1]
    columns = cell_values.reshape(4, levels, -1)
    phys_state = jnp.zeros((4, levels, columns.shape[2]), jnp.float32).at[:, :, column_owner_slot.reshape(-1)].set(columns)
    mean_thickness = lax.optimization_barrier(jnp.mean(phys_state[3], axis=0))
    return (prognostic_variables, phys_state, mean_thickness)
```

```python
import jax
import jax.numpy as jnp
import numpy as np
from jax import lax
from jax.sharding import PartitionSpec as P

COLS = 120
SUBSTEPS = 2


top_pressure = 10.0
time_increment = 0.05


def gll_slopes():
    root_five = np.sqrt(5.0)
    gll_nodes = [-1.0, -1.0 / root_five, 1.0 / root_five, 1.0]
    legendre_values = [-1.0, 1.0 / root_five, -1.0 / root_five, 1.0]
    slopes = np.zeros((4, 4))
    for row_node in range(4):
        for column in range(4):
            if row_node != column:
                slopes[row_node, column] = (
                    legendre_values[row_node]
                    / legendre_values[column]
                    / (gll_nodes[row_node] - gll_nodes[column])
                )
    slopes[0, 0] = -3.0
    slopes[3, 3] = 3.0
    return slopes


SLOPES = gll_slopes().astype(np.float32)


def rotation_tables():
    forward = np.zeros((4, 16), np.int32)
    for first_pos in range(4):
        for second_pos in range(4):
            canonical = 4 * first_pos + second_pos
            forward[0, canonical] = 4 * first_pos + second_pos
            forward[1, canonical] = 4 * (3 - second_pos) + first_pos
            forward[2, canonical] = 4 * (3 - first_pos) + (3 - second_pos)
            forward[3, canonical] = 4 * second_pos + 3 - first_pos
    backward = np.argsort(forward, axis=1).astype(np.int32)
    return (forward, backward)


def weighted_sum(terms):
    acc = None
    for coef, value in terms:
        if coef == 0.0:
            continue
        part = jnp.float32(coef) * value
        acc = part if acc is None else acc + part
    return acc


def first_deriv(f):
    return jnp.stack(
        [
            weighted_sum([(SLOPES[a, k], f[4 * k + j]) for k in range(4)])
            for a in range(4)
            for j in range(4)
        ]
    )


def second_deriv(f):
    return jnp.stack(
        [
            weighted_sum([(SLOPES[a, k], f[4 * i + k]) for k in range(4)])
            for i in range(4)
            for a in range(4)
        ]
    )


def carried_in(part, axis, reverse):
    count = lax.axis_size(axis)
    place = lax.axis_index(axis)
    gathered = lax.all_gather(part, axis)
    index = jnp.arange(count).reshape((count,) + (1,) * part.ndim)
    chosen = index > place if reverse else index < place
    return jnp.sum(jnp.where(chosen, gathered, jnp.zeros_like(gathered)), axis=0)


def site_potential_energy(thermal_reading, layer_depth):
    column_mass = jnp.sum(layer_depth, axis=1)
    above_sum = carried_in(column_mass, "lev", False)
    layer_midpoint_load = (
        top_pressure + above_sum[:, None, :] + jnp.cumsum(layer_depth, axis=1) - 0.5 * layer_depth
    )
    surface_change_rate = thermal_reading * layer_depth / layer_midpoint_load
    group_height = jnp.sum(surface_change_rate, axis=1)
    below_sum = carried_in(group_height, "lev", True)
    return (
        below_sum[:, None, :]
        + lax.cumsum(surface_change_rate, axis=1, reverse=True)
        - 0.5 * surface_change_rate
    )


def tendency_step(u, v, temp, dp, geopotential, jac, rot):
    energy = geopotential + 0.5 * (u * u + v * v)
    energy_first = first_deriv(energy)
    energy_second = second_deriv(energy)
    zonal_slope = jac[0] * energy_first + jac[1] * energy_second
    meridional_slope = jac[2] * energy_first + jac[3] * energy_second
    initial_transport = jac[0] * u + jac[2] * v
    latter_transport = jac[1] * u + jac[3] * v
    advect_with_motion = initial_transport * first_deriv(temp) + latter_transport * second_deriv(
        temp
    )
    distribute_onto_vertices = first_deriv(dp * initial_transport) + second_deriv(
        dp * latter_transport
    )
    return (
        u + time_increment * (rot * v - zonal_slope),
        v - time_increment * (rot * u + meridional_slope),
        temp - time_increment * advect_with_motion,
        dp - time_increment * distribute_onto_vertices,
    )


def reorder(values, rotation, table):
    rows = []
    for q in range(16):
        pick = values[int(table[3, q])]
        for w in (2, 1, 0):
            pick = jnp.where(rotation == w, values[int(table[w, q])], pick)
        rows.append(pick)
    return jnp.stack(rows)


def node_sum(canon, col, row, rows_dev):
    elements = canon.shape[-1]

    def roll(y, shift):
        return jnp.roll(y, shift, axis=-1)

    rows = [canon[q] for q in range(16)]
    for a in range(4):
        left = jnp.where(col == 0, roll(rows[4 * a + 3], -(COLS - 1)), roll(rows[4 * a + 3], 1))
        total = rows[4 * a] + left
        rows[4 * a] = total
        rows[4 * a + 3] = jnp.where(col == COLS - 1, roll(total, COLS - 1), roll(total, -1))
    seg_count = lax.axis_size("seg")
    up = [(i, (i + 1) % seg_count) for i in range(seg_count)]
    down = [(j, i) for i, j in up]
    last = jnp.stack([rows[12 + b][:, elements - COLS :] for b in range(4)])
    first = jnp.stack([rows[b][:, :COLS] for b in range(4)])
    prev_last = lax.ppermute(last, "seg", up)
    next_first = lax.ppermute(first, "seg", down)
    pad = jnp.zeros(prev_last.shape[1:-1] + (elements - COLS,), canon.dtype)
    out = list(rows)
    for b in range(4):
        halo_up = jnp.concatenate([prev_last[b], pad], axis=-1)
        from_up = jnp.where(row == 0, halo_up, roll(rows[12 + b], COLS))
        out[b] = rows[b] + from_up
        halo_down = jnp.concatenate([pad, next_first[b]], axis=-1)
        from_down = jnp.where(row == rows_dev - 1, halo_down, roll(rows[b], -COLS))
        out[12 + b] = rows[12 + b] + from_down
    return jnp.stack(out)


def local(
    velocity_pair,
    thermal_reading,
    layer_depth,
    jacobian_terms,
    rotation_frequency,
    integration_mass,
    shared_vertex_label,
    column_owner_slot,
):
    levels_dev = thermal_reading.shape[0]
    elements = thermal_reading.shape[2]
    seg_count = lax.axis_size("seg")
    lev_count = lax.axis_size("lev")
    rows_dev = elements // COLS
    node_cols = 3 * COLS
    first_row = 3 * rows_dev * lax.axis_index("seg")
    grid_rows = 3 * rows_dev * seg_count
    corner_ids = shared_vertex_label[0]
    element_pos = jnp.arange(elements)
    row_offset = (corner_ids // node_cols - first_row) % grid_rows - 3 * (element_pos // COLS)
    col_offset = (corner_ids % node_cols - 3 * (element_pos % COLS)) % node_cols
    rotation = jnp.where(
        row_offset == 0, jnp.where(col_offset == 0, 0, 1), jnp.where(col_offset == 3, 2, 3)
    )
    forward_order, backward_order = rotation_tables()
    col = element_pos % COLS
    row = element_pos // COLS

    def pm(x):
        return jnp.transpose(x, (1, 0, 2))

    u = pm(velocity_pair[0])
    v = pm(velocity_pair[1])
    temp = pm(thermal_reading)
    dp = pm(layer_depth)
    jac = jacobian_terms[:, :, None, :]
    rot = rotation_frequency[:, None, :]
    mass = integration_mass[:, None, :]
    mass_canon = reorder(mass, rotation, forward_order)
    mass_total = None
    results = []
    for substep in range(SUBSTEPS):
        geopotential = site_potential_energy(temp, dp)
        advanced = jnp.concatenate(
            tendency_step(u, v, temp, dp, geopotential, jac, rot), axis=1
        )
        weighted = reorder(advanced, rotation, forward_order) * mass_canon
        if mass_total is None:
            totals = node_sum(
                jnp.concatenate([weighted, mass_canon], axis=1), col, row, rows_dev
            )
            mass_total = totals[:, -1:]
            totals = totals[:, :-1]
        else:
            totals = node_sum(weighted, col, row, rows_dev)
        fields = reorder(totals / mass_total, rotation, backward_order)
        results.append(fields)
        u, v, temp, dp = jnp.split(fields, 4, axis=1)
    final = results[-1]
    running = results[0]
    for extra in results[1:]:
        running = running + extra
    average = running / SUBSTEPS
    channels = average.shape[1]
    groups = [(0, 1, 4, 5), (2, 3, 6, 7), (8, 9, 12, 13), (10, 11, 14, 15)]
    cells = []
    for group in groups:
        summed = (mass[group[0]] * average[group[0]] + mass[group[1]] * average[group[1]]) + (
            mass[group[2]] * average[group[2]] + mass[group[3]] * average[group[3]]
        )
        area = (mass[group[0]] + mass[group[1]]) + (mass[group[2]] + mass[group[3]])
        cells.append(summed / area)
    cell_values = jnp.stack(cells)
    payload = jnp.transpose(cell_values, (0, 2, 1)).reshape(4 * elements, channels)

    dev_count = seg_count * lev_count
    own_cols = 4 * elements * seg_count // dev_count
    per_pair = own_cols // seg_count
    capacity = per_pair + per_pair // 2
    assert capacity <= channels
    targets = column_owner_slot.reshape(-1)
    owner_index = targets // own_cols
    slot_index = targets % own_cols
    cell_count = targets.shape[0]
    cell_pos = jnp.arange(cell_count)
    same_owner = owner_index[:, None] == owner_index[None, :]
    earlier = cell_pos[None, :] < cell_pos[:, None]
    rank = jnp.sum(jnp.logical_and(same_owner, earlier).astype(jnp.int32), axis=1)
    destination = owner_index * capacity + rank
    slots = jnp.arange(dev_count * capacity)
    match = destination[None, :] == slots[:, None]
    has = jnp.any(match, axis=1)
    source_cell = jnp.sum(jnp.where(match, cell_pos[None, :], 0), axis=1)
    source_pos = jnp.sum(jnp.where(match, slot_index[None, :], 0), axis=1)
    outgoing = jnp.where(has[:, None], payload[source_cell], 0.0)
    ids = jnp.where(has, source_pos, -1).astype(jnp.float32).reshape(dev_count, capacity)
    ids = jnp.pad(ids, ((0, 0), (0, channels - capacity)), constant_values=-1.0)
    buffer = jnp.concatenate(
        [outgoing.reshape(dev_count, capacity, channels), ids[:, None, :]], axis=1
    )
    received = lax.all_to_all(buffer, ("seg", "lev"), split_axis=0, concat_axis=0, tiled=True)
    received_ids = jnp.round(received[:, capacity, :capacity]).astype(jnp.int32)
    received_rows = received[:, :capacity, :].reshape(dev_count * capacity, channels)
    flat = jnp.arange(dev_count * capacity).reshape(dev_count, capacity)
    source_lev = (jnp.arange(dev_count) % lev_count)[:, None]
    positions = jnp.arange(own_cols)
    picks = []
    for group in range(lev_count):
        hit = jnp.logical_and(
            received_ids[None, :, :] == positions[:, None, None], (source_lev == group)[None]
        )
        picks.append(jnp.sum(jnp.where(hit, flat[None], 0), axis=(1, 2)))
    arrived = received_rows[jnp.stack(picks)]
    arrived = arrived.reshape(lev_count, own_cols, 4, levels_dev).transpose(2, 0, 3, 1)
    phys_state = arrived.reshape(4, lev_count * levels_dev, own_cols)
    mean_thickness = jnp.mean(phys_state[3], axis=0)
    dyn_state = final.reshape(16, 4, levels_dev, elements).transpose(1, 2, 0, 3)
    return (dyn_state, phys_state, mean_thickness)


def solution(mesh):
    in_specs = (
        P(None, "lev", None, "seg"),
        P("lev", None, "seg"),
        P("lev", None, "seg"),
        P(None, None, "seg"),
        P(None, "seg"),
        P(None, "seg"),
        P(None, "seg"),
        P(None, "seg"),
    )
    out_specs = (P(None, "lev", None, "seg"), P(None, None, ("seg", "lev")), P(("seg", "lev")))
    return jax.shard_map(local, mesh=mesh, in_specs=in_specs, out_specs=out_specs, check_vma=False)
```

```python
import functools

import jax
import jax.numpy as jnp
import numpy as np
from jax import lax
from jax.experimental import pallas as pl
from jax.experimental.pallas import tpu as pltpu
from jax.sharding import PartitionSpec as P

COLS = 120
SUBSTEPS = 2


top_pressure = 10.0
time_increment = 0.05


def gll_slopes():
    root_five = np.sqrt(5.0)
    gll_nodes = [-1.0, -1.0 / root_five, 1.0 / root_five, 1.0]
    legendre_values = [-1.0, 1.0 / root_five, -1.0 / root_five, 1.0]
    slopes = np.zeros((4, 4))
    for row_node in range(4):
        for column in range(4):
            if row_node != column:
                slopes[row_node, column] = (
                    legendre_values[row_node]
                    / legendre_values[column]
                    / (gll_nodes[row_node] - gll_nodes[column])
                )
    slopes[0, 0] = -3.0
    slopes[3, 3] = 3.0
    return slopes


SLOPES = gll_slopes().astype(np.float32)


def rotation_tables():
    forward = np.zeros((4, 16), np.int32)
    for first_pos in range(4):
        for second_pos in range(4):
            canonical = 4 * first_pos + second_pos
            forward[0, canonical] = 4 * first_pos + second_pos
            forward[1, canonical] = 4 * (3 - second_pos) + first_pos
            forward[2, canonical] = 4 * (3 - first_pos) + (3 - second_pos)
            forward[3, canonical] = 4 * second_pos + 3 - first_pos
    backward = np.argsort(forward, axis=1).astype(np.int32)
    return (forward, backward)


def weighted_sum(terms):
    acc = None
    for coef, value in terms:
        if coef == 0.0:
            continue
        part = jnp.float32(coef) * value
        acc = part if acc is None else acc + part
    return acc


def first_deriv(f):
    return jnp.stack(
        [
            weighted_sum([(SLOPES[a, k], f[4 * k + j]) for k in range(4)])
            for a in range(4)
            for j in range(4)
        ]
    )


def second_deriv(f):
    return jnp.stack(
        [
            weighted_sum([(SLOPES[a, k], f[4 * i + k]) for k in range(4)])
            for i in range(4)
            for a in range(4)
        ]
    )


def carried_in(part, axis, reverse):
    count = lax.axis_size(axis)
    place = lax.axis_index(axis)
    gathered = lax.all_gather(part, axis)
    index = jnp.arange(count).reshape((count,) + (1,) * part.ndim)
    chosen = index > place if reverse else index < place
    return jnp.sum(jnp.where(chosen, gathered, jnp.zeros_like(gathered)), axis=0)


def site_potential_energy(thermal_reading, layer_depth):
    column_mass = jnp.sum(layer_depth, axis=1)
    above_sum = carried_in(column_mass, "lev", False)
    layer_midpoint_load = (
        top_pressure + above_sum[:, None, :] + jnp.cumsum(layer_depth, axis=1) - 0.5 * layer_depth
    )
    surface_change_rate = thermal_reading * layer_depth / layer_midpoint_load
    group_height = jnp.sum(surface_change_rate, axis=1)
    below_sum = carried_in(group_height, "lev", True)
    return (
        below_sum[:, None, :]
        + lax.cumsum(surface_change_rate, axis=1, reverse=True)
        - 0.5 * surface_change_rate
    )


def tendency_step(u, v, temp, dp, geopotential, jac, rot):
    energy = geopotential + 0.5 * (u * u + v * v)
    energy_first = first_deriv(energy)
    energy_second = second_deriv(energy)
    zonal_slope = jac[0] * energy_first + jac[1] * energy_second
    meridional_slope = jac[2] * energy_first + jac[3] * energy_second
    initial_transport = jac[0] * u + jac[2] * v
    latter_transport = jac[1] * u + jac[3] * v
    advect_with_motion = initial_transport * first_deriv(temp) + latter_transport * second_deriv(
        temp
    )
    distribute_onto_vertices = first_deriv(dp * initial_transport) + second_deriv(
        dp * latter_transport
    )
    return (
        u + time_increment * (rot * v - zonal_slope),
        v - time_increment * (rot * u + meridional_slope),
        temp - time_increment * advect_with_motion,
        dp - time_increment * distribute_onto_vertices,
    )


def reorder(values, rotation, table):
    rows = []
    for q in range(16):
        pick = values[int(table[3, q])]
        for w in (2, 1, 0):
            pick = jnp.where(rotation == w, values[int(table[w, q])], pick)
        rows.append(pick)
    return jnp.stack(rows)


def node_sum(canon, col, row, rows_dev):
    elements = canon.shape[-1]

    def roll(y, shift):
        return jnp.roll(y, shift, axis=-1)

    rows = [canon[q] for q in range(16)]
    for a in range(4):
        left = jnp.where(col == 0, roll(rows[4 * a + 3], -(COLS - 1)), roll(rows[4 * a + 3], 1))
        total = rows[4 * a] + left
        rows[4 * a] = total
        rows[4 * a + 3] = jnp.where(col == COLS - 1, roll(total, COLS - 1), roll(total, -1))
    seg_count = lax.axis_size("seg")
    up = [(i, (i + 1) % seg_count) for i in range(seg_count)]
    down = [(j, i) for i, j in up]
    last = jnp.stack([rows[12 + b][:, elements - COLS :] for b in range(4)])
    first = jnp.stack([rows[b][:, :COLS] for b in range(4)])
    prev_last = lax.ppermute(last, "seg", up)
    next_first = lax.ppermute(first, "seg", down)
    pad = jnp.zeros(prev_last.shape[1:-1] + (elements - COLS,), canon.dtype)
    out = list(rows)
    for b in range(4):
        halo_up = jnp.concatenate([prev_last[b], pad], axis=-1)
        from_up = jnp.where(row == 0, halo_up, roll(rows[12 + b], COLS))
        out[b] = rows[b] + from_up
        halo_down = jnp.concatenate([pad, next_first[b]], axis=-1)
        from_down = jnp.where(row == rows_dev - 1, halo_down, roll(rows[b], -COLS))
        out[12 + b] = rows[12 + b] + from_down
    return jnp.stack(out)


LANES = 512
CHUNK = 8
INTERPRET = None


def lane_info(rotation, elements):
    element_pos = jnp.arange(elements)
    info = jnp.stack(
        [rotation, element_pos % COLS, element_pos // COLS]
        + [jnp.zeros_like(rotation)] * 5
    ).astype(jnp.int32)
    return jnp.pad(info, ((0, 0), (0, LANES - elements)), constant_values=-1)


def pad_lanes(x, value=0.0):
    widths = [(0, 0)] * (x.ndim - 1) + [(0, LANES - x.shape[-1])]
    return jnp.pad(x, widths, constant_values=value)


def select_rows(values, rotation, table):
    rows = []
    for q in range(16):
        pick = values[int(table[3, q])]
        for w in (2, 1, 0):
            pick = jnp.where(rotation == w, values[int(table[w, q])], pick)
        rows.append(pick)
    return rows


def term_kernel(levels, f_ref, above_ref, g_ref, gh_ref):
    level = lax.broadcasted_iota(jnp.int32, (levels, LANES), 0)
    for p in range(f_ref.shape[1]):
        temp = f_ref[0, p]
        dp = f_ref[1, p]
        cum = dp
        shift = 1
        while shift < levels:
            cum = cum + jnp.where(level >= shift, pltpu.roll(cum, shift, 0), 0.0)
            shift *= 2
        load = top_pressure + above_ref[p] + cum - 0.5 * dp
        term = temp * dp / load
        gh_ref[p] = jnp.sum(term, axis=0, keepdims=True)
        rcum = term
        shift = 1
        while shift < levels:
            rcum = rcum + jnp.where(
                level + shift < levels, pltpu.roll(rcum, levels - shift, 0), 0.0
            )
            shift *= 2
        g_ref[p] = rcum - 0.5 * term


def term_call(fields, above):
    levels = fields.shape[2]
    group = 4
    return pl.pallas_call(
        functools.partial(term_kernel, levels),
        interpret=INTERPRET,
        grid=(16 // group,),
        in_specs=[
            pl.BlockSpec((2, group, levels, LANES), lambda i: (1, i, 0, 0)),
            pl.BlockSpec((group, 1, LANES), lambda i: (i, 0, 0)),
        ],
        out_specs=[
            pl.BlockSpec((group, levels, LANES), lambda i: (i, 0, 0)),
            pl.BlockSpec((group, 1, LANES), lambda i: (i, 0, 0)),
        ],
        out_shape=[
            jax.ShapeDtypeStruct((16, levels, LANES), jnp.float32),
            jax.ShapeDtypeStruct((16, 1, LANES), jnp.float32),
        ],
    )(fields, above)


def lane_roll(y, shift):
    return pltpu.roll(y, shift % LANES, 1)


def adv_kernel(f_ref, g_ref, below_ref, jac_ref, rot_ref, mc_ref, info_ref, out_ref):
    info = info_ref[...]
    rotation = info[0:1]
    col = info[1:2]
    forward_order, _ = rotation_tables()
    u = [f_ref[0, p] for p in range(16)]
    v = [f_ref[1, p] for p in range(16)]
    temp = [f_ref[2, p] for p in range(16)]
    dp = [f_ref[3, p] for p in range(16)]
    jac = [[jac_ref[k, p] for p in range(16)] for k in range(4)]
    energy = [
        (below_ref[p] + g_ref[p]) + 0.5 * (u[p] * u[p] + v[p] * v[p]) for p in range(16)
    ]
    e1 = first_rows(energy)
    e2 = second_rows(energy)
    it = [jac[0][p] * u[p] + jac[2][p] * v[p] for p in range(16)]
    lt = [jac[1][p] * u[p] + jac[3][p] * v[p] for p in range(16)]
    t1 = first_rows(temp)
    t2 = second_rows(temp)
    d1 = first_rows([dp[p] * it[p] for p in range(16)])
    d2 = second_rows([dp[p] * lt[p] for p in range(16)])
    advanced = []
    for p in range(16):
        rot = rot_ref[p]
        zonal_slope = jac[0][p] * e1[p] + jac[1][p] * e2[p]
        meridional_slope = jac[2][p] * e1[p] + jac[3][p] * e2[p]
        advanced.append(
            (
                u[p] + time_increment * (rot * v[p] - zonal_slope),
                v[p] - time_increment * (rot * u[p] + meridional_slope),
                temp[p] - time_increment * (it[p] * t1[p] + lt[p] * t2[p]),
                dp[p] - time_increment * (d1[p] + d2[p]),
            )
        )
    for f in range(4):
        rows = select_rows([advanced[p][f] for p in range(16)], rotation, forward_order)
        rows = [rows[q] * mc_ref[q] for q in range(16)]
        for a in range(4):
            edge = rows[4 * a + 3]
            left = jnp.where(col == 0, lane_roll(edge, -(COLS - 1)), lane_roll(edge, 1))
            total = rows[4 * a] + left
            rows[4 * a] = total
            rows[4 * a + 3] = jnp.where(
                col == COLS - 1, lane_roll(total, COLS - 1), lane_roll(total, -1)
            )
        for q in range(16):
            out_ref[f, q] = rows[q]


def first_rows(rows):
    return [
        weighted_sum([(SLOPES[a, k], rows[4 * k + j]) for k in range(4)])
        for a in range(4)
        for j in range(4)
    ]


def second_rows(rows):
    return [
        weighted_sum([(SLOPES[a, k], rows[4 * i + k]) for k in range(4)])
        for i in range(4)
        for a in range(4)
    ]


def adv_call(fields, g0, below, jac, rot, mass_canon, info):
    levels = fields.shape[2]
    steps = levels // CHUNK
    small = pl.BlockSpec((16, 1, LANES), lambda i: (0, 0, 0))
    return pl.pallas_call(
        adv_kernel,
        interpret=INTERPRET,
        grid=(steps,),
        in_specs=[
            pl.BlockSpec((4, 16, CHUNK, LANES), lambda i: (0, 0, i, 0)),
            pl.BlockSpec((16, CHUNK, LANES), lambda i: (0, i, 0)),
            small,
            pl.BlockSpec((4, 16, 1, LANES), lambda i: (0, 0, 0, 0)),
            small,
            small,
            pl.BlockSpec((8, LANES), lambda i: (0, 0)),
        ],
        out_specs=pl.BlockSpec((4, 16, CHUNK, LANES), lambda i: (0, 0, i, 0)),
        out_shape=jax.ShapeDtypeStruct(fields.shape, jnp.float32),
    )(fields, g0, below, jac, rot, mass_canon, info)


def fin_kernel(rows_dev, elements, with_cells, *refs):
    if with_cells:
        w_ref, hu_ref, hd_ref, mt_ref, info_ref, prev_ref, m_ref, out_ref, cm_ref, cell_ref = refs
    else:
        w_ref, hu_ref, hd_ref, mt_ref, info_ref, out_ref, cm_ref = refs
    info = info_ref[...]
    rotation = info[0:1]
    row = info[2:3]
    lane = lax.broadcasted_iota(jnp.int32, (1, LANES), 1)
    valid = lane < elements
    _, backward_order = rotation_tables()
    groups = [(0, 1, 4, 5), (2, 3, 6, 7), (8, 9, 12, 13), (10, 11, 14, 15)]
    for f in range(4):
        rows = [w_ref[f, q] for q in range(16)]
        out = list(rows)
        for b in range(4):
            from_up = jnp.where(row == 0, hu_ref[f, b], lane_roll(rows[12 + b], COLS))
            out[b] = rows[b] + from_up
            from_down = jnp.where(row == rows_dev - 1, hd_ref[f, b], lane_roll(rows[b], -COLS))
            out[12 + b] = rows[12 + b] + from_down
        out = [out[q] / mt_ref[q] for q in range(16)]
        new = select_rows(out, rotation, backward_order)
        new = [jnp.where(valid, new[p], 0.0) for p in range(16)]
        for p in range(16):
            out_ref[f, p] = new[p]
        if f == 3:
            for p in range(16):
                cm_ref[p] = jnp.sum(new[p], axis=0, keepdims=True)
        if with_cells:
            average = [(prev_ref[f, p] + new[p]) / SUBSTEPS for p in range(16)]
            for c, group in enumerate(groups):
                m = [m_ref[p] for p in group]
                summed = (m[0] * average[group[0]] + m[1] * average[group[1]]) + (
                    m[2] * average[group[2]] + m[3] * average[group[3]]
                )
                area = (m[0] + m[1]) + (m[2] + m[3])
                cell_ref[c, f] = summed / area


def fin_call(w, halo_up, halo_down, mass_total, info, rows_dev, elements, prev=None, mass=None):
    levels = w.shape[2]
    steps = levels // CHUNK
    block = pl.BlockSpec((4, 16, CHUNK, LANES), lambda i: (0, 0, i, 0))
    halo = pl.BlockSpec((4, 4, CHUNK, LANES), lambda i: (0, 0, i, 0))
    small = pl.BlockSpec((16, 1, LANES), lambda i: (0, 0, 0))
    with_cells = prev is not None
    in_specs = [block, halo, halo, small, pl.BlockSpec((8, LANES), lambda i: (0, 0))]
    args = [w, halo_up, halo_down, mass_total, info]
    out_specs = [block, pl.BlockSpec((16, 1, LANES), lambda i: (0, 0, 0))]
    out_shape = [
        jax.ShapeDtypeStruct(w.shape, jnp.float32),
        jax.ShapeDtypeStruct((steps, 16, 1, LANES), jnp.float32),
    ]
    out_specs[1] = pl.BlockSpec((None, 16, 1, LANES), lambda i: (i, 0, 0, 0))
    if with_cells:
        in_specs += [block, small]
        args += [prev, mass]
        out_specs.append(pl.BlockSpec((4, 4, CHUNK, LANES), lambda i: (0, 0, i, 0)))
        out_shape.append(jax.ShapeDtypeStruct((4, 4, levels, LANES), jnp.float32))
    return pl.pallas_call(
        functools.partial(fin_kernel, rows_dev, elements, with_cells),
        interpret=INTERPRET,
        grid=(steps,),
        in_specs=in_specs,
        out_specs=out_specs,
        out_shape=out_shape,
    )(*args)


def halo_exchange(w, elements):
    seg_count = lax.axis_size("seg")
    up = [(i, (i + 1) % seg_count) for i in range(seg_count)]
    down = [(j, i) for i, j in up]
    last = w[..., 12:16, :, elements - COLS : elements]
    first = w[..., 0:4, :, 0:COLS]
    prev_last = lax.ppermute(last, "seg", up)
    next_first = lax.ppermute(first, "seg", down)
    widths = [(0, 0)] * (w.ndim - 1)
    halo_up = jnp.pad(prev_last, widths + [(0, LANES - COLS)])
    halo_down = jnp.pad(next_first, widths + [(elements - COLS, LANES - elements)])
    return halo_up, halo_down


def mass_dss(mass_canon_rows, info, rows_dev, elements):
    col = info[1:2]
    row = info[2:3]
    rows = list(mass_canon_rows)
    for a in range(4):
        edge = rows[4 * a + 3]
        left = jnp.where(col == 0, jnp.roll(edge, -(COLS - 1), -1), jnp.roll(edge, 1, -1))
        total = rows[4 * a] + left
        rows[4 * a] = total
        rows[4 * a + 3] = jnp.where(
            col == COLS - 1, jnp.roll(total, COLS - 1, -1), jnp.roll(total, -1, -1)
        )
    w = jnp.stack(rows)
    halo_up, halo_down = halo_exchange(w, elements)
    out = list(rows)
    for b in range(4):
        from_up = jnp.where(row == 0, halo_up[b], jnp.roll(rows[12 + b], COLS, -1))
        out[b] = rows[b] + from_up
        from_down = jnp.where(row == rows_dev - 1, halo_down[b], jnp.roll(rows[b], -COLS, -1))
        out[12 + b] = rows[12 + b] + from_down
    total = jnp.stack(out)
    lane = jnp.arange(LANES)
    return jnp.where(lane < elements, total, 1.0)


def local(
    velocity_pair,
    thermal_reading,
    layer_depth,
    jacobian_terms,
    rotation_frequency,
    integration_mass,
    shared_vertex_label,
    column_owner_slot,
):
    levels_dev = thermal_reading.shape[0]
    elements = thermal_reading.shape[2]
    seg_count = lax.axis_size("seg")
    lev_count = lax.axis_size("lev")
    rows_dev = elements // COLS
    node_cols = 3 * COLS
    first_row = 3 * rows_dev * lax.axis_index("seg")
    grid_rows = 3 * rows_dev * seg_count
    corner_ids = shared_vertex_label[0]
    element_pos = jnp.arange(elements)
    row_offset = (corner_ids // node_cols - first_row) % grid_rows - 3 * (element_pos // COLS)
    col_offset = (corner_ids % node_cols - 3 * (element_pos % COLS)) % node_cols
    rotation = jnp.where(
        row_offset == 0, jnp.where(col_offset == 0, 0, 1), jnp.where(col_offset == 3, 2, 3)
    )
    info = lane_info(rotation, elements)
    forward_order, _ = rotation_tables()

    prognostic = jnp.concatenate([velocity_pair, thermal_reading[None], layer_depth[None]], axis=0)
    fields = pad_lanes(jnp.transpose(prognostic, (0, 2, 1, 3)))
    jac = pad_lanes(jacobian_terms[:, :, None, :])
    rot = pad_lanes(rotation_frequency[:, None, :])
    mass = pad_lanes(integration_mass[:, None, :])
    mass_one = pad_lanes(integration_mass[:, None, :], 1.0)
    mass_canon = jnp.stack(select_rows([mass[p] for p in range(16)], info[0:1], forward_order))
    mass_total = mass_dss(mass_canon, info, rows_dev, elements)
    column_mass = jnp.sum(fields[3], axis=1, keepdims=True)
    previous = None
    cells = None
    for substep in range(SUBSTEPS):
        above = carried_in(column_mass, "lev", False)
        g0, group_height = term_call(fields, above)
        below = carried_in(group_height, "lev", True)
        w = adv_call(fields, g0, below, jac, rot, mass_canon, info)
        halo_up, halo_down = halo_exchange(w, elements)
        if substep == SUBSTEPS - 1:
            fields, column_parts, cells = fin_call(
                w, halo_up, halo_down, mass_total, info, rows_dev, elements, previous, mass_one
            )
        else:
            fields, column_parts = fin_call(
                w, halo_up, halo_down, mass_total, info, rows_dev, elements
            )
            previous = fields
        column_mass = jnp.sum(column_parts, axis=0)
    channels = 4 * levels_dev
    cell_values = cells[..., :elements].reshape(4, channels, elements)
    payload = jnp.transpose(cell_values, (0, 2, 1)).reshape(4 * elements, channels)
    dev_count = seg_count * lev_count
    own_cols = 4 * elements * seg_count // dev_count
    per_pair = own_cols // seg_count
    capacity = per_pair + per_pair // 2
    assert capacity <= channels
    targets = column_owner_slot.reshape(-1)
    owner_index = targets // own_cols
    slot_index = targets % own_cols
    cell_count = targets.shape[0]
    cell_pos = jnp.arange(cell_count)
    same_owner = owner_index[:, None] == owner_index[None, :]
    earlier = cell_pos[None, :] < cell_pos[:, None]
    rank = jnp.sum(jnp.logical_and(same_owner, earlier).astype(jnp.int32), axis=1)
    destination = owner_index * capacity + rank
    slots = jnp.arange(dev_count * capacity)
    match = destination[None, :] == slots[:, None]
    has = jnp.any(match, axis=1)
    source_cell = jnp.sum(jnp.where(match, cell_pos[None, :], 0), axis=1)
    source_pos = jnp.sum(jnp.where(match, slot_index[None, :], 0), axis=1)
    outgoing = jnp.where(has[:, None], payload[source_cell], 0.0)
    ids = jnp.where(has, source_pos, -1).astype(jnp.float32).reshape(dev_count, capacity)
    ids = jnp.pad(ids, ((0, 0), (0, channels - capacity)), constant_values=-1.0)
    buffer = jnp.concatenate(
        [outgoing.reshape(dev_count, capacity, channels), ids[:, None, :]], axis=1
    )
    received = lax.all_to_all(buffer, ("seg", "lev"), split_axis=0, concat_axis=0, tiled=True)
    received_ids = jnp.round(received[:, capacity, :capacity]).astype(jnp.int32)
    received_rows = received[:, :capacity, :].reshape(dev_count * capacity, channels)
    flat = jnp.arange(dev_count * capacity).reshape(dev_count, capacity)
    source_lev = (jnp.arange(dev_count) % lev_count)[:, None]
    positions = jnp.arange(own_cols)
    picks = []
    for group in range(lev_count):
        hit = jnp.logical_and(
            received_ids[None, :, :] == positions[:, None, None], (source_lev == group)[None]
        )
        picks.append(jnp.sum(jnp.where(hit, flat[None], 0), axis=(1, 2)))
    arrived = received_rows[jnp.stack(picks)]
    arrived = arrived.reshape(lev_count, own_cols, 4, levels_dev).transpose(2, 0, 3, 1)
    phys_state = arrived.reshape(4, lev_count * levels_dev, own_cols)
    mean_thickness = jnp.mean(phys_state[3], axis=0)
    dyn_state = jnp.transpose(fields[..., :elements], (0, 2, 1, 3))
    return (dyn_state, phys_state, mean_thickness)


def solution(mesh):
    in_specs = (
        P(None, "lev", None, "seg"),
        P("lev", None, "seg"),
        P("lev", None, "seg"),
        P(None, None, "seg"),
        P(None, "seg"),
        P(None, "seg"),
        P(None, "seg"),
        P(None, "seg"),
    )
    out_specs = (P(None, "lev", None, "seg"), P(None, None, ("seg", "lev")), P(("seg", "lev")))
    return jax.shard_map(local, mesh=mesh, in_specs=in_specs, out_specs=out_specs, check_vma=False)
```

```python
import functools

import jax
import jax.numpy as jnp
import numpy as np
from jax import lax
from jax.experimental import pallas as pl
from jax.experimental.pallas import tpu as pltpu
from jax.sharding import PartitionSpec as P

COLS = 120
SUBSTEPS = 2


top_pressure = 10.0
time_increment = 0.05


def gll_slopes():
    root_five = np.sqrt(5.0)
    gll_nodes = [-1.0, -1.0 / root_five, 1.0 / root_five, 1.0]
    legendre_values = [-1.0, 1.0 / root_five, -1.0 / root_five, 1.0]
    slopes = np.zeros((4, 4))
    for row_node in range(4):
        for column in range(4):
            if row_node != column:
                slopes[row_node, column] = (
                    legendre_values[row_node]
                    / legendre_values[column]
                    / (gll_nodes[row_node] - gll_nodes[column])
                )
    slopes[0, 0] = -3.0
    slopes[3, 3] = 3.0
    return slopes


SLOPES = gll_slopes().astype(np.float32)


def rotation_tables():
    forward = np.zeros((4, 16), np.int32)
    for first_pos in range(4):
        for second_pos in range(4):
            canonical = 4 * first_pos + second_pos
            forward[0, canonical] = 4 * first_pos + second_pos
            forward[1, canonical] = 4 * (3 - second_pos) + first_pos
            forward[2, canonical] = 4 * (3 - first_pos) + (3 - second_pos)
            forward[3, canonical] = 4 * second_pos + 3 - first_pos
    backward = np.argsort(forward, axis=1).astype(np.int32)
    return (forward, backward)


def weighted_sum(terms):
    acc = None
    for coef, value in terms:
        if coef == 0.0:
            continue
        part = jnp.float32(coef) * value
        acc = part if acc is None else acc + part
    return acc


def first_deriv(f):
    return jnp.stack(
        [
            weighted_sum([(SLOPES[a, k], f[4 * k + j]) for k in range(4)])
            for a in range(4)
            for j in range(4)
        ]
    )


def second_deriv(f):
    return jnp.stack(
        [
            weighted_sum([(SLOPES[a, k], f[4 * i + k]) for k in range(4)])
            for i in range(4)
            for a in range(4)
        ]
    )


def carried_in(part, axis, reverse):
    count = lax.axis_size(axis)
    place = lax.axis_index(axis)
    gathered = lax.all_gather(part, axis)
    index = jnp.arange(count).reshape((count,) + (1,) * part.ndim)
    chosen = index > place if reverse else index < place
    return jnp.sum(jnp.where(chosen, gathered, jnp.zeros_like(gathered)), axis=0)


def site_potential_energy(thermal_reading, layer_depth):
    column_mass = jnp.sum(layer_depth, axis=1)
    above_sum = carried_in(column_mass, "lev", False)
    layer_midpoint_load = (
        top_pressure + above_sum[:, None, :] + jnp.cumsum(layer_depth, axis=1) - 0.5 * layer_depth
    )
    surface_change_rate = thermal_reading * layer_depth / layer_midpoint_load
    group_height = jnp.sum(surface_change_rate, axis=1)
    below_sum = carried_in(group_height, "lev", True)
    return (
        below_sum[:, None, :]
        + lax.cumsum(surface_change_rate, axis=1, reverse=True)
        - 0.5 * surface_change_rate
    )


def tendency_step(u, v, temp, dp, geopotential, jac, rot):
    energy = geopotential + 0.5 * (u * u + v * v)
    energy_first = first_deriv(energy)
    energy_second = second_deriv(energy)
    zonal_slope = jac[0] * energy_first + jac[1] * energy_second
    meridional_slope = jac[2] * energy_first + jac[3] * energy_second
    initial_transport = jac[0] * u + jac[2] * v
    latter_transport = jac[1] * u + jac[3] * v
    advect_with_motion = initial_transport * first_deriv(temp) + latter_transport * second_deriv(
        temp
    )
    distribute_onto_vertices = first_deriv(dp * initial_transport) + second_deriv(
        dp * latter_transport
    )
    return (
        u + time_increment * (rot * v - zonal_slope),
        v - time_increment * (rot * u + meridional_slope),
        temp - time_increment * advect_with_motion,
        dp - time_increment * distribute_onto_vertices,
    )


def reorder(values, rotation, table):
    rows = []
    for q in range(16):
        pick = values[int(table[3, q])]
        for w in (2, 1, 0):
            pick = jnp.where(rotation == w, values[int(table[w, q])], pick)
        rows.append(pick)
    return jnp.stack(rows)


def node_sum(canon, col, row, rows_dev):
    elements = canon.shape[-1]

    def roll(y, shift):
        return jnp.roll(y, shift, axis=-1)

    rows = [canon[q] for q in range(16)]
    for a in range(4):
        left = jnp.where(col == 0, roll(rows[4 * a + 3], -(COLS - 1)), roll(rows[4 * a + 3], 1))
        total = rows[4 * a] + left
        rows[4 * a] = total
        rows[4 * a + 3] = jnp.where(col == COLS - 1, roll(total, COLS - 1), roll(total, -1))
    seg_count = lax.axis_size("seg")
    up = [(i, (i + 1) % seg_count) for i in range(seg_count)]
    down = [(j, i) for i, j in up]
    last = jnp.stack([rows[12 + b][:, elements - COLS :] for b in range(4)])
    first = jnp.stack([rows[b][:, :COLS] for b in range(4)])
    prev_last = lax.ppermute(last, "seg", up)
    next_first = lax.ppermute(first, "seg", down)
    pad = jnp.zeros(prev_last.shape[1:-1] + (elements - COLS,), canon.dtype)
    out = list(rows)
    for b in range(4):
        halo_up = jnp.concatenate([prev_last[b], pad], axis=-1)
        from_up = jnp.where(row == 0, halo_up, roll(rows[12 + b], COLS))
        out[b] = rows[b] + from_up
        halo_down = jnp.concatenate([pad, next_first[b]], axis=-1)
        from_down = jnp.where(row == rows_dev - 1, halo_down, roll(rows[b], -COLS))
        out[12 + b] = rows[12 + b] + from_down
    return jnp.stack(out)


LANES = 512
CHUNK = 8
INTERPRET = None


def lane_info(rotation, elements):
    element_pos = jnp.arange(elements)
    info = jnp.stack(
        [rotation, element_pos % COLS, element_pos // COLS]
        + [jnp.zeros_like(rotation)] * 5
    ).astype(jnp.int32)
    return jnp.pad(info, ((0, 0), (0, LANES - elements)), constant_values=-1)


def pad_lanes(x, value=0.0):
    widths = [(0, 0)] * (x.ndim - 1) + [(0, LANES - x.shape[-1])]
    return jnp.pad(x, widths, constant_values=value)


def select_rows(values, rotation, table):
    rows = []
    for q in range(16):
        pick = values[int(table[3, q])]
        for w in (2, 1, 0):
            pick = jnp.where(rotation == w, values[int(table[w, q])], pick)
        rows.append(pick)
    return rows


def term_kernel(levels, f_ref, above_ref, g_ref, gh_ref):
    level = lax.broadcasted_iota(jnp.int32, (levels, LANES), 0)
    for p in range(f_ref.shape[1]):
        temp = f_ref[0, p]
        dp = f_ref[1, p]
        cum = dp
        shift = 1
        while shift < levels:
            cum = cum + jnp.where(level >= shift, pltpu.roll(cum, shift, 0), 0.0)
            shift *= 2
        load = top_pressure + above_ref[p] + cum - 0.5 * dp
        term = temp * dp / load
        gh_ref[p] = jnp.sum(term, axis=0, keepdims=True)
        rcum = term
        shift = 1
        while shift < levels:
            rcum = rcum + jnp.where(
                level + shift < levels, pltpu.roll(rcum, levels - shift, 0), 0.0
            )
            shift *= 2
        g_ref[p] = rcum - 0.5 * term


def term_call(fields, above):
    levels = fields.shape[2]
    group = 4
    return pl.pallas_call(
        functools.partial(term_kernel, levels),
        interpret=INTERPRET,
        grid=(16 // group,),
        in_specs=[
            pl.BlockSpec((2, group, levels, LANES), lambda i: (1, i, 0, 0)),
            pl.BlockSpec((group, 1, LANES), lambda i: (i, 0, 0)),
        ],
        out_specs=[
            pl.BlockSpec((group, levels, LANES), lambda i: (i, 0, 0)),
            pl.BlockSpec((group, 1, LANES), lambda i: (i, 0, 0)),
        ],
        out_shape=[
            jax.ShapeDtypeStruct((16, levels, LANES), jnp.float32),
            jax.ShapeDtypeStruct((16, 1, LANES), jnp.float32),
        ],
    )(fields, above)


def lane_roll(y, shift):
    return pltpu.roll(y, shift % LANES, 1)


def adv_kernel(elements, f_ref, g_ref, below_ref, jac_ref, rot_ref, mc_ref, info_ref, out_ref, last_ref, first_ref):
    info = info_ref[...]
    rotation = info[0:1]
    col = info[1:2]
    forward_order, _ = rotation_tables()
    u = [f_ref[0, p] for p in range(16)]
    v = [f_ref[1, p] for p in range(16)]
    temp = [f_ref[2, p] for p in range(16)]
    dp = [f_ref[3, p] for p in range(16)]
    jac = [[jac_ref[k, p] for p in range(16)] for k in range(4)]
    energy = [
        (below_ref[p] + g_ref[p]) + 0.5 * (u[p] * u[p] + v[p] * v[p]) for p in range(16)
    ]
    e1 = first_rows(energy)
    e2 = second_rows(energy)
    it = [jac[0][p] * u[p] + jac[2][p] * v[p] for p in range(16)]
    lt = [jac[1][p] * u[p] + jac[3][p] * v[p] for p in range(16)]
    t1 = first_rows(temp)
    t2 = second_rows(temp)
    d1 = first_rows([dp[p] * it[p] for p in range(16)])
    d2 = second_rows([dp[p] * lt[p] for p in range(16)])
    advanced = []
    for p in range(16):
        rot = rot_ref[p]
        zonal_slope = jac[0][p] * e1[p] + jac[1][p] * e2[p]
        meridional_slope = jac[2][p] * e1[p] + jac[3][p] * e2[p]
        advanced.append(
            (
                u[p] + time_increment * (rot * v[p] - zonal_slope),
                v[p] - time_increment * (rot * u[p] + meridional_slope),
                temp[p] - time_increment * (it[p] * t1[p] + lt[p] * t2[p]),
                dp[p] - time_increment * (d1[p] + d2[p]),
            )
        )
    for f in range(4):
        rows = select_rows([advanced[p][f] for p in range(16)], rotation, forward_order)
        rows = [rows[q] * mc_ref[q] for q in range(16)]
        for a in range(4):
            edge = rows[4 * a + 3]
            left = jnp.where(col == 0, lane_roll(edge, -(COLS - 1)), lane_roll(edge, 1))
            total = rows[4 * a] + left
            rows[4 * a] = total
            rows[4 * a + 3] = jnp.where(
                col == COLS - 1, lane_roll(total, COLS - 1), lane_roll(total, -1)
            )
        for q in range(16):
            out_ref[f, q] = rows[q]
        for b in range(4):
            last_ref[f, b] = lane_roll(rows[12 + b], COLS - elements)[:, :128]
            first_ref[f, b] = rows[b][:, :128]


def first_rows(rows):
    return [
        weighted_sum([(SLOPES[a, k], rows[4 * k + j]) for k in range(4)])
        for a in range(4)
        for j in range(4)
    ]


def second_rows(rows):
    return [
        weighted_sum([(SLOPES[a, k], rows[4 * i + k]) for k in range(4)])
        for i in range(4)
        for a in range(4)
    ]


def adv_call(fields, g0, below, jac, rot, mass_canon, info, elements):
    levels = fields.shape[2]
    steps = levels // CHUNK
    small = pl.BlockSpec((16, 1, LANES), lambda i: (0, 0, 0))
    edge = pl.BlockSpec((4, 4, CHUNK, 128), lambda i: (0, 0, i, 0))
    edge_shape = jax.ShapeDtypeStruct((4, 4, levels, 128), jnp.float32)
    return pl.pallas_call(
        functools.partial(adv_kernel, elements),
        interpret=INTERPRET,
        grid=(steps,),
        in_specs=[
            pl.BlockSpec((4, 16, CHUNK, LANES), lambda i: (0, 0, i, 0)),
            pl.BlockSpec((16, CHUNK, LANES), lambda i: (0, i, 0)),
            small,
            pl.BlockSpec((4, 16, 1, LANES), lambda i: (0, 0, 0, 0)),
            small,
            small,
            pl.BlockSpec((8, LANES), lambda i: (0, 0)),
        ],
        out_specs=[pl.BlockSpec((4, 16, CHUNK, LANES), lambda i: (0, 0, i, 0)), edge, edge],
        out_shape=[jax.ShapeDtypeStruct(fields.shape, jnp.float32), edge_shape, edge_shape],
    )(fields, g0, below, jac, rot, mass_canon, info)


def fin_kernel(rows_dev, elements, with_cells, *refs):
    if with_cells:
        w_ref, hu_ref, hd_ref, mt_ref, info_ref, prev_ref, m_ref, out_ref, cm_ref, cell_ref = refs
    else:
        w_ref, hu_ref, hd_ref, mt_ref, info_ref, out_ref, cm_ref = refs
    info = info_ref[...]
    rotation = info[0:1]
    row = info[2:3]
    lane = lax.broadcasted_iota(jnp.int32, (1, LANES), 1)
    valid = lane < elements
    _, backward_order = rotation_tables()
    groups = [(0, 1, 4, 5), (2, 3, 6, 7), (8, 9, 12, 13), (10, 11, 14, 15)]
    for f in range(4):
        rows = [w_ref[f, q] for q in range(16)]
        out = list(rows)
        for b in range(4):
            fill = jnp.zeros((rows[b].shape[0], LANES - 128), jnp.float32)
            halo_up = jnp.concatenate([hu_ref[f, b], fill], axis=1)
            halo_down = lane_roll(jnp.concatenate([hd_ref[f, b], fill], axis=1), elements - COLS)
            from_up = jnp.where(row == 0, halo_up, lane_roll(rows[12 + b], COLS))
            out[b] = rows[b] + from_up
            from_down = jnp.where(row == rows_dev - 1, halo_down, lane_roll(rows[b], -COLS))
            out[12 + b] = rows[12 + b] + from_down
        out = [out[q] / mt_ref[q] for q in range(16)]
        new = select_rows(out, rotation, backward_order)
        new = [jnp.where(valid, new[p], 0.0) for p in range(16)]
        for p in range(16):
            out_ref[f, p] = new[p]
        if f == 3:
            for p in range(16):
                cm_ref[p] = jnp.sum(new[p], axis=0, keepdims=True)
        if with_cells:
            average = [(prev_ref[f, p] + new[p]) / SUBSTEPS for p in range(16)]
            for c, group in enumerate(groups):
                m = [m_ref[p] for p in group]
                summed = (m[0] * average[group[0]] + m[1] * average[group[1]]) + (
                    m[2] * average[group[2]] + m[3] * average[group[3]]
                )
                area = (m[0] + m[1]) + (m[2] + m[3])
                cell_ref[c, f] = summed / area


def fin_call(w, halo_up, halo_down, mass_total, info, rows_dev, elements, prev=None, mass=None):
    levels = w.shape[2]
    steps = levels // CHUNK
    block = pl.BlockSpec((4, 16, CHUNK, LANES), lambda i: (0, 0, i, 0))
    halo = pl.BlockSpec((4, 4, CHUNK, 128), lambda i: (0, 0, i, 0))
    small = pl.BlockSpec((16, 1, LANES), lambda i: (0, 0, 0))
    with_cells = prev is not None
    in_specs = [block, halo, halo, small, pl.BlockSpec((8, LANES), lambda i: (0, 0))]
    args = [w, halo_up, halo_down, mass_total, info]
    out_specs = [block, pl.BlockSpec((16, 1, LANES), lambda i: (0, 0, 0))]
    out_shape = [
        jax.ShapeDtypeStruct(w.shape, jnp.float32),
        jax.ShapeDtypeStruct((steps, 16, 1, LANES), jnp.float32),
    ]
    out_specs[1] = pl.BlockSpec((None, 16, 1, LANES), lambda i: (i, 0, 0, 0))
    if with_cells:
        in_specs += [block, small]
        args += [prev, mass]
        out_specs.append(pl.BlockSpec((4, 4, CHUNK, LANES), lambda i: (0, 0, i, 0)))
        out_shape.append(jax.ShapeDtypeStruct((4, 4, levels, LANES), jnp.float32))
    return pl.pallas_call(
        functools.partial(fin_kernel, rows_dev, elements, with_cells),
        interpret=INTERPRET,
        grid=(steps,),
        in_specs=in_specs,
        out_specs=out_specs,
        out_shape=out_shape,
    )(*args)


def edge_exchange(last, first):
    seg_count = lax.axis_size("seg")
    up = [(i, (i + 1) % seg_count) for i in range(seg_count)]
    down = [(j, i) for i, j in up]
    return lax.ppermute(last, "seg", up), lax.ppermute(first, "seg", down)


def halo_exchange(w, elements):
    seg_count = lax.axis_size("seg")
    up = [(i, (i + 1) % seg_count) for i in range(seg_count)]
    down = [(j, i) for i, j in up]
    last = w[..., 12:16, :, elements - COLS : elements]
    first = w[..., 0:4, :, 0:COLS]
    prev_last = lax.ppermute(last, "seg", up)
    next_first = lax.ppermute(first, "seg", down)
    widths = [(0, 0)] * (w.ndim - 1)
    halo_up = jnp.pad(prev_last, widths + [(0, LANES - COLS)])
    halo_down = jnp.pad(next_first, widths + [(elements - COLS, LANES - elements)])
    return halo_up, halo_down


def mass_dss(mass_canon_rows, info, rows_dev, elements):
    col = info[1:2]
    row = info[2:3]
    rows = list(mass_canon_rows)
    for a in range(4):
        edge = rows[4 * a + 3]
        left = jnp.where(col == 0, jnp.roll(edge, -(COLS - 1), -1), jnp.roll(edge, 1, -1))
        total = rows[4 * a] + left
        rows[4 * a] = total
        rows[4 * a + 3] = jnp.where(
            col == COLS - 1, jnp.roll(total, COLS - 1, -1), jnp.roll(total, -1, -1)
        )
    w = jnp.stack(rows)
    halo_up, halo_down = halo_exchange(w, elements)
    out = list(rows)
    for b in range(4):
        from_up = jnp.where(row == 0, halo_up[b], jnp.roll(rows[12 + b], COLS, -1))
        out[b] = rows[b] + from_up
        from_down = jnp.where(row == rows_dev - 1, halo_down[b], jnp.roll(rows[b], -COLS, -1))
        out[12 + b] = rows[12 + b] + from_down
    total = jnp.stack(out)
    lane = jnp.arange(LANES)
    return jnp.where(lane < elements, total, 1.0)


def local(
    velocity_pair,
    thermal_reading,
    layer_depth,
    jacobian_terms,
    rotation_frequency,
    integration_mass,
    shared_vertex_label,
    column_owner_slot,
):
    levels_dev = thermal_reading.shape[0]
    elements = thermal_reading.shape[2]
    seg_count = lax.axis_size("seg")
    lev_count = lax.axis_size("lev")
    rows_dev = elements // COLS
    node_cols = 3 * COLS
    first_row = 3 * rows_dev * lax.axis_index("seg")
    grid_rows = 3 * rows_dev * seg_count
    corner_ids = shared_vertex_label[0]
    element_pos = jnp.arange(elements)
    row_offset = (corner_ids // node_cols - first_row) % grid_rows - 3 * (element_pos // COLS)
    col_offset = (corner_ids % node_cols - 3 * (element_pos % COLS)) % node_cols
    rotation = jnp.where(
        row_offset == 0, jnp.where(col_offset == 0, 0, 1), jnp.where(col_offset == 3, 2, 3)
    )
    info = lane_info(rotation, elements)
    forward_order, _ = rotation_tables()

    prognostic = jnp.concatenate([velocity_pair, thermal_reading[None], layer_depth[None]], axis=0)
    fields = pad_lanes(jnp.transpose(prognostic, (0, 2, 1, 3)))
    jac = pad_lanes(jacobian_terms[:, :, None, :])
    rot = pad_lanes(rotation_frequency[:, None, :])
    mass = pad_lanes(integration_mass[:, None, :])
    mass_one = pad_lanes(integration_mass[:, None, :], 1.0)
    mass_canon = jnp.stack(select_rows([mass[p] for p in range(16)], info[0:1], forward_order))
    mass_total = mass_dss(mass_canon, info, rows_dev, elements)
    column_mass = jnp.sum(fields[3], axis=1, keepdims=True)
    previous = None
    cells = None
    for substep in range(SUBSTEPS):
        above = carried_in(column_mass, "lev", False)
        g0, group_height = term_call(fields, above)
        below = carried_in(group_height, "lev", True)
        w, last, first = adv_call(fields, g0, below, jac, rot, mass_canon, info, elements)
        halo_up, halo_down = edge_exchange(last, first)
        if substep == SUBSTEPS - 1:
            fields, column_parts, cells = fin_call(
                w, halo_up, halo_down, mass_total, info, rows_dev, elements, previous, mass_one
            )
        else:
            fields, column_parts = fin_call(
                w, halo_up, halo_down, mass_total, info, rows_dev, elements
            )
            previous = fields
        column_mass = jnp.sum(column_parts, axis=0)
    channels = 4 * levels_dev
    cell_values = cells[..., :elements].reshape(4, channels, elements)
    payload = jnp.transpose(cell_values, (0, 2, 1)).reshape(4 * elements, channels)
    dev_count = seg_count * lev_count
    own_cols = 4 * elements * seg_count // dev_count
    per_pair = own_cols // seg_count
    capacity = per_pair + per_pair // 2
    assert capacity <= channels
    targets = column_owner_slot.reshape(-1)
    owner_index = targets // own_cols
    slot_index = targets % own_cols
    cell_count = targets.shape[0]
    cell_pos = jnp.arange(cell_count)
    same_owner = owner_index[:, None] == owner_index[None, :]
    earlier = cell_pos[None, :] < cell_pos[:, None]
    rank = jnp.sum(jnp.logical_and(same_owner, earlier).astype(jnp.int32), axis=1)
    destination = owner_index * capacity + rank
    slots = jnp.arange(dev_count * capacity)
    match = destination[None, :] == slots[:, None]
    has = jnp.any(match, axis=1)
    source_cell = jnp.sum(jnp.where(match, cell_pos[None, :], 0), axis=1)
    source_pos = jnp.sum(jnp.where(match, slot_index[None, :], 0), axis=1)
    outgoing = jnp.where(has[:, None], payload[source_cell], 0.0)
    ids = jnp.where(has, source_pos, -1).astype(jnp.float32).reshape(dev_count, capacity)
    ids = jnp.pad(ids, ((0, 0), (0, channels - capacity)), constant_values=-1.0)
    buffer = jnp.concatenate(
        [outgoing.reshape(dev_count, capacity, channels), ids[:, None, :]], axis=1
    )
    received = lax.all_to_all(buffer, ("seg", "lev"), split_axis=0, concat_axis=0, tiled=True)
    received_ids = jnp.round(received[:, capacity, :capacity]).astype(jnp.int32)
    received_rows = received[:, :capacity, :].reshape(dev_count * capacity, channels)
    flat = jnp.arange(dev_count * capacity).reshape(dev_count, capacity)
    source_lev = (jnp.arange(dev_count) % lev_count)[:, None]
    positions = jnp.arange(own_cols)
    picks = []
    for group in range(lev_count):
        hit = jnp.logical_and(
            received_ids[None, :, :] == positions[:, None, None], (source_lev == group)[None]
        )
        picks.append(jnp.sum(jnp.where(hit, flat[None], 0), axis=(1, 2)))
    arrived = received_rows[jnp.stack(picks)]
    arrived = arrived.reshape(lev_count, own_cols, 4, levels_dev).transpose(2, 0, 3, 1)
    phys_state = arrived.reshape(4, lev_count * levels_dev, own_cols)
    mean_thickness = jnp.mean(phys_state[3], axis=0)
    dyn_state = jnp.transpose(fields[..., :elements], (0, 2, 1, 3))
    return (dyn_state, phys_state, mean_thickness)


def solution(mesh):
    in_specs = (
        P(None, "lev", None, "seg"),
        P("lev", None, "seg"),
        P("lev", None, "seg"),
        P(None, None, "seg"),
        P(None, "seg"),
        P(None, "seg"),
        P(None, "seg"),
        P(None, "seg"),
    )
    out_specs = (P(None, "lev", None, "seg"), P(None, None, ("seg", "lev")), P(("seg", "lev")))
    return jax.shard_map(local, mesh=mesh, in_specs=in_specs, out_specs=out_specs, check_vma=False)
```

```python
import functools

import jax
import jax.numpy as jnp
import numpy as np
from jax import lax
from jax.experimental import pallas as pl
from jax.experimental.pallas import tpu as pltpu
from jax.sharding import PartitionSpec as P

COLS = 120
SUBSTEPS = 2


top_pressure = 10.0
time_increment = 0.05


def gll_slopes():
    root_five = np.sqrt(5.0)
    gll_nodes = [-1.0, -1.0 / root_five, 1.0 / root_five, 1.0]
    legendre_values = [-1.0, 1.0 / root_five, -1.0 / root_five, 1.0]
    slopes = np.zeros((4, 4))
    for row_node in range(4):
        for column in range(4):
            if row_node != column:
                slopes[row_node, column] = (
                    legendre_values[row_node]
                    / legendre_values[column]
                    / (gll_nodes[row_node] - gll_nodes[column])
                )
    slopes[0, 0] = -3.0
    slopes[3, 3] = 3.0
    return slopes


SLOPES = gll_slopes().astype(np.float32)


def rotation_tables():
    forward = np.zeros((4, 16), np.int32)
    for first_pos in range(4):
        for second_pos in range(4):
            canonical = 4 * first_pos + second_pos
            forward[0, canonical] = 4 * first_pos + second_pos
            forward[1, canonical] = 4 * (3 - second_pos) + first_pos
            forward[2, canonical] = 4 * (3 - first_pos) + (3 - second_pos)
            forward[3, canonical] = 4 * second_pos + 3 - first_pos
    backward = np.argsort(forward, axis=1).astype(np.int32)
    return (forward, backward)


def weighted_sum(terms):
    acc = None
    for coef, value in terms:
        if coef == 0.0:
            continue
        part = jnp.float32(coef) * value
        acc = part if acc is None else acc + part
    return acc


def first_deriv(f):
    return jnp.stack(
        [
            weighted_sum([(SLOPES[a, k], f[4 * k + j]) for k in range(4)])
            for a in range(4)
            for j in range(4)
        ]
    )


def second_deriv(f):
    return jnp.stack(
        [
            weighted_sum([(SLOPES[a, k], f[4 * i + k]) for k in range(4)])
            for i in range(4)
            for a in range(4)
        ]
    )


def carried_in(part, axis, reverse):
    count = lax.axis_size(axis)
    place = lax.axis_index(axis)
    gathered = lax.all_gather(part, axis)
    index = jnp.arange(count).reshape((count,) + (1,) * part.ndim)
    chosen = index > place if reverse else index < place
    return jnp.sum(jnp.where(chosen, gathered, jnp.zeros_like(gathered)), axis=0)


def site_potential_energy(thermal_reading, layer_depth):
    column_mass = jnp.sum(layer_depth, axis=1)
    above_sum = carried_in(column_mass, "lev", False)
    layer_midpoint_load = (
        top_pressure + above_sum[:, None, :] + jnp.cumsum(layer_depth, axis=1) - 0.5 * layer_depth
    )
    surface_change_rate = thermal_reading * layer_depth / layer_midpoint_load
    group_height = jnp.sum(surface_change_rate, axis=1)
    below_sum = carried_in(group_height, "lev", True)
    return (
        below_sum[:, None, :]
        + lax.cumsum(surface_change_rate, axis=1, reverse=True)
        - 0.5 * surface_change_rate
    )


def tendency_step(u, v, temp, dp, geopotential, jac, rot):
    energy = geopotential + 0.5 * (u * u + v * v)
    energy_first = first_deriv(energy)
    energy_second = second_deriv(energy)
    zonal_slope = jac[0] * energy_first + jac[1] * energy_second
    meridional_slope = jac[2] * energy_first + jac[3] * energy_second
    initial_transport = jac[0] * u + jac[2] * v
    latter_transport = jac[1] * u + jac[3] * v
    advect_with_motion = initial_transport * first_deriv(temp) + latter_transport * second_deriv(
        temp
    )
    distribute_onto_vertices = first_deriv(dp * initial_transport) + second_deriv(
        dp * latter_transport
    )
    return (
        u + time_increment * (rot * v - zonal_slope),
        v - time_increment * (rot * u + meridional_slope),
        temp - time_increment * advect_with_motion,
        dp - time_increment * distribute_onto_vertices,
    )


def reorder(values, rotation, table):
    rows = []
    for q in range(16):
        pick = values[int(table[3, q])]
        for w in (2, 1, 0):
            pick = jnp.where(rotation == w, values[int(table[w, q])], pick)
        rows.append(pick)
    return jnp.stack(rows)


def node_sum(canon, col, row, rows_dev):
    elements = canon.shape[-1]

    def roll(y, shift):
        return jnp.roll(y, shift, axis=-1)

    rows = [canon[q] for q in range(16)]
    for a in range(4):
        left = jnp.where(col == 0, roll(rows[4 * a + 3], -(COLS - 1)), roll(rows[4 * a + 3], 1))
        total = rows[4 * a] + left
        rows[4 * a] = total
        rows[4 * a + 3] = jnp.where(col == COLS - 1, roll(total, COLS - 1), roll(total, -1))
    seg_count = lax.axis_size("seg")
    up = [(i, (i + 1) % seg_count) for i in range(seg_count)]
    down = [(j, i) for i, j in up]
    last = jnp.stack([rows[12 + b][:, elements - COLS :] for b in range(4)])
    first = jnp.stack([rows[b][:, :COLS] for b in range(4)])
    prev_last = lax.ppermute(last, "seg", up)
    next_first = lax.ppermute(first, "seg", down)
    pad = jnp.zeros(prev_last.shape[1:-1] + (elements - COLS,), canon.dtype)
    out = list(rows)
    for b in range(4):
        halo_up = jnp.concatenate([prev_last[b], pad], axis=-1)
        from_up = jnp.where(row == 0, halo_up, roll(rows[12 + b], COLS))
        out[b] = rows[b] + from_up
        halo_down = jnp.concatenate([pad, next_first[b]], axis=-1)
        from_down = jnp.where(row == rows_dev - 1, halo_down, roll(rows[b], -COLS))
        out[12 + b] = rows[12 + b] + from_down
    return jnp.stack(out)


LANES = 512
CHUNK = 8
INTERPRET = None


def lane_info(rotation, elements):
    element_pos = jnp.arange(elements)
    info = jnp.stack(
        [rotation, element_pos % COLS, element_pos // COLS]
        + [jnp.zeros_like(rotation)] * 5
    ).astype(jnp.int32)
    return jnp.pad(info, ((0, 0), (0, LANES - elements)), constant_values=-1)


def pad_lanes(x, value=0.0):
    widths = [(0, 0)] * (x.ndim - 1) + [(0, LANES - x.shape[-1])]
    return jnp.pad(x, widths, constant_values=value)


def select_rows(values, rotation, table):
    rows = []
    for q in range(16):
        pick = values[int(table[3, q])]
        for w in (2, 1, 0):
            pick = jnp.where(rotation == w, values[int(table[w, q])], pick)
        rows.append(pick)
    return rows


def term_kernel(levels, f_ref, above_ref, g_ref, gh_ref):
    level = lax.broadcasted_iota(jnp.int32, (levels, LANES), 0)
    for p in range(f_ref.shape[1]):
        temp = f_ref[0, p]
        dp = f_ref[1, p]
        cum = dp
        shift = 1
        while shift < levels:
            cum = cum + jnp.where(level >= shift, pltpu.roll(cum, shift, 0), 0.0)
            shift *= 2
        load = top_pressure + above_ref[p] + cum - 0.5 * dp
        term = temp * dp / load
        gh_ref[p] = jnp.sum(term, axis=0, keepdims=True)
        rcum = term
        shift = 1
        while shift < levels:
            rcum = rcum + jnp.where(
                level + shift < levels, pltpu.roll(rcum, levels - shift, 0), 0.0
            )
            shift *= 2
        g_ref[p] = rcum - 0.5 * term


def term_call(fields, above):
    levels = fields.shape[2]
    group = 4
    return pl.pallas_call(
        functools.partial(term_kernel, levels),
        interpret=INTERPRET,
        grid=(16 // group,),
        in_specs=[
            pl.BlockSpec((2, group, levels, LANES), lambda i: (1, i, 0, 0)),
            pl.BlockSpec((group, 1, LANES), lambda i: (i, 0, 0)),
        ],
        out_specs=[
            pl.BlockSpec((group, levels, LANES), lambda i: (i, 0, 0)),
            pl.BlockSpec((group, 1, LANES), lambda i: (i, 0, 0)),
        ],
        out_shape=[
            jax.ShapeDtypeStruct((16, levels, LANES), jnp.float32),
            jax.ShapeDtypeStruct((16, 1, LANES), jnp.float32),
        ],
    )(fields, above)


def lane_roll(y, shift):
    return pltpu.roll(y, shift % LANES, 1)


def column_fold(rows, col):
    rows = list(rows)
    for a in range(4):
        edge = rows[4 * a + 3]
        left = jnp.where(col == 0, lane_roll(edge, -(COLS - 1)), lane_roll(edge, 1))
        total = rows[4 * a] + left
        rows[4 * a] = total
        rows[4 * a + 3] = jnp.where(
            col == COLS - 1, lane_roll(total, COLS - 1), lane_roll(total, -1)
        )
    return rows


def row_fold(rows, up_rows, down_rows, row, rows_dev, elements):
    out = list(rows)
    for b in range(4):
        fill = jnp.zeros((rows[b].shape[0], LANES - 128), jnp.float32)
        halo_up = jnp.concatenate([up_rows[b], fill], axis=1)
        halo_down = lane_roll(jnp.concatenate([down_rows[b], fill], axis=1), elements - COLS)
        from_up = jnp.where(row == 0, halo_up, lane_roll(rows[12 + b], COLS))
        out[b] = rows[b] + from_up
        from_down = jnp.where(row == rows_dev - 1, halo_down, lane_roll(rows[b], -COLS))
        out[12 + b] = rows[12 + b] + from_down
    return out


def mass_kernel(elements, m_ref, info_ref, mc_ref, mw_ref, last_ref, first_ref):
    info = info_ref[...]
    forward_order, _ = rotation_tables()
    canon = select_rows([m_ref[p] for p in range(16)], info[0:1], forward_order)
    rows = column_fold(canon, info[1:2])
    for q in range(16):
        mc_ref[q] = canon[q]
        mw_ref[q] = rows[q]
    for b in range(4):
        last_ref[b] = lane_roll(rows[12 + b], COLS - elements)[:, :128]
        first_ref[b] = rows[b][:, :128]


def mass_call(mass, info, elements):
    small = jax.ShapeDtypeStruct((16, 1, LANES), jnp.float32)
    edge = jax.ShapeDtypeStruct((4, 1, 128), jnp.float32)
    return pl.pallas_call(
        functools.partial(mass_kernel, elements),
        interpret=INTERPRET,
        out_shape=[small, small, edge, edge],
    )(mass, info)


def adv_kernel(elements, f_ref, g_ref, below_ref, jac_ref, rot_ref, mc_ref, info_ref, out_ref, last_ref, first_ref):
    info = info_ref[...]
    rotation = info[0:1]
    col = info[1:2]
    forward_order, _ = rotation_tables()
    u = [f_ref[0, p] for p in range(16)]
    v = [f_ref[1, p] for p in range(16)]
    temp = [f_ref[2, p] for p in range(16)]
    dp = [f_ref[3, p] for p in range(16)]
    jac = [[jac_ref[k, p] for p in range(16)] for k in range(4)]
    energy = [
        (below_ref[p] + g_ref[p]) + 0.5 * (u[p] * u[p] + v[p] * v[p]) for p in range(16)
    ]
    e1 = first_rows(energy)
    e2 = second_rows(energy)
    it = [jac[0][p] * u[p] + jac[2][p] * v[p] for p in range(16)]
    lt = [jac[1][p] * u[p] + jac[3][p] * v[p] for p in range(16)]
    t1 = first_rows(temp)
    t2 = second_rows(temp)
    d1 = first_rows([dp[p] * it[p] for p in range(16)])
    d2 = second_rows([dp[p] * lt[p] for p in range(16)])
    advanced = []
    for p in range(16):
        rot = rot_ref[p]
        zonal_slope = jac[0][p] * e1[p] + jac[1][p] * e2[p]
        meridional_slope = jac[2][p] * e1[p] + jac[3][p] * e2[p]
        advanced.append(
            (
                u[p] + time_increment * (rot * v[p] - zonal_slope),
                v[p] - time_increment * (rot * u[p] + meridional_slope),
                temp[p] - time_increment * (it[p] * t1[p] + lt[p] * t2[p]),
                dp[p] - time_increment * (d1[p] + d2[p]),
            )
        )
    for f in range(4):
        rows = select_rows([advanced[p][f] for p in range(16)], rotation, forward_order)
        rows = column_fold([rows[q] * mc_ref[q] for q in range(16)], col)
        for q in range(16):
            out_ref[f, q] = rows[q]
        for b in range(4):
            last_ref[f, b] = lane_roll(rows[12 + b], COLS - elements)[:, :128]
            first_ref[f, b] = rows[b][:, :128]


def first_rows(rows):
    return [
        weighted_sum([(SLOPES[a, k], rows[4 * k + j]) for k in range(4)])
        for a in range(4)
        for j in range(4)
    ]


def second_rows(rows):
    return [
        weighted_sum([(SLOPES[a, k], rows[4 * i + k]) for k in range(4)])
        for i in range(4)
        for a in range(4)
    ]


def adv_call(fields, g0, below, jac, rot, mass_canon, info, elements):
    levels = fields.shape[2]
    steps = levels // CHUNK
    small = pl.BlockSpec((16, 1, LANES), lambda i: (0, 0, 0))
    edge = pl.BlockSpec((4, 4, CHUNK, 128), lambda i: (0, 0, i, 0))
    edge_shape = jax.ShapeDtypeStruct((4, 4, levels, 128), jnp.float32)
    return pl.pallas_call(
        functools.partial(adv_kernel, elements),
        interpret=INTERPRET,
        grid=(steps,),
        in_specs=[
            pl.BlockSpec((4, 16, CHUNK, LANES), lambda i: (0, 0, i, 0)),
            pl.BlockSpec((16, CHUNK, LANES), lambda i: (0, i, 0)),
            small,
            pl.BlockSpec((4, 16, 1, LANES), lambda i: (0, 0, 0, 0)),
            small,
            small,
            pl.BlockSpec((8, LANES), lambda i: (0, 0)),
        ],
        out_specs=[pl.BlockSpec((4, 16, CHUNK, LANES), lambda i: (0, 0, i, 0)), edge, edge],
        out_shape=[jax.ShapeDtypeStruct(fields.shape, jnp.float32), edge_shape, edge_shape],
    )(fields, g0, below, jac, rot, mass_canon, info)


def fin_kernel(rows_dev, elements, with_cells, with_mass, *refs):
    refs = list(refs)
    w_ref, hu_ref, hd_ref = refs[:3]
    if with_mass:
        mw_ref, mhu_ref, mhd_ref = refs[3:6]
        refs = refs[6:]
    else:
        mt_ref = refs[3]
        refs = refs[4:]
    info_ref = refs.pop(0)
    if with_cells:
        prev_ref, m_ref = refs[:2]
        refs = refs[2:]
    out_ref, cm_ref = refs[:2]
    if with_cells:
        cell_ref = refs[2]
    info = info_ref[...]
    rotation = info[0:1]
    row = info[2:3]
    if with_mass:
        mass_total = row_fold(
            [mw_ref[q] for q in range(16)],
            [mhu_ref[b] for b in range(4)],
            [mhd_ref[b] for b in range(4)],
            row,
            rows_dev,
            elements,
        )
        lane_ok = lax.broadcasted_iota(jnp.int32, (1, LANES), 1) < elements
        mass_total = [jnp.where(lane_ok, m, 1.0) for m in mass_total]
        for q in range(16):
            refs[-1][q] = mass_total[q]
    else:
        mass_total = [mt_ref[q] for q in range(16)]
    lane = lax.broadcasted_iota(jnp.int32, (1, LANES), 1)
    valid = lane < elements
    _, backward_order = rotation_tables()
    groups = [(0, 1, 4, 5), (2, 3, 6, 7), (8, 9, 12, 13), (10, 11, 14, 15)]
    for f in range(4):
        out = row_fold(
            [w_ref[f, q] for q in range(16)],
            [hu_ref[f, b] for b in range(4)],
            [hd_ref[f, b] for b in range(4)],
            row,
            rows_dev,
            elements,
        )
        out = [out[q] / mass_total[q] for q in range(16)]
        new = select_rows(out, rotation, backward_order)
        new = [jnp.where(valid, new[p], 0.0) for p in range(16)]
        for p in range(16):
            out_ref[f, p] = new[p]
        if f == 3:
            for p in range(16):
                cm_ref[p] = jnp.sum(new[p], axis=0, keepdims=True)
        if with_cells:
            average = [(prev_ref[f, p] + new[p]) / SUBSTEPS for p in range(16)]
            for c, group in enumerate(groups):
                m = [m_ref[p] for p in group]
                summed = (m[0] * average[group[0]] + m[1] * average[group[1]]) + (
                    m[2] * average[group[2]] + m[3] * average[group[3]]
                )
                area = (m[0] + m[1]) + (m[2] + m[3])
                cell_ref[c, f] = summed / area


def fin_call(w, halo_up, halo_down, mass_parts, info, rows_dev, elements, prev=None, mass=None):
    levels = w.shape[2]
    steps = levels // CHUNK
    block = pl.BlockSpec((4, 16, CHUNK, LANES), lambda i: (0, 0, i, 0))
    halo = pl.BlockSpec((4, 4, CHUNK, 128), lambda i: (0, 0, i, 0))
    small = pl.BlockSpec((16, 1, LANES), lambda i: (0, 0, 0))
    mass_edge = pl.BlockSpec((4, 1, 128), lambda i: (0, 0, 0))
    with_cells = prev is not None
    with_mass = len(mass_parts) == 3
    in_specs = [block, halo, halo]
    args = [w, halo_up, halo_down] + list(mass_parts)
    in_specs += [small, mass_edge, mass_edge] if with_mass else [small]
    in_specs.append(pl.BlockSpec((8, LANES), lambda i: (0, 0)))
    args.append(info)
    out_specs = [block, pl.BlockSpec((None, 16, 1, LANES), lambda i: (i, 0, 0, 0))]
    out_shape = [
        jax.ShapeDtypeStruct(w.shape, jnp.float32),
        jax.ShapeDtypeStruct((steps, 16, 1, LANES), jnp.float32),
    ]
    if with_cells:
        in_specs += [block, small]
        args += [prev, mass]
        out_specs.append(pl.BlockSpec((4, 4, CHUNK, LANES), lambda i: (0, 0, i, 0)))
        out_shape.append(jax.ShapeDtypeStruct((4, 4, levels, LANES), jnp.float32))
    if with_mass:
        out_specs.append(small)
        out_shape.append(jax.ShapeDtypeStruct((16, 1, LANES), jnp.float32))
    return pl.pallas_call(
        functools.partial(fin_kernel, rows_dev, elements, with_cells, with_mass),
        interpret=INTERPRET,
        grid=(steps,),
        in_specs=in_specs,
        out_specs=out_specs,
        out_shape=out_shape,
    )(*args)


def edge_exchange(last, first):
    seg_count = lax.axis_size("seg")
    up = [(i, (i + 1) % seg_count) for i in range(seg_count)]
    down = [(j, i) for i, j in up]
    return lax.ppermute(last, "seg", up), lax.ppermute(first, "seg", down)


def halo_exchange(w, elements):
    seg_count = lax.axis_size("seg")
    up = [(i, (i + 1) % seg_count) for i in range(seg_count)]
    down = [(j, i) for i, j in up]
    last = w[..., 12:16, :, elements - COLS : elements]
    first = w[..., 0:4, :, 0:COLS]
    prev_last = lax.ppermute(last, "seg", up)
    next_first = lax.ppermute(first, "seg", down)
    widths = [(0, 0)] * (w.ndim - 1)
    halo_up = jnp.pad(prev_last, widths + [(0, LANES - COLS)])
    halo_down = jnp.pad(next_first, widths + [(elements - COLS, LANES - elements)])
    return halo_up, halo_down


def mass_dss(mass_canon_rows, info, rows_dev, elements):
    col = info[1:2]
    row = info[2:3]
    rows = list(mass_canon_rows)
    for a in range(4):
        edge = rows[4 * a + 3]
        left = jnp.where(col == 0, jnp.roll(edge, -(COLS - 1), -1), jnp.roll(edge, 1, -1))
        total = rows[4 * a] + left
        rows[4 * a] = total
        rows[4 * a + 3] = jnp.where(
            col == COLS - 1, jnp.roll(total, COLS - 1, -1), jnp.roll(total, -1, -1)
        )
    w = jnp.stack(rows)
    halo_up, halo_down = halo_exchange(w, elements)
    out = list(rows)
    for b in range(4):
        from_up = jnp.where(row == 0, halo_up[b], jnp.roll(rows[12 + b], COLS, -1))
        out[b] = rows[b] + from_up
        from_down = jnp.where(row == rows_dev - 1, halo_down[b], jnp.roll(rows[b], -COLS, -1))
        out[12 + b] = rows[12 + b] + from_down
    total = jnp.stack(out)
    lane = jnp.arange(LANES)
    return jnp.where(lane < elements, total, 1.0)


def local(
    velocity_pair,
    thermal_reading,
    layer_depth,
    jacobian_terms,
    rotation_frequency,
    integration_mass,
    shared_vertex_label,
    column_owner_slot,
):
    levels_dev = thermal_reading.shape[0]
    elements = thermal_reading.shape[2]
    seg_count = lax.axis_size("seg")
    lev_count = lax.axis_size("lev")
    rows_dev = elements // COLS
    node_cols = 3 * COLS
    first_row = 3 * rows_dev * lax.axis_index("seg")
    grid_rows = 3 * rows_dev * seg_count
    corner_ids = shared_vertex_label[0]
    element_pos = jnp.arange(elements)
    row_offset = (corner_ids // node_cols - first_row) % grid_rows - 3 * (element_pos // COLS)
    col_offset = (corner_ids % node_cols - 3 * (element_pos % COLS)) % node_cols
    rotation = jnp.where(
        row_offset == 0, jnp.where(col_offset == 0, 0, 1), jnp.where(col_offset == 3, 2, 3)
    )
    info = lane_info(rotation, elements)
    forward_order, _ = rotation_tables()

    prognostic = jnp.concatenate([velocity_pair, thermal_reading[None], layer_depth[None]], axis=0)
    fields = pad_lanes(jnp.transpose(prognostic, (0, 2, 1, 3)))
    jac = pad_lanes(jacobian_terms[:, :, None, :])
    rot = pad_lanes(rotation_frequency[:, None, :])
    mass = pad_lanes(integration_mass[:, None, :])
    mass_one = pad_lanes(integration_mass[:, None, :], 1.0)
    mass_canon, mass_folded, mass_last, mass_first = mass_call(mass, info, elements)
    mass_up, mass_down = edge_exchange(mass_last, mass_first)
    mass_parts = (mass_folded, mass_up, mass_down)
    column_mass = jnp.sum(fields[3], axis=1, keepdims=True)
    previous = None
    cells = None
    for substep in range(SUBSTEPS):
        above = carried_in(column_mass, "lev", False)
        g0, group_height = term_call(fields, above)
        below = carried_in(group_height, "lev", True)
        w, last, first = adv_call(fields, g0, below, jac, rot, mass_canon, info, elements)
        halo_up, halo_down = edge_exchange(last, first)
        outs = fin_call(
            w,
            halo_up,
            halo_down,
            mass_parts,
            info,
            rows_dev,
            elements,
            previous if substep == SUBSTEPS - 1 else None,
            mass_one,
        )
        fields, column_parts = outs[:2]
        if substep == SUBSTEPS - 1:
            cells = outs[2]
        if len(mass_parts) == 3:
            mass_parts = (outs[-1],)
        previous = fields
        column_mass = jnp.sum(column_parts, axis=0)
    channels = 4 * levels_dev
    cell_values = cells[..., :elements].reshape(4, channels, elements)
    payload = jnp.transpose(cell_values, (0, 2, 1)).reshape(4 * elements, channels)
    dev_count = seg_count * lev_count
    own_cols = 4 * elements * seg_count // dev_count
    per_pair = own_cols // seg_count
    capacity = per_pair + per_pair // 2
    assert capacity <= channels
    targets = column_owner_slot.reshape(-1)
    owner_index = targets // own_cols
    slot_index = targets % own_cols
    cell_count = targets.shape[0]
    cell_pos = jnp.arange(cell_count)
    same_owner = owner_index[:, None] == owner_index[None, :]
    earlier = cell_pos[:, None] < cell_pos[None, :]
    rank = jnp.sum(jnp.logical_and(same_owner, earlier).astype(jnp.int32), axis=0)
    destination = owner_index * capacity + rank
    slots = jnp.arange(dev_count * capacity)
    code = cell_pos * (own_cols + 1) + slot_index + 1
    match = destination[:, None] == slots[None, :]
    found = jnp.sum(jnp.where(match, code[:, None], 0), axis=0)
    has = found > 0
    source_cell = jnp.maximum(found - 1, 0) // (own_cols + 1)
    source_pos = jnp.maximum(found - 1, 0) % (own_cols + 1)
    outgoing = jnp.where(has[:, None], payload[source_cell], 0.0)
    ids = jnp.where(has, source_pos, -1).astype(jnp.float32).reshape(dev_count, capacity)
    ids = jnp.pad(ids, ((0, 0), (0, channels - capacity)), constant_values=-1.0)
    buffer = jnp.concatenate(
        [outgoing.reshape(dev_count, capacity, channels), ids[:, None, :]], axis=1
    )
    received = lax.all_to_all(buffer, ("seg", "lev"), split_axis=0, concat_axis=0, tiled=True)
    received_ids = jnp.round(received[:, capacity, :capacity]).astype(jnp.int32)
    received_rows = received[:, :capacity, :].reshape(dev_count * capacity, channels)
    flat = jnp.arange(dev_count * capacity).reshape(dev_count, capacity)
    source_lev = (jnp.arange(dev_count) % lev_count)[:, None]
    positions = jnp.arange(own_cols)
    picks = []
    for group in range(lev_count):
        hit = jnp.logical_and(
            received_ids[:, :, None] == positions[None, None, :], (source_lev == group)[:, :, None]
        )
        picks.append(jnp.sum(jnp.where(hit, flat[:, :, None], 0), axis=(0, 1)))
    arrived = received_rows[jnp.stack(picks)]
    arrived = arrived.reshape(lev_count, own_cols, 4, levels_dev).transpose(2, 0, 3, 1)
    phys_state = arrived.reshape(4, lev_count * levels_dev, own_cols)
    mean_thickness = jnp.mean(phys_state[3], axis=0)
    dyn_state = jnp.transpose(fields[..., :elements], (0, 2, 1, 3))
    return (dyn_state, phys_state, mean_thickness)


def solution(mesh):
    in_specs = (
        P(None, "lev", None, "seg"),
        P("lev", None, "seg"),
        P("lev", None, "seg"),
        P(None, None, "seg"),
        P(None, "seg"),
        P(None, "seg"),
        P(None, "seg"),
        P(None, "seg"),
    )
    out_specs = (P(None, "lev", None, "seg"), P(None, None, ("seg", "lev")), P(("seg", "lev")))
    return jax.shard_map(local, mesh=mesh, in_specs=in_specs, out_specs=out_specs, check_vma=False)
```

```python
import functools

import jax
import jax.numpy as jnp
import numpy as np
from jax import lax
from jax.experimental import pallas as pl
from jax.experimental.pallas import tpu as pltpu
from jax.sharding import PartitionSpec as P

COLS = 120
SUBSTEPS = 2


top_pressure = 10.0
time_increment = 0.05


def gll_slopes():
    root_five = np.sqrt(5.0)
    gll_nodes = [-1.0, -1.0 / root_five, 1.0 / root_five, 1.0]
    legendre_values = [-1.0, 1.0 / root_five, -1.0 / root_five, 1.0]
    slopes = np.zeros((4, 4))
    for row_node in range(4):
        for column in range(4):
            if row_node != column:
                slopes[row_node, column] = (
                    legendre_values[row_node]
                    / legendre_values[column]
                    / (gll_nodes[row_node] - gll_nodes[column])
                )
    slopes[0, 0] = -3.0
    slopes[3, 3] = 3.0
    return slopes


SLOPES = gll_slopes().astype(np.float32)


def rotation_tables():
    forward = np.zeros((4, 16), np.int32)
    for first_pos in range(4):
        for second_pos in range(4):
            canonical = 4 * first_pos + second_pos
            forward[0, canonical] = 4 * first_pos + second_pos
            forward[1, canonical] = 4 * (3 - second_pos) + first_pos
            forward[2, canonical] = 4 * (3 - first_pos) + (3 - second_pos)
            forward[3, canonical] = 4 * second_pos + 3 - first_pos
    backward = np.argsort(forward, axis=1).astype(np.int32)
    return (forward, backward)


def weighted_sum(terms):
    acc = None
    for coef, value in terms:
        if coef == 0.0:
            continue
        part = jnp.float32(coef) * value
        acc = part if acc is None else acc + part
    return acc


def first_deriv(f):
    return jnp.stack(
        [
            weighted_sum([(SLOPES[a, k], f[4 * k + j]) for k in range(4)])
            for a in range(4)
            for j in range(4)
        ]
    )


def second_deriv(f):
    return jnp.stack(
        [
            weighted_sum([(SLOPES[a, k], f[4 * i + k]) for k in range(4)])
            for i in range(4)
            for a in range(4)
        ]
    )


def carried_in(part, axis, reverse):
    count = lax.axis_size(axis)
    place = lax.axis_index(axis)
    gathered = lax.all_gather(part, axis)
    index = jnp.arange(count).reshape((count,) + (1,) * part.ndim)
    chosen = index > place if reverse else index < place
    return jnp.sum(jnp.where(chosen, gathered, jnp.zeros_like(gathered)), axis=0)


def site_potential_energy(thermal_reading, layer_depth):
    column_mass = jnp.sum(layer_depth, axis=1)
    above_sum = carried_in(column_mass, "lev", False)
    layer_midpoint_load = (
        top_pressure + above_sum[:, None, :] + jnp.cumsum(layer_depth, axis=1) - 0.5 * layer_depth
    )
    surface_change_rate = thermal_reading * layer_depth / layer_midpoint_load
    group_height = jnp.sum(surface_change_rate, axis=1)
    below_sum = carried_in(group_height, "lev", True)
    return (
        below_sum[:, None, :]
        + lax.cumsum(surface_change_rate, axis=1, reverse=True)
        - 0.5 * surface_change_rate
    )


def tendency_step(u, v, temp, dp, geopotential, jac, rot):
    energy = geopotential + 0.5 * (u * u + v * v)
    energy_first = first_deriv(energy)
    energy_second = second_deriv(energy)
    zonal_slope = jac[0] * energy_first + jac[1] * energy_second
    meridional_slope = jac[2] * energy_first + jac[3] * energy_second
    initial_transport = jac[0] * u + jac[2] * v
    latter_transport = jac[1] * u + jac[3] * v
    advect_with_motion = initial_transport * first_deriv(temp) + latter_transport * second_deriv(
        temp
    )
    distribute_onto_vertices = first_deriv(dp * initial_transport) + second_deriv(
        dp * latter_transport
    )
    return (
        u + time_increment * (rot * v - zonal_slope),
        v - time_increment * (rot * u + meridional_slope),
        temp - time_increment * advect_with_motion,
        dp - time_increment * distribute_onto_vertices,
    )


def reorder(values, rotation, table):
    rows = []
    for q in range(16):
        pick = values[int(table[3, q])]
        for w in (2, 1, 0):
            pick = jnp.where(rotation == w, values[int(table[w, q])], pick)
        rows.append(pick)
    return jnp.stack(rows)


def node_sum(canon, col, row, rows_dev):
    elements = canon.shape[-1]

    def roll(y, shift):
        return jnp.roll(y, shift, axis=-1)

    rows = [canon[q] for q in range(16)]
    for a in range(4):
        left = jnp.where(col == 0, roll(rows[4 * a + 3], -(COLS - 1)), roll(rows[4 * a + 3], 1))
        total = rows[4 * a] + left
        rows[4 * a] = total
        rows[4 * a + 3] = jnp.where(col == COLS - 1, roll(total, COLS - 1), roll(total, -1))
    seg_count = lax.axis_size("seg")
    up = [(i, (i + 1) % seg_count) for i in range(seg_count)]
    down = [(j, i) for i, j in up]
    last = jnp.stack([rows[12 + b][:, elements - COLS :] for b in range(4)])
    first = jnp.stack([rows[b][:, :COLS] for b in range(4)])
    prev_last = lax.ppermute(last, "seg", up)
    next_first = lax.ppermute(first, "seg", down)
    pad = jnp.zeros(prev_last.shape[1:-1] + (elements - COLS,), canon.dtype)
    out = list(rows)
    for b in range(4):
        halo_up = jnp.concatenate([prev_last[b], pad], axis=-1)
        from_up = jnp.where(row == 0, halo_up, roll(rows[12 + b], COLS))
        out[b] = rows[b] + from_up
        halo_down = jnp.concatenate([pad, next_first[b]], axis=-1)
        from_down = jnp.where(row == rows_dev - 1, halo_down, roll(rows[b], -COLS))
        out[12 + b] = rows[12 + b] + from_down
    return jnp.stack(out)


LANES = 512
CHUNK = 8
INTERPRET = None


def lane_info(rotation, elements):
    element_pos = jnp.arange(elements)
    info = jnp.stack(
        [rotation, element_pos % COLS, element_pos // COLS]
        + [jnp.zeros_like(rotation)] * 5
    ).astype(jnp.int32)
    return jnp.pad(info, ((0, 0), (0, LANES - elements)), constant_values=-1)


def pad_lanes(x, value=0.0):
    widths = [(0, 0)] * (x.ndim - 1) + [(0, LANES - x.shape[-1])]
    return jnp.pad(x, widths, constant_values=value)


def select_rows(values, rotation, table):
    rows = []
    for q in range(16):
        pick = values[int(table[3, q])]
        for w in (2, 1, 0):
            pick = jnp.where(rotation == w, values[int(table[w, q])], pick)
        rows.append(pick)
    return rows


def term_kernel(levels, f_ref, above_ref, g_ref, gh_ref):
    level = lax.broadcasted_iota(jnp.int32, (levels, LANES), 0)
    for p in range(f_ref.shape[1]):
        temp = f_ref[0, p]
        dp = f_ref[1, p]
        cum = dp
        shift = 1
        while shift < levels:
            cum = cum + jnp.where(level >= shift, pltpu.roll(cum, shift, 0), 0.0)
            shift *= 2
        load = top_pressure + above_ref[p] + cum - 0.5 * dp
        term = temp * dp / load
        gh_ref[p] = jnp.sum(term, axis=0, keepdims=True)
        rcum = term
        shift = 1
        while shift < levels:
            rcum = rcum + jnp.where(
                level + shift < levels, pltpu.roll(rcum, levels - shift, 0), 0.0
            )
            shift *= 2
        g_ref[p] = rcum - 0.5 * term


def term_call(fields, above):
    levels = fields.shape[2]
    group = 4
    return pl.pallas_call(
        functools.partial(term_kernel, levels),
        interpret=INTERPRET,
        grid=(16 // group,),
        in_specs=[
            pl.BlockSpec((2, group, levels, LANES), lambda i: (1, i, 0, 0)),
            pl.BlockSpec((group, 1, LANES), lambda i: (i, 0, 0)),
        ],
        out_specs=[
            pl.BlockSpec((group, levels, LANES), lambda i: (i, 0, 0)),
            pl.BlockSpec((group, 1, LANES), lambda i: (i, 0, 0)),
        ],
        out_shape=[
            jax.ShapeDtypeStruct((16, levels, LANES), jnp.float32),
            jax.ShapeDtypeStruct((16, 1, LANES), jnp.float32),
        ],
    )(fields, above)


def lane_roll(y, shift):
    return pltpu.roll(y, shift % LANES, 1)


def column_fold(rows, col):
    rows = list(rows)
    for a in range(4):
        edge = rows[4 * a + 3]
        left = jnp.where(col == 0, lane_roll(edge, -(COLS - 1)), lane_roll(edge, 1))
        total = rows[4 * a] + left
        rows[4 * a] = total
        rows[4 * a + 3] = jnp.where(
            col == COLS - 1, lane_roll(total, COLS - 1), lane_roll(total, -1)
        )
    return rows


def row_fold(rows, up_rows, down_rows, row, rows_dev, elements):
    out = list(rows)
    for b in range(4):
        fill = jnp.zeros((rows[b].shape[0], LANES - 128), jnp.float32)
        halo_up = jnp.concatenate([up_rows[b], fill], axis=1)
        halo_down = lane_roll(jnp.concatenate([down_rows[b], fill], axis=1), elements - COLS)
        from_up = jnp.where(row == 0, halo_up, lane_roll(rows[12 + b], COLS))
        out[b] = rows[b] + from_up
        from_down = jnp.where(row == rows_dev - 1, halo_down, lane_roll(rows[b], -COLS))
        out[12 + b] = rows[12 + b] + from_down
    return out


def mass_kernel(elements, m_ref, info_ref, mc_ref, mw_ref, last_ref, first_ref):
    info = info_ref[...]
    forward_order, _ = rotation_tables()
    canon = select_rows([m_ref[p] for p in range(16)], info[0:1], forward_order)
    rows = column_fold(canon, info[1:2])
    for q in range(16):
        mc_ref[q] = canon[q]
        mw_ref[q] = rows[q]
    for b in range(4):
        last_ref[b] = lane_roll(rows[12 + b], COLS - elements)[:, :128]
        first_ref[b] = rows[b][:, :128]


def mass_call(mass, info, elements):
    small = jax.ShapeDtypeStruct((16, 1, LANES), jnp.float32)
    edge = jax.ShapeDtypeStruct((4, 1, 128), jnp.float32)
    return pl.pallas_call(
        functools.partial(mass_kernel, elements),
        interpret=INTERPRET,
        out_shape=[small, small, edge, edge],
    )(mass, info)


def adv_kernel(elements, f_ref, g_ref, below_ref, jac_ref, rot_ref, mc_ref, info_ref, out_ref, last_ref, first_ref):
    info = info_ref[...]
    rotation = info[0:1]
    col = info[1:2]
    forward_order, _ = rotation_tables()
    u = [f_ref[0, p] for p in range(16)]
    v = [f_ref[1, p] for p in range(16)]
    temp = [f_ref[2, p] for p in range(16)]
    dp = [f_ref[3, p] for p in range(16)]
    jac = [[jac_ref[k, p] for p in range(16)] for k in range(4)]
    energy = [
        (below_ref[p] + g_ref[p]) + 0.5 * (u[p] * u[p] + v[p] * v[p]) for p in range(16)
    ]
    e1 = first_rows(energy)
    e2 = second_rows(energy)
    it = [jac[0][p] * u[p] + jac[2][p] * v[p] for p in range(16)]
    lt = [jac[1][p] * u[p] + jac[3][p] * v[p] for p in range(16)]
    t1 = first_rows(temp)
    t2 = second_rows(temp)
    d1 = first_rows([dp[p] * it[p] for p in range(16)])
    d2 = second_rows([dp[p] * lt[p] for p in range(16)])
    advanced = []
    for p in range(16):
        rot = rot_ref[p]
        zonal_slope = jac[0][p] * e1[p] + jac[1][p] * e2[p]
        meridional_slope = jac[2][p] * e1[p] + jac[3][p] * e2[p]
        advanced.append(
            (
                u[p] + time_increment * (rot * v[p] - zonal_slope),
                v[p] - time_increment * (rot * u[p] + meridional_slope),
                temp[p] - time_increment * (it[p] * t1[p] + lt[p] * t2[p]),
                dp[p] - time_increment * (d1[p] + d2[p]),
            )
        )
    for f in range(4):
        rows = select_rows([advanced[p][f] for p in range(16)], rotation, forward_order)
        rows = column_fold([rows[q] * mc_ref[q] for q in range(16)], col)
        for q in range(16):
            out_ref[f, q] = rows[q]
        for b in range(4):
            last_ref[f, b] = lane_roll(rows[12 + b], COLS - elements)[:, :128]
            first_ref[f, b] = rows[b][:, :128]


def first_rows(rows):
    return [
        weighted_sum([(SLOPES[a, k], rows[4 * k + j]) for k in range(4)])
        for a in range(4)
        for j in range(4)
    ]


def second_rows(rows):
    return [
        weighted_sum([(SLOPES[a, k], rows[4 * i + k]) for k in range(4)])
        for i in range(4)
        for a in range(4)
    ]


def adv_call(fields, g0, below, jac, rot, mass_canon, info, elements):
    levels = fields.shape[2]
    steps = levels // CHUNK
    small = pl.BlockSpec((16, 1, LANES), lambda i: (0, 0, 0))
    edge = pl.BlockSpec((4, 4, CHUNK, 128), lambda i: (0, 0, i, 0))
    edge_shape = jax.ShapeDtypeStruct((4, 4, levels, 128), jnp.float32)
    return pl.pallas_call(
        functools.partial(adv_kernel, elements),
        interpret=INTERPRET,
        grid=(steps,),
        in_specs=[
            pl.BlockSpec((4, 16, CHUNK, LANES), lambda i: (0, 0, i, 0)),
            pl.BlockSpec((16, CHUNK, LANES), lambda i: (0, i, 0)),
            small,
            pl.BlockSpec((4, 16, 1, LANES), lambda i: (0, 0, 0, 0)),
            small,
            small,
            pl.BlockSpec((8, LANES), lambda i: (0, 0)),
        ],
        out_specs=[pl.BlockSpec((4, 16, CHUNK, LANES), lambda i: (0, 0, i, 0)), edge, edge],
        out_shape=[jax.ShapeDtypeStruct(fields.shape, jnp.float32), edge_shape, edge_shape],
    )(fields, g0, below, jac, rot, mass_canon, info)


def fin_kernel(rows_dev, elements, with_cells, with_mass, *refs):
    refs = list(refs)
    w_ref, hu_ref, hd_ref = refs[:3]
    if with_mass:
        mw_ref, mhu_ref, mhd_ref = refs[3:6]
        refs = refs[6:]
    else:
        mt_ref = refs[3]
        refs = refs[4:]
    info_ref = refs.pop(0)
    if with_cells:
        prev_ref, m_ref = refs[:2]
        refs = refs[2:]
    out_ref, cm_ref = refs[:2]
    if with_cells:
        cell_ref = refs[2]
    info = info_ref[...]
    rotation = info[0:1]
    row = info[2:3]
    if with_mass:
        mass_total = row_fold(
            [mw_ref[q] for q in range(16)],
            [mhu_ref[b] for b in range(4)],
            [mhd_ref[b] for b in range(4)],
            row,
            rows_dev,
            elements,
        )
        lane_ok = lax.broadcasted_iota(jnp.int32, (1, LANES), 1) < elements
        mass_total = [jnp.where(lane_ok, m, 1.0) for m in mass_total]
        for q in range(16):
            refs[-1][q] = mass_total[q]
    else:
        mass_total = [mt_ref[q] for q in range(16)]
    lane = lax.broadcasted_iota(jnp.int32, (1, LANES), 1)
    valid = lane < elements
    _, backward_order = rotation_tables()
    groups = [(0, 1, 4, 5), (2, 3, 6, 7), (8, 9, 12, 13), (10, 11, 14, 15)]
    for f in range(4):
        out = row_fold(
            [w_ref[f, q] for q in range(16)],
            [hu_ref[f, b] for b in range(4)],
            [hd_ref[f, b] for b in range(4)],
            row,
            rows_dev,
            elements,
        )
        out = [out[q] / mass_total[q] for q in range(16)]
        new = select_rows(out, rotation, backward_order)
        new = [jnp.where(valid, new[p], 0.0) for p in range(16)]
        for p in range(16):
            out_ref[f, p] = new[p]
        if f == 3:
            for p in range(16):
                cm_ref[p] = jnp.sum(new[p], axis=0, keepdims=True)
        if with_cells:
            average = [(prev_ref[f, p] + new[p]) / SUBSTEPS for p in range(16)]
            for c, group in enumerate(groups):
                m = [m_ref[p] for p in group]
                summed = (m[0] * average[group[0]] + m[1] * average[group[1]]) + (
                    m[2] * average[group[2]] + m[3] * average[group[3]]
                )
                area = (m[0] + m[1]) + (m[2] + m[3])
                cell_ref[c, f] = summed / area


def fin_call(w, halo_up, halo_down, mass_parts, info, rows_dev, elements, prev=None, mass=None):
    levels = w.shape[2]
    steps = levels // CHUNK
    block = pl.BlockSpec((4, 16, CHUNK, LANES), lambda i: (0, 0, i, 0))
    halo = pl.BlockSpec((4, 4, CHUNK, 128), lambda i: (0, 0, i, 0))
    small = pl.BlockSpec((16, 1, LANES), lambda i: (0, 0, 0))
    mass_edge = pl.BlockSpec((4, 1, 128), lambda i: (0, 0, 0))
    with_cells = prev is not None
    with_mass = len(mass_parts) == 3
    in_specs = [block, halo, halo]
    args = [w, halo_up, halo_down] + list(mass_parts)
    in_specs += [small, mass_edge, mass_edge] if with_mass else [small]
    in_specs.append(pl.BlockSpec((8, LANES), lambda i: (0, 0)))
    args.append(info)
    out_specs = [block, pl.BlockSpec((None, 16, 1, LANES), lambda i: (i, 0, 0, 0))]
    out_shape = [
        jax.ShapeDtypeStruct(w.shape, jnp.float32),
        jax.ShapeDtypeStruct((steps, 16, 1, LANES), jnp.float32),
    ]
    if with_cells:
        in_specs += [block, small]
        args += [prev, mass]
        out_specs.append(pl.BlockSpec((4, 4, CHUNK, LANES), lambda i: (0, 0, i, 0)))
        out_shape.append(jax.ShapeDtypeStruct((4, 4, levels, LANES), jnp.float32))
    if with_mass:
        out_specs.append(small)
        out_shape.append(jax.ShapeDtypeStruct((16, 1, LANES), jnp.float32))
    return pl.pallas_call(
        functools.partial(fin_kernel, rows_dev, elements, with_cells, with_mass),
        interpret=INTERPRET,
        grid=(steps,),
        in_specs=in_specs,
        out_specs=out_specs,
        out_shape=out_shape,
    )(*args)


def edge_exchange(last, first):
    seg_count = lax.axis_size("seg")
    up = [(i, (i + 1) % seg_count) for i in range(seg_count)]
    down = [(j, i) for i, j in up]
    return lax.ppermute(last, "seg", up), lax.ppermute(first, "seg", down)


def halo_exchange(w, elements):
    seg_count = lax.axis_size("seg")
    up = [(i, (i + 1) % seg_count) for i in range(seg_count)]
    down = [(j, i) for i, j in up]
    last = w[..., 12:16, :, elements - COLS : elements]
    first = w[..., 0:4, :, 0:COLS]
    prev_last = lax.ppermute(last, "seg", up)
    next_first = lax.ppermute(first, "seg", down)
    widths = [(0, 0)] * (w.ndim - 1)
    halo_up = jnp.pad(prev_last, widths + [(0, LANES - COLS)])
    halo_down = jnp.pad(next_first, widths + [(elements - COLS, LANES - elements)])
    return halo_up, halo_down


def mass_dss(mass_canon_rows, info, rows_dev, elements):
    col = info[1:2]
    row = info[2:3]
    rows = list(mass_canon_rows)
    for a in range(4):
        edge = rows[4 * a + 3]
        left = jnp.where(col == 0, jnp.roll(edge, -(COLS - 1), -1), jnp.roll(edge, 1, -1))
        total = rows[4 * a] + left
        rows[4 * a] = total
        rows[4 * a + 3] = jnp.where(
            col == COLS - 1, jnp.roll(total, COLS - 1, -1), jnp.roll(total, -1, -1)
        )
    w = jnp.stack(rows)
    halo_up, halo_down = halo_exchange(w, elements)
    out = list(rows)
    for b in range(4):
        from_up = jnp.where(row == 0, halo_up[b], jnp.roll(rows[12 + b], COLS, -1))
        out[b] = rows[b] + from_up
        from_down = jnp.where(row == rows_dev - 1, halo_down[b], jnp.roll(rows[b], -COLS, -1))
        out[12 + b] = rows[12 + b] + from_down
    total = jnp.stack(out)
    lane = jnp.arange(LANES)
    return jnp.where(lane < elements, total, 1.0)


def local(
    velocity_pair,
    thermal_reading,
    layer_depth,
    jacobian_terms,
    rotation_frequency,
    integration_mass,
    shared_vertex_label,
    column_owner_slot,
):
    levels_dev = thermal_reading.shape[0]
    elements = thermal_reading.shape[2]
    seg_count = lax.axis_size("seg")
    lev_count = lax.axis_size("lev")
    rows_dev = elements // COLS
    node_cols = 3 * COLS
    first_row = 3 * rows_dev * lax.axis_index("seg")
    grid_rows = 3 * rows_dev * seg_count
    corner_ids = shared_vertex_label[0]
    element_pos = jnp.arange(elements)
    row_offset = (corner_ids // node_cols - first_row) % grid_rows - 3 * (element_pos // COLS)
    col_offset = (corner_ids % node_cols - 3 * (element_pos % COLS)) % node_cols
    rotation = jnp.where(
        row_offset == 0, jnp.where(col_offset == 0, 0, 1), jnp.where(col_offset == 3, 2, 3)
    )
    info = lane_info(rotation, elements)
    forward_order, _ = rotation_tables()

    prognostic = jnp.concatenate([velocity_pair, thermal_reading[None], layer_depth[None]], axis=0)
    fields = pad_lanes(jnp.transpose(prognostic, (0, 2, 1, 3)))
    jac = pad_lanes(jacobian_terms[:, :, None, :])
    rot = pad_lanes(rotation_frequency[:, None, :])
    mass = pad_lanes(integration_mass[:, None, :])
    mass_one = pad_lanes(integration_mass[:, None, :], 1.0)
    mass_canon, mass_folded, mass_last, mass_first = mass_call(mass, info, elements)
    mass_up, mass_down = edge_exchange(mass_last, mass_first)
    mass_parts = (mass_folded, mass_up, mass_down)
    column_mass = jnp.sum(fields[3], axis=1, keepdims=True)
    previous = None
    cells = None
    for substep in range(SUBSTEPS):
        above = carried_in(column_mass, "lev", False)
        g0, group_height = term_call(fields, above)
        below = carried_in(group_height, "lev", True)
        w, last, first = adv_call(fields, g0, below, jac, rot, mass_canon, info, elements)
        halo_up, halo_down = edge_exchange(last, first)
        outs = fin_call(
            w,
            halo_up,
            halo_down,
            mass_parts,
            info,
            rows_dev,
            elements,
            previous if substep == SUBSTEPS - 1 else None,
            mass_one,
        )
        fields, column_parts = outs[:2]
        if substep == SUBSTEPS - 1:
            cells = outs[2]
        if len(mass_parts) == 3:
            mass_parts = (outs[-1],)
        previous = fields
        column_mass = jnp.sum(column_parts, axis=0)
    channels = 4 * levels_dev
    cell_values = cells[..., :elements].reshape(4, channels, elements)
    payload = jnp.transpose(cell_values, (0, 2, 1)).reshape(4 * elements, channels)
    dev_count = seg_count * lev_count
    own_cols = 4 * elements * seg_count // dev_count
    per_pair = own_cols // seg_count
    capacity = per_pair + per_pair // 2
    targets = column_owner_slot.reshape(-1)
    owner_index = targets // own_cols
    slot_index = targets % own_cols
    cell_count = targets.shape[0]
    cell_pos = jnp.arange(cell_count)
    same_owner = owner_index[:, None] == owner_index[None, :]
    earlier = cell_pos[:, None] < cell_pos[None, :]
    rank = jnp.sum(jnp.logical_and(same_owner, earlier).astype(jnp.int32), axis=0)
    destination = owner_index * capacity + rank
    slots = jnp.arange(dev_count * capacity)
    code = cell_pos * (own_cols + 1) + slot_index + 1
    match = destination[:, None] == slots[None, :]
    found = jnp.sum(jnp.where(match, code[:, None], 0), axis=0)
    has = found > 0
    source_cell = jnp.maximum(found - 1, 0) // (own_cols + 1)
    source_pos = jnp.maximum(found - 1, 0) % (own_cols + 1)
    outgoing = jnp.where(has[:, None], payload[source_cell], 0.0)
    ids = jnp.where(has, source_pos, -1).reshape(dev_count, capacity)
    received_ids = lax.all_to_all(ids, ("seg", "lev"), split_axis=0, concat_axis=0, tiled=True)
    flat = jnp.arange(dev_count * capacity).reshape(dev_count, capacity)
    source_lev = (jnp.arange(dev_count) % lev_count)[:, None]
    positions = jnp.arange(own_cols)
    picks = []
    for group in range(lev_count):
        hit = jnp.logical_and(
            received_ids[:, :, None] == positions[None, None, :], (source_lev == group)[:, :, None]
        )
        picks.append(jnp.sum(jnp.where(hit, flat[:, :, None], 0), axis=(0, 1)))
    buffer = outgoing.reshape(dev_count, capacity, channels)
    received = lax.all_to_all(buffer, ("seg", "lev"), split_axis=0, concat_axis=0, tiled=True)
    received_rows = received.reshape(dev_count * capacity, channels)
    arrived = received_rows[jnp.stack(picks)]
    arrived = arrived.reshape(lev_count, own_cols, 4, levels_dev).transpose(2, 0, 3, 1)
    phys_state = arrived.reshape(4, lev_count * levels_dev, own_cols)
    mean_thickness = jnp.mean(phys_state[3], axis=0)
    dyn_state = jnp.transpose(fields[..., :elements], (0, 2, 1, 3))
    return (dyn_state, phys_state, mean_thickness)


def solution(mesh):
    in_specs = (
        P(None, "lev", None, "seg"),
        P("lev", None, "seg"),
        P("lev", None, "seg"),
        P(None, None, "seg"),
        P(None, "seg"),
        P(None, "seg"),
        P(None, "seg"),
        P(None, "seg"),
    )
    out_specs = (P(None, "lev", None, "seg"), P(None, None, ("seg", "lev")), P(("seg", "lev")))
    return jax.shard_map(local, mesh=mesh, in_specs=in_specs, out_specs=out_specs, check_vma=False)
```

```python
import functools

import jax
import jax.numpy as jnp
import numpy as np
from jax import lax
from jax.experimental import pallas as pl
from jax.experimental.pallas import tpu as pltpu
from jax.sharding import PartitionSpec as P

COLS = 120
SUBSTEPS = 2


top_pressure = 10.0
time_increment = 0.05


def gll_slopes():
    root_five = np.sqrt(5.0)
    gll_nodes = [-1.0, -1.0 / root_five, 1.0 / root_five, 1.0]
    legendre_values = [-1.0, 1.0 / root_five, -1.0 / root_five, 1.0]
    slopes = np.zeros((4, 4))
    for row_node in range(4):
        for column in range(4):
            if row_node != column:
                slopes[row_node, column] = (
                    legendre_values[row_node]
                    / legendre_values[column]
                    / (gll_nodes[row_node] - gll_nodes[column])
                )
    slopes[0, 0] = -3.0
    slopes[3, 3] = 3.0
    return slopes


SLOPES = gll_slopes().astype(np.float32)


def rotation_tables():
    forward = np.zeros((4, 16), np.int32)
    for first_pos in range(4):
        for second_pos in range(4):
            canonical = 4 * first_pos + second_pos
            forward[0, canonical] = 4 * first_pos + second_pos
            forward[1, canonical] = 4 * (3 - second_pos) + first_pos
            forward[2, canonical] = 4 * (3 - first_pos) + (3 - second_pos)
            forward[3, canonical] = 4 * second_pos + 3 - first_pos
    backward = np.argsort(forward, axis=1).astype(np.int32)
    return (forward, backward)


def weighted_sum(terms):
    acc = None
    for coef, value in terms:
        if coef == 0.0:
            continue
        part = jnp.float32(coef) * value
        acc = part if acc is None else acc + part
    return acc


def first_deriv(f):
    return jnp.stack(
        [
            weighted_sum([(SLOPES[a, k], f[4 * k + j]) for k in range(4)])
            for a in range(4)
            for j in range(4)
        ]
    )


def second_deriv(f):
    return jnp.stack(
        [
            weighted_sum([(SLOPES[a, k], f[4 * i + k]) for k in range(4)])
            for i in range(4)
            for a in range(4)
        ]
    )


def carried_in(part, axis, reverse):
    count = lax.axis_size(axis)
    place = lax.axis_index(axis)
    gathered = lax.all_gather(part, axis)
    index = jnp.arange(count).reshape((count,) + (1,) * part.ndim)
    chosen = index > place if reverse else index < place
    return jnp.sum(jnp.where(chosen, gathered, jnp.zeros_like(gathered)), axis=0)


def site_potential_energy(thermal_reading, layer_depth):
    column_mass = jnp.sum(layer_depth, axis=1)
    above_sum = carried_in(column_mass, "lev", False)
    layer_midpoint_load = (
        top_pressure + above_sum[:, None, :] + jnp.cumsum(layer_depth, axis=1) - 0.5 * layer_depth
    )
    surface_change_rate = thermal_reading * layer_depth / layer_midpoint_load
    group_height = jnp.sum(surface_change_rate, axis=1)
    below_sum = carried_in(group_height, "lev", True)
    return (
        below_sum[:, None, :]
        + lax.cumsum(surface_change_rate, axis=1, reverse=True)
        - 0.5 * surface_change_rate
    )


def tendency_step(u, v, temp, dp, geopotential, jac, rot):
    energy = geopotential + 0.5 * (u * u + v * v)
    energy_first = first_deriv(energy)
    energy_second = second_deriv(energy)
    zonal_slope = jac[0] * energy_first + jac[1] * energy_second
    meridional_slope = jac[2] * energy_first + jac[3] * energy_second
    initial_transport = jac[0] * u + jac[2] * v
    latter_transport = jac[1] * u + jac[3] * v
    advect_with_motion = initial_transport * first_deriv(temp) + latter_transport * second_deriv(
        temp
    )
    distribute_onto_vertices = first_deriv(dp * initial_transport) + second_deriv(
        dp * latter_transport
    )
    return (
        u + time_increment * (rot * v - zonal_slope),
        v - time_increment * (rot * u + meridional_slope),
        temp - time_increment * advect_with_motion,
        dp - time_increment * distribute_onto_vertices,
    )


def reorder(values, rotation, table):
    rows = []
    for q in range(16):
        pick = values[int(table[3, q])]
        for w in (2, 1, 0):
            pick = jnp.where(rotation == w, values[int(table[w, q])], pick)
        rows.append(pick)
    return jnp.stack(rows)


def node_sum(canon, col, row, rows_dev):
    elements = canon.shape[-1]

    def roll(y, shift):
        return jnp.roll(y, shift, axis=-1)

    rows = [canon[q] for q in range(16)]
    for a in range(4):
        left = jnp.where(col == 0, roll(rows[4 * a + 3], -(COLS - 1)), roll(rows[4 * a + 3], 1))
        total = rows[4 * a] + left
        rows[4 * a] = total
        rows[4 * a + 3] = jnp.where(col == COLS - 1, roll(total, COLS - 1), roll(total, -1))
    seg_count = lax.axis_size("seg")
    up = [(i, (i + 1) % seg_count) for i in range(seg_count)]
    down = [(j, i) for i, j in up]
    last = jnp.stack([rows[12 + b][:, elements - COLS :] for b in range(4)])
    first = jnp.stack([rows[b][:, :COLS] for b in range(4)])
    prev_last = lax.ppermute(last, "seg", up)
    next_first = lax.ppermute(first, "seg", down)
    pad = jnp.zeros(prev_last.shape[1:-1] + (elements - COLS,), canon.dtype)
    out = list(rows)
    for b in range(4):
        halo_up = jnp.concatenate([prev_last[b], pad], axis=-1)
        from_up = jnp.where(row == 0, halo_up, roll(rows[12 + b], COLS))
        out[b] = rows[b] + from_up
        halo_down = jnp.concatenate([pad, next_first[b]], axis=-1)
        from_down = jnp.where(row == rows_dev - 1, halo_down, roll(rows[b], -COLS))
        out[12 + b] = rows[12 + b] + from_down
    return jnp.stack(out)


LANES = 512
CHUNK = 8
INTERPRET = None


def lane_info(rotation, elements):
    element_pos = jnp.arange(elements)
    info = jnp.stack(
        [rotation, element_pos % COLS, element_pos // COLS]
        + [jnp.zeros_like(rotation)] * 5
    ).astype(jnp.int32)
    return jnp.pad(info, ((0, 0), (0, LANES - elements)), constant_values=-1)


def pad_lanes(x, value=0.0):
    widths = [(0, 0)] * (x.ndim - 1) + [(0, LANES - x.shape[-1])]
    return jnp.pad(x, widths, constant_values=value)


def select_rows(values, rotation, table):
    rows = []
    for q in range(16):
        pick = values[int(table[3, q])]
        for w in (2, 1, 0):
            pick = jnp.where(rotation == w, values[int(table[w, q])], pick)
        rows.append(pick)
    return rows


def term_kernel(levels, f_ref, above_ref, g_ref, gh_ref):
    level = lax.broadcasted_iota(jnp.int32, (levels, LANES), 0)
    for p in range(f_ref.shape[1]):
        temp = f_ref[0, p]
        dp = f_ref[1, p]
        cum = dp
        shift = 1
        while shift < levels:
            cum = cum + jnp.where(level >= shift, pltpu.roll(cum, shift, 0), 0.0)
            shift *= 2
        load = top_pressure + above_ref[p] + cum - 0.5 * dp
        term = temp * dp / load
        gh_ref[p] = jnp.sum(term, axis=0, keepdims=True)
        rcum = term
        shift = 1
        while shift < levels:
            rcum = rcum + jnp.where(
                level + shift < levels, pltpu.roll(rcum, levels - shift, 0), 0.0
            )
            shift *= 2
        g_ref[p] = rcum - 0.5 * term


def term_call(fields, above):
    levels = fields.shape[2]
    group = 4
    return pl.pallas_call(
        functools.partial(term_kernel, levels),
        interpret=INTERPRET,
        grid=(16 // group,),
        in_specs=[
            pl.BlockSpec((2, group, levels, LANES), lambda i: (1, i, 0, 0)),
            pl.BlockSpec((group, 1, LANES), lambda i: (i, 0, 0)),
        ],
        out_specs=[
            pl.BlockSpec((group, levels, LANES), lambda i: (i, 0, 0)),
            pl.BlockSpec((group, 1, LANES), lambda i: (i, 0, 0)),
        ],
        out_shape=[
            jax.ShapeDtypeStruct((16, levels, LANES), jnp.float32),
            jax.ShapeDtypeStruct((16, 1, LANES), jnp.float32),
        ],
    )(fields, above)


def lane_roll(y, shift):
    return pltpu.roll(y, shift % LANES, 1)


def column_fold(rows, col):
    rows = list(rows)
    for a in range(4):
        edge = rows[4 * a + 3]
        left = jnp.where(col == 0, lane_roll(edge, -(COLS - 1)), lane_roll(edge, 1))
        total = rows[4 * a] + left
        rows[4 * a] = total
        rows[4 * a + 3] = jnp.where(
            col == COLS - 1, lane_roll(total, COLS - 1), lane_roll(total, -1)
        )
    return rows


def shift_right(y, col):
    return jnp.where(col == COLS - 1, lane_roll(y, COLS - 1), lane_roll(y, -1))


def row_fold(rows, up_rows, down_rows, row, col, rows_dev, elements):
    fill = jnp.zeros((rows[0].shape[0], LANES - 128), jnp.float32)
    halo_up = [jnp.concatenate([up_rows[b], fill], axis=1) for b in range(3)]
    halo_down = [
        lane_roll(jnp.concatenate([down_rows[b], fill], axis=1), elements - COLS) for b in range(3)
    ]
    halo_up.append(shift_right(halo_up[0], col))
    halo_down.append(shift_right(halo_down[0], col))
    out = list(rows)
    for b in range(4):
        from_up = jnp.where(row == 0, halo_up[b], lane_roll(rows[12 + b], COLS))
        out[b] = rows[b] + from_up
        from_down = jnp.where(row == rows_dev - 1, halo_down[b], lane_roll(rows[b], -COLS))
        out[12 + b] = rows[12 + b] + from_down
    return out


def mass_kernel(elements, m_ref, info_ref, mc_ref, mw_ref, last_ref, first_ref):
    info = info_ref[...]
    forward_order, _ = rotation_tables()
    canon = select_rows([m_ref[p] for p in range(16)], info[0:1], forward_order)
    rows = column_fold(canon, info[1:2])
    for q in range(16):
        mc_ref[q] = canon[q]
        mw_ref[q] = rows[q]
    for b in range(4):
        last_ref[b] = lane_roll(rows[12 + b], COLS - elements)[:, :128]
        first_ref[b] = rows[b][:, :128]


def mass_call(mass, info, elements):
    small = jax.ShapeDtypeStruct((16, 1, LANES), jnp.float32)
    edge = jax.ShapeDtypeStruct((4, 1, 128), jnp.float32)
    return pl.pallas_call(
        functools.partial(mass_kernel, elements),
        interpret=INTERPRET,
        out_shape=[small, small, edge, edge],
    )(mass, info)


def adv_kernel(elements, with_mass, *refs):
    f_ref, g_ref, below_ref, jac_ref, rot_ref, mc_ref, info_ref = refs[:7]
    if with_mass:
        mlast_ref, mfirst_ref = refs[7:9]
    out_ref, last_ref, first_ref = refs[-3:]
    info = info_ref[...]
    rotation = info[0:1]
    col = info[1:2]
    forward_order, _ = rotation_tables()
    u = [f_ref[0, p] for p in range(16)]
    v = [f_ref[1, p] for p in range(16)]
    temp = [f_ref[2, p] for p in range(16)]
    dp = [f_ref[3, p] for p in range(16)]
    jac = [[jac_ref[k, p] for p in range(16)] for k in range(4)]
    energy = [
        (below_ref[p] + g_ref[p]) + 0.5 * (u[p] * u[p] + v[p] * v[p]) for p in range(16)
    ]
    e1 = first_rows(energy)
    e2 = second_rows(energy)
    it = [jac[0][p] * u[p] + jac[2][p] * v[p] for p in range(16)]
    lt = [jac[1][p] * u[p] + jac[3][p] * v[p] for p in range(16)]
    t1 = first_rows(temp)
    t2 = second_rows(temp)
    d1 = first_rows([dp[p] * it[p] for p in range(16)])
    d2 = second_rows([dp[p] * lt[p] for p in range(16)])
    advanced = []
    for p in range(16):
        rot = rot_ref[p]
        zonal_slope = jac[0][p] * e1[p] + jac[1][p] * e2[p]
        meridional_slope = jac[2][p] * e1[p] + jac[3][p] * e2[p]
        advanced.append(
            (
                u[p] + time_increment * (rot * v[p] - zonal_slope),
                v[p] - time_increment * (rot * u[p] + meridional_slope),
                temp[p] - time_increment * (it[p] * t1[p] + lt[p] * t2[p]),
                dp[p] - time_increment * (d1[p] + d2[p]),
            )
        )
    for f in range(4):
        rows = select_rows([advanced[p][f] for p in range(16)], rotation, forward_order)
        rows = column_fold([rows[q] * mc_ref[q] for q in range(16)], col)
        for q in range(16):
            out_ref[f, q] = rows[q]
        for b in range(3):
            last_ref[f, b] = lane_roll(rows[12 + b], COLS - elements)[:, :128]
            first_ref[f, b] = rows[b][:, :128]
    if with_mass:
        shape = last_ref.shape[2:]
        for b in range(3):
            last_ref[4, b] = jnp.broadcast_to(mlast_ref[b], shape)
            first_ref[4, b] = jnp.broadcast_to(mfirst_ref[b], shape)


def first_rows(rows):
    return [
        weighted_sum([(SLOPES[a, k], rows[4 * k + j]) for k in range(4)])
        for a in range(4)
        for j in range(4)
    ]


def second_rows(rows):
    return [
        weighted_sum([(SLOPES[a, k], rows[4 * i + k]) for k in range(4)])
        for i in range(4)
        for a in range(4)
    ]


def adv_call(fields, g0, below, jac, rot, mass_canon, info, elements, mass_edges=None):
    levels = fields.shape[2]
    steps = levels // CHUNK
    with_mass = mass_edges is not None
    width = 5 if with_mass else 4
    small = pl.BlockSpec((16, 1, LANES), lambda i: (0, 0, 0))
    edge = pl.BlockSpec((width, 3, CHUNK, 128), lambda i: (0, 0, i, 0))
    edge_shape = jax.ShapeDtypeStruct((width, 3, levels, 128), jnp.float32)
    in_specs = [
        pl.BlockSpec((4, 16, CHUNK, LANES), lambda i: (0, 0, i, 0)),
        pl.BlockSpec((16, CHUNK, LANES), lambda i: (0, i, 0)),
        small,
        pl.BlockSpec((4, 16, 1, LANES), lambda i: (0, 0, 0, 0)),
        small,
        small,
        pl.BlockSpec((8, LANES), lambda i: (0, 0)),
    ]
    args = [fields, g0, below, jac, rot, mass_canon, info]
    if with_mass:
        in_specs += [pl.BlockSpec((4, 1, 128), lambda i: (0, 0, 0))] * 2
        args += list(mass_edges)
    return pl.pallas_call(
        functools.partial(adv_kernel, elements, with_mass),
        interpret=INTERPRET,
        grid=(steps,),
        in_specs=in_specs,
        out_specs=[pl.BlockSpec((4, 16, CHUNK, LANES), lambda i: (0, 0, i, 0)), edge, edge],
        out_shape=[jax.ShapeDtypeStruct(fields.shape, jnp.float32), edge_shape, edge_shape],
    )(*args)


def fin_kernel(rows_dev, elements, with_cells, with_mass, *refs):
    refs = list(refs)
    w_ref, hu_ref, hd_ref = refs[:3]
    if with_mass:
        mw_ref = refs[3]
        refs = refs[4:]
    else:
        mt_ref = refs[3]
        refs = refs[4:]
    info_ref = refs.pop(0)
    if with_cells:
        prev_ref, m_ref = refs[:2]
        refs = refs[2:]
    out_ref, cm_ref = refs[:2]
    if with_cells:
        cell_ref = refs[2]
    info = info_ref[...]
    rotation = info[0:1]
    col = info[1:2]
    row = info[2:3]
    if with_mass:
        mass_total = row_fold(
            [mw_ref[q] for q in range(16)],
            [hu_ref[4, b][0:1] for b in range(3)],
            [hd_ref[4, b][0:1] for b in range(3)],
            row,
            col,
            rows_dev,
            elements,
        )
        lane_ok = lax.broadcasted_iota(jnp.int32, (1, LANES), 1) < elements
        mass_total = [jnp.where(lane_ok, m, 1.0) for m in mass_total]
        for q in range(16):
            refs[-1][q] = mass_total[q]
    else:
        mass_total = [mt_ref[q] for q in range(16)]
    lane = lax.broadcasted_iota(jnp.int32, (1, LANES), 1)
    valid = lane < elements
    _, backward_order = rotation_tables()
    groups = [(0, 1, 4, 5), (2, 3, 6, 7), (8, 9, 12, 13), (10, 11, 14, 15)]
    for f in range(4):
        out = row_fold(
            [w_ref[f, q] for q in range(16)],
            [hu_ref[f, b] for b in range(3)],
            [hd_ref[f, b] for b in range(3)],
            row,
            col,
            rows_dev,
            elements,
        )
        out = [out[q] / mass_total[q] for q in range(16)]
        new = select_rows(out, rotation, backward_order)
        new = [jnp.where(valid, new[p], 0.0) for p in range(16)]
        for p in range(16):
            out_ref[f, p] = new[p]
        if f == 3:
            for p in range(16):
                cm_ref[p] = jnp.sum(new[p], axis=0, keepdims=True)
        if with_cells:
            average = [(prev_ref[f, p] + new[p]) / SUBSTEPS for p in range(16)]
            for c, group in enumerate(groups):
                m = [m_ref[p] for p in group]
                summed = (m[0] * average[group[0]] + m[1] * average[group[1]]) + (
                    m[2] * average[group[2]] + m[3] * average[group[3]]
                )
                area = (m[0] + m[1]) + (m[2] + m[3])
                cell_ref[c, f] = summed / area


def fin_call(w, halo_up, halo_down, mass_parts, info, rows_dev, elements, prev=None, mass=None):
    levels = w.shape[2]
    steps = levels // CHUNK
    block = pl.BlockSpec((4, 16, CHUNK, LANES), lambda i: (0, 0, i, 0))
    halo = pl.BlockSpec((halo_up.shape[0], 3, CHUNK, 128), lambda i: (0, 0, i, 0))
    small = pl.BlockSpec((16, 1, LANES), lambda i: (0, 0, 0))
    with_cells = prev is not None
    with_mass = halo_up.shape[0] == 5
    in_specs = [block, halo, halo, small]
    args = [w, halo_up, halo_down, mass_parts]
    in_specs.append(pl.BlockSpec((8, LANES), lambda i: (0, 0)))
    args.append(info)
    out_specs = [block, pl.BlockSpec((None, 16, 1, LANES), lambda i: (i, 0, 0, 0))]
    out_shape = [
        jax.ShapeDtypeStruct(w.shape, jnp.float32),
        jax.ShapeDtypeStruct((steps, 16, 1, LANES), jnp.float32),
    ]
    if with_cells:
        in_specs += [block, small]
        args += [prev, mass]
        out_specs.append(pl.BlockSpec((4, 4, CHUNK, LANES), lambda i: (0, 0, i, 0)))
        out_shape.append(jax.ShapeDtypeStruct((4, 4, levels, LANES), jnp.float32))
    if with_mass:
        out_specs.append(small)
        out_shape.append(jax.ShapeDtypeStruct((16, 1, LANES), jnp.float32))
    return pl.pallas_call(
        functools.partial(fin_kernel, rows_dev, elements, with_cells, with_mass),
        interpret=INTERPRET,
        grid=(steps,),
        in_specs=in_specs,
        out_specs=out_specs,
        out_shape=out_shape,
    )(*args)


def edge_exchange(last, first):
    seg_count = lax.axis_size("seg")
    up = [(i, (i + 1) % seg_count) for i in range(seg_count)]
    down = [(j, i) for i, j in up]
    return lax.ppermute(last, "seg", up), lax.ppermute(first, "seg", down)


def halo_exchange(w, elements):
    seg_count = lax.axis_size("seg")
    up = [(i, (i + 1) % seg_count) for i in range(seg_count)]
    down = [(j, i) for i, j in up]
    last = w[..., 12:16, :, elements - COLS : elements]
    first = w[..., 0:4, :, 0:COLS]
    prev_last = lax.ppermute(last, "seg", up)
    next_first = lax.ppermute(first, "seg", down)
    widths = [(0, 0)] * (w.ndim - 1)
    halo_up = jnp.pad(prev_last, widths + [(0, LANES - COLS)])
    halo_down = jnp.pad(next_first, widths + [(elements - COLS, LANES - elements)])
    return halo_up, halo_down


def mass_dss(mass_canon_rows, info, rows_dev, elements):
    col = info[1:2]
    row = info[2:3]
    rows = list(mass_canon_rows)
    for a in range(4):
        edge = rows[4 * a + 3]
        left = jnp.where(col == 0, jnp.roll(edge, -(COLS - 1), -1), jnp.roll(edge, 1, -1))
        total = rows[4 * a] + left
        rows[4 * a] = total
        rows[4 * a + 3] = jnp.where(
            col == COLS - 1, jnp.roll(total, COLS - 1, -1), jnp.roll(total, -1, -1)
        )
    w = jnp.stack(rows)
    halo_up, halo_down = halo_exchange(w, elements)
    out = list(rows)
    for b in range(4):
        from_up = jnp.where(row == 0, halo_up[b], jnp.roll(rows[12 + b], COLS, -1))
        out[b] = rows[b] + from_up
        from_down = jnp.where(row == rows_dev - 1, halo_down[b], jnp.roll(rows[b], -COLS, -1))
        out[12 + b] = rows[12 + b] + from_down
    total = jnp.stack(out)
    lane = jnp.arange(LANES)
    return jnp.where(lane < elements, total, 1.0)


def local(
    velocity_pair,
    thermal_reading,
    layer_depth,
    jacobian_terms,
    rotation_frequency,
    integration_mass,
    shared_vertex_label,
    column_owner_slot,
):
    levels_dev = thermal_reading.shape[0]
    elements = thermal_reading.shape[2]
    seg_count = lax.axis_size("seg")
    lev_count = lax.axis_size("lev")
    rows_dev = elements // COLS
    node_cols = 3 * COLS
    first_row = 3 * rows_dev * lax.axis_index("seg")
    grid_rows = 3 * rows_dev * seg_count
    corner_ids = shared_vertex_label[0]
    element_pos = jnp.arange(elements)
    row_offset = (corner_ids // node_cols - first_row) % grid_rows - 3 * (element_pos // COLS)
    col_offset = (corner_ids % node_cols - 3 * (element_pos % COLS)) % node_cols
    rotation = jnp.where(
        row_offset == 0, jnp.where(col_offset == 0, 0, 1), jnp.where(col_offset == 3, 2, 3)
    )
    info = lane_info(rotation, elements)
    forward_order, _ = rotation_tables()

    prognostic = jnp.concatenate([velocity_pair, thermal_reading[None], layer_depth[None]], axis=0)
    fields = pad_lanes(jnp.transpose(prognostic, (0, 2, 1, 3)))
    jac = pad_lanes(jacobian_terms[:, :, None, :])
    rot = pad_lanes(rotation_frequency[:, None, :])
    mass = pad_lanes(integration_mass[:, None, :])
    mass_one = pad_lanes(integration_mass[:, None, :], 1.0)
    mass_canon, mass_folded, mass_last, mass_first = mass_call(mass, info, elements)
    mass_parts = mass_folded
    mass_edges = (mass_last, mass_first)
    column_mass = jnp.sum(fields[3], axis=1, keepdims=True)
    previous = None
    cells = None
    for substep in range(SUBSTEPS):
        above = carried_in(column_mass, "lev", False)
        g0, group_height = term_call(fields, above)
        below = carried_in(group_height, "lev", True)
        w, last, first = adv_call(
            fields, g0, below, jac, rot, mass_canon, info, elements, mass_edges
        )
        mass_edges = None
        halo_up, halo_down = edge_exchange(last, first)
        outs = fin_call(
            w,
            halo_up,
            halo_down,
            mass_parts,
            info,
            rows_dev,
            elements,
            previous if substep == SUBSTEPS - 1 else None,
            mass_one,
        )
        fields, column_parts = outs[:2]
        if substep == SUBSTEPS - 1:
            cells = outs[2]
        if substep == 0:
            mass_parts = outs[-1]
        previous = fields
        column_mass = jnp.sum(column_parts, axis=0)
    channels = 4 * levels_dev
    cell_values = cells[..., :elements].reshape(4, channels, elements)
    payload = jnp.transpose(cell_values, (0, 2, 1)).reshape(4 * elements, channels)
    dev_count = seg_count * lev_count
    own_cols = 4 * elements * seg_count // dev_count
    per_pair = own_cols // seg_count
    capacity = per_pair + per_pair // 2
    targets = column_owner_slot.reshape(-1)
    owner_index = targets // own_cols
    slot_index = targets % own_cols
    cell_count = targets.shape[0]
    cell_pos = jnp.arange(cell_count)
    same_owner = owner_index[:, None] == owner_index[None, :]
    earlier = cell_pos[:, None] < cell_pos[None, :]
    rank = jnp.sum(jnp.logical_and(same_owner, earlier).astype(jnp.int32), axis=0)
    destination = owner_index * capacity + rank
    slots = jnp.arange(dev_count * capacity)
    code = cell_pos * (own_cols + 1) + slot_index + 1
    match = destination[:, None] == slots[None, :]
    found = jnp.sum(jnp.where(match, code[:, None], 0), axis=0)
    has = found > 0
    source_cell = jnp.maximum(found - 1, 0) // (own_cols + 1)
    source_pos = jnp.maximum(found - 1, 0) % (own_cols + 1)
    outgoing = jnp.where(has[:, None], payload[source_cell], 0.0)
    ids = jnp.where(has, source_pos, -1).reshape(dev_count, capacity)
    received_ids = lax.all_to_all(ids, ("seg", "lev"), split_axis=0, concat_axis=0, tiled=True)
    flat = jnp.arange(dev_count * capacity).reshape(dev_count, capacity)
    source_lev = (jnp.arange(dev_count) % lev_count)[:, None]
    positions = jnp.arange(own_cols)
    picks = []
    for group in range(lev_count):
        hit = jnp.logical_and(
            received_ids[:, :, None] == positions[None, None, :], (source_lev == group)[:, :, None]
        )
        picks.append(jnp.sum(jnp.where(hit, flat[:, :, None], 0), axis=(0, 1)))
    buffer = outgoing.reshape(dev_count, capacity, channels)
    received = lax.all_to_all(buffer, ("seg", "lev"), split_axis=0, concat_axis=0, tiled=True)
    received_rows = received.reshape(dev_count * capacity, channels)
    arrived = received_rows[jnp.stack(picks)]
    arrived = arrived.reshape(lev_count, own_cols, 4, levels_dev).transpose(2, 0, 3, 1)
    phys_state = arrived.reshape(4, lev_count * levels_dev, own_cols)
    mean_thickness = jnp.mean(phys_state[3], axis=0)
    dyn_state = jnp.transpose(fields[..., :elements], (0, 2, 1, 3))
    return (dyn_state, phys_state, mean_thickness)


def solution(mesh):
    in_specs = (
        P(None, "lev", None, "seg"),
        P("lev", None, "seg"),
        P("lev", None, "seg"),
        P(None, None, "seg"),
        P(None, "seg"),
        P(None, "seg"),
        P(None, "seg"),
        P(None, "seg"),
    )
    out_specs = (P(None, "lev", None, "seg"), P(None, None, ("seg", "lev")), P(("seg", "lev")))
    return jax.shard_map(local, mesh=mesh, in_specs=in_specs, out_specs=out_specs, check_vma=False)
```

```python
import functools

import jax
import jax.numpy as jnp
import numpy as np
from jax import lax
from jax.experimental import pallas as pl
from jax.experimental.pallas import tpu as pltpu
from jax.sharding import PartitionSpec as P

COLS = 120
SUBSTEPS = 2


top_pressure = 10.0
time_increment = 0.05


def gll_slopes():
    root_five = np.sqrt(5.0)
    gll_nodes = [-1.0, -1.0 / root_five, 1.0 / root_five, 1.0]
    legendre_values = [-1.0, 1.0 / root_five, -1.0 / root_five, 1.0]
    slopes = np.zeros((4, 4))
    for row_node in range(4):
        for column in range(4):
            if row_node != column:
                slopes[row_node, column] = (
                    legendre_values[row_node]
                    / legendre_values[column]
                    / (gll_nodes[row_node] - gll_nodes[column])
                )
    slopes[0, 0] = -3.0
    slopes[3, 3] = 3.0
    return slopes


SLOPES = gll_slopes().astype(np.float32)


def rotation_tables():
    forward = np.zeros((4, 16), np.int32)
    for first_pos in range(4):
        for second_pos in range(4):
            canonical = 4 * first_pos + second_pos
            forward[0, canonical] = 4 * first_pos + second_pos
            forward[1, canonical] = 4 * (3 - second_pos) + first_pos
            forward[2, canonical] = 4 * (3 - first_pos) + (3 - second_pos)
            forward[3, canonical] = 4 * second_pos + 3 - first_pos
    backward = np.argsort(forward, axis=1).astype(np.int32)
    return (forward, backward)


def weighted_sum(terms):
    acc = None
    for coef, value in terms:
        if coef == 0.0:
            continue
        part = jnp.float32(coef) * value
        acc = part if acc is None else acc + part
    return acc


def first_deriv(f):
    return jnp.stack(
        [
            weighted_sum([(SLOPES[a, k], f[4 * k + j]) for k in range(4)])
            for a in range(4)
            for j in range(4)
        ]
    )


def second_deriv(f):
    return jnp.stack(
        [
            weighted_sum([(SLOPES[a, k], f[4 * i + k]) for k in range(4)])
            for i in range(4)
            for a in range(4)
        ]
    )


def carried_in(part, axis, reverse):
    count = lax.axis_size(axis)
    place = lax.axis_index(axis)
    gathered = lax.all_gather(part, axis)
    index = jnp.arange(count).reshape((count,) + (1,) * part.ndim)
    chosen = index > place if reverse else index < place
    return jnp.sum(jnp.where(chosen, gathered, jnp.zeros_like(gathered)), axis=0)


def site_potential_energy(thermal_reading, layer_depth):
    column_mass = jnp.sum(layer_depth, axis=1)
    above_sum = carried_in(column_mass, "lev", False)
    layer_midpoint_load = (
        top_pressure + above_sum[:, None, :] + jnp.cumsum(layer_depth, axis=1) - 0.5 * layer_depth
    )
    surface_change_rate = thermal_reading * layer_depth / layer_midpoint_load
    group_height = jnp.sum(surface_change_rate, axis=1)
    below_sum = carried_in(group_height, "lev", True)
    return (
        below_sum[:, None, :]
        + lax.cumsum(surface_change_rate, axis=1, reverse=True)
        - 0.5 * surface_change_rate
    )


def tendency_step(u, v, temp, dp, geopotential, jac, rot):
    energy = geopotential + 0.5 * (u * u + v * v)
    energy_first = first_deriv(energy)
    energy_second = second_deriv(energy)
    zonal_slope = jac[0] * energy_first + jac[1] * energy_second
    meridional_slope = jac[2] * energy_first + jac[3] * energy_second
    initial_transport = jac[0] * u + jac[2] * v
    latter_transport = jac[1] * u + jac[3] * v
    advect_with_motion = initial_transport * first_deriv(temp) + latter_transport * second_deriv(
        temp
    )
    distribute_onto_vertices = first_deriv(dp * initial_transport) + second_deriv(
        dp * latter_transport
    )
    return (
        u + time_increment * (rot * v - zonal_slope),
        v - time_increment * (rot * u + meridional_slope),
        temp - time_increment * advect_with_motion,
        dp - time_increment * distribute_onto_vertices,
    )


def reorder(values, rotation, table):
    rows = []
    for q in range(16):
        pick = values[int(table[3, q])]
        for w in (2, 1, 0):
            pick = jnp.where(rotation == w, values[int(table[w, q])], pick)
        rows.append(pick)
    return jnp.stack(rows)


def node_sum(canon, col, row, rows_dev):
    elements = canon.shape[-1]

    def roll(y, shift):
        return jnp.roll(y, shift, axis=-1)

    rows = [canon[q] for q in range(16)]
    for a in range(4):
        left = jnp.where(col == 0, roll(rows[4 * a + 3], -(COLS - 1)), roll(rows[4 * a + 3], 1))
        total = rows[4 * a] + left
        rows[4 * a] = total
        rows[4 * a + 3] = jnp.where(col == COLS - 1, roll(total, COLS - 1), roll(total, -1))
    seg_count = lax.axis_size("seg")
    up = [(i, (i + 1) % seg_count) for i in range(seg_count)]
    down = [(j, i) for i, j in up]
    last = jnp.stack([rows[12 + b][:, elements - COLS :] for b in range(4)])
    first = jnp.stack([rows[b][:, :COLS] for b in range(4)])
    prev_last = lax.ppermute(last, "seg", up)
    next_first = lax.ppermute(first, "seg", down)
    pad = jnp.zeros(prev_last.shape[1:-1] + (elements - COLS,), canon.dtype)
    out = list(rows)
    for b in range(4):
        halo_up = jnp.concatenate([prev_last[b], pad], axis=-1)
        from_up = jnp.where(row == 0, halo_up, roll(rows[12 + b], COLS))
        out[b] = rows[b] + from_up
        halo_down = jnp.concatenate([pad, next_first[b]], axis=-1)
        from_down = jnp.where(row == rows_dev - 1, halo_down, roll(rows[b], -COLS))
        out[12 + b] = rows[12 + b] + from_down
    return jnp.stack(out)


LANES = 512
CHUNK = 8
INTERPRET = None


def lane_info(rotation, elements):
    element_pos = jnp.arange(elements)
    info = jnp.stack(
        [rotation, element_pos % COLS, element_pos // COLS]
        + [jnp.zeros_like(rotation)] * 5
    ).astype(jnp.int32)
    return jnp.pad(info, ((0, 0), (0, LANES - elements)), constant_values=-1)


def pad_lanes(x, value=0.0):
    widths = [(0, 0)] * (x.ndim - 1) + [(0, LANES - x.shape[-1])]
    return jnp.pad(x, widths, constant_values=value)


def select_rows(values, rotation, table):
    rows = []
    for q in range(16):
        pick = values[int(table[3, q])]
        for w in (2, 1, 0):
            pick = jnp.where(rotation == w, values[int(table[w, q])], pick)
        rows.append(pick)
    return rows


def term_kernel(levels, f_ref, above_ref, g_ref, gh_ref):
    row = lax.broadcasted_iota(jnp.int32, (levels, levels), 0)
    column = lax.broadcasted_iota(jnp.int32, (levels, levels), 1)
    lower = (column <= row).astype(jnp.float32)
    upper = (column >= row).astype(jnp.float32)

    def mix(matrix, x):
        return lax.dot_general(
            matrix,
            x,
            (((1,), (0,)), ((), ())),
            precision=lax.Precision.HIGHEST,
            preferred_element_type=jnp.float32,
        )

    for p in range(f_ref.shape[1]):
        temp = f_ref[0, p]
        dp = f_ref[1, p]
        load = top_pressure + above_ref[p] + mix(lower, dp) - 0.5 * dp
        term = temp * dp / load
        gh_ref[p] = jnp.sum(term, axis=0, keepdims=True)
        g_ref[p] = mix(upper, term) - 0.5 * term


def term_call(fields, above):
    levels = fields.shape[2]
    group = 4
    return pl.pallas_call(
        functools.partial(term_kernel, levels),
        interpret=INTERPRET,
        grid=(16 // group,),
        in_specs=[
            pl.BlockSpec((2, group, levels, LANES), lambda i: (1, i, 0, 0)),
            pl.BlockSpec((group, 1, LANES), lambda i: (i, 0, 0)),
        ],
        out_specs=[
            pl.BlockSpec((group, levels, LANES), lambda i: (i, 0, 0)),
            pl.BlockSpec((group, 1, LANES), lambda i: (i, 0, 0)),
        ],
        out_shape=[
            jax.ShapeDtypeStruct((16, levels, LANES), jnp.float32),
            jax.ShapeDtypeStruct((16, 1, LANES), jnp.float32),
        ],
    )(fields, above)


def lane_roll(y, shift):
    return pltpu.roll(y, shift % LANES, 1)


def column_fold(rows, col):
    rows = list(rows)
    for a in range(4):
        edge = rows[4 * a + 3]
        left = jnp.where(col == 0, lane_roll(edge, -(COLS - 1)), lane_roll(edge, 1))
        total = rows[4 * a] + left
        rows[4 * a] = total
        rows[4 * a + 3] = jnp.where(
            col == COLS - 1, lane_roll(total, COLS - 1), lane_roll(total, -1)
        )
    return rows


def shift_right(y, col):
    return jnp.where(col == COLS - 1, lane_roll(y, COLS - 1), lane_roll(y, -1))


def row_fold(rows, up_rows, down_rows, row, col, rows_dev, elements):
    fill = jnp.zeros((rows[0].shape[0], LANES - 128), jnp.float32)
    halo_up = [jnp.concatenate([up_rows[b], fill], axis=1) for b in range(3)]
    halo_down = [
        lane_roll(jnp.concatenate([down_rows[b], fill], axis=1), elements - COLS) for b in range(3)
    ]
    halo_up.append(shift_right(halo_up[0], col))
    halo_down.append(shift_right(halo_down[0], col))
    out = list(rows)
    for b in range(4):
        from_up = jnp.where(row == 0, halo_up[b], lane_roll(rows[12 + b], COLS))
        out[b] = rows[b] + from_up
        from_down = jnp.where(row == rows_dev - 1, halo_down[b], lane_roll(rows[b], -COLS))
        out[12 + b] = rows[12 + b] + from_down
    return out


def mass_kernel(elements, m_ref, info_ref, mc_ref, mw_ref, last_ref, first_ref):
    info = info_ref[...]
    forward_order, _ = rotation_tables()
    canon = select_rows([m_ref[p] for p in range(16)], info[0:1], forward_order)
    rows = column_fold(canon, info[1:2])
    for q in range(16):
        mc_ref[q] = canon[q]
        mw_ref[q] = rows[q]
    for b in range(4):
        last_ref[b] = lane_roll(rows[12 + b], COLS - elements)[:, :128]
        first_ref[b] = rows[b][:, :128]


def mass_call(mass, info, elements):
    small = jax.ShapeDtypeStruct((16, 1, LANES), jnp.float32)
    edge = jax.ShapeDtypeStruct((4, 1, 128), jnp.float32)
    return pl.pallas_call(
        functools.partial(mass_kernel, elements),
        interpret=INTERPRET,
        out_shape=[small, small, edge, edge],
    )(mass, info)


def adv_kernel(elements, with_mass, *refs):
    f_ref, g_ref, below_ref, jac_ref, rot_ref, mc_ref, info_ref = refs[:7]
    if with_mass:
        mlast_ref, mfirst_ref = refs[7:9]
    out_ref, last_ref, first_ref = refs[-3:]
    info = info_ref[...]
    rotation = info[0:1]
    col = info[1:2]
    forward_order, _ = rotation_tables()
    u = [f_ref[0, p] for p in range(16)]
    v = [f_ref[1, p] for p in range(16)]
    temp = [f_ref[2, p] for p in range(16)]
    dp = [f_ref[3, p] for p in range(16)]
    jac = [[jac_ref[k, p] for p in range(16)] for k in range(4)]
    energy = [
        (below_ref[p] + g_ref[p]) + 0.5 * (u[p] * u[p] + v[p] * v[p]) for p in range(16)
    ]
    e1 = first_rows(energy)
    e2 = second_rows(energy)
    it = [jac[0][p] * u[p] + jac[2][p] * v[p] for p in range(16)]
    lt = [jac[1][p] * u[p] + jac[3][p] * v[p] for p in range(16)]
    t1 = first_rows(temp)
    t2 = second_rows(temp)
    d1 = first_rows([dp[p] * it[p] for p in range(16)])
    d2 = second_rows([dp[p] * lt[p] for p in range(16)])
    advanced = []
    for p in range(16):
        rot = rot_ref[p]
        zonal_slope = jac[0][p] * e1[p] + jac[1][p] * e2[p]
        meridional_slope = jac[2][p] * e1[p] + jac[3][p] * e2[p]
        advanced.append(
            (
                u[p] + time_increment * (rot * v[p] - zonal_slope),
                v[p] - time_increment * (rot * u[p] + meridional_slope),
                temp[p] - time_increment * (it[p] * t1[p] + lt[p] * t2[p]),
                dp[p] - time_increment * (d1[p] + d2[p]),
            )
        )
    for f in range(4):
        rows = select_rows([advanced[p][f] for p in range(16)], rotation, forward_order)
        rows = column_fold([rows[q] * mc_ref[q] for q in range(16)], col)
        for q in range(16):
            out_ref[f, q] = rows[q]
        for b in range(3):
            last_ref[f, b] = lane_roll(rows[12 + b], COLS - elements)[:, :128]
            first_ref[f, b] = rows[b][:, :128]
    if with_mass:
        shape = last_ref.shape[2:]
        for b in range(3):
            last_ref[4, b] = jnp.broadcast_to(mlast_ref[b], shape)
            first_ref[4, b] = jnp.broadcast_to(mfirst_ref[b], shape)


def first_rows(rows):
    return [
        weighted_sum([(SLOPES[a, k], rows[4 * k + j]) for k in range(4)])
        for a in range(4)
        for j in range(4)
    ]


def second_rows(rows):
    return [
        weighted_sum([(SLOPES[a, k], rows[4 * i + k]) for k in range(4)])
        for i in range(4)
        for a in range(4)
    ]


def adv_call(fields, g0, below, jac, rot, mass_canon, info, elements, mass_edges=None):
    levels = fields.shape[2]
    steps = levels // CHUNK
    with_mass = mass_edges is not None
    width = 5 if with_mass else 4
    small = pl.BlockSpec((16, 1, LANES), lambda i: (0, 0, 0))
    edge = pl.BlockSpec((width, 3, CHUNK, 128), lambda i: (0, 0, i, 0))
    edge_shape = jax.ShapeDtypeStruct((width, 3, levels, 128), jnp.float32)
    in_specs = [
        pl.BlockSpec((4, 16, CHUNK, LANES), lambda i: (0, 0, i, 0)),
        pl.BlockSpec((16, CHUNK, LANES), lambda i: (0, i, 0)),
        small,
        pl.BlockSpec((4, 16, 1, LANES), lambda i: (0, 0, 0, 0)),
        small,
        small,
        pl.BlockSpec((8, LANES), lambda i: (0, 0)),
    ]
    args = [fields, g0, below, jac, rot, mass_canon, info]
    if with_mass:
        in_specs += [pl.BlockSpec((4, 1, 128), lambda i: (0, 0, 0))] * 2
        args += list(mass_edges)
    return pl.pallas_call(
        functools.partial(adv_kernel, elements, with_mass),
        interpret=INTERPRET,
        grid=(steps,),
        in_specs=in_specs,
        out_specs=[pl.BlockSpec((4, 16, CHUNK, LANES), lambda i: (0, 0, i, 0)), edge, edge],
        out_shape=[jax.ShapeDtypeStruct(fields.shape, jnp.float32), edge_shape, edge_shape],
    )(*args)


def fin_kernel(rows_dev, elements, with_cells, with_mass, *refs):
    refs = list(refs)
    w_ref, hu_ref, hd_ref = refs[:3]
    if with_mass:
        mw_ref = refs[3]
        refs = refs[4:]
    else:
        mt_ref = refs[3]
        refs = refs[4:]
    info_ref = refs.pop(0)
    if with_cells:
        prev_ref, m_ref = refs[:2]
        refs = refs[2:]
    out_ref, cm_ref = refs[:2]
    if with_cells:
        cell_ref = refs[2]
    info = info_ref[...]
    rotation = info[0:1]
    col = info[1:2]
    row = info[2:3]
    if with_mass:
        mass_total = row_fold(
            [mw_ref[q] for q in range(16)],
            [hu_ref[4, b][0:1] for b in range(3)],
            [hd_ref[4, b][0:1] for b in range(3)],
            row,
            col,
            rows_dev,
            elements,
        )
        lane_ok = lax.broadcasted_iota(jnp.int32, (1, LANES), 1) < elements
        mass_total = [jnp.where(lane_ok, m, 1.0) for m in mass_total]
        for q in range(16):
            refs[-1][q] = mass_total[q]
    else:
        mass_total = [mt_ref[q] for q in range(16)]
    lane = lax.broadcasted_iota(jnp.int32, (1, LANES), 1)
    valid = lane < elements
    _, backward_order = rotation_tables()
    groups = [(0, 1, 4, 5), (2, 3, 6, 7), (8, 9, 12, 13), (10, 11, 14, 15)]
    for f in range(4):
        out = row_fold(
            [w_ref[f, q] for q in range(16)],
            [hu_ref[f, b] for b in range(3)],
            [hd_ref[f, b] for b in range(3)],
            row,
            col,
            rows_dev,
            elements,
        )
        out = [out[q] / mass_total[q] for q in range(16)]
        new = select_rows(out, rotation, backward_order)
        new = [jnp.where(valid, new[p], 0.0) for p in range(16)]
        for p in range(16):
            out_ref[f, p] = new[p]
        if f == 3:
            for p in range(16):
                cm_ref[p] = jnp.sum(new[p], axis=0, keepdims=True)
        if with_cells:
            average = [(prev_ref[f, p] + new[p]) / SUBSTEPS for p in range(16)]
            for c, group in enumerate(groups):
                m = [m_ref[p] for p in group]
                summed = (m[0] * average[group[0]] + m[1] * average[group[1]]) + (
                    m[2] * average[group[2]] + m[3] * average[group[3]]
                )
                area = (m[0] + m[1]) + (m[2] + m[3])
                cell_ref[c, f] = summed / area


def fin_call(w, halo_up, halo_down, mass_parts, info, rows_dev, elements, prev=None, mass=None):
    levels = w.shape[2]
    steps = levels // CHUNK
    block = pl.BlockSpec((4, 16, CHUNK, LANES), lambda i: (0, 0, i, 0))
    halo = pl.BlockSpec((halo_up.shape[0], 3, CHUNK, 128), lambda i: (0, 0, i, 0))
    small = pl.BlockSpec((16, 1, LANES), lambda i: (0, 0, 0))
    with_cells = prev is not None
    with_mass = halo_up.shape[0] == 5
    in_specs = [block, halo, halo, small]
    args = [w, halo_up, halo_down, mass_parts]
    in_specs.append(pl.BlockSpec((8, LANES), lambda i: (0, 0)))
    args.append(info)
    out_specs = [block, pl.BlockSpec((None, 16, 1, LANES), lambda i: (i, 0, 0, 0))]
    out_shape = [
        jax.ShapeDtypeStruct(w.shape, jnp.float32),
        jax.ShapeDtypeStruct((steps, 16, 1, LANES), jnp.float32),
    ]
    if with_cells:
        in_specs += [block, small]
        args += [prev, mass]
        out_specs.append(pl.BlockSpec((4, 4, CHUNK, LANES), lambda i: (0, 0, i, 0)))
        out_shape.append(jax.ShapeDtypeStruct((4, 4, levels, LANES), jnp.float32))
    if with_mass:
        out_specs.append(small)
        out_shape.append(jax.ShapeDtypeStruct((16, 1, LANES), jnp.float32))
    return pl.pallas_call(
        functools.partial(fin_kernel, rows_dev, elements, with_cells, with_mass),
        interpret=INTERPRET,
        grid=(steps,),
        in_specs=in_specs,
        out_specs=out_specs,
        out_shape=out_shape,
    )(*args)


def edge_exchange(last, first):
    seg_count = lax.axis_size("seg")
    up = [(i, (i + 1) % seg_count) for i in range(seg_count)]
    down = [(j, i) for i, j in up]
    return lax.ppermute(last, "seg", up), lax.ppermute(first, "seg", down)


def halo_exchange(w, elements):
    seg_count = lax.axis_size("seg")
    up = [(i, (i + 1) % seg_count) for i in range(seg_count)]
    down = [(j, i) for i, j in up]
    last = w[..., 12:16, :, elements - COLS : elements]
    first = w[..., 0:4, :, 0:COLS]
    prev_last = lax.ppermute(last, "seg", up)
    next_first = lax.ppermute(first, "seg", down)
    widths = [(0, 0)] * (w.ndim - 1)
    halo_up = jnp.pad(prev_last, widths + [(0, LANES - COLS)])
    halo_down = jnp.pad(next_first, widths + [(elements - COLS, LANES - elements)])
    return halo_up, halo_down


def mass_dss(mass_canon_rows, info, rows_dev, elements):
    col = info[1:2]
    row = info[2:3]
    rows = list(mass_canon_rows)
    for a in range(4):
        edge = rows[4 * a + 3]
        left = jnp.where(col == 0, jnp.roll(edge, -(COLS - 1), -1), jnp.roll(edge, 1, -1))
        total = rows[4 * a] + left
        rows[4 * a] = total
        rows[4 * a + 3] = jnp.where(
            col == COLS - 1, jnp.roll(total, COLS - 1, -1), jnp.roll(total, -1, -1)
        )
    w = jnp.stack(rows)
    halo_up, halo_down = halo_exchange(w, elements)
    out = list(rows)
    for b in range(4):
        from_up = jnp.where(row == 0, halo_up[b], jnp.roll(rows[12 + b], COLS, -1))
        out[b] = rows[b] + from_up
        from_down = jnp.where(row == rows_dev - 1, halo_down[b], jnp.roll(rows[b], -COLS, -1))
        out[12 + b] = rows[12 + b] + from_down
    total = jnp.stack(out)
    lane = jnp.arange(LANES)
    return jnp.where(lane < elements, total, 1.0)


def local(
    velocity_pair,
    thermal_reading,
    layer_depth,
    jacobian_terms,
    rotation_frequency,
    integration_mass,
    shared_vertex_label,
    column_owner_slot,
):
    levels_dev = thermal_reading.shape[0]
    elements = thermal_reading.shape[2]
    seg_count = lax.axis_size("seg")
    lev_count = lax.axis_size("lev")
    rows_dev = elements // COLS
    node_cols = 3 * COLS
    first_row = 3 * rows_dev * lax.axis_index("seg")
    grid_rows = 3 * rows_dev * seg_count
    corner_ids = shared_vertex_label[0]
    element_pos = jnp.arange(elements)
    row_offset = (corner_ids // node_cols - first_row) % grid_rows - 3 * (element_pos // COLS)
    col_offset = (corner_ids % node_cols - 3 * (element_pos % COLS)) % node_cols
    rotation = jnp.where(
        row_offset == 0, jnp.where(col_offset == 0, 0, 1), jnp.where(col_offset == 3, 2, 3)
    )
    info = lane_info(rotation, elements)
    forward_order, _ = rotation_tables()

    prognostic = jnp.concatenate([velocity_pair, thermal_reading[None], layer_depth[None]], axis=0)
    fields = pad_lanes(jnp.transpose(prognostic, (0, 2, 1, 3)))
    jac = pad_lanes(jacobian_terms[:, :, None, :])
    rot = pad_lanes(rotation_frequency[:, None, :])
    mass = pad_lanes(integration_mass[:, None, :])
    mass_one = pad_lanes(integration_mass[:, None, :], 1.0)
    mass_canon, mass_folded, mass_last, mass_first = mass_call(mass, info, elements)
    mass_parts = mass_folded
    mass_edges = (mass_last, mass_first)
    column_mass = jnp.sum(fields[3], axis=1, keepdims=True)
    previous = None
    cells = None
    for substep in range(SUBSTEPS):
        above = carried_in(column_mass, "lev", False)
        g0, group_height = term_call(fields, above)
        below = carried_in(group_height, "lev", True)
        w, last, first = adv_call(
            fields, g0, below, jac, rot, mass_canon, info, elements, mass_edges
        )
        mass_edges = None
        halo_up, halo_down = edge_exchange(last, first)
        outs = fin_call(
            w,
            halo_up,
            halo_down,
            mass_parts,
            info,
            rows_dev,
            elements,
            previous if substep == SUBSTEPS - 1 else None,
            mass_one,
        )
        fields, column_parts = outs[:2]
        if substep == SUBSTEPS - 1:
            cells = outs[2]
        if substep == 0:
            mass_parts = outs[-1]
        previous = fields
        column_mass = jnp.sum(column_parts, axis=0)
    channels = 4 * levels_dev
    cell_values = cells[..., :elements].reshape(4, channels, elements)
    payload = jnp.transpose(cell_values, (0, 2, 1)).reshape(4 * elements, channels)
    dev_count = seg_count * lev_count
    own_cols = 4 * elements * seg_count // dev_count
    per_pair = own_cols // seg_count
    capacity = per_pair + per_pair // 2
    targets = column_owner_slot.reshape(-1)
    owner_index = targets // own_cols
    slot_index = targets % own_cols
    cell_count = targets.shape[0]
    cell_pos = jnp.arange(cell_count)
    same_owner = owner_index[:, None] == owner_index[None, :]
    earlier = cell_pos[:, None] < cell_pos[None, :]
    rank = jnp.sum(jnp.logical_and(same_owner, earlier).astype(jnp.int32), axis=0)
    destination = owner_index * capacity + rank
    slots = jnp.arange(dev_count * capacity)
    code = cell_pos * (own_cols + 1) + slot_index + 1
    match = destination[:, None] == slots[None, :]
    found = jnp.sum(jnp.where(match, code[:, None], 0), axis=0)
    has = found > 0
    source_cell = jnp.maximum(found - 1, 0) // (own_cols + 1)
    source_pos = jnp.maximum(found - 1, 0) % (own_cols + 1)
    outgoing = payload[source_cell]
    ids = jnp.where(has, source_pos, -1).reshape(dev_count, capacity)
    received_ids = lax.all_to_all(ids, ("seg", "lev"), split_axis=0, concat_axis=0, tiled=True)
    flat = jnp.arange(dev_count * capacity).reshape(dev_count, capacity)
    source_lev = (jnp.arange(dev_count) % lev_count)[:, None]
    positions = jnp.arange(own_cols)
    picks = []
    for group in range(lev_count):
        hit = jnp.logical_and(
            received_ids[:, :, None] == positions[None, None, :], (source_lev == group)[:, :, None]
        )
        picks.append(jnp.sum(jnp.where(hit, flat[:, :, None], 0), axis=(0, 1)))
    buffer = outgoing.reshape(dev_count, capacity, channels)
    received = lax.all_to_all(buffer, ("seg", "lev"), split_axis=0, concat_axis=0, tiled=True)
    received_rows = received.reshape(dev_count * capacity, channels)
    arrived = received_rows[jnp.stack(picks)]
    arrived = arrived.reshape(lev_count, own_cols, 4, levels_dev).transpose(2, 0, 3, 1)
    phys_state = arrived.reshape(4, lev_count * levels_dev, own_cols)
    mean_thickness = jnp.mean(phys_state[3], axis=0)
    dyn_state = jnp.transpose(fields[..., :elements], (0, 2, 1, 3))
    return (dyn_state, phys_state, mean_thickness)


def solution(mesh):
    in_specs = (
        P(None, "lev", None, "seg"),
        P("lev", None, "seg"),
        P("lev", None, "seg"),
        P(None, None, "seg"),
        P(None, "seg"),
        P(None, "seg"),
        P(None, "seg"),
        P(None, "seg"),
    )
    out_specs = (P(None, "lev", None, "seg"), P(None, None, ("seg", "lev")), P(("seg", "lev")))
    return jax.shard_map(local, mesh=mesh, in_specs=in_specs, out_specs=out_specs, check_vma=False)
```

```python
import functools

import jax
import jax.numpy as jnp
import numpy as np
from jax import lax
from jax.experimental import pallas as pl
from jax.experimental.pallas import tpu as pltpu
from jax.sharding import PartitionSpec as P

COLS = 120
SUBSTEPS = 2


top_pressure = 10.0
time_increment = 0.05


def gll_slopes():
    root_five = np.sqrt(5.0)
    gll_nodes = [-1.0, -1.0 / root_five, 1.0 / root_five, 1.0]
    legendre_values = [-1.0, 1.0 / root_five, -1.0 / root_five, 1.0]
    slopes = np.zeros((4, 4))
    for row_node in range(4):
        for column in range(4):
            if row_node != column:
                slopes[row_node, column] = (
                    legendre_values[row_node]
                    / legendre_values[column]
                    / (gll_nodes[row_node] - gll_nodes[column])
                )
    slopes[0, 0] = -3.0
    slopes[3, 3] = 3.0
    return slopes


SLOPES = gll_slopes().astype(np.float32)


def rotation_tables():
    forward = np.zeros((4, 16), np.int32)
    for first_pos in range(4):
        for second_pos in range(4):
            canonical = 4 * first_pos + second_pos
            forward[0, canonical] = 4 * first_pos + second_pos
            forward[1, canonical] = 4 * (3 - second_pos) + first_pos
            forward[2, canonical] = 4 * (3 - first_pos) + (3 - second_pos)
            forward[3, canonical] = 4 * second_pos + 3 - first_pos
    backward = np.argsort(forward, axis=1).astype(np.int32)
    return (forward, backward)


def weighted_sum(terms):
    acc = None
    for coef, value in terms:
        if coef == 0.0:
            continue
        part = jnp.float32(coef) * value
        acc = part if acc is None else acc + part
    return acc


def first_deriv(f):
    return jnp.stack(
        [
            weighted_sum([(SLOPES[a, k], f[4 * k + j]) for k in range(4)])
            for a in range(4)
            for j in range(4)
        ]
    )


def second_deriv(f):
    return jnp.stack(
        [
            weighted_sum([(SLOPES[a, k], f[4 * i + k]) for k in range(4)])
            for i in range(4)
            for a in range(4)
        ]
    )


def carried_in(part, axis, reverse):
    count = lax.axis_size(axis)
    place = lax.axis_index(axis)
    gathered = lax.all_gather(part, axis)
    index = jnp.arange(count).reshape((count,) + (1,) * part.ndim)
    chosen = index > place if reverse else index < place
    return jnp.sum(jnp.where(chosen, gathered, jnp.zeros_like(gathered)), axis=0)


def site_potential_energy(thermal_reading, layer_depth):
    column_mass = jnp.sum(layer_depth, axis=1)
    above_sum = carried_in(column_mass, "lev", False)
    layer_midpoint_load = (
        top_pressure + above_sum[:, None, :] + jnp.cumsum(layer_depth, axis=1) - 0.5 * layer_depth
    )
    surface_change_rate = thermal_reading * layer_depth / layer_midpoint_load
    group_height = jnp.sum(surface_change_rate, axis=1)
    below_sum = carried_in(group_height, "lev", True)
    return (
        below_sum[:, None, :]
        + lax.cumsum(surface_change_rate, axis=1, reverse=True)
        - 0.5 * surface_change_rate
    )


def tendency_step(u, v, temp, dp, geopotential, jac, rot):
    energy = geopotential + 0.5 * (u * u + v * v)
    energy_first = first_deriv(energy)
    energy_second = second_deriv(energy)
    zonal_slope = jac[0] * energy_first + jac[1] * energy_second
    meridional_slope = jac[2] * energy_first + jac[3] * energy_second
    initial_transport = jac[0] * u + jac[2] * v
    latter_transport = jac[1] * u + jac[3] * v
    advect_with_motion = initial_transport * first_deriv(temp) + latter_transport * second_deriv(
        temp
    )
    distribute_onto_vertices = first_deriv(dp * initial_transport) + second_deriv(
        dp * latter_transport
    )
    return (
        u + time_increment * (rot * v - zonal_slope),
        v - time_increment * (rot * u + meridional_slope),
        temp - time_increment * advect_with_motion,
        dp - time_increment * distribute_onto_vertices,
    )


def reorder(values, rotation, table):
    rows = []
    for q in range(16):
        pick = values[int(table[3, q])]
        for w in (2, 1, 0):
            pick = jnp.where(rotation == w, values[int(table[w, q])], pick)
        rows.append(pick)
    return jnp.stack(rows)


def node_sum(canon, col, row, rows_dev):
    elements = canon.shape[-1]

    def roll(y, shift):
        return jnp.roll(y, shift, axis=-1)

    rows = [canon[q] for q in range(16)]
    for a in range(4):
        left = jnp.where(col == 0, roll(rows[4 * a + 3], -(COLS - 1)), roll(rows[4 * a + 3], 1))
        total = rows[4 * a] + left
        rows[4 * a] = total
        rows[4 * a + 3] = jnp.where(col == COLS - 1, roll(total, COLS - 1), roll(total, -1))
    seg_count = lax.axis_size("seg")
    up = [(i, (i + 1) % seg_count) for i in range(seg_count)]
    down = [(j, i) for i, j in up]
    last = jnp.stack([rows[12 + b][:, elements - COLS :] for b in range(4)])
    first = jnp.stack([rows[b][:, :COLS] for b in range(4)])
    prev_last = lax.ppermute(last, "seg", up)
    next_first = lax.ppermute(first, "seg", down)
    pad = jnp.zeros(prev_last.shape[1:-1] + (elements - COLS,), canon.dtype)
    out = list(rows)
    for b in range(4):
        halo_up = jnp.concatenate([prev_last[b], pad], axis=-1)
        from_up = jnp.where(row == 0, halo_up, roll(rows[12 + b], COLS))
        out[b] = rows[b] + from_up
        halo_down = jnp.concatenate([pad, next_first[b]], axis=-1)
        from_down = jnp.where(row == rows_dev - 1, halo_down, roll(rows[b], -COLS))
        out[12 + b] = rows[12 + b] + from_down
    return jnp.stack(out)


LANES = 512
CHUNK = 8
INTERPRET = None


def lane_info(rotation, elements):
    element_pos = jnp.arange(elements)
    info = jnp.stack(
        [rotation, element_pos % COLS, element_pos // COLS]
        + [jnp.zeros_like(rotation)] * 5
    ).astype(jnp.int32)
    return jnp.pad(info, ((0, 0), (0, LANES - elements)), constant_values=-1)


def pad_lanes(x, value=0.0):
    widths = [(0, 0)] * (x.ndim - 1) + [(0, LANES - x.shape[-1])]
    return jnp.pad(x, widths, constant_values=value)


def select_rows(values, rotation, table):
    rows = []
    for q in range(16):
        pick = values[int(table[3, q])]
        for w in (2, 1, 0):
            pick = jnp.where(rotation == w, values[int(table[w, q])], pick)
        rows.append(pick)
    return rows


def term_kernel(levels, f_ref, above_ref, g_ref, gh_ref):
    level = lax.broadcasted_iota(jnp.int32, (levels, LANES), 0)
    for p in range(f_ref.shape[1]):
        temp = f_ref[0, p]
        dp = f_ref[1, p]
        cum = dp
        shift = 1
        while shift < levels:
            cum = cum + jnp.where(level >= shift, pltpu.roll(cum, shift, 0), 0.0)
            shift *= 2
        load = top_pressure + above_ref[p] + cum - 0.5 * dp
        term = temp * dp / load
        gh_ref[p] = jnp.sum(term, axis=0, keepdims=True)
        rcum = term
        shift = 1
        while shift < levels:
            rcum = rcum + jnp.where(
                level + shift < levels, pltpu.roll(rcum, levels - shift, 0), 0.0
            )
            shift *= 2
        g_ref[p] = rcum - 0.5 * term


def term_call(fields, above):
    levels = fields.shape[2]
    group = 4
    return pl.pallas_call(
        functools.partial(term_kernel, levels),
        interpret=INTERPRET,
        grid=(16 // group,),
        in_specs=[
            pl.BlockSpec((2, group, levels, LANES), lambda i: (1, i, 0, 0)),
            pl.BlockSpec((group, 1, LANES), lambda i: (i, 0, 0)),
        ],
        out_specs=[
            pl.BlockSpec((group, levels, LANES), lambda i: (i, 0, 0)),
            pl.BlockSpec((group, 1, LANES), lambda i: (i, 0, 0)),
        ],
        out_shape=[
            jax.ShapeDtypeStruct((16, levels, LANES), jnp.float32),
            jax.ShapeDtypeStruct((16, 1, LANES), jnp.float32),
        ],
    )(fields, above)


def lane_roll(y, shift):
    return pltpu.roll(y, shift % LANES, 1)


def column_fold(rows, col):
    rows = list(rows)
    for a in range(4):
        edge = rows[4 * a + 3]
        left = jnp.where(col == 0, lane_roll(edge, -(COLS - 1)), lane_roll(edge, 1))
        total = rows[4 * a] + left
        rows[4 * a] = total
        rows[4 * a + 3] = jnp.where(
            col == COLS - 1, lane_roll(total, COLS - 1), lane_roll(total, -1)
        )
    return rows


def shift_right(y, col):
    return jnp.where(col == COLS - 1, lane_roll(y, COLS - 1), lane_roll(y, -1))


def row_fold(rows, up_rows, down_rows, row, col, rows_dev, elements):
    fill = jnp.zeros((rows[0].shape[0], LANES - 128), jnp.float32)
    halo_up = [jnp.concatenate([up_rows[b], fill], axis=1) for b in range(3)]
    halo_down = [
        lane_roll(jnp.concatenate([down_rows[b], fill], axis=1), elements - COLS) for b in range(3)
    ]
    halo_up.append(shift_right(halo_up[0], col))
    halo_down.append(shift_right(halo_down[0], col))
    out = list(rows)
    for b in range(4):
        from_up = jnp.where(row == 0, halo_up[b], lane_roll(rows[12 + b], COLS))
        out[b] = rows[b] + from_up
        from_down = jnp.where(row == rows_dev - 1, halo_down[b], lane_roll(rows[b], -COLS))
        out[12 + b] = rows[12 + b] + from_down
    return out


def mass_kernel(elements, m_ref, info_ref, mc_ref, mw_ref, last_ref, first_ref):
    info = info_ref[...]
    forward_order, _ = rotation_tables()
    canon = select_rows([m_ref[p] for p in range(16)], info[0:1], forward_order)
    rows = column_fold(canon, info[1:2])
    for q in range(16):
        mc_ref[q] = canon[q]
        mw_ref[q] = rows[q]
    for b in range(4):
        last_ref[b] = lane_roll(rows[12 + b], COLS - elements)[:, :128]
        first_ref[b] = rows[b][:, :128]


def mass_call(mass, info, elements):
    small = jax.ShapeDtypeStruct((16, 1, LANES), jnp.float32)
    edge = jax.ShapeDtypeStruct((4, 1, 128), jnp.float32)
    return pl.pallas_call(
        functools.partial(mass_kernel, elements),
        interpret=INTERPRET,
        out_shape=[small, small, edge, edge],
    )(mass, info)


def adv_kernel(elements, with_mass, *refs):
    f_ref, g_ref, below_ref, jac_ref, rot_ref, mc_ref, info_ref = refs[:7]
    if with_mass:
        mlast_ref, mfirst_ref = refs[7:9]
    out_ref, last_ref, first_ref = refs[-3:]
    info = info_ref[...]
    rotation = info[0:1]
    col = info[1:2]
    forward_order, _ = rotation_tables()
    u = [f_ref[0, p] for p in range(16)]
    v = [f_ref[1, p] for p in range(16)]
    temp = [f_ref[2, p] for p in range(16)]
    dp = [f_ref[3, p] for p in range(16)]
    jac = [[jac_ref[k, p] for p in range(16)] for k in range(4)]
    energy = [
        (below_ref[p] + g_ref[p]) + 0.5 * (u[p] * u[p] + v[p] * v[p]) for p in range(16)
    ]
    e1 = first_rows(energy)
    e2 = second_rows(energy)
    it = [jac[0][p] * u[p] + jac[2][p] * v[p] for p in range(16)]
    lt = [jac[1][p] * u[p] + jac[3][p] * v[p] for p in range(16)]
    t1 = first_rows(temp)
    t2 = second_rows(temp)
    d1 = first_rows([dp[p] * it[p] for p in range(16)])
    d2 = second_rows([dp[p] * lt[p] for p in range(16)])
    advanced = []
    for p in range(16):
        rot = rot_ref[p]
        zonal_slope = jac[0][p] * e1[p] + jac[1][p] * e2[p]
        meridional_slope = jac[2][p] * e1[p] + jac[3][p] * e2[p]
        advanced.append(
            (
                u[p] + time_increment * (rot * v[p] - zonal_slope),
                v[p] - time_increment * (rot * u[p] + meridional_slope),
                temp[p] - time_increment * (it[p] * t1[p] + lt[p] * t2[p]),
                dp[p] - time_increment * (d1[p] + d2[p]),
            )
        )
    for f in range(4):
        rows = select_rows([advanced[p][f] for p in range(16)], rotation, forward_order)
        rows = column_fold([rows[q] * mc_ref[q] for q in range(16)], col)
        for q in range(16):
            out_ref[f, q] = rows[q]
        for b in range(3):
            last_ref[f, b] = lane_roll(rows[12 + b], COLS - elements)[:, :128]
            first_ref[f, b] = rows[b][:, :128]
    if with_mass:
        shape = last_ref.shape[2:]
        for b in range(3):
            last_ref[4, b] = jnp.broadcast_to(mlast_ref[b], shape)
            first_ref[4, b] = jnp.broadcast_to(mfirst_ref[b], shape)


def first_rows(rows):
    return [
        weighted_sum([(SLOPES[a, k], rows[4 * k + j]) for k in range(4)])
        for a in range(4)
        for j in range(4)
    ]


def second_rows(rows):
    return [
        weighted_sum([(SLOPES[a, k], rows[4 * i + k]) for k in range(4)])
        for i in range(4)
        for a in range(4)
    ]


def adv_call(fields, g0, below, jac, rot, mass_canon, info, elements, mass_edges=None):
    levels = fields.shape[2]
    steps = levels // CHUNK
    with_mass = mass_edges is not None
    width = 5 if with_mass else 4
    small = pl.BlockSpec((16, 1, LANES), lambda i: (0, 0, 0))
    edge = pl.BlockSpec((width, 3, CHUNK, 128), lambda i: (0, 0, i, 0))
    edge_shape = jax.ShapeDtypeStruct((width, 3, levels, 128), jnp.float32)
    in_specs = [
        pl.BlockSpec((4, 16, CHUNK, LANES), lambda i: (0, 0, i, 0)),
        pl.BlockSpec((16, CHUNK, LANES), lambda i: (0, i, 0)),
        small,
        pl.BlockSpec((4, 16, 1, LANES), lambda i: (0, 0, 0, 0)),
        small,
        small,
        pl.BlockSpec((8, LANES), lambda i: (0, 0)),
    ]
    args = [fields, g0, below, jac, rot, mass_canon, info]
    if with_mass:
        in_specs += [pl.BlockSpec((4, 1, 128), lambda i: (0, 0, 0))] * 2
        args += list(mass_edges)
    return pl.pallas_call(
        functools.partial(adv_kernel, elements, with_mass),
        interpret=INTERPRET,
        grid=(steps,),
        in_specs=in_specs,
        out_specs=[pl.BlockSpec((4, 16, CHUNK, LANES), lambda i: (0, 0, i, 0)), edge, edge],
        out_shape=[jax.ShapeDtypeStruct(fields.shape, jnp.float32), edge_shape, edge_shape],
    )(*args)


def fin_kernel(rows_dev, elements, with_cells, with_mass, *refs):
    refs = list(refs)
    w_ref, hu_ref, hd_ref = refs[:3]
    if with_mass:
        mw_ref = refs[3]
        refs = refs[4:]
    else:
        mt_ref = refs[3]
        refs = refs[4:]
    info_ref = refs.pop(0)
    if with_cells:
        prev_ref, m_ref = refs[:2]
        refs = refs[2:]
    out_ref, cm_ref = refs[:2]
    if with_cells:
        cell_ref = refs[2]
    info = info_ref[...]
    rotation = info[0:1]
    col = info[1:2]
    row = info[2:3]
    if with_mass:
        mass_total = row_fold(
            [mw_ref[q] for q in range(16)],
            [hu_ref[4, b][0:1] for b in range(3)],
            [hd_ref[4, b][0:1] for b in range(3)],
            row,
            col,
            rows_dev,
            elements,
        )
        lane_ok = lax.broadcasted_iota(jnp.int32, (1, LANES), 1) < elements
        mass_total = [jnp.where(lane_ok, m, 1.0) for m in mass_total]
        for q in range(16):
            refs[-1][q] = mass_total[q]
    else:
        mass_total = [mt_ref[q] for q in range(16)]
    lane = lax.broadcasted_iota(jnp.int32, (1, LANES), 1)
    valid = lane < elements
    _, backward_order = rotation_tables()
    groups = [(0, 1, 4, 5), (2, 3, 6, 7), (8, 9, 12, 13), (10, 11, 14, 15)]
    for f in range(4):
        out = row_fold(
            [w_ref[f, q] for q in range(16)],
            [hu_ref[f, b] for b in range(3)],
            [hd_ref[f, b] for b in range(3)],
            row,
            col,
            rows_dev,
            elements,
        )
        out = [out[q] / mass_total[q] for q in range(16)]
        new = select_rows(out, rotation, backward_order)
        new = [jnp.where(valid, new[p], 0.0) for p in range(16)]
        for p in range(16):
            out_ref[f, p] = new[p]
        if f == 3:
            for p in range(16):
                cm_ref[p] = jnp.sum(new[p], axis=0, keepdims=True)
        if with_cells:
            average = [(prev_ref[f, p] + new[p]) / SUBSTEPS for p in range(16)]
            for c, group in enumerate(groups):
                m = [m_ref[p] for p in group]
                summed = (m[0] * average[group[0]] + m[1] * average[group[1]]) + (
                    m[2] * average[group[2]] + m[3] * average[group[3]]
                )
                area = (m[0] + m[1]) + (m[2] + m[3])
                cell_ref[c, f] = summed / area


def fin_call(w, halo_up, halo_down, mass_parts, info, rows_dev, elements, prev=None, mass=None):
    levels = w.shape[2]
    steps = levels // CHUNK
    block = pl.BlockSpec((4, 16, CHUNK, LANES), lambda i: (0, 0, i, 0))
    halo = pl.BlockSpec((halo_up.shape[0], 3, CHUNK, 128), lambda i: (0, 0, i, 0))
    small = pl.BlockSpec((16, 1, LANES), lambda i: (0, 0, 0))
    with_cells = prev is not None
    with_mass = halo_up.shape[0] == 5
    in_specs = [block, halo, halo, small]
    args = [w, halo_up, halo_down, mass_parts]
    in_specs.append(pl.BlockSpec((8, LANES), lambda i: (0, 0)))
    args.append(info)
    out_specs = [block, pl.BlockSpec((None, 16, 1, LANES), lambda i: (i, 0, 0, 0))]
    out_shape = [
        jax.ShapeDtypeStruct(w.shape, jnp.float32),
        jax.ShapeDtypeStruct((steps, 16, 1, LANES), jnp.float32),
    ]
    if with_cells:
        in_specs += [block, small]
        args += [prev, mass]
        out_specs.append(pl.BlockSpec((4, 4, CHUNK, LANES), lambda i: (0, 0, i, 0)))
        out_shape.append(jax.ShapeDtypeStruct((4, 4, levels, LANES), jnp.float32))
    if with_mass:
        out_specs.append(small)
        out_shape.append(jax.ShapeDtypeStruct((16, 1, LANES), jnp.float32))
    return pl.pallas_call(
        functools.partial(fin_kernel, rows_dev, elements, with_cells, with_mass),
        interpret=INTERPRET,
        grid=(steps,),
        in_specs=in_specs,
        out_specs=out_specs,
        out_shape=out_shape,
    )(*args)


def edge_exchange(last, first):
    seg_count = lax.axis_size("seg")
    up = [(i, (i + 1) % seg_count) for i in range(seg_count)]
    down = [(j, i) for i, j in up]
    return lax.ppermute(last, "seg", up), lax.ppermute(first, "seg", down)


def halo_exchange(w, elements):
    seg_count = lax.axis_size("seg")
    up = [(i, (i + 1) % seg_count) for i in range(seg_count)]
    down = [(j, i) for i, j in up]
    last = w[..., 12:16, :, elements - COLS : elements]
    first = w[..., 0:4, :, 0:COLS]
    prev_last = lax.ppermute(last, "seg", up)
    next_first = lax.ppermute(first, "seg", down)
    widths = [(0, 0)] * (w.ndim - 1)
    halo_up = jnp.pad(prev_last, widths + [(0, LANES - COLS)])
    halo_down = jnp.pad(next_first, widths + [(elements - COLS, LANES - elements)])
    return halo_up, halo_down


def mass_dss(mass_canon_rows, info, rows_dev, elements):
    col = info[1:2]
    row = info[2:3]
    rows = list(mass_canon_rows)
    for a in range(4):
        edge = rows[4 * a + 3]
        left = jnp.where(col == 0, jnp.roll(edge, -(COLS - 1), -1), jnp.roll(edge, 1, -1))
        total = rows[4 * a] + left
        rows[4 * a] = total
        rows[4 * a + 3] = jnp.where(
            col == COLS - 1, jnp.roll(total, COLS - 1, -1), jnp.roll(total, -1, -1)
        )
    w = jnp.stack(rows)
    halo_up, halo_down = halo_exchange(w, elements)
    out = list(rows)
    for b in range(4):
        from_up = jnp.where(row == 0, halo_up[b], jnp.roll(rows[12 + b], COLS, -1))
        out[b] = rows[b] + from_up
        from_down = jnp.where(row == rows_dev - 1, halo_down[b], jnp.roll(rows[b], -COLS, -1))
        out[12 + b] = rows[12 + b] + from_down
    total = jnp.stack(out)
    lane = jnp.arange(LANES)
    return jnp.where(lane < elements, total, 1.0)


def prep_kernel(elements, vel_ref, temp_ref, dp_ref, out_ref, cm_ref):
    chunk = out_ref.shape[2]
    zeros = jnp.zeros((chunk, 128), jnp.float32)
    blocks = [vel_ref[0], vel_ref[1], temp_ref[...], dp_ref[...]]
    for f, block in enumerate(blocks):
        grouped = block.reshape(chunk, 16, elements)
        for p in range(16):
            rows = grouped[:, p, :]
            out_ref[f, p, :, pl.ds(LANES - 128, 128)] = zeros
            out_ref[f, p, :, pl.ds(0, elements)] = rows
            if f == 3:
                cm_ref[p, :, pl.ds(LANES - 128, 128)] = jnp.zeros((1, 128), jnp.float32)
                cm_ref[p, :, pl.ds(0, elements)] = jnp.sum(rows, axis=0, keepdims=True)


def prep_call(velocity_pair, thermal_reading, layer_depth):
    levels, points, elements = thermal_reading.shape
    steps = levels // CHUNK
    rows = CHUNK * points
    vel = velocity_pair.reshape(2, levels * points, elements)
    temp = thermal_reading.reshape(levels * points, elements)
    dp = layer_depth.reshape(levels * points, elements)
    return pl.pallas_call(
        functools.partial(prep_kernel, elements),
        interpret=INTERPRET,
        grid=(steps,),
        in_specs=[
            pl.BlockSpec((2, rows, elements), lambda i: (0, i, 0)),
            pl.BlockSpec((rows, elements), lambda i: (i, 0)),
            pl.BlockSpec((rows, elements), lambda i: (i, 0)),
        ],
        out_specs=[
            pl.BlockSpec((4, 16, CHUNK, LANES), lambda i: (0, 0, i, 0)),
            pl.BlockSpec((None, 16, 1, LANES), lambda i: (i, 0, 0, 0)),
        ],
        out_shape=[
            jax.ShapeDtypeStruct((4, 16, levels, LANES), jnp.float32),
            jax.ShapeDtypeStruct((steps, 16, 1, LANES), jnp.float32),
        ],
    )(vel, temp, dp)


def local(
    velocity_pair,
    thermal_reading,
    layer_depth,
    jacobian_terms,
    rotation_frequency,
    integration_mass,
    shared_vertex_label,
    column_owner_slot,
):
    levels_dev = thermal_reading.shape[0]
    elements = thermal_reading.shape[2]
    seg_count = lax.axis_size("seg")
    lev_count = lax.axis_size("lev")
    rows_dev = elements // COLS
    node_cols = 3 * COLS
    first_row = 3 * rows_dev * lax.axis_index("seg")
    grid_rows = 3 * rows_dev * seg_count
    corner_ids = shared_vertex_label[0]
    element_pos = jnp.arange(elements)
    row_offset = (corner_ids // node_cols - first_row) % grid_rows - 3 * (element_pos // COLS)
    col_offset = (corner_ids % node_cols - 3 * (element_pos % COLS)) % node_cols
    rotation = jnp.where(
        row_offset == 0, jnp.where(col_offset == 0, 0, 1), jnp.where(col_offset == 3, 2, 3)
    )
    info = lane_info(rotation, elements)
    forward_order, _ = rotation_tables()

    fields, column_parts = prep_call(velocity_pair, thermal_reading, layer_depth)
    jac = pad_lanes(jacobian_terms[:, :, None, :])
    rot = pad_lanes(rotation_frequency[:, None, :])
    mass = pad_lanes(integration_mass[:, None, :])
    mass_one = pad_lanes(integration_mass[:, None, :], 1.0)
    mass_canon, mass_folded, mass_last, mass_first = mass_call(mass, info, elements)
    mass_parts = mass_folded
    mass_edges = (mass_last, mass_first)
    column_mass = jnp.sum(column_parts, axis=0)
    previous = None
    cells = None
    for substep in range(SUBSTEPS):
        above = carried_in(column_mass, "lev", False)
        g0, group_height = term_call(fields, above)
        below = carried_in(group_height, "lev", True)
        w, last, first = adv_call(
            fields, g0, below, jac, rot, mass_canon, info, elements, mass_edges
        )
        mass_edges = None
        halo_up, halo_down = edge_exchange(last, first)
        outs = fin_call(
            w,
            halo_up,
            halo_down,
            mass_parts,
            info,
            rows_dev,
            elements,
            previous if substep == SUBSTEPS - 1 else None,
            mass_one,
        )
        fields, column_parts = outs[:2]
        if substep == SUBSTEPS - 1:
            cells = outs[2]
        if substep == 0:
            mass_parts = outs[-1]
        previous = fields
        column_mass = jnp.sum(column_parts, axis=0)
    channels = 4 * levels_dev
    cell_values = cells[..., :elements].reshape(4, channels, elements)
    payload = jnp.transpose(cell_values, (0, 2, 1)).reshape(4 * elements, channels)
    dev_count = seg_count * lev_count
    own_cols = 4 * elements * seg_count // dev_count
    per_pair = own_cols // seg_count
    capacity = per_pair + per_pair // 2
    targets = column_owner_slot.reshape(-1)
    owner_index = targets // own_cols
    slot_index = targets % own_cols
    cell_count = targets.shape[0]
    cell_pos = jnp.arange(cell_count)
    same_owner = owner_index[:, None] == owner_index[None, :]
    earlier = cell_pos[:, None] < cell_pos[None, :]
    rank = jnp.sum(jnp.logical_and(same_owner, earlier).astype(jnp.int32), axis=0)
    destination = owner_index * capacity + rank
    slots = jnp.arange(dev_count * capacity)
    code = cell_pos * (own_cols + 1) + slot_index + 1
    match = destination[:, None] == slots[None, :]
    found = jnp.sum(jnp.where(match, code[:, None], 0), axis=0)
    has = found > 0
    source_cell = jnp.maximum(found - 1, 0) // (own_cols + 1)
    source_pos = jnp.maximum(found - 1, 0) % (own_cols + 1)
    outgoing = payload[source_cell]
    ids = jnp.where(has, source_pos, -1).reshape(dev_count, capacity)
    received_ids = lax.all_to_all(ids, ("seg", "lev"), split_axis=0, concat_axis=0, tiled=True)
    flat = jnp.arange(dev_count * capacity).reshape(dev_count, capacity)
    source_lev = (jnp.arange(dev_count) % lev_count)[:, None]
    positions = jnp.arange(own_cols)
    picks = []
    for group in range(lev_count):
        hit = jnp.logical_and(
            received_ids[:, :, None] == positions[None, None, :], (source_lev == group)[:, :, None]
        )
        picks.append(jnp.sum(jnp.where(hit, flat[:, :, None], 0), axis=(0, 1)))
    buffer = outgoing.reshape(dev_count, capacity, channels)
    received = lax.all_to_all(buffer, ("seg", "lev"), split_axis=0, concat_axis=0, tiled=True)
    received_rows = received.reshape(dev_count * capacity, channels)
    arrived = received_rows[jnp.stack(picks)]
    arrived = arrived.reshape(lev_count, own_cols, 4, levels_dev).transpose(2, 0, 3, 1)
    phys_state = arrived.reshape(4, lev_count * levels_dev, own_cols)
    mean_thickness = jnp.mean(phys_state[3], axis=0)
    dyn_state = jnp.transpose(fields[..., :elements], (0, 2, 1, 3))
    return (dyn_state, phys_state, mean_thickness)


def solution(mesh):
    in_specs = (
        P(None, "lev", None, "seg"),
        P("lev", None, "seg"),
        P("lev", None, "seg"),
        P(None, None, "seg"),
        P(None, "seg"),
        P(None, "seg"),
        P(None, "seg"),
        P(None, "seg"),
    )
    out_specs = (P(None, "lev", None, "seg"), P(None, None, ("seg", "lev")), P(("seg", "lev")))
    return jax.shard_map(local, mesh=mesh, in_specs=in_specs, out_specs=out_specs, check_vma=False)
```

```python
import functools

import jax
import jax.numpy as jnp
import numpy as np
from jax import lax
from jax.experimental import pallas as pl
from jax.experimental.pallas import tpu as pltpu
from jax.sharding import PartitionSpec as P

COLS = 120
SUBSTEPS = 2


top_pressure = 10.0
time_increment = 0.05


def gll_slopes():
    root_five = np.sqrt(5.0)
    gll_nodes = [-1.0, -1.0 / root_five, 1.0 / root_five, 1.0]
    legendre_values = [-1.0, 1.0 / root_five, -1.0 / root_five, 1.0]
    slopes = np.zeros((4, 4))
    for row_node in range(4):
        for column in range(4):
            if row_node != column:
                slopes[row_node, column] = (
                    legendre_values[row_node]
                    / legendre_values[column]
                    / (gll_nodes[row_node] - gll_nodes[column])
                )
    slopes[0, 0] = -3.0
    slopes[3, 3] = 3.0
    return slopes


SLOPES = gll_slopes().astype(np.float32)


def rotation_tables():
    forward = np.zeros((4, 16), np.int32)
    for first_pos in range(4):
        for second_pos in range(4):
            canonical = 4 * first_pos + second_pos
            forward[0, canonical] = 4 * first_pos + second_pos
            forward[1, canonical] = 4 * (3 - second_pos) + first_pos
            forward[2, canonical] = 4 * (3 - first_pos) + (3 - second_pos)
            forward[3, canonical] = 4 * second_pos + 3 - first_pos
    backward = np.argsort(forward, axis=1).astype(np.int32)
    return (forward, backward)


def weighted_sum(terms):
    acc = None
    for coef, value in terms:
        if coef == 0.0:
            continue
        part = jnp.float32(coef) * value
        acc = part if acc is None else acc + part
    return acc


def first_deriv(f):
    return jnp.stack(
        [
            weighted_sum([(SLOPES[a, k], f[4 * k + j]) for k in range(4)])
            for a in range(4)
            for j in range(4)
        ]
    )


def second_deriv(f):
    return jnp.stack(
        [
            weighted_sum([(SLOPES[a, k], f[4 * i + k]) for k in range(4)])
            for i in range(4)
            for a in range(4)
        ]
    )


def carried_in(part, axis, reverse):
    count = lax.axis_size(axis)
    place = lax.axis_index(axis)
    gathered = lax.all_gather(part, axis)
    index = jnp.arange(count).reshape((count,) + (1,) * part.ndim)
    chosen = index > place if reverse else index < place
    return jnp.sum(jnp.where(chosen, gathered, jnp.zeros_like(gathered)), axis=0)


def site_potential_energy(thermal_reading, layer_depth):
    column_mass = jnp.sum(layer_depth, axis=1)
    above_sum = carried_in(column_mass, "lev", False)
    layer_midpoint_load = (
        top_pressure + above_sum[:, None, :] + jnp.cumsum(layer_depth, axis=1) - 0.5 * layer_depth
    )
    surface_change_rate = thermal_reading * layer_depth / layer_midpoint_load
    group_height = jnp.sum(surface_change_rate, axis=1)
    below_sum = carried_in(group_height, "lev", True)
    return (
        below_sum[:, None, :]
        + lax.cumsum(surface_change_rate, axis=1, reverse=True)
        - 0.5 * surface_change_rate
    )


def tendency_step(u, v, temp, dp, geopotential, jac, rot):
    energy = geopotential + 0.5 * (u * u + v * v)
    energy_first = first_deriv(energy)
    energy_second = second_deriv(energy)
    zonal_slope = jac[0] * energy_first + jac[1] * energy_second
    meridional_slope = jac[2] * energy_first + jac[3] * energy_second
    initial_transport = jac[0] * u + jac[2] * v
    latter_transport = jac[1] * u + jac[3] * v
    advect_with_motion = initial_transport * first_deriv(temp) + latter_transport * second_deriv(
        temp
    )
    distribute_onto_vertices = first_deriv(dp * initial_transport) + second_deriv(
        dp * latter_transport
    )
    return (
        u + time_increment * (rot * v - zonal_slope),
        v - time_increment * (rot * u + meridional_slope),
        temp - time_increment * advect_with_motion,
        dp - time_increment * distribute_onto_vertices,
    )


def reorder(values, rotation, table):
    rows = []
    for q in range(16):
        pick = values[int(table[3, q])]
        for w in (2, 1, 0):
            pick = jnp.where(rotation == w, values[int(table[w, q])], pick)
        rows.append(pick)
    return jnp.stack(rows)


def node_sum(canon, col, row, rows_dev):
    elements = canon.shape[-1]

    def roll(y, shift):
        return jnp.roll(y, shift, axis=-1)

    rows = [canon[q] for q in range(16)]
    for a in range(4):
        left = jnp.where(col == 0, roll(rows[4 * a + 3], -(COLS - 1)), roll(rows[4 * a + 3], 1))
        total = rows[4 * a] + left
        rows[4 * a] = total
        rows[4 * a + 3] = jnp.where(col == COLS - 1, roll(total, COLS - 1), roll(total, -1))
    seg_count = lax.axis_size("seg")
    up = [(i, (i + 1) % seg_count) for i in range(seg_count)]
    down = [(j, i) for i, j in up]
    last = jnp.stack([rows[12 + b][:, elements - COLS :] for b in range(4)])
    first = jnp.stack([rows[b][:, :COLS] for b in range(4)])
    prev_last = lax.ppermute(last, "seg", up)
    next_first = lax.ppermute(first, "seg", down)
    pad = jnp.zeros(prev_last.shape[1:-1] + (elements - COLS,), canon.dtype)
    out = list(rows)
    for b in range(4):
        halo_up = jnp.concatenate([prev_last[b], pad], axis=-1)
        from_up = jnp.where(row == 0, halo_up, roll(rows[12 + b], COLS))
        out[b] = rows[b] + from_up
        halo_down = jnp.concatenate([pad, next_first[b]], axis=-1)
        from_down = jnp.where(row == rows_dev - 1, halo_down, roll(rows[b], -COLS))
        out[12 + b] = rows[12 + b] + from_down
    return jnp.stack(out)


LANES = 512
CHUNK = 8
INTERPRET = None


def lane_info(rotation, elements):
    element_pos = jnp.arange(elements)
    info = jnp.stack(
        [rotation, element_pos % COLS, element_pos // COLS]
        + [jnp.zeros_like(rotation)] * 5
    ).astype(jnp.int32)
    return jnp.pad(info, ((0, 0), (0, LANES - elements)), constant_values=-1)


def pad_lanes(x, value=0.0):
    widths = [(0, 0)] * (x.ndim - 1) + [(0, LANES - x.shape[-1])]
    return jnp.pad(x, widths, constant_values=value)


def select_rows(values, rotation, table):
    rows = []
    for q in range(16):
        pick = values[int(table[3, q])]
        for w in (2, 1, 0):
            pick = jnp.where(rotation == w, values[int(table[w, q])], pick)
        rows.append(pick)
    return rows


def term_kernel(levels, f_ref, above_ref, g_ref, gh_ref):
    level = lax.broadcasted_iota(jnp.int32, (levels, LANES), 0)
    for p in range(f_ref.shape[1]):
        temp = f_ref[0, p]
        dp = f_ref[1, p]
        cum = dp
        shift = 1
        while shift < levels:
            cum = cum + jnp.where(level >= shift, pltpu.roll(cum, shift, 0), 0.0)
            shift *= 2
        load = top_pressure + above_ref[p] + cum - 0.5 * dp
        term = temp * dp / load
        gh_ref[p] = jnp.sum(term, axis=0, keepdims=True)
        rcum = term
        shift = 1
        while shift < levels:
            rcum = rcum + jnp.where(
                level + shift < levels, pltpu.roll(rcum, levels - shift, 0), 0.0
            )
            shift *= 2
        g_ref[p] = rcum - 0.5 * term


def term_call(fields, above):
    levels = fields.shape[2]
    group = 4
    return pl.pallas_call(
        functools.partial(term_kernel, levels),
        interpret=INTERPRET,
        grid=(16 // group,),
        in_specs=[
            pl.BlockSpec((2, group, levels, LANES), lambda i: (1, i, 0, 0)),
            pl.BlockSpec((group, 1, LANES), lambda i: (i, 0, 0)),
        ],
        out_specs=[
            pl.BlockSpec((group, levels, LANES), lambda i: (i, 0, 0)),
            pl.BlockSpec((group, 1, LANES), lambda i: (i, 0, 0)),
        ],
        out_shape=[
            jax.ShapeDtypeStruct((16, levels, LANES), jnp.float32),
            jax.ShapeDtypeStruct((16, 1, LANES), jnp.float32),
        ],
    )(fields, above)


def lane_roll(y, shift):
    return pltpu.roll(y, shift % LANES, 1)


def column_fold(rows, col):
    rows = list(rows)
    for a in range(4):
        edge = rows[4 * a + 3]
        left = jnp.where(col == 0, lane_roll(edge, -(COLS - 1)), lane_roll(edge, 1))
        total = rows[4 * a] + left
        rows[4 * a] = total
        rows[4 * a + 3] = jnp.where(
            col == COLS - 1, lane_roll(total, COLS - 1), lane_roll(total, -1)
        )
    return rows


def shift_right(y, col):
    return jnp.where(col == COLS - 1, lane_roll(y, COLS - 1), lane_roll(y, -1))


def row_fold(rows, up_rows, down_rows, row, col, rows_dev, elements):
    fill = jnp.zeros((rows[0].shape[0], LANES - 128), jnp.float32)
    halo_up = [jnp.concatenate([up_rows[b], fill], axis=1) for b in range(3)]
    halo_down = [
        lane_roll(jnp.concatenate([down_rows[b], fill], axis=1), elements - COLS) for b in range(3)
    ]
    halo_up.append(shift_right(halo_up[0], col))
    halo_down.append(shift_right(halo_down[0], col))
    out = list(rows)
    for b in range(4):
        from_up = jnp.where(row == 0, halo_up[b], lane_roll(rows[12 + b], COLS))
        out[b] = rows[b] + from_up
        from_down = jnp.where(row == rows_dev - 1, halo_down[b], lane_roll(rows[b], -COLS))
        out[12 + b] = rows[12 + b] + from_down
    return out


def mass_kernel(elements, m_ref, j_ref, r_ref, info_ref, mc_ref, mw_ref, last_ref, first_ref, mp_ref, mo_ref, jp_ref, rp_ref):
    info = info_ref[...]
    forward_order, _ = rotation_tables()
    zero = jnp.zeros((1, 128), jnp.float32)
    one = jnp.ones((1, 128), jnp.float32)
    for p in range(16):
        row = m_ref[pl.ds(p, 1), :]
        mp_ref[p, :, pl.ds(LANES - 128, 128)] = zero
        mp_ref[p, :, pl.ds(0, elements)] = row
        mo_ref[p, :, pl.ds(LANES - 128, 128)] = one
        mo_ref[p, :, pl.ds(0, elements)] = row
        rp_ref[p, :, pl.ds(LANES - 128, 128)] = zero
        rp_ref[p, :, pl.ds(0, elements)] = r_ref[pl.ds(p, 1), :]
        for k in range(4):
            jp_ref[k, p, :, pl.ds(LANES - 128, 128)] = zero
            jp_ref[k, p, :, pl.ds(0, elements)] = j_ref[k, pl.ds(p, 1), :]
    canon = select_rows([mp_ref[p] for p in range(16)], info[0:1], forward_order)
    rows = column_fold(canon, info[1:2])
    for q in range(16):
        mc_ref[q] = canon[q]
        mw_ref[q] = rows[q]
    for b in range(4):
        last_ref[b] = lane_roll(rows[12 + b], COLS - elements)[:, :128]
        first_ref[b] = rows[b][:, :128]


def mass_call(mass, jac, rot, info):
    elements = mass.shape[-1]
    small = jax.ShapeDtypeStruct((16, 1, LANES), jnp.float32)
    edge = jax.ShapeDtypeStruct((4, 1, 128), jnp.float32)
    return pl.pallas_call(
        functools.partial(mass_kernel, elements),
        interpret=INTERPRET,
        out_shape=[
            small,
            small,
            edge,
            edge,
            small,
            small,
            jax.ShapeDtypeStruct((4, 16, 1, LANES), jnp.float32),
            small,
        ],
    )(mass, jac, rot, info)


def adv_kernel(elements, with_mass, *refs):
    f_ref, g_ref, below_ref, jac_ref, rot_ref, mc_ref, info_ref = refs[:7]
    if with_mass:
        mlast_ref, mfirst_ref = refs[7:9]
    out_ref, last_ref, first_ref = refs[-3:]
    info = info_ref[...]
    rotation = info[0:1]
    col = info[1:2]
    forward_order, _ = rotation_tables()
    u = [f_ref[0, p] for p in range(16)]
    v = [f_ref[1, p] for p in range(16)]
    temp = [f_ref[2, p] for p in range(16)]
    dp = [f_ref[3, p] for p in range(16)]
    jac = [[jac_ref[k, p] for p in range(16)] for k in range(4)]
    energy = [
        (below_ref[p] + g_ref[p]) + 0.5 * (u[p] * u[p] + v[p] * v[p]) for p in range(16)
    ]
    e1 = first_rows(energy)
    e2 = second_rows(energy)
    it = [jac[0][p] * u[p] + jac[2][p] * v[p] for p in range(16)]
    lt = [jac[1][p] * u[p] + jac[3][p] * v[p] for p in range(16)]
    t1 = first_rows(temp)
    t2 = second_rows(temp)
    d1 = first_rows([dp[p] * it[p] for p in range(16)])
    d2 = second_rows([dp[p] * lt[p] for p in range(16)])
    advanced = []
    for p in range(16):
        rot = rot_ref[p]
        zonal_slope = jac[0][p] * e1[p] + jac[1][p] * e2[p]
        meridional_slope = jac[2][p] * e1[p] + jac[3][p] * e2[p]
        advanced.append(
            (
                u[p] + time_increment * (rot * v[p] - zonal_slope),
                v[p] - time_increment * (rot * u[p] + meridional_slope),
                temp[p] - time_increment * (it[p] * t1[p] + lt[p] * t2[p]),
                dp[p] - time_increment * (d1[p] + d2[p]),
            )
        )
    for f in range(4):
        rows = select_rows([advanced[p][f] for p in range(16)], rotation, forward_order)
        rows = column_fold([rows[q] * mc_ref[q] for q in range(16)], col)
        for q in range(16):
            out_ref[f, q] = rows[q]
        for b in range(3):
            last_ref[f, b] = lane_roll(rows[12 + b], COLS - elements)[:, :128]
            first_ref[f, b] = rows[b][:, :128]
    if with_mass:
        shape = last_ref.shape[2:]
        for b in range(3):
            last_ref[4, b] = jnp.broadcast_to(mlast_ref[b], shape)
            first_ref[4, b] = jnp.broadcast_to(mfirst_ref[b], shape)


def first_rows(rows):
    return [
        weighted_sum([(SLOPES[a, k], rows[4 * k + j]) for k in range(4)])
        for a in range(4)
        for j in range(4)
    ]


def second_rows(rows):
    return [
        weighted_sum([(SLOPES[a, k], rows[4 * i + k]) for k in range(4)])
        for i in range(4)
        for a in range(4)
    ]


def adv_call(fields, g0, below, jac, rot, mass_canon, info, elements, mass_edges=None):
    levels = fields.shape[2]
    steps = levels // CHUNK
    with_mass = mass_edges is not None
    width = 5 if with_mass else 4
    small = pl.BlockSpec((16, 1, LANES), lambda i: (0, 0, 0))
    edge = pl.BlockSpec((width, 3, CHUNK, 128), lambda i: (0, 0, i, 0))
    edge_shape = jax.ShapeDtypeStruct((width, 3, levels, 128), jnp.float32)
    in_specs = [
        pl.BlockSpec((4, 16, CHUNK, LANES), lambda i: (0, 0, i, 0)),
        pl.BlockSpec((16, CHUNK, LANES), lambda i: (0, i, 0)),
        small,
        pl.BlockSpec((4, 16, 1, LANES), lambda i: (0, 0, 0, 0)),
        small,
        small,
        pl.BlockSpec((8, LANES), lambda i: (0, 0)),
    ]
    args = [fields, g0, below, jac, rot, mass_canon, info]
    if with_mass:
        in_specs += [pl.BlockSpec((4, 1, 128), lambda i: (0, 0, 0))] * 2
        args += list(mass_edges)
    return pl.pallas_call(
        functools.partial(adv_kernel, elements, with_mass),
        interpret=INTERPRET,
        grid=(steps,),
        in_specs=in_specs,
        out_specs=[pl.BlockSpec((4, 16, CHUNK, LANES), lambda i: (0, 0, i, 0)), edge, edge],
        out_shape=[jax.ShapeDtypeStruct(fields.shape, jnp.float32), edge_shape, edge_shape],
    )(*args)


def fin_kernel(rows_dev, elements, with_cells, with_mass, *refs):
    refs = list(refs)
    w_ref, hu_ref, hd_ref = refs[:3]
    if with_mass:
        mw_ref = refs[3]
        refs = refs[4:]
    else:
        mt_ref = refs[3]
        refs = refs[4:]
    info_ref = refs.pop(0)
    if with_cells:
        prev_ref, m_ref = refs[:2]
        refs = refs[2:]
    out_ref, cm_ref = refs[:2]
    if with_cells:
        cell_ref = refs[2]
    info = info_ref[...]
    rotation = info[0:1]
    col = info[1:2]
    row = info[2:3]
    if with_mass:
        mass_total = row_fold(
            [mw_ref[q] for q in range(16)],
            [hu_ref[4, b][0:1] for b in range(3)],
            [hd_ref[4, b][0:1] for b in range(3)],
            row,
            col,
            rows_dev,
            elements,
        )
        lane_ok = lax.broadcasted_iota(jnp.int32, (1, LANES), 1) < elements
        mass_total = [jnp.where(lane_ok, m, 1.0) for m in mass_total]
        for q in range(16):
            refs[-1][q] = mass_total[q]
    else:
        mass_total = [mt_ref[q] for q in range(16)]
    lane = lax.broadcasted_iota(jnp.int32, (1, LANES), 1)
    valid = lane < elements
    _, backward_order = rotation_tables()
    groups = [(0, 1, 4, 5), (2, 3, 6, 7), (8, 9, 12, 13), (10, 11, 14, 15)]
    for f in range(4):
        out = row_fold(
            [w_ref[f, q] for q in range(16)],
            [hu_ref[f, b] for b in range(3)],
            [hd_ref[f, b] for b in range(3)],
            row,
            col,
            rows_dev,
            elements,
        )
        out = [out[q] / mass_total[q] for q in range(16)]
        new = select_rows(out, rotation, backward_order)
        new = [jnp.where(valid, new[p], 0.0) for p in range(16)]
        for p in range(16):
            out_ref[f, p] = new[p]
        if f == 3:
            for p in range(16):
                cm_ref[p] = jnp.sum(new[p], axis=0, keepdims=True)
        if with_cells:
            average = [(prev_ref[f, p] + new[p]) / SUBSTEPS for p in range(16)]
            for c, group in enumerate(groups):
                m = [m_ref[p] for p in group]
                summed = (m[0] * average[group[0]] + m[1] * average[group[1]]) + (
                    m[2] * average[group[2]] + m[3] * average[group[3]]
                )
                area = (m[0] + m[1]) + (m[2] + m[3])
                cell_ref[c, f] = summed / area


def fin_call(w, halo_up, halo_down, mass_parts, info, rows_dev, elements, prev=None, mass=None):
    levels = w.shape[2]
    steps = levels // CHUNK
    block = pl.BlockSpec((4, 16, CHUNK, LANES), lambda i: (0, 0, i, 0))
    halo = pl.BlockSpec((halo_up.shape[0], 3, CHUNK, 128), lambda i: (0, 0, i, 0))
    small = pl.BlockSpec((16, 1, LANES), lambda i: (0, 0, 0))
    with_cells = prev is not None
    with_mass = halo_up.shape[0] == 5
    in_specs = [block, halo, halo, small]
    args = [w, halo_up, halo_down, mass_parts]
    in_specs.append(pl.BlockSpec((8, LANES), lambda i: (0, 0)))
    args.append(info)
    out_specs = [block, pl.BlockSpec((None, 16, 1, LANES), lambda i: (i, 0, 0, 0))]
    out_shape = [
        jax.ShapeDtypeStruct(w.shape, jnp.float32),
        jax.ShapeDtypeStruct((steps, 16, 1, LANES), jnp.float32),
    ]
    if with_cells:
        in_specs += [block, small]
        args += [prev, mass]
        out_specs.append(pl.BlockSpec((4, 4, CHUNK, LANES), lambda i: (0, 0, i, 0)))
        out_shape.append(jax.ShapeDtypeStruct((4, 4, levels, LANES), jnp.float32))
    if with_mass:
        out_specs.append(small)
        out_shape.append(jax.ShapeDtypeStruct((16, 1, LANES), jnp.float32))
    return pl.pallas_call(
        functools.partial(fin_kernel, rows_dev, elements, with_cells, with_mass),
        interpret=INTERPRET,
        grid=(steps,),
        in_specs=in_specs,
        out_specs=out_specs,
        out_shape=out_shape,
    )(*args)


def edge_exchange(last, first):
    seg_count = lax.axis_size("seg")
    up = [(i, (i + 1) % seg_count) for i in range(seg_count)]
    down = [(j, i) for i, j in up]
    return lax.ppermute(last, "seg", up), lax.ppermute(first, "seg", down)


def halo_exchange(w, elements):
    seg_count = lax.axis_size("seg")
    up = [(i, (i + 1) % seg_count) for i in range(seg_count)]
    down = [(j, i) for i, j in up]
    last = w[..., 12:16, :, elements - COLS : elements]
    first = w[..., 0:4, :, 0:COLS]
    prev_last = lax.ppermute(last, "seg", up)
    next_first = lax.ppermute(first, "seg", down)
    widths = [(0, 0)] * (w.ndim - 1)
    halo_up = jnp.pad(prev_last, widths + [(0, LANES - COLS)])
    halo_down = jnp.pad(next_first, widths + [(elements - COLS, LANES - elements)])
    return halo_up, halo_down


def mass_dss(mass_canon_rows, info, rows_dev, elements):
    col = info[1:2]
    row = info[2:3]
    rows = list(mass_canon_rows)
    for a in range(4):
        edge = rows[4 * a + 3]
        left = jnp.where(col == 0, jnp.roll(edge, -(COLS - 1), -1), jnp.roll(edge, 1, -1))
        total = rows[4 * a] + left
        rows[4 * a] = total
        rows[4 * a + 3] = jnp.where(
            col == COLS - 1, jnp.roll(total, COLS - 1, -1), jnp.roll(total, -1, -1)
        )
    w = jnp.stack(rows)
    halo_up, halo_down = halo_exchange(w, elements)
    out = list(rows)
    for b in range(4):
        from_up = jnp.where(row == 0, halo_up[b], jnp.roll(rows[12 + b], COLS, -1))
        out[b] = rows[b] + from_up
        from_down = jnp.where(row == rows_dev - 1, halo_down[b], jnp.roll(rows[b], -COLS, -1))
        out[12 + b] = rows[12 + b] + from_down
    total = jnp.stack(out)
    lane = jnp.arange(LANES)
    return jnp.where(lane < elements, total, 1.0)


def prep_kernel(elements, vel_ref, temp_ref, dp_ref, out_ref, cm_ref):
    chunk = out_ref.shape[2]
    zeros = jnp.zeros((chunk, 128), jnp.float32)
    blocks = [vel_ref[0], vel_ref[1], temp_ref[...], dp_ref[...]]
    for f, block in enumerate(blocks):
        grouped = block.reshape(chunk, 16, elements)
        for p in range(16):
            rows = grouped[:, p, :]
            out_ref[f, p, :, pl.ds(LANES - 128, 128)] = zeros
            out_ref[f, p, :, pl.ds(0, elements)] = rows
            if f == 3:
                cm_ref[p, :, pl.ds(LANES - 128, 128)] = jnp.zeros((1, 128), jnp.float32)
                cm_ref[p, :, pl.ds(0, elements)] = jnp.sum(rows, axis=0, keepdims=True)


def prep_call(velocity_pair, thermal_reading, layer_depth):
    levels, points, elements = thermal_reading.shape
    steps = levels // CHUNK
    rows = CHUNK * points
    vel = velocity_pair.reshape(2, levels * points, elements)
    temp = thermal_reading.reshape(levels * points, elements)
    dp = layer_depth.reshape(levels * points, elements)
    return pl.pallas_call(
        functools.partial(prep_kernel, elements),
        interpret=INTERPRET,
        grid=(steps,),
        in_specs=[
            pl.BlockSpec((2, rows, elements), lambda i: (0, i, 0)),
            pl.BlockSpec((rows, elements), lambda i: (i, 0)),
            pl.BlockSpec((rows, elements), lambda i: (i, 0)),
        ],
        out_specs=[
            pl.BlockSpec((4, 16, CHUNK, LANES), lambda i: (0, 0, i, 0)),
            pl.BlockSpec((None, 16, 1, LANES), lambda i: (i, 0, 0, 0)),
        ],
        out_shape=[
            jax.ShapeDtypeStruct((4, 16, levels, LANES), jnp.float32),
            jax.ShapeDtypeStruct((steps, 16, 1, LANES), jnp.float32),
        ],
    )(vel, temp, dp)


def local(
    velocity_pair,
    thermal_reading,
    layer_depth,
    jacobian_terms,
    rotation_frequency,
    integration_mass,
    shared_vertex_label,
    column_owner_slot,
):
    levels_dev = thermal_reading.shape[0]
    elements = thermal_reading.shape[2]
    seg_count = lax.axis_size("seg")
    lev_count = lax.axis_size("lev")
    rows_dev = elements // COLS
    node_cols = 3 * COLS
    first_row = 3 * rows_dev * lax.axis_index("seg")
    grid_rows = 3 * rows_dev * seg_count
    corner_ids = shared_vertex_label[0]
    element_pos = jnp.arange(elements)
    row_offset = (corner_ids // node_cols - first_row) % grid_rows - 3 * (element_pos // COLS)
    col_offset = (corner_ids % node_cols - 3 * (element_pos % COLS)) % node_cols
    rotation = jnp.where(
        row_offset == 0, jnp.where(col_offset == 0, 0, 1), jnp.where(col_offset == 3, 2, 3)
    )
    info = lane_info(rotation, elements)
    forward_order, _ = rotation_tables()

    fields, column_parts = prep_call(velocity_pair, thermal_reading, layer_depth)
    (
        mass_canon,
        mass_folded,
        mass_last,
        mass_first,
        mass,
        mass_one,
        jac,
        rot,
    ) = mass_call(integration_mass, jacobian_terms, rotation_frequency, info)
    mass_parts = mass_folded
    mass_edges = (mass_last, mass_first)
    column_mass = jnp.sum(column_parts, axis=0)
    previous = None
    cells = None
    for substep in range(SUBSTEPS):
        above = carried_in(column_mass, "lev", False)
        g0, group_height = term_call(fields, above)
        below = carried_in(group_height, "lev", True)
        w, last, first = adv_call(
            fields, g0, below, jac, rot, mass_canon, info, elements, mass_edges
        )
        mass_edges = None
        halo_up, halo_down = edge_exchange(last, first)
        outs = fin_call(
            w,
            halo_up,
            halo_down,
            mass_parts,
            info,
            rows_dev,
            elements,
            previous if substep == SUBSTEPS - 1 else None,
            mass_one,
        )
        fields, column_parts = outs[:2]
        if substep == SUBSTEPS - 1:
            cells = outs[2]
        if substep == 0:
            mass_parts = outs[-1]
        previous = fields
        column_mass = jnp.sum(column_parts, axis=0)
    channels = 4 * levels_dev
    cell_values = cells[..., :elements].reshape(4, channels, elements)
    payload = jnp.transpose(cell_values, (0, 2, 1)).reshape(4 * elements, channels)
    dev_count = seg_count * lev_count
    own_cols = 4 * elements * seg_count // dev_count
    per_pair = own_cols // seg_count
    capacity = per_pair + per_pair // 2
    targets = column_owner_slot.reshape(-1)
    owner_index = targets // own_cols
    slot_index = targets % own_cols
    cell_count = targets.shape[0]
    cell_pos = jnp.arange(cell_count)
    same_owner = owner_index[:, None] == owner_index[None, :]
    earlier = cell_pos[:, None] < cell_pos[None, :]
    rank = jnp.sum(jnp.logical_and(same_owner, earlier).astype(jnp.int32), axis=0)
    destination = owner_index * capacity + rank
    slots = jnp.arange(dev_count * capacity)
    code = cell_pos * (own_cols + 1) + slot_index + 1
    match = destination[:, None] == slots[None, :]
    found = jnp.sum(jnp.where(match, code[:, None], 0), axis=0)
    has = found > 0
    source_cell = jnp.maximum(found - 1, 0) // (own_cols + 1)
    source_pos = jnp.maximum(found - 1, 0) % (own_cols + 1)
    outgoing = payload[source_cell.reshape(dev_count, capacity)]
    ids = jnp.where(has, source_pos, -1).reshape(dev_count, capacity)
    received_ids = lax.all_to_all(ids, ("seg", "lev"), split_axis=0, concat_axis=0, tiled=True)
    flat = jnp.arange(dev_count * capacity).reshape(dev_count, capacity)
    source_lev = (jnp.arange(dev_count) % lev_count)[:, None]
    positions = jnp.arange(own_cols)
    picks = []
    for group in range(lev_count):
        hit = jnp.logical_and(
            received_ids[:, :, None] == positions[None, None, :], (source_lev == group)[:, :, None]
        )
        picks.append(jnp.sum(jnp.where(hit, flat[:, :, None], 0), axis=(0, 1)))
    received = lax.all_to_all(outgoing, ("seg", "lev"), split_axis=0, concat_axis=0, tiled=True)
    picked = jnp.stack(picks)
    arrived = received[picked // capacity, picked % capacity]
    arrived = arrived.reshape(lev_count, own_cols, 4, levels_dev).transpose(2, 0, 3, 1)
    phys_state = arrived.reshape(4, lev_count * levels_dev, own_cols)
    mean_thickness = jnp.mean(phys_state[3], axis=0)
    dyn_state = jnp.transpose(fields[..., :elements], (0, 2, 1, 3))
    return (dyn_state, phys_state, mean_thickness)


def solution(mesh):
    in_specs = (
        P(None, "lev", None, "seg"),
        P("lev", None, "seg"),
        P("lev", None, "seg"),
        P(None, None, "seg"),
        P(None, "seg"),
        P(None, "seg"),
        P(None, "seg"),
        P(None, "seg"),
    )
    out_specs = (P(None, "lev", None, "seg"), P(None, None, ("seg", "lev")), P(("seg", "lev")))
    return jax.shard_map(local, mesh=mesh, in_specs=in_specs, out_specs=out_specs, check_vma=False)
```

```python
import functools

import jax
import jax.numpy as jnp
import numpy as np
from jax import lax
from jax.experimental import pallas as pl
from jax.experimental.pallas import tpu as pltpu
from jax.sharding import PartitionSpec as P

COLS = 120
SUBSTEPS = 2


top_pressure = 10.0
time_increment = 0.05


def gll_slopes():
    root_five = np.sqrt(5.0)
    gll_nodes = [-1.0, -1.0 / root_five, 1.0 / root_five, 1.0]
    legendre_values = [-1.0, 1.0 / root_five, -1.0 / root_five, 1.0]
    slopes = np.zeros((4, 4))
    for row_node in range(4):
        for column in range(4):
            if row_node != column:
                slopes[row_node, column] = (
                    legendre_values[row_node]
                    / legendre_values[column]
                    / (gll_nodes[row_node] - gll_nodes[column])
                )
    slopes[0, 0] = -3.0
    slopes[3, 3] = 3.0
    return slopes


SLOPES = gll_slopes().astype(np.float32)


def rotation_tables():
    forward = np.zeros((4, 16), np.int32)
    for first_pos in range(4):
        for second_pos in range(4):
            canonical = 4 * first_pos + second_pos
            forward[0, canonical] = 4 * first_pos + second_pos
            forward[1, canonical] = 4 * (3 - second_pos) + first_pos
            forward[2, canonical] = 4 * (3 - first_pos) + (3 - second_pos)
            forward[3, canonical] = 4 * second_pos + 3 - first_pos
    backward = np.argsort(forward, axis=1).astype(np.int32)
    return (forward, backward)


def weighted_sum(terms):
    acc = None
    for coef, value in terms:
        if coef == 0.0:
            continue
        part = jnp.float32(coef) * value
        acc = part if acc is None else acc + part
    return acc


def first_deriv(f):
    return jnp.stack(
        [
            weighted_sum([(SLOPES[a, k], f[4 * k + j]) for k in range(4)])
            for a in range(4)
            for j in range(4)
        ]
    )


def second_deriv(f):
    return jnp.stack(
        [
            weighted_sum([(SLOPES[a, k], f[4 * i + k]) for k in range(4)])
            for i in range(4)
            for a in range(4)
        ]
    )


def carried_in(part, axis, reverse):
    count = lax.axis_size(axis)
    place = lax.axis_index(axis)
    gathered = lax.all_gather(part, axis)
    index = jnp.arange(count).reshape((count,) + (1,) * part.ndim)
    chosen = index > place if reverse else index < place
    return jnp.sum(jnp.where(chosen, gathered, jnp.zeros_like(gathered)), axis=0)


def site_potential_energy(thermal_reading, layer_depth):
    column_mass = jnp.sum(layer_depth, axis=1)
    above_sum = carried_in(column_mass, "lev", False)
    layer_midpoint_load = (
        top_pressure + above_sum[:, None, :] + jnp.cumsum(layer_depth, axis=1) - 0.5 * layer_depth
    )
    surface_change_rate = thermal_reading * layer_depth / layer_midpoint_load
    group_height = jnp.sum(surface_change_rate, axis=1)
    below_sum = carried_in(group_height, "lev", True)
    return (
        below_sum[:, None, :]
        + lax.cumsum(surface_change_rate, axis=1, reverse=True)
        - 0.5 * surface_change_rate
    )


def tendency_step(u, v, temp, dp, geopotential, jac, rot):
    energy = geopotential + 0.5 * (u * u + v * v)
    energy_first = first_deriv(energy)
    energy_second = second_deriv(energy)
    zonal_slope = jac[0] * energy_first + jac[1] * energy_second
    meridional_slope = jac[2] * energy_first + jac[3] * energy_second
    initial_transport = jac[0] * u + jac[2] * v
    latter_transport = jac[1] * u + jac[3] * v
    advect_with_motion = initial_transport * first_deriv(temp) + latter_transport * second_deriv(
        temp
    )
    distribute_onto_vertices = first_deriv(dp * initial_transport) + second_deriv(
        dp * latter_transport
    )
    return (
        u + time_increment * (rot * v - zonal_slope),
        v - time_increment * (rot * u + meridional_slope),
        temp - time_increment * advect_with_motion,
        dp - time_increment * distribute_onto_vertices,
    )


def reorder(values, rotation, table):
    rows = []
    for q in range(16):
        pick = values[int(table[3, q])]
        for w in (2, 1, 0):
            pick = jnp.where(rotation == w, values[int(table[w, q])], pick)
        rows.append(pick)
    return jnp.stack(rows)


def node_sum(canon, col, row, rows_dev):
    elements = canon.shape[-1]

    def roll(y, shift):
        return jnp.roll(y, shift, axis=-1)

    rows = [canon[q] for q in range(16)]
    for a in range(4):
        left = jnp.where(col == 0, roll(rows[4 * a + 3], -(COLS - 1)), roll(rows[4 * a + 3], 1))
        total = rows[4 * a] + left
        rows[4 * a] = total
        rows[4 * a + 3] = jnp.where(col == COLS - 1, roll(total, COLS - 1), roll(total, -1))
    seg_count = lax.axis_size("seg")
    up = [(i, (i + 1) % seg_count) for i in range(seg_count)]
    down = [(j, i) for i, j in up]
    last = jnp.stack([rows[12 + b][:, elements - COLS :] for b in range(4)])
    first = jnp.stack([rows[b][:, :COLS] for b in range(4)])
    prev_last = lax.ppermute(last, "seg", up)
    next_first = lax.ppermute(first, "seg", down)
    pad = jnp.zeros(prev_last.shape[1:-1] + (elements - COLS,), canon.dtype)
    out = list(rows)
    for b in range(4):
        halo_up = jnp.concatenate([prev_last[b], pad], axis=-1)
        from_up = jnp.where(row == 0, halo_up, roll(rows[12 + b], COLS))
        out[b] = rows[b] + from_up
        halo_down = jnp.concatenate([pad, next_first[b]], axis=-1)
        from_down = jnp.where(row == rows_dev - 1, halo_down, roll(rows[b], -COLS))
        out[12 + b] = rows[12 + b] + from_down
    return jnp.stack(out)


LANES = 512
CHUNK = 8
INTERPRET = None


def lane_info(rotation, elements):
    element_pos = jnp.arange(elements)
    info = jnp.stack(
        [rotation, element_pos % COLS, element_pos // COLS]
        + [jnp.zeros_like(rotation)] * 5
    ).astype(jnp.int32)
    return jnp.pad(info, ((0, 0), (0, LANES - elements)), constant_values=-1)


def pad_lanes(x, value=0.0):
    widths = [(0, 0)] * (x.ndim - 1) + [(0, LANES - x.shape[-1])]
    return jnp.pad(x, widths, constant_values=value)


def select_rows(values, rotation, table):
    rows = []
    for q in range(16):
        pick = values[int(table[3, q])]
        for w in (2, 1, 0):
            pick = jnp.where(rotation == w, values[int(table[w, q])], pick)
        rows.append(pick)
    return rows


def term_kernel(levels, f_ref, above_ref, g_ref, gh_ref):
    level = lax.broadcasted_iota(jnp.int32, (levels, LANES), 0)
    for p in range(f_ref.shape[1]):
        temp = f_ref[0, p]
        dp = f_ref[1, p]
        cum = dp
        shift = 1
        while shift < levels:
            cum = cum + jnp.where(level >= shift, pltpu.roll(cum, shift, 0), 0.0)
            shift *= 2
        load = top_pressure + above_ref[p] + cum - 0.5 * dp
        term = temp * dp / load
        gh_ref[p] = jnp.sum(term, axis=0, keepdims=True)
        rcum = term
        shift = 1
        while shift < levels:
            rcum = rcum + jnp.where(
                level + shift < levels, pltpu.roll(rcum, levels - shift, 0), 0.0
            )
            shift *= 2
        g_ref[p] = rcum - 0.5 * term


def term_call(fields, above):
    levels = fields.shape[2]
    group = 4
    return pl.pallas_call(
        functools.partial(term_kernel, levels),
        interpret=INTERPRET,
        grid=(16 // group,),
        in_specs=[
            pl.BlockSpec((2, group, levels, LANES), lambda i: (1, i, 0, 0)),
            pl.BlockSpec((group, 1, LANES), lambda i: (i, 0, 0)),
        ],
        out_specs=[
            pl.BlockSpec((group, levels, LANES), lambda i: (i, 0, 0)),
            pl.BlockSpec((group, 1, LANES), lambda i: (i, 0, 0)),
        ],
        out_shape=[
            jax.ShapeDtypeStruct((16, levels, LANES), jnp.float32),
            jax.ShapeDtypeStruct((16, 1, LANES), jnp.float32),
        ],
    )(fields, above)


def lane_roll(y, shift):
    return pltpu.roll(y, shift % LANES, 1)


def column_fold(rows, col):
    rows = list(rows)
    for a in range(4):
        edge = rows[4 * a + 3]
        left = jnp.where(col == 0, lane_roll(edge, -(COLS - 1)), lane_roll(edge, 1))
        total = rows[4 * a] + left
        rows[4 * a] = total
        rows[4 * a + 3] = jnp.where(
            col == COLS - 1, lane_roll(total, COLS - 1), lane_roll(total, -1)
        )
    return rows


def shift_right(y, col):
    return jnp.where(col == COLS - 1, lane_roll(y, COLS - 1), lane_roll(y, -1))


def row_fold(rows, up_rows, down_rows, row, col, rows_dev, elements):
    fill = jnp.zeros((rows[0].shape[0], LANES - 128), jnp.float32)
    halo_up = [jnp.concatenate([up_rows[b], fill], axis=1) for b in range(3)]
    halo_down = [
        lane_roll(jnp.concatenate([down_rows[b], fill], axis=1), elements - COLS) for b in range(3)
    ]
    halo_up.append(shift_right(halo_up[0], col))
    halo_down.append(shift_right(halo_down[0], col))
    out = list(rows)
    for b in range(4):
        from_up = jnp.where(row == 0, halo_up[b], lane_roll(rows[12 + b], COLS))
        out[b] = rows[b] + from_up
        from_down = jnp.where(row == rows_dev - 1, halo_down[b], lane_roll(rows[b], -COLS))
        out[12 + b] = rows[12 + b] + from_down
    return out


def mass_kernel(elements, m_ref, j_ref, r_ref, info_ref, mc_ref, mw_ref, last_ref, first_ref, mp_ref, mo_ref, jp_ref, rp_ref):
    info = info_ref[...]
    forward_order, _ = rotation_tables()
    zero = jnp.zeros((1, 128), jnp.float32)
    one = jnp.ones((1, 128), jnp.float32)
    for p in range(16):
        row = m_ref[pl.ds(p, 1), :]
        mp_ref[p, :, pl.ds(LANES - 128, 128)] = zero
        mp_ref[p, :, pl.ds(0, elements)] = row
        mo_ref[p, :, pl.ds(LANES - 128, 128)] = one
        mo_ref[p, :, pl.ds(0, elements)] = row
        rp_ref[p, :, pl.ds(LANES - 128, 128)] = zero
        rp_ref[p, :, pl.ds(0, elements)] = r_ref[pl.ds(p, 1), :]
        for k in range(4):
            jp_ref[k, p, :, pl.ds(LANES - 128, 128)] = zero
            jp_ref[k, p, :, pl.ds(0, elements)] = j_ref[k, pl.ds(p, 1), :]
    canon = select_rows([mp_ref[p] for p in range(16)], info[0:1], forward_order)
    rows = column_fold(canon, info[1:2])
    for q in range(16):
        mc_ref[q] = canon[q]
        mw_ref[q] = rows[q]
    for b in range(4):
        last_ref[b] = lane_roll(rows[12 + b], COLS - elements)[:, :128]
        first_ref[b] = rows[b][:, :128]


def mass_call(mass, jac, rot, info):
    elements = mass.shape[-1]
    small = jax.ShapeDtypeStruct((16, 1, LANES), jnp.float32)
    edge = jax.ShapeDtypeStruct((4, 1, 128), jnp.float32)
    return pl.pallas_call(
        functools.partial(mass_kernel, elements),
        interpret=INTERPRET,
        out_shape=[
            small,
            small,
            edge,
            edge,
            small,
            small,
            jax.ShapeDtypeStruct((4, 16, 1, LANES), jnp.float32),
            small,
        ],
    )(mass, jac, rot, info)


def adv_kernel(elements, with_mass, *refs):
    f_ref, g_ref, below_ref, jac_ref, rot_ref, mc_ref, info_ref = refs[:7]
    if with_mass:
        mlast_ref, mfirst_ref = refs[7:9]
    out_ref, last_ref, first_ref = refs[-3:]
    info = info_ref[...]
    rotation = info[0:1]
    col = info[1:2]
    forward_order, _ = rotation_tables()
    u = [f_ref[0, p] for p in range(16)]
    v = [f_ref[1, p] for p in range(16)]
    temp = [f_ref[2, p] for p in range(16)]
    dp = [f_ref[3, p] for p in range(16)]
    jac = [[jac_ref[k, p] for p in range(16)] for k in range(4)]
    energy = [
        (below_ref[p] + g_ref[p]) + 0.5 * (u[p] * u[p] + v[p] * v[p]) for p in range(16)
    ]
    e1 = first_rows(energy)
    e2 = second_rows(energy)
    it = [jac[0][p] * u[p] + jac[2][p] * v[p] for p in range(16)]
    lt = [jac[1][p] * u[p] + jac[3][p] * v[p] for p in range(16)]
    t1 = first_rows(temp)
    t2 = second_rows(temp)
    d1 = first_rows([dp[p] * it[p] for p in range(16)])
    d2 = second_rows([dp[p] * lt[p] for p in range(16)])
    advanced = []
    for p in range(16):
        rot = rot_ref[p]
        zonal_slope = jac[0][p] * e1[p] + jac[1][p] * e2[p]
        meridional_slope = jac[2][p] * e1[p] + jac[3][p] * e2[p]
        advanced.append(
            (
                u[p] + time_increment * (rot * v[p] - zonal_slope),
                v[p] - time_increment * (rot * u[p] + meridional_slope),
                temp[p] - time_increment * (it[p] * t1[p] + lt[p] * t2[p]),
                dp[p] - time_increment * (d1[p] + d2[p]),
            )
        )
    for f in range(4):
        rows = select_rows([advanced[p][f] for p in range(16)], rotation, forward_order)
        rows = column_fold([rows[q] * mc_ref[q] for q in range(16)], col)
        for q in range(16):
            out_ref[f, q] = rows[q]
        for b in range(3):
            last_ref[f, b] = lane_roll(rows[12 + b], COLS - elements)[:, :128]
            first_ref[f, b] = rows[b][:, :128]
    if with_mass:
        shape = last_ref.shape[2:]
        for b in range(3):
            last_ref[4, b] = jnp.broadcast_to(mlast_ref[b], shape)
            first_ref[4, b] = jnp.broadcast_to(mfirst_ref[b], shape)


def first_rows(rows):
    return [
        weighted_sum([(SLOPES[a, k], rows[4 * k + j]) for k in range(4)])
        for a in range(4)
        for j in range(4)
    ]


def second_rows(rows):
    return [
        weighted_sum([(SLOPES[a, k], rows[4 * i + k]) for k in range(4)])
        for i in range(4)
        for a in range(4)
    ]


def adv_call(fields, g0, below, jac, rot, mass_canon, info, elements, mass_edges=None):
    levels = fields.shape[2]
    steps = levels // CHUNK
    with_mass = mass_edges is not None
    width = 5 if with_mass else 4
    small = pl.BlockSpec((16, 1, LANES), lambda i: (0, 0, 0))
    edge = pl.BlockSpec((width, 3, CHUNK, 128), lambda i: (0, 0, i, 0))
    edge_shape = jax.ShapeDtypeStruct((width, 3, levels, 128), jnp.float32)
    in_specs = [
        pl.BlockSpec((4, 16, CHUNK, LANES), lambda i: (0, 0, i, 0)),
        pl.BlockSpec((16, CHUNK, LANES), lambda i: (0, i, 0)),
        small,
        pl.BlockSpec((4, 16, 1, LANES), lambda i: (0, 0, 0, 0)),
        small,
        small,
        pl.BlockSpec((8, LANES), lambda i: (0, 0)),
    ]
    args = [fields, g0, below, jac, rot, mass_canon, info]
    if with_mass:
        in_specs += [pl.BlockSpec((4, 1, 128), lambda i: (0, 0, 0))] * 2
        args += list(mass_edges)
    return pl.pallas_call(
        functools.partial(adv_kernel, elements, with_mass),
        interpret=INTERPRET,
        grid=(steps,),
        in_specs=in_specs,
        out_specs=[pl.BlockSpec((4, 16, CHUNK, LANES), lambda i: (0, 0, i, 0)), edge, edge],
        out_shape=[jax.ShapeDtypeStruct(fields.shape, jnp.float32), edge_shape, edge_shape],
    )(*args)


def fin_kernel(rows_dev, elements, with_cells, with_mass, *refs):
    refs = list(refs)
    w_ref, hu_ref, hd_ref = refs[:3]
    if with_mass:
        mw_ref = refs[3]
        refs = refs[4:]
    else:
        mt_ref = refs[3]
        refs = refs[4:]
    info_ref = refs.pop(0)
    if with_cells:
        prev_ref, m_ref = refs[:2]
        refs = refs[2:]
    out_ref, cm_ref = refs[:2]
    if with_cells:
        cell_ref = refs[2]
    info = info_ref[...]
    rotation = info[0:1]
    col = info[1:2]
    row = info[2:3]
    if with_mass:
        mass_total = row_fold(
            [mw_ref[q] for q in range(16)],
            [hu_ref[4, b][0:1] for b in range(3)],
            [hd_ref[4, b][0:1] for b in range(3)],
            row,
            col,
            rows_dev,
            elements,
        )
        lane_ok = lax.broadcasted_iota(jnp.int32, (1, LANES), 1) < elements
        mass_total = [jnp.where(lane_ok, m, 1.0) for m in mass_total]
        for q in range(16):
            refs[-1][q] = mass_total[q]
    else:
        mass_total = [mt_ref[q] for q in range(16)]
    lane = lax.broadcasted_iota(jnp.int32, (1, LANES), 1)
    valid = lane < elements
    _, backward_order = rotation_tables()
    groups = [(0, 1, 4, 5), (2, 3, 6, 7), (8, 9, 12, 13), (10, 11, 14, 15)]
    for f in range(4):
        out = row_fold(
            [w_ref[f, q] for q in range(16)],
            [hu_ref[f, b] for b in range(3)],
            [hd_ref[f, b] for b in range(3)],
            row,
            col,
            rows_dev,
            elements,
        )
        out = [out[q] / mass_total[q] for q in range(16)]
        new = select_rows(out, rotation, backward_order)
        new = [jnp.where(valid, new[p], 0.0) for p in range(16)]
        for p in range(16):
            out_ref[f, p] = new[p]
        if f == 3:
            for p in range(16):
                cm_ref[p] = jnp.sum(new[p], axis=0, keepdims=True)
        if with_cells:
            average = [(prev_ref[f, p] + new[p]) / SUBSTEPS for p in range(16)]
            for c, group in enumerate(groups):
                m = [m_ref[p] for p in group]
                summed = (m[0] * average[group[0]] + m[1] * average[group[1]]) + (
                    m[2] * average[group[2]] + m[3] * average[group[3]]
                )
                area = (m[0] + m[1]) + (m[2] + m[3])
                cell_ref[c, f] = summed / area


def fin_call(w, halo_up, halo_down, mass_parts, info, rows_dev, elements, prev=None, mass=None):
    levels = w.shape[2]
    steps = levels // CHUNK
    block = pl.BlockSpec((4, 16, CHUNK, LANES), lambda i: (0, 0, i, 0))
    halo = pl.BlockSpec((halo_up.shape[0], 3, CHUNK, 128), lambda i: (0, 0, i, 0))
    small = pl.BlockSpec((16, 1, LANES), lambda i: (0, 0, 0))
    with_cells = prev is not None
    with_mass = halo_up.shape[0] == 5
    in_specs = [block, halo, halo, small]
    args = [w, halo_up, halo_down, mass_parts]
    in_specs.append(pl.BlockSpec((8, LANES), lambda i: (0, 0)))
    args.append(info)
    out_specs = [block, pl.BlockSpec((None, 16, 1, LANES), lambda i: (i, 0, 0, 0))]
    out_shape = [
        jax.ShapeDtypeStruct(w.shape, jnp.float32),
        jax.ShapeDtypeStruct((steps, 16, 1, LANES), jnp.float32),
    ]
    if with_cells:
        in_specs += [block, small]
        args += [prev, mass]
        out_specs.append(pl.BlockSpec((4, 4, CHUNK, LANES), lambda i: (0, 0, i, 0)))
        out_shape.append(jax.ShapeDtypeStruct((4, 4, levels, LANES), jnp.float32))
    if with_mass:
        out_specs.append(small)
        out_shape.append(jax.ShapeDtypeStruct((16, 1, LANES), jnp.float32))
    return pl.pallas_call(
        functools.partial(fin_kernel, rows_dev, elements, with_cells, with_mass),
        interpret=INTERPRET,
        grid=(steps,),
        in_specs=in_specs,
        out_specs=out_specs,
        out_shape=out_shape,
    )(*args)


def edge_exchange(last, first):
    seg_count = lax.axis_size("seg")
    up = [(i, (i + 1) % seg_count) for i in range(seg_count)]
    down = [(j, i) for i, j in up]
    return lax.ppermute(last, "seg", up), lax.ppermute(first, "seg", down)


def halo_exchange(w, elements):
    seg_count = lax.axis_size("seg")
    up = [(i, (i + 1) % seg_count) for i in range(seg_count)]
    down = [(j, i) for i, j in up]
    last = w[..., 12:16, :, elements - COLS : elements]
    first = w[..., 0:4, :, 0:COLS]
    prev_last = lax.ppermute(last, "seg", up)
    next_first = lax.ppermute(first, "seg", down)
    widths = [(0, 0)] * (w.ndim - 1)
    halo_up = jnp.pad(prev_last, widths + [(0, LANES - COLS)])
    halo_down = jnp.pad(next_first, widths + [(elements - COLS, LANES - elements)])
    return halo_up, halo_down


def mass_dss(mass_canon_rows, info, rows_dev, elements):
    col = info[1:2]
    row = info[2:3]
    rows = list(mass_canon_rows)
    for a in range(4):
        edge = rows[4 * a + 3]
        left = jnp.where(col == 0, jnp.roll(edge, -(COLS - 1), -1), jnp.roll(edge, 1, -1))
        total = rows[4 * a] + left
        rows[4 * a] = total
        rows[4 * a + 3] = jnp.where(
            col == COLS - 1, jnp.roll(total, COLS - 1, -1), jnp.roll(total, -1, -1)
        )
    w = jnp.stack(rows)
    halo_up, halo_down = halo_exchange(w, elements)
    out = list(rows)
    for b in range(4):
        from_up = jnp.where(row == 0, halo_up[b], jnp.roll(rows[12 + b], COLS, -1))
        out[b] = rows[b] + from_up
        from_down = jnp.where(row == rows_dev - 1, halo_down[b], jnp.roll(rows[b], -COLS, -1))
        out[12 + b] = rows[12 + b] + from_down
    total = jnp.stack(out)
    lane = jnp.arange(LANES)
    return jnp.where(lane < elements, total, 1.0)


def prep_kernel(elements, vel_ref, temp_ref, dp_ref, out_ref, cm_ref):
    chunk = out_ref.shape[2]
    zeros = jnp.zeros((chunk, 128), jnp.float32)
    blocks = [vel_ref[0], vel_ref[1], temp_ref[...], dp_ref[...]]
    for f, block in enumerate(blocks):
        grouped = block.reshape(chunk, 16, elements)
        for p in range(16):
            rows = grouped[:, p, :]
            out_ref[f, p, :, pl.ds(LANES - 128, 128)] = zeros
            out_ref[f, p, :, pl.ds(0, elements)] = rows
            if f == 3:
                cm_ref[p, :, pl.ds(LANES - 128, 128)] = jnp.zeros((1, 128), jnp.float32)
                cm_ref[p, :, pl.ds(0, elements)] = jnp.sum(rows, axis=0, keepdims=True)


def prep_call(velocity_pair, thermal_reading, layer_depth):
    levels, points, elements = thermal_reading.shape
    steps = levels // CHUNK
    rows = CHUNK * points
    vel = velocity_pair.reshape(2, levels * points, elements)
    temp = thermal_reading.reshape(levels * points, elements)
    dp = layer_depth.reshape(levels * points, elements)
    return pl.pallas_call(
        functools.partial(prep_kernel, elements),
        interpret=INTERPRET,
        grid=(steps,),
        in_specs=[
            pl.BlockSpec((2, rows, elements), lambda i: (0, i, 0)),
            pl.BlockSpec((rows, elements), lambda i: (i, 0)),
            pl.BlockSpec((rows, elements), lambda i: (i, 0)),
        ],
        out_specs=[
            pl.BlockSpec((4, 16, CHUNK, LANES), lambda i: (0, 0, i, 0)),
            pl.BlockSpec((None, 16, 1, LANES), lambda i: (i, 0, 0, 0)),
        ],
        out_shape=[
            jax.ShapeDtypeStruct((4, 16, levels, LANES), jnp.float32),
            jax.ShapeDtypeStruct((steps, 16, 1, LANES), jnp.float32),
        ],
    )(vel, temp, dp)


def local(
    velocity_pair,
    thermal_reading,
    layer_depth,
    jacobian_terms,
    rotation_frequency,
    integration_mass,
    shared_vertex_label,
    column_owner_slot,
):
    levels_dev = thermal_reading.shape[0]
    elements = thermal_reading.shape[2]
    seg_count = lax.axis_size("seg")
    lev_count = lax.axis_size("lev")
    rows_dev = elements // COLS
    node_cols = 3 * COLS
    first_row = 3 * rows_dev * lax.axis_index("seg")
    grid_rows = 3 * rows_dev * seg_count
    corner_ids = shared_vertex_label[0]
    element_pos = jnp.arange(elements)
    row_offset = (corner_ids // node_cols - first_row) % grid_rows - 3 * (element_pos // COLS)
    col_offset = (corner_ids % node_cols - 3 * (element_pos % COLS)) % node_cols
    rotation = jnp.where(
        row_offset == 0, jnp.where(col_offset == 0, 0, 1), jnp.where(col_offset == 3, 2, 3)
    )
    info = lane_info(rotation, elements)
    forward_order, _ = rotation_tables()

    fields, column_parts = prep_call(velocity_pair, thermal_reading, layer_depth)
    (
        mass_canon,
        mass_folded,
        mass_last,
        mass_first,
        mass,
        mass_one,
        jac,
        rot,
    ) = mass_call(integration_mass, jacobian_terms, rotation_frequency, info)
    mass_parts = mass_folded
    mass_edges = (mass_last, mass_first)
    column_mass = jnp.sum(column_parts, axis=0)
    previous = None
    cells = None
    for substep in range(SUBSTEPS):
        above = carried_in(column_mass, "lev", False)
        g0, group_height = term_call(fields, above)
        below = carried_in(group_height, "lev", True)
        w, last, first = adv_call(
            fields, g0, below, jac, rot, mass_canon, info, elements, mass_edges
        )
        mass_edges = None
        halo_up, halo_down = edge_exchange(last, first)
        outs = fin_call(
            w,
            halo_up,
            halo_down,
            mass_parts,
            info,
            rows_dev,
            elements,
            previous if substep == SUBSTEPS - 1 else None,
            mass_one,
        )
        fields, column_parts = outs[:2]
        if substep == SUBSTEPS - 1:
            cells = outs[2]
        if substep == 0:
            mass_parts = outs[-1]
        previous = fields
        column_mass = jnp.sum(column_parts, axis=0)
    channels = 4 * levels_dev
    cell_values = cells[..., :elements].reshape(4, channels, elements)
    payload = jnp.transpose(cell_values, (0, 2, 1)).reshape(4 * elements, channels)
    dev_count = seg_count * lev_count
    own_cols = 4 * elements * seg_count // dev_count
    per_pair = own_cols // seg_count
    capacity = per_pair + per_pair // 2
    targets = column_owner_slot.reshape(-1)
    owner_index = targets // own_cols
    slot_index = targets % own_cols
    cell_count = targets.shape[0]
    cell_pos = jnp.arange(cell_count)
    same_owner = owner_index[:, None] == owner_index[None, :]
    earlier = cell_pos[:, None] < cell_pos[None, :]
    rank = jnp.sum(jnp.logical_and(same_owner, earlier).astype(jnp.int32), axis=0)
    destination = owner_index * capacity + rank
    slots = jnp.arange(dev_count * capacity)
    code = cell_pos * (own_cols + 1) + slot_index + 1
    match = destination[:, None] == slots[None, :]
    found = jnp.sum(jnp.where(match, code[:, None], 0), axis=0)
    has = found > 0
    source_cell = jnp.maximum(found - 1, 0) // (own_cols + 1)
    source_pos = jnp.maximum(found - 1, 0) % (own_cols + 1)
    outgoing = payload[source_cell].reshape(dev_count, capacity, channels)
    ids = jnp.where(has, source_pos, -1).reshape(dev_count, capacity)
    received_ids = lax.all_to_all(ids, ("seg", "lev"), split_axis=0, concat_axis=0, tiled=True)
    flat = jnp.arange(dev_count * capacity).reshape(dev_count, capacity)
    source_lev = (jnp.arange(dev_count) % lev_count)[:, None]
    positions = jnp.arange(own_cols)
    picks = []
    for group in range(lev_count):
        hit = jnp.logical_and(
            received_ids[:, :, None] == positions[None, None, :], (source_lev == group)[:, :, None]
        )
        picks.append(jnp.sum(jnp.where(hit, flat[:, :, None], 0), axis=(0, 1)))
    received = lax.all_to_all(outgoing, ("seg", "lev"), split_axis=0, concat_axis=0, tiled=True)
    arrived = received.reshape(dev_count * capacity, channels)[jnp.stack(picks)]
    arrived = arrived.reshape(lev_count, own_cols, 4, levels_dev).transpose(2, 0, 3, 1)
    phys_state = arrived.reshape(4, lev_count * levels_dev, own_cols)
    mean_thickness = jnp.mean(phys_state[3], axis=0)
    dyn_state = jnp.transpose(fields[..., :elements], (0, 2, 1, 3))
    return (dyn_state, phys_state, mean_thickness)


def solution(mesh):
    in_specs = (
        P(None, "lev", None, "seg"),
        P("lev", None, "seg"),
        P("lev", None, "seg"),
        P(None, None, "seg"),
        P(None, "seg"),
        P(None, "seg"),
        P(None, "seg"),
        P(None, "seg"),
    )
    out_specs = (P(None, "lev", None, "seg"), P(None, None, ("seg", "lev")), P(("seg", "lev")))
    return jax.shard_map(local, mesh=mesh, in_specs=in_specs, out_specs=out_specs, check_vma=False)
```

```python
import functools

import jax
import jax.numpy as jnp
import numpy as np
from jax import lax
from jax.experimental import pallas as pl
from jax.experimental.pallas import tpu as pltpu
from jax.sharding import PartitionSpec as P

COLS = 120
SUBSTEPS = 2


top_pressure = 10.0
time_increment = 0.05


def gll_slopes():
    root_five = np.sqrt(5.0)
    gll_nodes = [-1.0, -1.0 / root_five, 1.0 / root_five, 1.0]
    legendre_values = [-1.0, 1.0 / root_five, -1.0 / root_five, 1.0]
    slopes = np.zeros((4, 4))
    for row_node in range(4):
        for column in range(4):
            if row_node != column:
                slopes[row_node, column] = (
                    legendre_values[row_node]
                    / legendre_values[column]
                    / (gll_nodes[row_node] - gll_nodes[column])
                )
    slopes[0, 0] = -3.0
    slopes[3, 3] = 3.0
    return slopes


SLOPES = gll_slopes().astype(np.float32)


def rotation_tables():
    forward = np.zeros((4, 16), np.int32)
    for first_pos in range(4):
        for second_pos in range(4):
            canonical = 4 * first_pos + second_pos
            forward[0, canonical] = 4 * first_pos + second_pos
            forward[1, canonical] = 4 * (3 - second_pos) + first_pos
            forward[2, canonical] = 4 * (3 - first_pos) + (3 - second_pos)
            forward[3, canonical] = 4 * second_pos + 3 - first_pos
    backward = np.argsort(forward, axis=1).astype(np.int32)
    return (forward, backward)


def weighted_sum(terms):
    acc = None
    for coef, value in terms:
        if coef == 0.0:
            continue
        part = jnp.float32(coef) * value
        acc = part if acc is None else acc + part
    return acc


def first_deriv(f):
    return jnp.stack(
        [
            weighted_sum([(SLOPES[a, k], f[4 * k + j]) for k in range(4)])
            for a in range(4)
            for j in range(4)
        ]
    )


def second_deriv(f):
    return jnp.stack(
        [
            weighted_sum([(SLOPES[a, k], f[4 * i + k]) for k in range(4)])
            for i in range(4)
            for a in range(4)
        ]
    )


def carried_in(part, axis, reverse):
    count = lax.axis_size(axis)
    place = lax.axis_index(axis)
    gathered = lax.all_gather(part, axis)
    index = jnp.arange(count).reshape((count,) + (1,) * part.ndim)
    chosen = index > place if reverse else index < place
    return jnp.sum(jnp.where(chosen, gathered, jnp.zeros_like(gathered)), axis=0)


def site_potential_energy(thermal_reading, layer_depth):
    column_mass = jnp.sum(layer_depth, axis=1)
    above_sum = carried_in(column_mass, "lev", False)
    layer_midpoint_load = (
        top_pressure + above_sum[:, None, :] + jnp.cumsum(layer_depth, axis=1) - 0.5 * layer_depth
    )
    surface_change_rate = thermal_reading * layer_depth / layer_midpoint_load
    group_height = jnp.sum(surface_change_rate, axis=1)
    below_sum = carried_in(group_height, "lev", True)
    return (
        below_sum[:, None, :]
        + lax.cumsum(surface_change_rate, axis=1, reverse=True)
        - 0.5 * surface_change_rate
    )


def tendency_step(u, v, temp, dp, geopotential, jac, rot):
    energy = geopotential + 0.5 * (u * u + v * v)
    energy_first = first_deriv(energy)
    energy_second = second_deriv(energy)
    zonal_slope = jac[0] * energy_first + jac[1] * energy_second
    meridional_slope = jac[2] * energy_first + jac[3] * energy_second
    initial_transport = jac[0] * u + jac[2] * v
    latter_transport = jac[1] * u + jac[3] * v
    advect_with_motion = initial_transport * first_deriv(temp) + latter_transport * second_deriv(
        temp
    )
    distribute_onto_vertices = first_deriv(dp * initial_transport) + second_deriv(
        dp * latter_transport
    )
    return (
        u + time_increment * (rot * v - zonal_slope),
        v - time_increment * (rot * u + meridional_slope),
        temp - time_increment * advect_with_motion,
        dp - time_increment * distribute_onto_vertices,
    )


def reorder(values, rotation, table):
    rows = []
    for q in range(16):
        pick = values[int(table[3, q])]
        for w in (2, 1, 0):
            pick = jnp.where(rotation == w, values[int(table[w, q])], pick)
        rows.append(pick)
    return jnp.stack(rows)


def node_sum(canon, col, row, rows_dev):
    elements = canon.shape[-1]

    def roll(y, shift):
        return jnp.roll(y, shift, axis=-1)

    rows = [canon[q] for q in range(16)]
    for a in range(4):
        left = jnp.where(col == 0, roll(rows[4 * a + 3], -(COLS - 1)), roll(rows[4 * a + 3], 1))
        total = rows[4 * a] + left
        rows[4 * a] = total
        rows[4 * a + 3] = jnp.where(col == COLS - 1, roll(total, COLS - 1), roll(total, -1))
    seg_count = lax.axis_size("seg")
    up = [(i, (i + 1) % seg_count) for i in range(seg_count)]
    down = [(j, i) for i, j in up]
    last = jnp.stack([rows[12 + b][:, elements - COLS :] for b in range(4)])
    first = jnp.stack([rows[b][:, :COLS] for b in range(4)])
    prev_last = lax.ppermute(last, "seg", up)
    next_first = lax.ppermute(first, "seg", down)
    pad = jnp.zeros(prev_last.shape[1:-1] + (elements - COLS,), canon.dtype)
    out = list(rows)
    for b in range(4):
        halo_up = jnp.concatenate([prev_last[b], pad], axis=-1)
        from_up = jnp.where(row == 0, halo_up, roll(rows[12 + b], COLS))
        out[b] = rows[b] + from_up
        halo_down = jnp.concatenate([pad, next_first[b]], axis=-1)
        from_down = jnp.where(row == rows_dev - 1, halo_down, roll(rows[b], -COLS))
        out[12 + b] = rows[12 + b] + from_down
    return jnp.stack(out)


LANES = 512
CHUNK = 8
INTERPRET = None


def lane_info(rotation, elements):
    element_pos = jnp.arange(elements)
    info = jnp.stack(
        [rotation, element_pos % COLS, element_pos // COLS]
        + [jnp.zeros_like(rotation)] * 5
    ).astype(jnp.int32)
    return jnp.pad(info, ((0, 0), (0, LANES - elements)), constant_values=-1)


def pad_lanes(x, value=0.0):
    widths = [(0, 0)] * (x.ndim - 1) + [(0, LANES - x.shape[-1])]
    return jnp.pad(x, widths, constant_values=value)


def select_rows(values, rotation, table):
    rows = []
    for q in range(16):
        pick = values[int(table[3, q])]
        for w in (2, 1, 0):
            pick = jnp.where(rotation == w, values[int(table[w, q])], pick)
        rows.append(pick)
    return rows


def term_kernel(levels, f_ref, above_ref, g_ref, gh_ref):
    level = lax.broadcasted_iota(jnp.int32, (levels, LANES), 0)
    for p in range(f_ref.shape[1]):
        temp = f_ref[0, p]
        dp = f_ref[1, p]
        cum = dp
        shift = 1
        while shift < levels:
            cum = cum + jnp.where(level >= shift, pltpu.roll(cum, shift, 0), 0.0)
            shift *= 2
        load = top_pressure + above_ref[p] + cum - 0.5 * dp
        term = temp * dp / load
        gh_ref[p] = jnp.sum(term, axis=0, keepdims=True)
        rcum = term
        shift = 1
        while shift < levels:
            rcum = rcum + jnp.where(
                level + shift < levels, pltpu.roll(rcum, levels - shift, 0), 0.0
            )
            shift *= 2
        g_ref[p] = rcum - 0.5 * term


def term_call(fields, above):
    levels = fields.shape[2]
    group = 4
    return pl.pallas_call(
        functools.partial(term_kernel, levels),
        interpret=INTERPRET,
        grid=(16 // group,),
        in_specs=[
            pl.BlockSpec((2, group, levels, LANES), lambda i: (1, i, 0, 0)),
            pl.BlockSpec((group, 1, LANES), lambda i: (i, 0, 0)),
        ],
        out_specs=[
            pl.BlockSpec((group, levels, LANES), lambda i: (i, 0, 0)),
            pl.BlockSpec((group, 1, LANES), lambda i: (i, 0, 0)),
        ],
        out_shape=[
            jax.ShapeDtypeStruct((16, levels, LANES), jnp.float32),
            jax.ShapeDtypeStruct((16, 1, LANES), jnp.float32),
        ],
    )(fields, above)


def lane_roll(y, shift):
    return pltpu.roll(y, shift % LANES, 1)


def column_fold(rows, col):
    rows = list(rows)
    for a in range(4):
        edge = rows[4 * a + 3]
        left = jnp.where(col == 0, lane_roll(edge, -(COLS - 1)), lane_roll(edge, 1))
        total = rows[4 * a] + left
        rows[4 * a] = total
        rows[4 * a + 3] = jnp.where(
            col == COLS - 1, lane_roll(total, COLS - 1), lane_roll(total, -1)
        )
    return rows


def shift_right(y, col):
    return jnp.where(col == COLS - 1, lane_roll(y, COLS - 1), lane_roll(y, -1))


def row_fold(rows, up_rows, down_rows, row, col, rows_dev, elements):
    fill = jnp.zeros((rows[0].shape[0], LANES - 128), jnp.float32)
    halo_up = [jnp.concatenate([up_rows[b], fill], axis=1) for b in range(3)]
    halo_down = [
        lane_roll(jnp.concatenate([down_rows[b], fill], axis=1), elements - COLS) for b in range(3)
    ]
    halo_up.append(shift_right(halo_up[0], col))
    halo_down.append(shift_right(halo_down[0], col))
    out = list(rows)
    for b in range(4):
        from_up = jnp.where(row == 0, halo_up[b], lane_roll(rows[12 + b], COLS))
        out[b] = rows[b] + from_up
        from_down = jnp.where(row == rows_dev - 1, halo_down[b], lane_roll(rows[b], -COLS))
        out[12 + b] = rows[12 + b] + from_down
    return out


def mass_kernel(elements, m_ref, j_ref, r_ref, info_ref, mc_ref, mw_ref, last_ref, first_ref, mp_ref, mo_ref, jp_ref, rp_ref):
    info = info_ref[...]
    forward_order, _ = rotation_tables()
    zero = jnp.zeros((1, 128), jnp.float32)
    one = jnp.ones((1, 128), jnp.float32)
    for p in range(16):
        row = m_ref[pl.ds(p, 1), :]
        mp_ref[p, :, pl.ds(LANES - 128, 128)] = zero
        mp_ref[p, :, pl.ds(0, elements)] = row
        mo_ref[p, :, pl.ds(LANES - 128, 128)] = one
        mo_ref[p, :, pl.ds(0, elements)] = row
        rp_ref[p, :, pl.ds(LANES - 128, 128)] = zero
        rp_ref[p, :, pl.ds(0, elements)] = r_ref[pl.ds(p, 1), :]
        for k in range(4):
            jp_ref[k, p, :, pl.ds(LANES - 128, 128)] = zero
            jp_ref[k, p, :, pl.ds(0, elements)] = j_ref[k, pl.ds(p, 1), :]
    canon = select_rows([mp_ref[p] for p in range(16)], info[0:1], forward_order)
    rows = column_fold(canon, info[1:2])
    for q in range(16):
        mc_ref[q] = canon[q]
        mw_ref[q] = rows[q]
    for b in range(4):
        last_ref[b] = lane_roll(rows[12 + b], COLS - elements)[:, :128]
        first_ref[b] = rows[b][:, :128]


def mass_call(mass, jac, rot, info):
    elements = mass.shape[-1]
    small = jax.ShapeDtypeStruct((16, 1, LANES), jnp.float32)
    edge = jax.ShapeDtypeStruct((4, 1, 128), jnp.float32)
    return pl.pallas_call(
        functools.partial(mass_kernel, elements),
        interpret=INTERPRET,
        out_shape=[
            small,
            small,
            edge,
            edge,
            small,
            small,
            jax.ShapeDtypeStruct((4, 16, 1, LANES), jnp.float32),
            small,
        ],
    )(mass, jac, rot, info)


def adv_kernel(elements, with_mass, *refs):
    f_ref, g_ref, below_ref, jac_ref, rot_ref, mc_ref, info_ref = refs[:7]
    if with_mass:
        mlast_ref, mfirst_ref = refs[7:9]
    out_ref, last_ref, first_ref = refs[-3:]
    info = info_ref[...]
    rotation = info[0:1]
    col = info[1:2]
    forward_order, _ = rotation_tables()
    u = [f_ref[0, p] for p in range(16)]
    v = [f_ref[1, p] for p in range(16)]
    temp = [f_ref[2, p] for p in range(16)]
    dp = [f_ref[3, p] for p in range(16)]
    jac = [[jac_ref[k, p] for p in range(16)] for k in range(4)]
    energy = [
        (below_ref[p] + g_ref[p]) + 0.5 * (u[p] * u[p] + v[p] * v[p]) for p in range(16)
    ]
    e1 = first_rows(energy)
    e2 = second_rows(energy)
    it = [jac[0][p] * u[p] + jac[2][p] * v[p] for p in range(16)]
    lt = [jac[1][p] * u[p] + jac[3][p] * v[p] for p in range(16)]
    t1 = first_rows(temp)
    t2 = second_rows(temp)
    d1 = first_rows([dp[p] * it[p] for p in range(16)])
    d2 = second_rows([dp[p] * lt[p] for p in range(16)])
    advanced = []
    for p in range(16):
        rot = rot_ref[p]
        zonal_slope = jac[0][p] * e1[p] + jac[1][p] * e2[p]
        meridional_slope = jac[2][p] * e1[p] + jac[3][p] * e2[p]
        advanced.append(
            (
                u[p] + time_increment * (rot * v[p] - zonal_slope),
                v[p] - time_increment * (rot * u[p] + meridional_slope),
                temp[p] - time_increment * (it[p] * t1[p] + lt[p] * t2[p]),
                dp[p] - time_increment * (d1[p] + d2[p]),
            )
        )
    for f in range(4):
        rows = select_rows([advanced[p][f] for p in range(16)], rotation, forward_order)
        rows = column_fold([rows[q] * mc_ref[q] for q in range(16)], col)
        for q in range(16):
            out_ref[f, q] = rows[q]
        for b in range(3):
            last_ref[f, b] = lane_roll(rows[12 + b], COLS - elements)[:, :128]
            first_ref[f, b] = rows[b][:, :128]
    if with_mass:
        shape = last_ref.shape[2:]
        for b in range(3):
            last_ref[4, b] = jnp.broadcast_to(mlast_ref[b], shape)
            first_ref[4, b] = jnp.broadcast_to(mfirst_ref[b], shape)


def first_rows(rows):
    return [
        weighted_sum([(SLOPES[a, k], rows[4 * k + j]) for k in range(4)])
        for a in range(4)
        for j in range(4)
    ]


def second_rows(rows):
    return [
        weighted_sum([(SLOPES[a, k], rows[4 * i + k]) for k in range(4)])
        for i in range(4)
        for a in range(4)
    ]


def adv_call(fields, g0, below, jac, rot, mass_canon, info, elements, mass_edges=None):
    levels = fields.shape[2]
    steps = levels // CHUNK
    with_mass = mass_edges is not None
    width = 5 if with_mass else 4
    small = pl.BlockSpec((16, 1, LANES), lambda i: (0, 0, 0))
    edge = pl.BlockSpec((width, 3, CHUNK, 128), lambda i: (0, 0, i, 0))
    edge_shape = jax.ShapeDtypeStruct((width, 3, levels, 128), jnp.float32)
    in_specs = [
        pl.BlockSpec((4, 16, CHUNK, LANES), lambda i: (0, 0, i, 0)),
        pl.BlockSpec((16, CHUNK, LANES), lambda i: (0, i, 0)),
        small,
        pl.BlockSpec((4, 16, 1, LANES), lambda i: (0, 0, 0, 0)),
        small,
        small,
        pl.BlockSpec((8, LANES), lambda i: (0, 0)),
    ]
    args = [fields, g0, below, jac, rot, mass_canon, info]
    if with_mass:
        in_specs += [pl.BlockSpec((4, 1, 128), lambda i: (0, 0, 0))] * 2
        args += list(mass_edges)
    return pl.pallas_call(
        functools.partial(adv_kernel, elements, with_mass),
        interpret=INTERPRET,
        grid=(steps,),
        in_specs=in_specs,
        out_specs=[pl.BlockSpec((4, 16, CHUNK, LANES), lambda i: (0, 0, i, 0)), edge, edge],
        out_shape=[jax.ShapeDtypeStruct(fields.shape, jnp.float32), edge_shape, edge_shape],
    )(*args)


def fin_kernel(rows_dev, elements, with_cells, with_mass, *refs):
    refs = list(refs)
    w_ref, hu_ref, hd_ref = refs[:3]
    if with_mass:
        mw_ref = refs[3]
        refs = refs[4:]
    else:
        mt_ref = refs[3]
        refs = refs[4:]
    info_ref = refs.pop(0)
    if with_cells:
        prev_ref, m_ref = refs[:2]
        refs = refs[2:]
    out_ref, cm_ref = refs[:2]
    if with_cells:
        cell_ref = refs[2]
    info = info_ref[...]
    rotation = info[0:1]
    col = info[1:2]
    row = info[2:3]
    if with_mass:
        mass_total = row_fold(
            [mw_ref[q] for q in range(16)],
            [hu_ref[4, b][0:1] for b in range(3)],
            [hd_ref[4, b][0:1] for b in range(3)],
            row,
            col,
            rows_dev,
            elements,
        )
        lane_ok = lax.broadcasted_iota(jnp.int32, (1, LANES), 1) < elements
        mass_total = [jnp.where(lane_ok, m, 1.0) for m in mass_total]
        for q in range(16):
            refs[-1][q] = mass_total[q]
    else:
        mass_total = [mt_ref[q] for q in range(16)]
    lane = lax.broadcasted_iota(jnp.int32, (1, LANES), 1)
    valid = lane < elements
    _, backward_order = rotation_tables()
    groups = [(0, 1, 4, 5), (2, 3, 6, 7), (8, 9, 12, 13), (10, 11, 14, 15)]
    for f in range(4):
        out = row_fold(
            [w_ref[f, q] for q in range(16)],
            [hu_ref[f, b] for b in range(3)],
            [hd_ref[f, b] for b in range(3)],
            row,
            col,
            rows_dev,
            elements,
        )
        out = [out[q] / mass_total[q] for q in range(16)]
        new = select_rows(out, rotation, backward_order)
        new = [jnp.where(valid, new[p], 0.0) for p in range(16)]
        for p in range(16):
            out_ref[f, p] = new[p]
        if f == 3:
            for p in range(16):
                part = jnp.sum(new[p], axis=0, keepdims=True)

                @pl.when(pl.program_id(0) == 0)
                def _():
                    cm_ref[p] = part

                @pl.when(pl.program_id(0) > 0)
                def _():
                    cm_ref[p] = cm_ref[p] + part
        if with_cells:
            average = [(prev_ref[f, p] + new[p]) / SUBSTEPS for p in range(16)]
            for c, group in enumerate(groups):
                m = [m_ref[p] for p in group]
                summed = (m[0] * average[group[0]] + m[1] * average[group[1]]) + (
                    m[2] * average[group[2]] + m[3] * average[group[3]]
                )
                area = (m[0] + m[1]) + (m[2] + m[3])
                cell_ref[c, f] = summed / area


def fin_call(w, halo_up, halo_down, mass_parts, info, rows_dev, elements, prev=None, mass=None):
    levels = w.shape[2]
    steps = levels // CHUNK
    block = pl.BlockSpec((4, 16, CHUNK, LANES), lambda i: (0, 0, i, 0))
    halo = pl.BlockSpec((halo_up.shape[0], 3, CHUNK, 128), lambda i: (0, 0, i, 0))
    small = pl.BlockSpec((16, 1, LANES), lambda i: (0, 0, 0))
    with_cells = prev is not None
    with_mass = halo_up.shape[0] == 5
    in_specs = [block, halo, halo, small]
    args = [w, halo_up, halo_down, mass_parts]
    in_specs.append(pl.BlockSpec((8, LANES), lambda i: (0, 0)))
    args.append(info)
    out_specs = [block, small]
    out_shape = [
        jax.ShapeDtypeStruct(w.shape, jnp.float32),
        jax.ShapeDtypeStruct((16, 1, LANES), jnp.float32),
    ]
    if with_cells:
        in_specs += [block, small]
        args += [prev, mass]
        out_specs.append(pl.BlockSpec((4, 4, CHUNK, LANES), lambda i: (0, 0, i, 0)))
        out_shape.append(jax.ShapeDtypeStruct((4, 4, levels, LANES), jnp.float32))
    if with_mass:
        out_specs.append(small)
        out_shape.append(jax.ShapeDtypeStruct((16, 1, LANES), jnp.float32))
    return pl.pallas_call(
        functools.partial(fin_kernel, rows_dev, elements, with_cells, with_mass),
        interpret=INTERPRET,
        grid=(steps,),
        in_specs=in_specs,
        out_specs=out_specs,
        out_shape=out_shape,
    )(*args)


def edge_exchange(last, first):
    seg_count = lax.axis_size("seg")
    up = [(i, (i + 1) % seg_count) for i in range(seg_count)]
    down = [(j, i) for i, j in up]
    return lax.ppermute(last, "seg", up), lax.ppermute(first, "seg", down)


def halo_exchange(w, elements):
    seg_count = lax.axis_size("seg")
    up = [(i, (i + 1) % seg_count) for i in range(seg_count)]
    down = [(j, i) for i, j in up]
    last = w[..., 12:16, :, elements - COLS : elements]
    first = w[..., 0:4, :, 0:COLS]
    prev_last = lax.ppermute(last, "seg", up)
    next_first = lax.ppermute(first, "seg", down)
    widths = [(0, 0)] * (w.ndim - 1)
    halo_up = jnp.pad(prev_last, widths + [(0, LANES - COLS)])
    halo_down = jnp.pad(next_first, widths + [(elements - COLS, LANES - elements)])
    return halo_up, halo_down


def mass_dss(mass_canon_rows, info, rows_dev, elements):
    col = info[1:2]
    row = info[2:3]
    rows = list(mass_canon_rows)
    for a in range(4):
        edge = rows[4 * a + 3]
        left = jnp.where(col == 0, jnp.roll(edge, -(COLS - 1), -1), jnp.roll(edge, 1, -1))
        total = rows[4 * a] + left
        rows[4 * a] = total
        rows[4 * a + 3] = jnp.where(
            col == COLS - 1, jnp.roll(total, COLS - 1, -1), jnp.roll(total, -1, -1)
        )
    w = jnp.stack(rows)
    halo_up, halo_down = halo_exchange(w, elements)
    out = list(rows)
    for b in range(4):
        from_up = jnp.where(row == 0, halo_up[b], jnp.roll(rows[12 + b], COLS, -1))
        out[b] = rows[b] + from_up
        from_down = jnp.where(row == rows_dev - 1, halo_down[b], jnp.roll(rows[b], -COLS, -1))
        out[12 + b] = rows[12 + b] + from_down
    total = jnp.stack(out)
    lane = jnp.arange(LANES)
    return jnp.where(lane < elements, total, 1.0)


def prep_kernel(elements, vel_ref, temp_ref, dp_ref, out_ref, cm_ref):
    chunk = out_ref.shape[2]
    zeros = jnp.zeros((chunk, 128), jnp.float32)
    blocks = [vel_ref[0], vel_ref[1], temp_ref[...], dp_ref[...]]
    for f, block in enumerate(blocks):
        grouped = block.reshape(chunk, 16, elements)
        for p in range(16):
            rows = grouped[:, p, :]
            out_ref[f, p, :, pl.ds(LANES - 128, 128)] = zeros
            out_ref[f, p, :, pl.ds(0, elements)] = rows
            if f == 3:
                part = jnp.sum(out_ref[f, p], axis=0, keepdims=True)

                @pl.when(pl.program_id(0) == 0)
                def _():
                    cm_ref[p] = part

                @pl.when(pl.program_id(0) > 0)
                def _():
                    cm_ref[p] = cm_ref[p] + part


def prep_call(velocity_pair, thermal_reading, layer_depth):
    levels, points, elements = thermal_reading.shape
    steps = levels // CHUNK
    rows = CHUNK * points
    vel = velocity_pair.reshape(2, levels * points, elements)
    temp = thermal_reading.reshape(levels * points, elements)
    dp = layer_depth.reshape(levels * points, elements)
    return pl.pallas_call(
        functools.partial(prep_kernel, elements),
        interpret=INTERPRET,
        grid=(steps,),
        in_specs=[
            pl.BlockSpec((2, rows, elements), lambda i: (0, i, 0)),
            pl.BlockSpec((rows, elements), lambda i: (i, 0)),
            pl.BlockSpec((rows, elements), lambda i: (i, 0)),
        ],
        out_specs=[
            pl.BlockSpec((4, 16, CHUNK, LANES), lambda i: (0, 0, i, 0)),
            pl.BlockSpec((16, 1, LANES), lambda i: (0, 0, 0)),
        ],
        out_shape=[
            jax.ShapeDtypeStruct((4, 16, levels, LANES), jnp.float32),
            jax.ShapeDtypeStruct((16, 1, LANES), jnp.float32),
        ],
    )(vel, temp, dp)


def local(
    velocity_pair,
    thermal_reading,
    layer_depth,
    jacobian_terms,
    rotation_frequency,
    integration_mass,
    shared_vertex_label,
    column_owner_slot,
):
    levels_dev = thermal_reading.shape[0]
    elements = thermal_reading.shape[2]
    seg_count = lax.axis_size("seg")
    lev_count = lax.axis_size("lev")
    rows_dev = elements // COLS
    node_cols = 3 * COLS
    first_row = 3 * rows_dev * lax.axis_index("seg")
    grid_rows = 3 * rows_dev * seg_count
    corner_ids = shared_vertex_label[0]
    element_pos = jnp.arange(elements)
    row_offset = (corner_ids // node_cols - first_row) % grid_rows - 3 * (element_pos // COLS)
    col_offset = (corner_ids % node_cols - 3 * (element_pos % COLS)) % node_cols
    rotation = jnp.where(
        row_offset == 0, jnp.where(col_offset == 0, 0, 1), jnp.where(col_offset == 3, 2, 3)
    )
    info = lane_info(rotation, elements)
    forward_order, _ = rotation_tables()

    fields, column_parts = prep_call(velocity_pair, thermal_reading, layer_depth)
    (
        mass_canon,
        mass_folded,
        mass_last,
        mass_first,
        mass,
        mass_one,
        jac,
        rot,
    ) = mass_call(integration_mass, jacobian_terms, rotation_frequency, info)
    mass_parts = mass_folded
    mass_edges = (mass_last, mass_first)
    column_mass = column_parts
    previous = None
    cells = None
    for substep in range(SUBSTEPS):
        above = carried_in(column_mass, "lev", False)
        g0, group_height = term_call(fields, above)
        below = carried_in(group_height, "lev", True)
        w, last, first = adv_call(
            fields, g0, below, jac, rot, mass_canon, info, elements, mass_edges
        )
        mass_edges = None
        halo_up, halo_down = edge_exchange(last, first)
        outs = fin_call(
            w,
            halo_up,
            halo_down,
            mass_parts,
            info,
            rows_dev,
            elements,
            previous if substep == SUBSTEPS - 1 else None,
            mass_one,
        )
        fields, column_parts = outs[:2]
        if substep == SUBSTEPS - 1:
            cells = outs[2]
        if substep == 0:
            mass_parts = outs[-1]
        previous = fields
        column_mass = column_parts
    channels = 4 * levels_dev
    cell_values = cells[..., :elements].reshape(4, channels, elements)
    payload = jnp.transpose(cell_values, (0, 2, 1)).reshape(4 * elements, channels)
    dev_count = seg_count * lev_count
    own_cols = 4 * elements * seg_count // dev_count
    per_pair = own_cols // seg_count
    capacity = per_pair + per_pair // 2
    targets = column_owner_slot.reshape(-1)
    owner_index = targets // own_cols
    slot_index = targets % own_cols
    cell_count = targets.shape[0]
    cell_pos = jnp.arange(cell_count)
    same_owner = owner_index[:, None] == owner_index[None, :]
    earlier = cell_pos[:, None] < cell_pos[None, :]
    rank = jnp.sum(jnp.logical_and(same_owner, earlier).astype(jnp.int32), axis=0)
    destination = owner_index * capacity + rank
    slots = jnp.arange(dev_count * capacity)
    code = cell_pos * (own_cols + 1) + slot_index + 1
    match = destination[:, None] == slots[None, :]
    found = jnp.sum(jnp.where(match, code[:, None], 0), axis=0)
    has = found > 0
    source_cell = jnp.maximum(found - 1, 0) // (own_cols + 1)
    source_pos = jnp.maximum(found - 1, 0) % (own_cols + 1)
    outgoing = payload[source_cell].reshape(dev_count, capacity, channels)
    ids = jnp.where(has, source_pos, -1).reshape(dev_count, capacity)
    received_ids = lax.all_to_all(ids, ("seg", "lev"), split_axis=0, concat_axis=0, tiled=True)
    flat = jnp.arange(dev_count * capacity).reshape(dev_count, capacity)
    source_lev = (jnp.arange(dev_count) % lev_count)[:, None]
    positions = jnp.arange(own_cols)
    picks = []
    for group in range(lev_count):
        hit = jnp.logical_and(
            received_ids[:, :, None] == positions[None, None, :], (source_lev == group)[:, :, None]
        )
        picks.append(jnp.sum(jnp.where(hit, flat[:, :, None], 0), axis=(0, 1)))
    received = lax.all_to_all(outgoing, ("seg", "lev"), split_axis=0, concat_axis=0, tiled=True)
    arrived = received.reshape(dev_count * capacity, channels)[jnp.stack(picks)]
    arrived = arrived.reshape(lev_count, own_cols, 4, levels_dev).transpose(2, 0, 3, 1)
    phys_state = arrived.reshape(4, lev_count * levels_dev, own_cols)
    mean_thickness = jnp.mean(phys_state[3], axis=0)
    dyn_state = jnp.transpose(fields[..., :elements], (0, 2, 1, 3))
    return (dyn_state, phys_state, mean_thickness)


def solution(mesh):
    in_specs = (
        P(None, "lev", None, "seg"),
        P("lev", None, "seg"),
        P("lev", None, "seg"),
        P(None, None, "seg"),
        P(None, "seg"),
        P(None, "seg"),
        P(None, "seg"),
        P(None, "seg"),
    )
    out_specs = (P(None, "lev", None, "seg"), P(None, None, ("seg", "lev")), P(("seg", "lev")))
    return jax.shard_map(local, mesh=mesh, in_specs=in_specs, out_specs=out_specs, check_vma=False)
```

```python
import functools

import jax
import jax.numpy as jnp
import numpy as np
from jax import lax
from jax.experimental import pallas as pl
from jax.experimental.pallas import tpu as pltpu
from jax.sharding import PartitionSpec as P

COLS = 120
SUBSTEPS = 2


top_pressure = 10.0
time_increment = 0.05


def gll_slopes():
    root_five = np.sqrt(5.0)
    gll_nodes = [-1.0, -1.0 / root_five, 1.0 / root_five, 1.0]
    legendre_values = [-1.0, 1.0 / root_five, -1.0 / root_five, 1.0]
    slopes = np.zeros((4, 4))
    for row_node in range(4):
        for column in range(4):
            if row_node != column:
                slopes[row_node, column] = (
                    legendre_values[row_node]
                    / legendre_values[column]
                    / (gll_nodes[row_node] - gll_nodes[column])
                )
    slopes[0, 0] = -3.0
    slopes[3, 3] = 3.0
    return slopes


SLOPES = gll_slopes().astype(np.float32)


def rotation_tables():
    forward = np.zeros((4, 16), np.int32)
    for first_pos in range(4):
        for second_pos in range(4):
            canonical = 4 * first_pos + second_pos
            forward[0, canonical] = 4 * first_pos + second_pos
            forward[1, canonical] = 4 * (3 - second_pos) + first_pos
            forward[2, canonical] = 4 * (3 - first_pos) + (3 - second_pos)
            forward[3, canonical] = 4 * second_pos + 3 - first_pos
    backward = np.argsort(forward, axis=1).astype(np.int32)
    return (forward, backward)


def weighted_sum(terms):
    acc = None
    for coef, value in terms:
        if coef == 0.0:
            continue
        part = jnp.float32(coef) * value
        acc = part if acc is None else acc + part
    return acc


def first_deriv(f):
    return jnp.stack(
        [
            weighted_sum([(SLOPES[a, k], f[4 * k + j]) for k in range(4)])
            for a in range(4)
            for j in range(4)
        ]
    )


def second_deriv(f):
    return jnp.stack(
        [
            weighted_sum([(SLOPES[a, k], f[4 * i + k]) for k in range(4)])
            for i in range(4)
            for a in range(4)
        ]
    )


def carried_in(part, axis, reverse):
    count = lax.axis_size(axis)
    place = lax.axis_index(axis)
    gathered = lax.all_gather(part, axis)
    index = jnp.arange(count).reshape((count,) + (1,) * part.ndim)
    chosen = index > place if reverse else index < place
    return jnp.sum(jnp.where(chosen, gathered, jnp.zeros_like(gathered)), axis=0)


def site_potential_energy(thermal_reading, layer_depth):
    column_mass = jnp.sum(layer_depth, axis=1)
    above_sum = carried_in(column_mass, "lev", False)
    layer_midpoint_load = (
        top_pressure + above_sum[:, None, :] + jnp.cumsum(layer_depth, axis=1) - 0.5 * layer_depth
    )
    surface_change_rate = thermal_reading * layer_depth / layer_midpoint_load
    group_height = jnp.sum(surface_change_rate, axis=1)
    below_sum = carried_in(group_height, "lev", True)
    return (
        below_sum[:, None, :]
        + lax.cumsum(surface_change_rate, axis=1, reverse=True)
        - 0.5 * surface_change_rate
    )


def tendency_step(u, v, temp, dp, geopotential, jac, rot):
    energy = geopotential + 0.5 * (u * u + v * v)
    energy_first = first_deriv(energy)
    energy_second = second_deriv(energy)
    zonal_slope = jac[0] * energy_first + jac[1] * energy_second
    meridional_slope = jac[2] * energy_first + jac[3] * energy_second
    initial_transport = jac[0] * u + jac[2] * v
    latter_transport = jac[1] * u + jac[3] * v
    advect_with_motion = initial_transport * first_deriv(temp) + latter_transport * second_deriv(
        temp
    )
    distribute_onto_vertices = first_deriv(dp * initial_transport) + second_deriv(
        dp * latter_transport
    )
    return (
        u + time_increment * (rot * v - zonal_slope),
        v - time_increment * (rot * u + meridional_slope),
        temp - time_increment * advect_with_motion,
        dp - time_increment * distribute_onto_vertices,
    )


def reorder(values, rotation, table):
    rows = []
    for q in range(16):
        pick = values[int(table[3, q])]
        for w in (2, 1, 0):
            pick = jnp.where(rotation == w, values[int(table[w, q])], pick)
        rows.append(pick)
    return jnp.stack(rows)


def node_sum(canon, col, row, rows_dev):
    elements = canon.shape[-1]

    def roll(y, shift):
        return jnp.roll(y, shift, axis=-1)

    rows = [canon[q] for q in range(16)]
    for a in range(4):
        left = jnp.where(col == 0, roll(rows[4 * a + 3], -(COLS - 1)), roll(rows[4 * a + 3], 1))
        total = rows[4 * a] + left
        rows[4 * a] = total
        rows[4 * a + 3] = jnp.where(col == COLS - 1, roll(total, COLS - 1), roll(total, -1))
    seg_count = lax.axis_size("seg")
    up = [(i, (i + 1) % seg_count) for i in range(seg_count)]
    down = [(j, i) for i, j in up]
    last = jnp.stack([rows[12 + b][:, elements - COLS :] for b in range(4)])
    first = jnp.stack([rows[b][:, :COLS] for b in range(4)])
    prev_last = lax.ppermute(last, "seg", up)
    next_first = lax.ppermute(first, "seg", down)
    pad = jnp.zeros(prev_last.shape[1:-1] + (elements - COLS,), canon.dtype)
    out = list(rows)
    for b in range(4):
        halo_up = jnp.concatenate([prev_last[b], pad], axis=-1)
        from_up = jnp.where(row == 0, halo_up, roll(rows[12 + b], COLS))
        out[b] = rows[b] + from_up
        halo_down = jnp.concatenate([pad, next_first[b]], axis=-1)
        from_down = jnp.where(row == rows_dev - 1, halo_down, roll(rows[b], -COLS))
        out[12 + b] = rows[12 + b] + from_down
    return jnp.stack(out)


LANES = 512
CHUNK = 16
INTERPRET = None


def lane_info(rotation, elements):
    element_pos = jnp.arange(elements)
    info = jnp.stack(
        [rotation, element_pos % COLS, element_pos // COLS]
        + [jnp.zeros_like(rotation)] * 5
    ).astype(jnp.int32)
    return jnp.pad(info, ((0, 0), (0, LANES - elements)), constant_values=-1)


def pad_lanes(x, value=0.0):
    widths = [(0, 0)] * (x.ndim - 1) + [(0, LANES - x.shape[-1])]
    return jnp.pad(x, widths, constant_values=value)


def select_rows(values, rotation, table):
    rows = []
    for q in range(16):
        pick = values[int(table[3, q])]
        for w in (2, 1, 0):
            pick = jnp.where(rotation == w, values[int(table[w, q])], pick)
        rows.append(pick)
    return rows


def term_kernel(levels, f_ref, above_ref, g_ref, gh_ref):
    level = lax.broadcasted_iota(jnp.int32, (levels, LANES), 0)
    for p in range(f_ref.shape[1]):
        temp = f_ref[0, p]
        dp = f_ref[1, p]
        cum = dp
        shift = 1
        while shift < levels:
            cum = cum + jnp.where(level >= shift, pltpu.roll(cum, shift, 0), 0.0)
            shift *= 2
        load = top_pressure + above_ref[p] + cum - 0.5 * dp
        term = temp * dp / load
        gh_ref[p] = jnp.sum(term, axis=0, keepdims=True)
        rcum = term
        shift = 1
        while shift < levels:
            rcum = rcum + jnp.where(
                level + shift < levels, pltpu.roll(rcum, levels - shift, 0), 0.0
            )
            shift *= 2
        g_ref[p] = rcum - 0.5 * term


def term_call(fields, above):
    levels = fields.shape[2]
    group = 4
    return pl.pallas_call(
        functools.partial(term_kernel, levels),
        interpret=INTERPRET,
        grid=(16 // group,),
        in_specs=[
            pl.BlockSpec((2, group, levels, LANES), lambda i: (1, i, 0, 0)),
            pl.BlockSpec((group, 1, LANES), lambda i: (i, 0, 0)),
        ],
        out_specs=[
            pl.BlockSpec((group, levels, LANES), lambda i: (i, 0, 0)),
            pl.BlockSpec((group, 1, LANES), lambda i: (i, 0, 0)),
        ],
        out_shape=[
            jax.ShapeDtypeStruct((16, levels, LANES), jnp.float32),
            jax.ShapeDtypeStruct((16, 1, LANES), jnp.float32),
        ],
    )(fields, above)


def lane_roll(y, shift):
    return pltpu.roll(y, shift % LANES, 1)


def column_fold(rows, col):
    rows = list(rows)
    for a in range(4):
        edge = rows[4 * a + 3]
        left = jnp.where(col == 0, lane_roll(edge, -(COLS - 1)), lane_roll(edge, 1))
        total = rows[4 * a] + left
        rows[4 * a] = total
        rows[4 * a + 3] = jnp.where(
            col == COLS - 1, lane_roll(total, COLS - 1), lane_roll(total, -1)
        )
    return rows


def shift_right(y, col):
    return jnp.where(col == COLS - 1, lane_roll(y, COLS - 1), lane_roll(y, -1))


def row_fold(rows, up_rows, down_rows, row, col, rows_dev, elements):
    fill = jnp.zeros((rows[0].shape[0], LANES - 128), jnp.float32)
    halo_up = [jnp.concatenate([up_rows[b], fill], axis=1) for b in range(3)]
    halo_down = [
        lane_roll(jnp.concatenate([down_rows[b], fill], axis=1), elements - COLS) for b in range(3)
    ]
    halo_up.append(shift_right(halo_up[0], col))
    halo_down.append(shift_right(halo_down[0], col))
    out = list(rows)
    for b in range(4):
        from_up = jnp.where(row == 0, halo_up[b], lane_roll(rows[12 + b], COLS))
        out[b] = rows[b] + from_up
        from_down = jnp.where(row == rows_dev - 1, halo_down[b], lane_roll(rows[b], -COLS))
        out[12 + b] = rows[12 + b] + from_down
    return out


def mass_kernel(elements, m_ref, j_ref, r_ref, info_ref, mc_ref, mw_ref, last_ref, first_ref, mp_ref, mo_ref, jp_ref, rp_ref):
    info = info_ref[...]
    forward_order, _ = rotation_tables()
    zero = jnp.zeros((1, 128), jnp.float32)
    one = jnp.ones((1, 128), jnp.float32)
    for p in range(16):
        row = m_ref[pl.ds(p, 1), :]
        mp_ref[p, :, pl.ds(LANES - 128, 128)] = zero
        mp_ref[p, :, pl.ds(0, elements)] = row
        mo_ref[p, :, pl.ds(LANES - 128, 128)] = one
        mo_ref[p, :, pl.ds(0, elements)] = row
        rp_ref[p, :, pl.ds(LANES - 128, 128)] = zero
        rp_ref[p, :, pl.ds(0, elements)] = r_ref[pl.ds(p, 1), :]
        for k in range(4):
            jp_ref[k, p, :, pl.ds(LANES - 128, 128)] = zero
            jp_ref[k, p, :, pl.ds(0, elements)] = j_ref[k, pl.ds(p, 1), :]
    canon = select_rows([mp_ref[p] for p in range(16)], info[0:1], forward_order)
    rows = column_fold(canon, info[1:2])
    for q in range(16):
        mc_ref[q] = canon[q]
        mw_ref[q] = rows[q]
    for b in range(4):
        last_ref[b] = lane_roll(rows[12 + b], COLS - elements)[:, :128]
        first_ref[b] = rows[b][:, :128]


def mass_call(mass, jac, rot, info):
    elements = mass.shape[-1]
    small = jax.ShapeDtypeStruct((16, 1, LANES), jnp.float32)
    edge = jax.ShapeDtypeStruct((4, 1, 128), jnp.float32)
    return pl.pallas_call(
        functools.partial(mass_kernel, elements),
        interpret=INTERPRET,
        out_shape=[
            small,
            small,
            edge,
            edge,
            small,
            small,
            jax.ShapeDtypeStruct((4, 16, 1, LANES), jnp.float32),
            small,
        ],
    )(mass, jac, rot, info)


def adv_kernel(elements, with_mass, *refs):
    f_ref, g_ref, below_ref, jac_ref, rot_ref, mc_ref, info_ref = refs[:7]
    if with_mass:
        mlast_ref, mfirst_ref = refs[7:9]
    out_ref, last_ref, first_ref = refs[-3:]
    info = info_ref[...]
    rotation = info[0:1]
    col = info[1:2]
    forward_order, _ = rotation_tables()
    u = [f_ref[0, p] for p in range(16)]
    v = [f_ref[1, p] for p in range(16)]
    temp = [f_ref[2, p] for p in range(16)]
    dp = [f_ref[3, p] for p in range(16)]
    jac = [[jac_ref[k, p] for p in range(16)] for k in range(4)]
    energy = [
        (below_ref[p] + g_ref[p]) + 0.5 * (u[p] * u[p] + v[p] * v[p]) for p in range(16)
    ]
    e1 = first_rows(energy)
    e2 = second_rows(energy)
    it = [jac[0][p] * u[p] + jac[2][p] * v[p] for p in range(16)]
    lt = [jac[1][p] * u[p] + jac[3][p] * v[p] for p in range(16)]
    t1 = first_rows(temp)
    t2 = second_rows(temp)
    d1 = first_rows([dp[p] * it[p] for p in range(16)])
    d2 = second_rows([dp[p] * lt[p] for p in range(16)])
    advanced = []
    for p in range(16):
        rot = rot_ref[p]
        zonal_slope = jac[0][p] * e1[p] + jac[1][p] * e2[p]
        meridional_slope = jac[2][p] * e1[p] + jac[3][p] * e2[p]
        advanced.append(
            (
                u[p] + time_increment * (rot * v[p] - zonal_slope),
                v[p] - time_increment * (rot * u[p] + meridional_slope),
                temp[p] - time_increment * (it[p] * t1[p] + lt[p] * t2[p]),
                dp[p] - time_increment * (d1[p] + d2[p]),
            )
        )
    for f in range(4):
        rows = select_rows([advanced[p][f] for p in range(16)], rotation, forward_order)
        rows = column_fold([rows[q] * mc_ref[q] for q in range(16)], col)
        for q in range(16):
            out_ref[f, q] = rows[q]
        for b in range(3):
            last_ref[f, b] = lane_roll(rows[12 + b], COLS - elements)[:, :128]
            first_ref[f, b] = rows[b][:, :128]
    if with_mass:
        shape = last_ref.shape[2:]
        for b in range(3):
            last_ref[4, b] = jnp.broadcast_to(mlast_ref[b], shape)
            first_ref[4, b] = jnp.broadcast_to(mfirst_ref[b], shape)


def first_rows(rows):
    return [
        weighted_sum([(SLOPES[a, k], rows[4 * k + j]) for k in range(4)])
        for a in range(4)
        for j in range(4)
    ]


def second_rows(rows):
    return [
        weighted_sum([(SLOPES[a, k], rows[4 * i + k]) for k in range(4)])
        for i in range(4)
        for a in range(4)
    ]


def adv_call(fields, g0, below, jac, rot, mass_canon, info, elements, mass_edges=None):
    levels = fields.shape[2]
    steps = levels // CHUNK
    with_mass = mass_edges is not None
    width = 5 if with_mass else 4
    small = pl.BlockSpec((16, 1, LANES), lambda i: (0, 0, 0))
    edge = pl.BlockSpec((width, 3, CHUNK, 128), lambda i: (0, 0, i, 0))
    edge_shape = jax.ShapeDtypeStruct((width, 3, levels, 128), jnp.float32)
    in_specs = [
        pl.BlockSpec((4, 16, CHUNK, LANES), lambda i: (0, 0, i, 0)),
        pl.BlockSpec((16, CHUNK, LANES), lambda i: (0, i, 0)),
        small,
        pl.BlockSpec((4, 16, 1, LANES), lambda i: (0, 0, 0, 0)),
        small,
        small,
        pl.BlockSpec((8, LANES), lambda i: (0, 0)),
    ]
    args = [fields, g0, below, jac, rot, mass_canon, info]
    if with_mass:
        in_specs += [pl.BlockSpec((4, 1, 128), lambda i: (0, 0, 0))] * 2
        args += list(mass_edges)
    return pl.pallas_call(
        functools.partial(adv_kernel, elements, with_mass),
        interpret=INTERPRET,
        grid=(steps,),
        in_specs=in_specs,
        out_specs=[pl.BlockSpec((4, 16, CHUNK, LANES), lambda i: (0, 0, i, 0)), edge, edge],
        out_shape=[jax.ShapeDtypeStruct(fields.shape, jnp.float32), edge_shape, edge_shape],
    )(*args)


def fin_kernel(rows_dev, elements, with_cells, with_mass, *refs):
    refs = list(refs)
    w_ref, hu_ref, hd_ref = refs[:3]
    if with_mass:
        mw_ref = refs[3]
        refs = refs[4:]
    else:
        mt_ref = refs[3]
        refs = refs[4:]
    info_ref = refs.pop(0)
    if with_cells:
        prev_ref, m_ref = refs[:2]
        refs = refs[2:]
    out_ref, cm_ref = refs[:2]
    if with_cells:
        cell_ref = refs[2]
    info = info_ref[...]
    rotation = info[0:1]
    col = info[1:2]
    row = info[2:3]
    if with_mass:
        mass_total = row_fold(
            [mw_ref[q] for q in range(16)],
            [hu_ref[4, b][0:1] for b in range(3)],
            [hd_ref[4, b][0:1] for b in range(3)],
            row,
            col,
            rows_dev,
            elements,
        )
        lane_ok = lax.broadcasted_iota(jnp.int32, (1, LANES), 1) < elements
        mass_total = [jnp.where(lane_ok, m, 1.0) for m in mass_total]
        for q in range(16):
            refs[-1][q] = mass_total[q]
    else:
        mass_total = [mt_ref[q] for q in range(16)]
    lane = lax.broadcasted_iota(jnp.int32, (1, LANES), 1)
    valid = lane < elements
    _, backward_order = rotation_tables()
    groups = [(0, 1, 4, 5), (2, 3, 6, 7), (8, 9, 12, 13), (10, 11, 14, 15)]
    for f in range(4):
        out = row_fold(
            [w_ref[f, q] for q in range(16)],
            [hu_ref[f, b] for b in range(3)],
            [hd_ref[f, b] for b in range(3)],
            row,
            col,
            rows_dev,
            elements,
        )
        out = [out[q] / mass_total[q] for q in range(16)]
        new = select_rows(out, rotation, backward_order)
        new = [jnp.where(valid, new[p], 0.0) for p in range(16)]
        for p in range(16):
            out_ref[f, p] = new[p]
        if f == 3:
            for p in range(16):
                part = jnp.sum(new[p], axis=0, keepdims=True)

                @pl.when(pl.program_id(0) == 0)
                def _():
                    cm_ref[p] = part

                @pl.when(pl.program_id(0) > 0)
                def _():
                    cm_ref[p] = cm_ref[p] + part
        if with_cells:
            average = [(prev_ref[f, p] + new[p]) / SUBSTEPS for p in range(16)]
            for c, group in enumerate(groups):
                m = [m_ref[p] for p in group]
                summed = (m[0] * average[group[0]] + m[1] * average[group[1]]) + (
                    m[2] * average[group[2]] + m[3] * average[group[3]]
                )
                area = (m[0] + m[1]) + (m[2] + m[3])
                cell_ref[c, f] = summed / area


def fin_call(w, halo_up, halo_down, mass_parts, info, rows_dev, elements, prev=None, mass=None):
    levels = w.shape[2]
    steps = levels // CHUNK
    block = pl.BlockSpec((4, 16, CHUNK, LANES), lambda i: (0, 0, i, 0))
    halo = pl.BlockSpec((halo_up.shape[0], 3, CHUNK, 128), lambda i: (0, 0, i, 0))
    small = pl.BlockSpec((16, 1, LANES), lambda i: (0, 0, 0))
    with_cells = prev is not None
    with_mass = halo_up.shape[0] == 5
    in_specs = [block, halo, halo, small]
    args = [w, halo_up, halo_down, mass_parts]
    in_specs.append(pl.BlockSpec((8, LANES), lambda i: (0, 0)))
    args.append(info)
    out_specs = [block, small]
    out_shape = [
        jax.ShapeDtypeStruct(w.shape, jnp.float32),
        jax.ShapeDtypeStruct((16, 1, LANES), jnp.float32),
    ]
    if with_cells:
        in_specs += [block, small]
        args += [prev, mass]
        out_specs.append(pl.BlockSpec((4, 4, CHUNK, LANES), lambda i: (0, 0, i, 0)))
        out_shape.append(jax.ShapeDtypeStruct((4, 4, levels, LANES), jnp.float32))
    if with_mass:
        out_specs.append(small)
        out_shape.append(jax.ShapeDtypeStruct((16, 1, LANES), jnp.float32))
    return pl.pallas_call(
        functools.partial(fin_kernel, rows_dev, elements, with_cells, with_mass),
        interpret=INTERPRET,
        grid=(steps,),
        in_specs=in_specs,
        out_specs=out_specs,
        out_shape=out_shape,
    )(*args)


def edge_exchange(last, first):
    seg_count = lax.axis_size("seg")
    up = [(i, (i + 1) % seg_count) for i in range(seg_count)]
    down = [(j, i) for i, j in up]
    return lax.ppermute(last, "seg", up), lax.ppermute(first, "seg", down)


def halo_exchange(w, elements):
    seg_count = lax.axis_size("seg")
    up = [(i, (i + 1) % seg_count) for i in range(seg_count)]
    down = [(j, i) for i, j in up]
    last = w[..., 12:16, :, elements - COLS : elements]
    first = w[..., 0:4, :, 0:COLS]
    prev_last = lax.ppermute(last, "seg", up)
    next_first = lax.ppermute(first, "seg", down)
    widths = [(0, 0)] * (w.ndim - 1)
    halo_up = jnp.pad(prev_last, widths + [(0, LANES - COLS)])
    halo_down = jnp.pad(next_first, widths + [(elements - COLS, LANES - elements)])
    return halo_up, halo_down


def mass_dss(mass_canon_rows, info, rows_dev, elements):
    col = info[1:2]
    row = info[2:3]
    rows = list(mass_canon_rows)
    for a in range(4):
        edge = rows[4 * a + 3]
        left = jnp.where(col == 0, jnp.roll(edge, -(COLS - 1), -1), jnp.roll(edge, 1, -1))
        total = rows[4 * a] + left
        rows[4 * a] = total
        rows[4 * a + 3] = jnp.where(
            col == COLS - 1, jnp.roll(total, COLS - 1, -1), jnp.roll(total, -1, -1)
        )
    w = jnp.stack(rows)
    halo_up, halo_down = halo_exchange(w, elements)
    out = list(rows)
    for b in range(4):
        from_up = jnp.where(row == 0, halo_up[b], jnp.roll(rows[12 + b], COLS, -1))
        out[b] = rows[b] + from_up
        from_down = jnp.where(row == rows_dev - 1, halo_down[b], jnp.roll(rows[b], -COLS, -1))
        out[12 + b] = rows[12 + b] + from_down
    total = jnp.stack(out)
    lane = jnp.arange(LANES)
    return jnp.where(lane < elements, total, 1.0)


def prep_kernel(elements, vel_ref, temp_ref, dp_ref, out_ref, cm_ref):
    chunk = out_ref.shape[2]
    zeros = jnp.zeros((chunk, 128), jnp.float32)
    blocks = [vel_ref[0], vel_ref[1], temp_ref[...], dp_ref[...]]
    for f, block in enumerate(blocks):
        grouped = block.reshape(chunk, 16, elements)
        for p in range(16):
            rows = grouped[:, p, :]
            out_ref[f, p, :, pl.ds(LANES - 128, 128)] = zeros
            out_ref[f, p, :, pl.ds(0, elements)] = rows
            if f == 3:
                part = jnp.sum(out_ref[f, p], axis=0, keepdims=True)

                @pl.when(pl.program_id(0) == 0)
                def _():
                    cm_ref[p] = part

                @pl.when(pl.program_id(0) > 0)
                def _():
                    cm_ref[p] = cm_ref[p] + part


def prep_call(velocity_pair, thermal_reading, layer_depth):
    levels, points, elements = thermal_reading.shape
    steps = levels // CHUNK
    rows = CHUNK * points
    vel = velocity_pair.reshape(2, levels * points, elements)
    temp = thermal_reading.reshape(levels * points, elements)
    dp = layer_depth.reshape(levels * points, elements)
    return pl.pallas_call(
        functools.partial(prep_kernel, elements),
        interpret=INTERPRET,
        grid=(steps,),
        in_specs=[
            pl.BlockSpec((2, rows, elements), lambda i: (0, i, 0)),
            pl.BlockSpec((rows, elements), lambda i: (i, 0)),
            pl.BlockSpec((rows, elements), lambda i: (i, 0)),
        ],
        out_specs=[
            pl.BlockSpec((4, 16, CHUNK, LANES), lambda i: (0, 0, i, 0)),
            pl.BlockSpec((16, 1, LANES), lambda i: (0, 0, 0)),
        ],
        out_shape=[
            jax.ShapeDtypeStruct((4, 16, levels, LANES), jnp.float32),
            jax.ShapeDtypeStruct((16, 1, LANES), jnp.float32),
        ],
    )(vel, temp, dp)


def local(
    velocity_pair,
    thermal_reading,
    layer_depth,
    jacobian_terms,
    rotation_frequency,
    integration_mass,
    shared_vertex_label,
    column_owner_slot,
):
    levels_dev = thermal_reading.shape[0]
    elements = thermal_reading.shape[2]
    seg_count = lax.axis_size("seg")
    lev_count = lax.axis_size("lev")
    rows_dev = elements // COLS
    node_cols = 3 * COLS
    first_row = 3 * rows_dev * lax.axis_index("seg")
    grid_rows = 3 * rows_dev * seg_count
    corner_ids = shared_vertex_label[0]
    element_pos = jnp.arange(elements)
    row_offset = (corner_ids // node_cols - first_row) % grid_rows - 3 * (element_pos // COLS)
    col_offset = (corner_ids % node_cols - 3 * (element_pos % COLS)) % node_cols
    rotation = jnp.where(
        row_offset == 0, jnp.where(col_offset == 0, 0, 1), jnp.where(col_offset == 3, 2, 3)
    )
    info = lane_info(rotation, elements)
    forward_order, _ = rotation_tables()

    fields, column_parts = prep_call(velocity_pair, thermal_reading, layer_depth)
    (
        mass_canon,
        mass_folded,
        mass_last,
        mass_first,
        mass,
        mass_one,
        jac,
        rot,
    ) = mass_call(integration_mass, jacobian_terms, rotation_frequency, info)
    mass_parts = mass_folded
    mass_edges = (mass_last, mass_first)
    column_mass = column_parts
    previous = None
    cells = None
    for substep in range(SUBSTEPS):
        above = carried_in(column_mass, "lev", False)
        g0, group_height = term_call(fields, above)
        below = carried_in(group_height, "lev", True)
        w, last, first = adv_call(
            fields, g0, below, jac, rot, mass_canon, info, elements, mass_edges
        )
        mass_edges = None
        halo_up, halo_down = edge_exchange(last, first)
        outs = fin_call(
            w,
            halo_up,
            halo_down,
            mass_parts,
            info,
            rows_dev,
            elements,
            previous if substep == SUBSTEPS - 1 else None,
            mass_one,
        )
        fields, column_parts = outs[:2]
        if substep == SUBSTEPS - 1:
            cells = outs[2]
        if substep == 0:
            mass_parts = outs[-1]
        previous = fields
        column_mass = column_parts
    channels = 4 * levels_dev
    cell_values = cells[..., :elements].reshape(4, channels, elements)
    payload = jnp.transpose(cell_values, (0, 2, 1)).reshape(4 * elements, channels)
    dev_count = seg_count * lev_count
    own_cols = 4 * elements * seg_count // dev_count
    per_pair = own_cols // seg_count
    capacity = per_pair + per_pair // 2
    targets = column_owner_slot.reshape(-1)
    owner_index = targets // own_cols
    slot_index = targets % own_cols
    cell_count = targets.shape[0]
    cell_pos = jnp.arange(cell_count)
    same_owner = owner_index[:, None] == owner_index[None, :]
    earlier = cell_pos[:, None] < cell_pos[None, :]
    rank = jnp.sum(jnp.logical_and(same_owner, earlier).astype(jnp.int32), axis=0)
    destination = owner_index * capacity + rank
    slots = jnp.arange(dev_count * capacity)
    code = cell_pos * (own_cols + 1) + slot_index + 1
    match = destination[:, None] == slots[None, :]
    found = jnp.sum(jnp.where(match, code[:, None], 0), axis=0)
    has = found > 0
    source_cell = jnp.maximum(found - 1, 0) // (own_cols + 1)
    source_pos = jnp.maximum(found - 1, 0) % (own_cols + 1)
    outgoing = payload[source_cell].reshape(dev_count, capacity, channels)
    ids = jnp.where(has, source_pos, -1).reshape(dev_count, capacity)
    received_ids = lax.all_to_all(ids, ("seg", "lev"), split_axis=0, concat_axis=0, tiled=True)
    flat = jnp.arange(dev_count * capacity).reshape(dev_count, capacity)
    source_lev = (jnp.arange(dev_count) % lev_count)[:, None]
    positions = jnp.arange(own_cols)
    picks = []
    for group in range(lev_count):
        hit = jnp.logical_and(
            received_ids[:, :, None] == positions[None, None, :], (source_lev == group)[:, :, None]
        )
        picks.append(jnp.sum(jnp.where(hit, flat[:, :, None], 0), axis=(0, 1)))
    received = lax.all_to_all(outgoing, ("seg", "lev"), split_axis=0, concat_axis=0, tiled=True)
    arrived = received.reshape(dev_count * capacity, channels)[jnp.stack(picks)]
    arrived = arrived.reshape(lev_count, own_cols, 4, levels_dev).transpose(2, 0, 3, 1)
    phys_state = arrived.reshape(4, lev_count * levels_dev, own_cols)
    mean_thickness = jnp.mean(phys_state[3], axis=0)
    dyn_state = jnp.transpose(fields[..., :elements], (0, 2, 1, 3))
    return (dyn_state, phys_state, mean_thickness)


def solution(mesh):
    in_specs = (
        P(None, "lev", None, "seg"),
        P("lev", None, "seg"),
        P("lev", None, "seg"),
        P(None, None, "seg"),
        P(None, "seg"),
        P(None, "seg"),
        P(None, "seg"),
        P(None, "seg"),
    )
    out_specs = (P(None, "lev", None, "seg"), P(None, None, ("seg", "lev")), P(("seg", "lev")))
    return jax.shard_map(local, mesh=mesh, in_specs=in_specs, out_specs=out_specs, check_vma=False)
```

```python
import functools

import jax
import jax.numpy as jnp
import numpy as np
from jax import lax
from jax.experimental import pallas as pl
from jax.experimental.pallas import tpu as pltpu
from jax.sharding import PartitionSpec as P

COLS = 120
SUBSTEPS = 2


top_pressure = 10.0
time_increment = 0.05


def gll_slopes():
    root_five = np.sqrt(5.0)
    gll_nodes = [-1.0, -1.0 / root_five, 1.0 / root_five, 1.0]
    legendre_values = [-1.0, 1.0 / root_five, -1.0 / root_five, 1.0]
    slopes = np.zeros((4, 4))
    for row_node in range(4):
        for column in range(4):
            if row_node != column:
                slopes[row_node, column] = (
                    legendre_values[row_node]
                    / legendre_values[column]
                    / (gll_nodes[row_node] - gll_nodes[column])
                )
    slopes[0, 0] = -3.0
    slopes[3, 3] = 3.0
    return slopes


SLOPES = gll_slopes().astype(np.float32)


def rotation_tables():
    forward = np.zeros((4, 16), np.int32)
    for first_pos in range(4):
        for second_pos in range(4):
            canonical = 4 * first_pos + second_pos
            forward[0, canonical] = 4 * first_pos + second_pos
            forward[1, canonical] = 4 * (3 - second_pos) + first_pos
            forward[2, canonical] = 4 * (3 - first_pos) + (3 - second_pos)
            forward[3, canonical] = 4 * second_pos + 3 - first_pos
    backward = np.argsort(forward, axis=1).astype(np.int32)
    return (forward, backward)


def weighted_sum(terms):
    acc = None
    for coef, value in terms:
        if coef == 0.0:
            continue
        part = jnp.float32(coef) * value
        acc = part if acc is None else acc + part
    return acc


def first_deriv(f):
    return jnp.stack(
        [
            weighted_sum([(SLOPES[a, k], f[4 * k + j]) for k in range(4)])
            for a in range(4)
            for j in range(4)
        ]
    )


def second_deriv(f):
    return jnp.stack(
        [
            weighted_sum([(SLOPES[a, k], f[4 * i + k]) for k in range(4)])
            for i in range(4)
            for a in range(4)
        ]
    )


def carried_in(part, axis, reverse):
    count = lax.axis_size(axis)
    place = lax.axis_index(axis)
    gathered = lax.all_gather(part, axis)
    index = jnp.arange(count).reshape((count,) + (1,) * part.ndim)
    chosen = index > place if reverse else index < place
    return jnp.sum(jnp.where(chosen, gathered, jnp.zeros_like(gathered)), axis=0)


def site_potential_energy(thermal_reading, layer_depth):
    column_mass = jnp.sum(layer_depth, axis=1)
    above_sum = carried_in(column_mass, "lev", False)
    layer_midpoint_load = (
        top_pressure + above_sum[:, None, :] + jnp.cumsum(layer_depth, axis=1) - 0.5 * layer_depth
    )
    surface_change_rate = thermal_reading * layer_depth / layer_midpoint_load
    group_height = jnp.sum(surface_change_rate, axis=1)
    below_sum = carried_in(group_height, "lev", True)
    return (
        below_sum[:, None, :]
        + lax.cumsum(surface_change_rate, axis=1, reverse=True)
        - 0.5 * surface_change_rate
    )


def tendency_step(u, v, temp, dp, geopotential, jac, rot):
    energy = geopotential + 0.5 * (u * u + v * v)
    energy_first = first_deriv(energy)
    energy_second = second_deriv(energy)
    zonal_slope = jac[0] * energy_first + jac[1] * energy_second
    meridional_slope = jac[2] * energy_first + jac[3] * energy_second
    initial_transport = jac[0] * u + jac[2] * v
    latter_transport = jac[1] * u + jac[3] * v
    advect_with_motion = initial_transport * first_deriv(temp) + latter_transport * second_deriv(
        temp
    )
    distribute_onto_vertices = first_deriv(dp * initial_transport) + second_deriv(
        dp * latter_transport
    )
    return (
        u + time_increment * (rot * v - zonal_slope),
        v - time_increment * (rot * u + meridional_slope),
        temp - time_increment * advect_with_motion,
        dp - time_increment * distribute_onto_vertices,
    )


def reorder(values, rotation, table):
    rows = []
    for q in range(16):
        pick = values[int(table[3, q])]
        for w in (2, 1, 0):
            pick = jnp.where(rotation == w, values[int(table[w, q])], pick)
        rows.append(pick)
    return jnp.stack(rows)


def node_sum(canon, col, row, rows_dev):
    elements = canon.shape[-1]

    def roll(y, shift):
        return jnp.roll(y, shift, axis=-1)

    rows = [canon[q] for q in range(16)]
    for a in range(4):
        left = jnp.where(col == 0, roll(rows[4 * a + 3], -(COLS - 1)), roll(rows[4 * a + 3], 1))
        total = rows[4 * a] + left
        rows[4 * a] = total
        rows[4 * a + 3] = jnp.where(col == COLS - 1, roll(total, COLS - 1), roll(total, -1))
    seg_count = lax.axis_size("seg")
    up = [(i, (i + 1) % seg_count) for i in range(seg_count)]
    down = [(j, i) for i, j in up]
    last = jnp.stack([rows[12 + b][:, elements - COLS :] for b in range(4)])
    first = jnp.stack([rows[b][:, :COLS] for b in range(4)])
    prev_last = lax.ppermute(last, "seg", up)
    next_first = lax.ppermute(first, "seg", down)
    pad = jnp.zeros(prev_last.shape[1:-1] + (elements - COLS,), canon.dtype)
    out = list(rows)
    for b in range(4):
        halo_up = jnp.concatenate([prev_last[b], pad], axis=-1)
        from_up = jnp.where(row == 0, halo_up, roll(rows[12 + b], COLS))
        out[b] = rows[b] + from_up
        halo_down = jnp.concatenate([pad, next_first[b]], axis=-1)
        from_down = jnp.where(row == rows_dev - 1, halo_down, roll(rows[b], -COLS))
        out[12 + b] = rows[12 + b] + from_down
    return jnp.stack(out)


LANES = 512
CHUNK = 32
INTERPRET = None


def lane_info(rotation, elements):
    element_pos = jnp.arange(elements)
    info = jnp.stack(
        [rotation, element_pos % COLS, element_pos // COLS]
        + [jnp.zeros_like(rotation)] * 5
    ).astype(jnp.int32)
    return jnp.pad(info, ((0, 0), (0, LANES - elements)), constant_values=-1)


def pad_lanes(x, value=0.0):
    widths = [(0, 0)] * (x.ndim - 1) + [(0, LANES - x.shape[-1])]
    return jnp.pad(x, widths, constant_values=value)


def select_rows(values, rotation, table):
    rows = []
    for q in range(16):
        pick = values[int(table[3, q])]
        for w in (2, 1, 0):
            pick = jnp.where(rotation == w, values[int(table[w, q])], pick)
        rows.append(pick)
    return rows


def term_kernel(levels, f_ref, above_ref, g_ref, gh_ref):
    level = lax.broadcasted_iota(jnp.int32, (levels, LANES), 0)
    for p in range(f_ref.shape[1]):
        temp = f_ref[0, p]
        dp = f_ref[1, p]
        cum = dp
        shift = 1
        while shift < levels:
            cum = cum + jnp.where(level >= shift, pltpu.roll(cum, shift, 0), 0.0)
            shift *= 2
        load = top_pressure + above_ref[p] + cum - 0.5 * dp
        term = temp * dp / load
        gh_ref[p] = jnp.sum(term, axis=0, keepdims=True)
        rcum = term
        shift = 1
        while shift < levels:
            rcum = rcum + jnp.where(
                level + shift < levels, pltpu.roll(rcum, levels - shift, 0), 0.0
            )
            shift *= 2
        g_ref[p] = rcum - 0.5 * term


def term_call(fields, above):
    levels = fields.shape[2]
    group = 4
    return pl.pallas_call(
        functools.partial(term_kernel, levels),
        interpret=INTERPRET,
        grid=(16 // group,),
        in_specs=[
            pl.BlockSpec((2, group, levels, LANES), lambda i: (1, i, 0, 0)),
            pl.BlockSpec((group, 1, LANES), lambda i: (i, 0, 0)),
        ],
        out_specs=[
            pl.BlockSpec((group, levels, LANES), lambda i: (i, 0, 0)),
            pl.BlockSpec((group, 1, LANES), lambda i: (i, 0, 0)),
        ],
        out_shape=[
            jax.ShapeDtypeStruct((16, levels, LANES), jnp.float32),
            jax.ShapeDtypeStruct((16, 1, LANES), jnp.float32),
        ],
    )(fields, above)


def lane_roll(y, shift):
    return pltpu.roll(y, shift % LANES, 1)


def column_fold(rows, col):
    rows = list(rows)
    for a in range(4):
        edge = rows[4 * a + 3]
        left = jnp.where(col == 0, lane_roll(edge, -(COLS - 1)), lane_roll(edge, 1))
        total = rows[4 * a] + left
        rows[4 * a] = total
        rows[4 * a + 3] = jnp.where(
            col == COLS - 1, lane_roll(total, COLS - 1), lane_roll(total, -1)
        )
    return rows


def shift_right(y, col):
    return jnp.where(col == COLS - 1, lane_roll(y, COLS - 1), lane_roll(y, -1))


def row_fold(rows, up_rows, down_rows, row, col, rows_dev, elements):
    fill = jnp.zeros((rows[0].shape[0], LANES - 128), jnp.float32)
    halo_up = [jnp.concatenate([up_rows[b], fill], axis=1) for b in range(3)]
    halo_down = [
        lane_roll(jnp.concatenate([down_rows[b], fill], axis=1), elements - COLS) for b in range(3)
    ]
    halo_up.append(shift_right(halo_up[0], col))
    halo_down.append(shift_right(halo_down[0], col))
    out = list(rows)
    for b in range(4):
        from_up = jnp.where(row == 0, halo_up[b], lane_roll(rows[12 + b], COLS))
        out[b] = rows[b] + from_up
        from_down = jnp.where(row == rows_dev - 1, halo_down[b], lane_roll(rows[b], -COLS))
        out[12 + b] = rows[12 + b] + from_down
    return out


def mass_kernel(elements, m_ref, j_ref, r_ref, info_ref, mc_ref, mw_ref, last_ref, first_ref, mp_ref, mo_ref, jp_ref, rp_ref):
    info = info_ref[...]
    forward_order, _ = rotation_tables()
    zero = jnp.zeros((1, 128), jnp.float32)
    one = jnp.ones((1, 128), jnp.float32)
    for p in range(16):
        row = m_ref[pl.ds(p, 1), :]
        mp_ref[p, :, pl.ds(LANES - 128, 128)] = zero
        mp_ref[p, :, pl.ds(0, elements)] = row
        mo_ref[p, :, pl.ds(LANES - 128, 128)] = one
        mo_ref[p, :, pl.ds(0, elements)] = row
        rp_ref[p, :, pl.ds(LANES - 128, 128)] = zero
        rp_ref[p, :, pl.ds(0, elements)] = r_ref[pl.ds(p, 1), :]
        for k in range(4):
            jp_ref[k, p, :, pl.ds(LANES - 128, 128)] = zero
            jp_ref[k, p, :, pl.ds(0, elements)] = j_ref[k, pl.ds(p, 1), :]
    canon = select_rows([mp_ref[p] for p in range(16)], info[0:1], forward_order)
    rows = column_fold(canon, info[1:2])
    for q in range(16):
        mc_ref[q] = canon[q]
        mw_ref[q] = rows[q]
    for b in range(4):
        last_ref[b] = lane_roll(rows[12 + b], COLS - elements)[:, :128]
        first_ref[b] = rows[b][:, :128]


def mass_call(mass, jac, rot, info):
    elements = mass.shape[-1]
    small = jax.ShapeDtypeStruct((16, 1, LANES), jnp.float32)
    edge = jax.ShapeDtypeStruct((4, 1, 128), jnp.float32)
    return pl.pallas_call(
        functools.partial(mass_kernel, elements),
        interpret=INTERPRET,
        out_shape=[
            small,
            small,
            edge,
            edge,
            small,
            small,
            jax.ShapeDtypeStruct((4, 16, 1, LANES), jnp.float32),
            small,
        ],
    )(mass, jac, rot, info)


def adv_kernel(elements, with_mass, *refs):
    f_ref, g_ref, below_ref, jac_ref, rot_ref, mc_ref, info_ref = refs[:7]
    if with_mass:
        mlast_ref, mfirst_ref = refs[7:9]
    out_ref, last_ref, first_ref = refs[-3:]
    info = info_ref[...]
    rotation = info[0:1]
    col = info[1:2]
    forward_order, _ = rotation_tables()
    u = [f_ref[0, p] for p in range(16)]
    v = [f_ref[1, p] for p in range(16)]
    temp = [f_ref[2, p] for p in range(16)]
    dp = [f_ref[3, p] for p in range(16)]
    jac = [[jac_ref[k, p] for p in range(16)] for k in range(4)]
    energy = [
        (below_ref[p] + g_ref[p]) + 0.5 * (u[p] * u[p] + v[p] * v[p]) for p in range(16)
    ]
    e1 = first_rows(energy)
    e2 = second_rows(energy)
    it = [jac[0][p] * u[p] + jac[2][p] * v[p] for p in range(16)]
    lt = [jac[1][p] * u[p] + jac[3][p] * v[p] for p in range(16)]
    t1 = first_rows(temp)
    t2 = second_rows(temp)
    d1 = first_rows([dp[p] * it[p] for p in range(16)])
    d2 = second_rows([dp[p] * lt[p] for p in range(16)])
    advanced = []
    for p in range(16):
        rot = rot_ref[p]
        zonal_slope = jac[0][p] * e1[p] + jac[1][p] * e2[p]
        meridional_slope = jac[2][p] * e1[p] + jac[3][p] * e2[p]
        advanced.append(
            (
                u[p] + time_increment * (rot * v[p] - zonal_slope),
                v[p] - time_increment * (rot * u[p] + meridional_slope),
                temp[p] - time_increment * (it[p] * t1[p] + lt[p] * t2[p]),
                dp[p] - time_increment * (d1[p] + d2[p]),
            )
        )
    for f in range(4):
        rows = select_rows([advanced[p][f] for p in range(16)], rotation, forward_order)
        rows = column_fold([rows[q] * mc_ref[q] for q in range(16)], col)
        for q in range(16):
            out_ref[f, q] = rows[q]
        for b in range(3):
            last_ref[f, b] = lane_roll(rows[12 + b], COLS - elements)[:, :128]
            first_ref[f, b] = rows[b][:, :128]
    if with_mass:
        shape = last_ref.shape[2:]
        for b in range(3):
            last_ref[4, b] = jnp.broadcast_to(mlast_ref[b], shape)
            first_ref[4, b] = jnp.broadcast_to(mfirst_ref[b], shape)


def first_rows(rows):
    return [
        weighted_sum([(SLOPES[a, k], rows[4 * k + j]) for k in range(4)])
        for a in range(4)
        for j in range(4)
    ]


def second_rows(rows):
    return [
        weighted_sum([(SLOPES[a, k], rows[4 * i + k]) for k in range(4)])
        for i in range(4)
        for a in range(4)
    ]


def adv_call(fields, g0, below, jac, rot, mass_canon, info, elements, mass_edges=None):
    levels = fields.shape[2]
    steps = levels // CHUNK
    with_mass = mass_edges is not None
    width = 5 if with_mass else 4
    small = pl.BlockSpec((16, 1, LANES), lambda i: (0, 0, 0))
    edge = pl.BlockSpec((width, 3, CHUNK, 128), lambda i: (0, 0, i, 0))
    edge_shape = jax.ShapeDtypeStruct((width, 3, levels, 128), jnp.float32)
    in_specs = [
        pl.BlockSpec((4, 16, CHUNK, LANES), lambda i: (0, 0, i, 0)),
        pl.BlockSpec((16, CHUNK, LANES), lambda i: (0, i, 0)),
        small,
        pl.BlockSpec((4, 16, 1, LANES), lambda i: (0, 0, 0, 0)),
        small,
        small,
        pl.BlockSpec((8, LANES), lambda i: (0, 0)),
    ]
    args = [fields, g0, below, jac, rot, mass_canon, info]
    if with_mass:
        in_specs += [pl.BlockSpec((4, 1, 128), lambda i: (0, 0, 0))] * 2
        args += list(mass_edges)
    return pl.pallas_call(
        functools.partial(adv_kernel, elements, with_mass),
        interpret=INTERPRET,
        grid=(steps,),
        in_specs=in_specs,
        out_specs=[pl.BlockSpec((4, 16, CHUNK, LANES), lambda i: (0, 0, i, 0)), edge, edge],
        out_shape=[jax.ShapeDtypeStruct(fields.shape, jnp.float32), edge_shape, edge_shape],
    )(*args)


def fin_kernel(rows_dev, elements, with_cells, with_mass, *refs):
    refs = list(refs)
    w_ref, hu_ref, hd_ref = refs[:3]
    if with_mass:
        mw_ref = refs[3]
        refs = refs[4:]
    else:
        mt_ref = refs[3]
        refs = refs[4:]
    info_ref = refs.pop(0)
    if with_cells:
        prev_ref, m_ref = refs[:2]
        refs = refs[2:]
    out_ref, cm_ref = refs[:2]
    if with_cells:
        cell_ref = refs[2]
    info = info_ref[...]
    rotation = info[0:1]
    col = info[1:2]
    row = info[2:3]
    if with_mass:
        mass_total = row_fold(
            [mw_ref[q] for q in range(16)],
            [hu_ref[4, b][0:1] for b in range(3)],
            [hd_ref[4, b][0:1] for b in range(3)],
            row,
            col,
            rows_dev,
            elements,
        )
        lane_ok = lax.broadcasted_iota(jnp.int32, (1, LANES), 1) < elements
        mass_total = [jnp.where(lane_ok, m, 1.0) for m in mass_total]
        for q in range(16):
            refs[-1][q] = mass_total[q]
    else:
        mass_total = [mt_ref[q] for q in range(16)]
    lane = lax.broadcasted_iota(jnp.int32, (1, LANES), 1)
    valid = lane < elements
    _, backward_order = rotation_tables()
    groups = [(0, 1, 4, 5), (2, 3, 6, 7), (8, 9, 12, 13), (10, 11, 14, 15)]
    for f in range(4):
        out = row_fold(
            [w_ref[f, q] for q in range(16)],
            [hu_ref[f, b] for b in range(3)],
            [hd_ref[f, b] for b in range(3)],
            row,
            col,
            rows_dev,
            elements,
        )
        out = [out[q] / mass_total[q] for q in range(16)]
        new = select_rows(out, rotation, backward_order)
        new = [jnp.where(valid, new[p], 0.0) for p in range(16)]
        for p in range(16):
            out_ref[f, p] = new[p]
        if f == 3:
            for p in range(16):
                part = jnp.sum(new[p], axis=0, keepdims=True)

                @pl.when(pl.program_id(0) == 0)
                def _():
                    cm_ref[p] = part

                @pl.when(pl.program_id(0) > 0)
                def _():
                    cm_ref[p] = cm_ref[p] + part
        if with_cells:
            average = [(prev_ref[f, p] + new[p]) / SUBSTEPS for p in range(16)]
            for c, group in enumerate(groups):
                m = [m_ref[p] for p in group]
                summed = (m[0] * average[group[0]] + m[1] * average[group[1]]) + (
                    m[2] * average[group[2]] + m[3] * average[group[3]]
                )
                area = (m[0] + m[1]) + (m[2] + m[3])
                cell_ref[c, f] = summed / area


def fin_call(w, halo_up, halo_down, mass_parts, info, rows_dev, elements, prev=None, mass=None):
    levels = w.shape[2]
    steps = levels // CHUNK
    block = pl.BlockSpec((4, 16, CHUNK, LANES), lambda i: (0, 0, i, 0))
    halo = pl.BlockSpec((halo_up.shape[0], 3, CHUNK, 128), lambda i: (0, 0, i, 0))
    small = pl.BlockSpec((16, 1, LANES), lambda i: (0, 0, 0))
    with_cells = prev is not None
    with_mass = halo_up.shape[0] == 5
    in_specs = [block, halo, halo, small]
    args = [w, halo_up, halo_down, mass_parts]
    in_specs.append(pl.BlockSpec((8, LANES), lambda i: (0, 0)))
    args.append(info)
    out_specs = [block, small]
    out_shape = [
        jax.ShapeDtypeStruct(w.shape, jnp.float32),
        jax.ShapeDtypeStruct((16, 1, LANES), jnp.float32),
    ]
    if with_cells:
        in_specs += [block, small]
        args += [prev, mass]
        out_specs.append(pl.BlockSpec((4, 4, CHUNK, LANES), lambda i: (0, 0, i, 0)))
        out_shape.append(jax.ShapeDtypeStruct((4, 4, levels, LANES), jnp.float32))
    if with_mass:
        out_specs.append(small)
        out_shape.append(jax.ShapeDtypeStruct((16, 1, LANES), jnp.float32))
    return pl.pallas_call(
        functools.partial(fin_kernel, rows_dev, elements, with_cells, with_mass),
        interpret=INTERPRET,
        grid=(steps,),
        in_specs=in_specs,
        out_specs=out_specs,
        out_shape=out_shape,
    )(*args)


def edge_exchange(last, first):
    seg_count = lax.axis_size("seg")
    up = [(i, (i + 1) % seg_count) for i in range(seg_count)]
    down = [(j, i) for i, j in up]
    return lax.ppermute(last, "seg", up), lax.ppermute(first, "seg", down)


def halo_exchange(w, elements):
    seg_count = lax.axis_size("seg")
    up = [(i, (i + 1) % seg_count) for i in range(seg_count)]
    down = [(j, i) for i, j in up]
    last = w[..., 12:16, :, elements - COLS : elements]
    first = w[..., 0:4, :, 0:COLS]
    prev_last = lax.ppermute(last, "seg", up)
    next_first = lax.ppermute(first, "seg", down)
    widths = [(0, 0)] * (w.ndim - 1)
    halo_up = jnp.pad(prev_last, widths + [(0, LANES - COLS)])
    halo_down = jnp.pad(next_first, widths + [(elements - COLS, LANES - elements)])
    return halo_up, halo_down


def mass_dss(mass_canon_rows, info, rows_dev, elements):
    col = info[1:2]
    row = info[2:3]
    rows = list(mass_canon_rows)
    for a in range(4):
        edge = rows[4 * a + 3]
        left = jnp.where(col == 0, jnp.roll(edge, -(COLS - 1), -1), jnp.roll(edge, 1, -1))
        total = rows[4 * a] + left
        rows[4 * a] = total
        rows[4 * a + 3] = jnp.where(
            col == COLS - 1, jnp.roll(total, COLS - 1, -1), jnp.roll(total, -1, -1)
        )
    w = jnp.stack(rows)
    halo_up, halo_down = halo_exchange(w, elements)
    out = list(rows)
    for b in range(4):
        from_up = jnp.where(row == 0, halo_up[b], jnp.roll(rows[12 + b], COLS, -1))
        out[b] = rows[b] + from_up
        from_down = jnp.where(row == rows_dev - 1, halo_down[b], jnp.roll(rows[b], -COLS, -1))
        out[12 + b] = rows[12 + b] + from_down
    total = jnp.stack(out)
    lane = jnp.arange(LANES)
    return jnp.where(lane < elements, total, 1.0)


def prep_kernel(elements, vel_ref, temp_ref, dp_ref, out_ref, cm_ref):
    chunk = out_ref.shape[2]
    zeros = jnp.zeros((chunk, 128), jnp.float32)
    blocks = [vel_ref[0], vel_ref[1], temp_ref[...], dp_ref[...]]
    for f, block in enumerate(blocks):
        grouped = block.reshape(chunk, 16, elements)
        for p in range(16):
            rows = grouped[:, p, :]
            out_ref[f, p, :, pl.ds(LANES - 128, 128)] = zeros
            out_ref[f, p, :, pl.ds(0, elements)] = rows
            if f == 3:
                part = jnp.sum(out_ref[f, p], axis=0, keepdims=True)

                @pl.when(pl.program_id(0) == 0)
                def _():
                    cm_ref[p] = part

                @pl.when(pl.program_id(0) > 0)
                def _():
                    cm_ref[p] = cm_ref[p] + part


def prep_call(velocity_pair, thermal_reading, layer_depth):
    levels, points, elements = thermal_reading.shape
    steps = levels // CHUNK
    rows = CHUNK * points
    vel = velocity_pair.reshape(2, levels * points, elements)
    temp = thermal_reading.reshape(levels * points, elements)
    dp = layer_depth.reshape(levels * points, elements)
    return pl.pallas_call(
        functools.partial(prep_kernel, elements),
        interpret=INTERPRET,
        grid=(steps,),
        in_specs=[
            pl.BlockSpec((2, rows, elements), lambda i: (0, i, 0)),
            pl.BlockSpec((rows, elements), lambda i: (i, 0)),
            pl.BlockSpec((rows, elements), lambda i: (i, 0)),
        ],
        out_specs=[
            pl.BlockSpec((4, 16, CHUNK, LANES), lambda i: (0, 0, i, 0)),
            pl.BlockSpec((16, 1, LANES), lambda i: (0, 0, 0)),
        ],
        out_shape=[
            jax.ShapeDtypeStruct((4, 16, levels, LANES), jnp.float32),
            jax.ShapeDtypeStruct((16, 1, LANES), jnp.float32),
        ],
    )(vel, temp, dp)


def local(
    velocity_pair,
    thermal_reading,
    layer_depth,
    jacobian_terms,
    rotation_frequency,
    integration_mass,
    shared_vertex_label,
    column_owner_slot,
):
    levels_dev = thermal_reading.shape[0]
    elements = thermal_reading.shape[2]
    seg_count = lax.axis_size("seg")
    lev_count = lax.axis_size("lev")
    rows_dev = elements // COLS
    node_cols = 3 * COLS
    first_row = 3 * rows_dev * lax.axis_index("seg")
    grid_rows = 3 * rows_dev * seg_count
    corner_ids = shared_vertex_label[0]
    element_pos = jnp.arange(elements)
    row_offset = (corner_ids // node_cols - first_row) % grid_rows - 3 * (element_pos // COLS)
    col_offset = (corner_ids % node_cols - 3 * (element_pos % COLS)) % node_cols
    rotation = jnp.where(
        row_offset == 0, jnp.where(col_offset == 0, 0, 1), jnp.where(col_offset == 3, 2, 3)
    )
    info = lane_info(rotation, elements)
    forward_order, _ = rotation_tables()

    fields, column_parts = prep_call(velocity_pair, thermal_reading, layer_depth)
    (
        mass_canon,
        mass_folded,
        mass_last,
        mass_first,
        mass,
        mass_one,
        jac,
        rot,
    ) = mass_call(integration_mass, jacobian_terms, rotation_frequency, info)
    mass_parts = mass_folded
    mass_edges = (mass_last, mass_first)
    column_mass = column_parts
    previous = None
    cells = None
    for substep in range(SUBSTEPS):
        above = carried_in(column_mass, "lev", False)
        g0, group_height = term_call(fields, above)
        below = carried_in(group_height, "lev", True)
        w, last, first = adv_call(
            fields, g0, below, jac, rot, mass_canon, info, elements, mass_edges
        )
        mass_edges = None
        halo_up, halo_down = edge_exchange(last, first)
        outs = fin_call(
            w,
            halo_up,
            halo_down,
            mass_parts,
            info,
            rows_dev,
            elements,
            previous if substep == SUBSTEPS - 1 else None,
            mass_one,
        )
        fields, column_parts = outs[:2]
        if substep == SUBSTEPS - 1:
            cells = outs[2]
        if substep == 0:
            mass_parts = outs[-1]
        previous = fields
        column_mass = column_parts
    channels = 4 * levels_dev
    cell_values = cells[..., :elements].reshape(4, channels, elements)
    payload = jnp.transpose(cell_values, (0, 2, 1)).reshape(4 * elements, channels)
    dev_count = seg_count * lev_count
    own_cols = 4 * elements * seg_count // dev_count
    per_pair = own_cols // seg_count
    capacity = per_pair + per_pair // 2
    targets = column_owner_slot.reshape(-1)
    owner_index = targets // own_cols
    slot_index = targets % own_cols
    cell_count = targets.shape[0]
    cell_pos = jnp.arange(cell_count)
    same_owner = owner_index[:, None] == owner_index[None, :]
    earlier = cell_pos[:, None] < cell_pos[None, :]
    rank = jnp.sum(jnp.logical_and(same_owner, earlier).astype(jnp.int32), axis=0)
    destination = owner_index * capacity + rank
    slots = jnp.arange(dev_count * capacity)
    code = cell_pos * (own_cols + 1) + slot_index + 1
    match = destination[:, None] == slots[None, :]
    found = jnp.sum(jnp.where(match, code[:, None], 0), axis=0)
    has = found > 0
    source_cell = jnp.maximum(found - 1, 0) // (own_cols + 1)
    source_pos = jnp.maximum(found - 1, 0) % (own_cols + 1)
    outgoing = payload[source_cell].reshape(dev_count, capacity, channels)
    ids = jnp.where(has, source_pos, -1).reshape(dev_count, capacity)
    received_ids = lax.all_to_all(ids, ("seg", "lev"), split_axis=0, concat_axis=0, tiled=True)
    flat = jnp.arange(dev_count * capacity).reshape(dev_count, capacity)
    source_lev = (jnp.arange(dev_count) % lev_count)[:, None]
    positions = jnp.arange(own_cols)
    picks = []
    for group in range(lev_count):
        hit = jnp.logical_and(
            received_ids[:, :, None] == positions[None, None, :], (source_lev == group)[:, :, None]
        )
        picks.append(jnp.sum(jnp.where(hit, flat[:, :, None], 0), axis=(0, 1)))
    received = lax.all_to_all(outgoing, ("seg", "lev"), split_axis=0, concat_axis=0, tiled=True)
    arrived = received.reshape(dev_count * capacity, channels)[jnp.stack(picks)]
    arrived = arrived.reshape(lev_count, own_cols, 4, levels_dev).transpose(2, 0, 3, 1)
    phys_state = arrived.reshape(4, lev_count * levels_dev, own_cols)
    mean_thickness = jnp.mean(phys_state[3], axis=0)
    dyn_state = jnp.transpose(fields[..., :elements], (0, 2, 1, 3))
    return (dyn_state, phys_state, mean_thickness)


def solution(mesh):
    in_specs = (
        P(None, "lev", None, "seg"),
        P("lev", None, "seg"),
        P("lev", None, "seg"),
        P(None, None, "seg"),
        P(None, "seg"),
        P(None, "seg"),
        P(None, "seg"),
        P(None, "seg"),
    )
    out_specs = (P(None, "lev", None, "seg"), P(None, None, ("seg", "lev")), P(("seg", "lev")))
    return jax.shard_map(local, mesh=mesh, in_specs=in_specs, out_specs=out_specs, check_vma=False)
```

```python
import functools

import jax
import jax.numpy as jnp
import numpy as np
from jax import lax
from jax.experimental import pallas as pl
from jax.experimental.pallas import tpu as pltpu
from jax.sharding import PartitionSpec as P

COLS = 120
SUBSTEPS = 2


top_pressure = 10.0
time_increment = 0.05


def gll_slopes():
    root_five = np.sqrt(5.0)
    gll_nodes = [-1.0, -1.0 / root_five, 1.0 / root_five, 1.0]
    legendre_values = [-1.0, 1.0 / root_five, -1.0 / root_five, 1.0]
    slopes = np.zeros((4, 4))
    for row_node in range(4):
        for column in range(4):
            if row_node != column:
                slopes[row_node, column] = (
                    legendre_values[row_node]
                    / legendre_values[column]
                    / (gll_nodes[row_node] - gll_nodes[column])
                )
    slopes[0, 0] = -3.0
    slopes[3, 3] = 3.0
    return slopes


SLOPES = gll_slopes().astype(np.float32)


def rotation_tables():
    forward = np.zeros((4, 16), np.int32)
    for first_pos in range(4):
        for second_pos in range(4):
            canonical = 4 * first_pos + second_pos
            forward[0, canonical] = 4 * first_pos + second_pos
            forward[1, canonical] = 4 * (3 - second_pos) + first_pos
            forward[2, canonical] = 4 * (3 - first_pos) + (3 - second_pos)
            forward[3, canonical] = 4 * second_pos + 3 - first_pos
    backward = np.argsort(forward, axis=1).astype(np.int32)
    return (forward, backward)


def weighted_sum(terms):
    acc = None
    for coef, value in terms:
        if coef == 0.0:
            continue
        part = jnp.float32(coef) * value
        acc = part if acc is None else acc + part
    return acc


def first_deriv(f):
    return jnp.stack(
        [
            weighted_sum([(SLOPES[a, k], f[4 * k + j]) for k in range(4)])
            for a in range(4)
            for j in range(4)
        ]
    )


def second_deriv(f):
    return jnp.stack(
        [
            weighted_sum([(SLOPES[a, k], f[4 * i + k]) for k in range(4)])
            for i in range(4)
            for a in range(4)
        ]
    )


def carried_in(part, axis, reverse):
    count = lax.axis_size(axis)
    place = lax.axis_index(axis)
    gathered = lax.all_gather(part, axis)
    index = jnp.arange(count).reshape((count,) + (1,) * part.ndim)
    chosen = index > place if reverse else index < place
    return jnp.sum(jnp.where(chosen, gathered, jnp.zeros_like(gathered)), axis=0)


def site_potential_energy(thermal_reading, layer_depth):
    column_mass = jnp.sum(layer_depth, axis=1)
    above_sum = carried_in(column_mass, "lev", False)
    layer_midpoint_load = (
        top_pressure + above_sum[:, None, :] + jnp.cumsum(layer_depth, axis=1) - 0.5 * layer_depth
    )
    surface_change_rate = thermal_reading * layer_depth / layer_midpoint_load
    group_height = jnp.sum(surface_change_rate, axis=1)
    below_sum = carried_in(group_height, "lev", True)
    return (
        below_sum[:, None, :]
        + lax.cumsum(surface_change_rate, axis=1, reverse=True)
        - 0.5 * surface_change_rate
    )


def tendency_step(u, v, temp, dp, geopotential, jac, rot):
    energy = geopotential + 0.5 * (u * u + v * v)
    energy_first = first_deriv(energy)
    energy_second = second_deriv(energy)
    zonal_slope = jac[0] * energy_first + jac[1] * energy_second
    meridional_slope = jac[2] * energy_first + jac[3] * energy_second
    initial_transport = jac[0] * u + jac[2] * v
    latter_transport = jac[1] * u + jac[3] * v
    advect_with_motion = initial_transport * first_deriv(temp) + latter_transport * second_deriv(
        temp
    )
    distribute_onto_vertices = first_deriv(dp * initial_transport) + second_deriv(
        dp * latter_transport
    )
    return (
        u + time_increment * (rot * v - zonal_slope),
        v - time_increment * (rot * u + meridional_slope),
        temp - time_increment * advect_with_motion,
        dp - time_increment * distribute_onto_vertices,
    )


def reorder(values, rotation, table):
    rows = []
    for q in range(16):
        pick = values[int(table[3, q])]
        for w in (2, 1, 0):
            pick = jnp.where(rotation == w, values[int(table[w, q])], pick)
        rows.append(pick)
    return jnp.stack(rows)


def node_sum(canon, col, row, rows_dev):
    elements = canon.shape[-1]

    def roll(y, shift):
        return jnp.roll(y, shift, axis=-1)

    rows = [canon[q] for q in range(16)]
    for a in range(4):
        left = jnp.where(col == 0, roll(rows[4 * a + 3], -(COLS - 1)), roll(rows[4 * a + 3], 1))
        total = rows[4 * a] + left
        rows[4 * a] = total
        rows[4 * a + 3] = jnp.where(col == COLS - 1, roll(total, COLS - 1), roll(total, -1))
    seg_count = lax.axis_size("seg")
    up = [(i, (i + 1) % seg_count) for i in range(seg_count)]
    down = [(j, i) for i, j in up]
    last = jnp.stack([rows[12 + b][:, elements - COLS :] for b in range(4)])
    first = jnp.stack([rows[b][:, :COLS] for b in range(4)])
    prev_last = lax.ppermute(last, "seg", up)
    next_first = lax.ppermute(first, "seg", down)
    pad = jnp.zeros(prev_last.shape[1:-1] + (elements - COLS,), canon.dtype)
    out = list(rows)
    for b in range(4):
        halo_up = jnp.concatenate([prev_last[b], pad], axis=-1)
        from_up = jnp.where(row == 0, halo_up, roll(rows[12 + b], COLS))
        out[b] = rows[b] + from_up
        halo_down = jnp.concatenate([pad, next_first[b]], axis=-1)
        from_down = jnp.where(row == rows_dev - 1, halo_down, roll(rows[b], -COLS))
        out[12 + b] = rows[12 + b] + from_down
    return jnp.stack(out)


LANES = 512
CHUNK = 16
INTERPRET = None


def lane_info(rotation, elements):
    element_pos = jnp.arange(elements)
    info = jnp.stack(
        [rotation, element_pos % COLS, element_pos // COLS]
        + [jnp.zeros_like(rotation)] * 5
    ).astype(jnp.int32)
    return jnp.pad(info, ((0, 0), (0, LANES - elements)), constant_values=-1)


def pad_lanes(x, value=0.0):
    widths = [(0, 0)] * (x.ndim - 1) + [(0, LANES - x.shape[-1])]
    return jnp.pad(x, widths, constant_values=value)


def select_rows(values, rotation, table):
    rows = []
    for q in range(16):
        pick = values[int(table[3, q])]
        for w in (2, 1, 0):
            pick = jnp.where(rotation == w, values[int(table[w, q])], pick)
        rows.append(pick)
    return rows


def term_kernel(levels, f_ref, above_ref, g_ref, gh_ref):
    level = lax.broadcasted_iota(jnp.int32, (levels, LANES), 0)
    for p in range(f_ref.shape[1]):
        temp = f_ref[0, p]
        dp = f_ref[1, p]
        cum = dp
        shift = 1
        while shift < levels:
            cum = cum + jnp.where(level >= shift, pltpu.roll(cum, shift, 0), 0.0)
            shift *= 2
        load = top_pressure + above_ref[p] + cum - 0.5 * dp
        term = temp * dp / load
        gh_ref[p] = jnp.sum(term, axis=0, keepdims=True)
        rcum = term
        shift = 1
        while shift < levels:
            rcum = rcum + jnp.where(
                level + shift < levels, pltpu.roll(rcum, levels - shift, 0), 0.0
            )
            shift *= 2
        g_ref[p] = rcum - 0.5 * term


def term_call(fields, above):
    levels = fields.shape[2]
    group = 8
    return pl.pallas_call(
        functools.partial(term_kernel, levels),
        interpret=INTERPRET,
        grid=(16 // group,),
        in_specs=[
            pl.BlockSpec((2, group, levels, LANES), lambda i: (1, i, 0, 0)),
            pl.BlockSpec((group, 1, LANES), lambda i: (i, 0, 0)),
        ],
        out_specs=[
            pl.BlockSpec((group, levels, LANES), lambda i: (i, 0, 0)),
            pl.BlockSpec((group, 1, LANES), lambda i: (i, 0, 0)),
        ],
        out_shape=[
            jax.ShapeDtypeStruct((16, levels, LANES), jnp.float32),
            jax.ShapeDtypeStruct((16, 1, LANES), jnp.float32),
        ],
    )(fields, above)


def lane_roll(y, shift):
    return pltpu.roll(y, shift % LANES, 1)


def column_fold(rows, col):
    rows = list(rows)
    for a in range(4):
        edge = rows[4 * a + 3]
        left = jnp.where(col == 0, lane_roll(edge, -(COLS - 1)), lane_roll(edge, 1))
        total = rows[4 * a] + left
        rows[4 * a] = total
        rows[4 * a + 3] = jnp.where(
            col == COLS - 1, lane_roll(total, COLS - 1), lane_roll(total, -1)
        )
    return rows


def shift_right(y, col):
    return jnp.where(col == COLS - 1, lane_roll(y, COLS - 1), lane_roll(y, -1))


def row_fold(rows, up_rows, down_rows, row, col, rows_dev, elements):
    fill = jnp.zeros((rows[0].shape[0], LANES - 128), jnp.float32)
    halo_up = [jnp.concatenate([up_rows[b], fill], axis=1) for b in range(3)]
    halo_down = [
        lane_roll(jnp.concatenate([down_rows[b], fill], axis=1), elements - COLS) for b in range(3)
    ]
    halo_up.append(shift_right(halo_up[0], col))
    halo_down.append(shift_right(halo_down[0], col))
    out = list(rows)
    for b in range(4):
        from_up = jnp.where(row == 0, halo_up[b], lane_roll(rows[12 + b], COLS))
        out[b] = rows[b] + from_up
        from_down = jnp.where(row == rows_dev - 1, halo_down[b], lane_roll(rows[b], -COLS))
        out[12 + b] = rows[12 + b] + from_down
    return out


def mass_kernel(elements, m_ref, j_ref, r_ref, info_ref, mc_ref, mw_ref, last_ref, first_ref, mp_ref, mo_ref, jp_ref, rp_ref):
    info = info_ref[...]
    forward_order, _ = rotation_tables()
    zero = jnp.zeros((1, 128), jnp.float32)
    one = jnp.ones((1, 128), jnp.float32)
    for p in range(16):
        row = m_ref[pl.ds(p, 1), :]
        mp_ref[p, :, pl.ds(LANES - 128, 128)] = zero
        mp_ref[p, :, pl.ds(0, elements)] = row
        mo_ref[p, :, pl.ds(LANES - 128, 128)] = one
        mo_ref[p, :, pl.ds(0, elements)] = row
        rp_ref[p, :, pl.ds(LANES - 128, 128)] = zero
        rp_ref[p, :, pl.ds(0, elements)] = r_ref[pl.ds(p, 1), :]
        for k in range(4):
            jp_ref[k, p, :, pl.ds(LANES - 128, 128)] = zero
            jp_ref[k, p, :, pl.ds(0, elements)] = j_ref[k, pl.ds(p, 1), :]
    canon = select_rows([mp_ref[p] for p in range(16)], info[0:1], forward_order)
    rows = column_fold(canon, info[1:2])
    for q in range(16):
        mc_ref[q] = canon[q]
        mw_ref[q] = rows[q]
    for b in range(4):
        last_ref[b] = lane_roll(rows[12 + b], COLS - elements)[:, :128]
        first_ref[b] = rows[b][:, :128]


def mass_call(mass, jac, rot, info):
    elements = mass.shape[-1]
    small = jax.ShapeDtypeStruct((16, 1, LANES), jnp.float32)
    edge = jax.ShapeDtypeStruct((4, 1, 128), jnp.float32)
    return pl.pallas_call(
        functools.partial(mass_kernel, elements),
        interpret=INTERPRET,
        out_shape=[
            small,
            small,
            edge,
            edge,
            small,
            small,
            jax.ShapeDtypeStruct((4, 16, 1, LANES), jnp.float32),
            small,
        ],
    )(mass, jac, rot, info)


def adv_kernel(elements, with_mass, *refs):
    f_ref, g_ref, below_ref, jac_ref, rot_ref, mc_ref, info_ref = refs[:7]
    if with_mass:
        mlast_ref, mfirst_ref = refs[7:9]
    out_ref, last_ref, first_ref = refs[-3:]
    info = info_ref[...]
    rotation = info[0:1]
    col = info[1:2]
    forward_order, _ = rotation_tables()
    u = [f_ref[0, p] for p in range(16)]
    v = [f_ref[1, p] for p in range(16)]
    temp = [f_ref[2, p] for p in range(16)]
    dp = [f_ref[3, p] for p in range(16)]
    jac = [[jac_ref[k, p] for p in range(16)] for k in range(4)]
    energy = [
        (below_ref[p] + g_ref[p]) + 0.5 * (u[p] * u[p] + v[p] * v[p]) for p in range(16)
    ]
    e1 = first_rows(energy)
    e2 = second_rows(energy)
    it = [jac[0][p] * u[p] + jac[2][p] * v[p] for p in range(16)]
    lt = [jac[1][p] * u[p] + jac[3][p] * v[p] for p in range(16)]
    t1 = first_rows(temp)
    t2 = second_rows(temp)
    d1 = first_rows([dp[p] * it[p] for p in range(16)])
    d2 = second_rows([dp[p] * lt[p] for p in range(16)])
    advanced = []
    for p in range(16):
        rot = rot_ref[p]
        zonal_slope = jac[0][p] * e1[p] + jac[1][p] * e2[p]
        meridional_slope = jac[2][p] * e1[p] + jac[3][p] * e2[p]
        advanced.append(
            (
                u[p] + time_increment * (rot * v[p] - zonal_slope),
                v[p] - time_increment * (rot * u[p] + meridional_slope),
                temp[p] - time_increment * (it[p] * t1[p] + lt[p] * t2[p]),
                dp[p] - time_increment * (d1[p] + d2[p]),
            )
        )
    for f in range(4):
        rows = select_rows([advanced[p][f] for p in range(16)], rotation, forward_order)
        rows = column_fold([rows[q] * mc_ref[q] for q in range(16)], col)
        for q in range(16):
            out_ref[f, q] = rows[q]
        for b in range(3):
            last_ref[f, b] = lane_roll(rows[12 + b], COLS - elements)[:, :128]
            first_ref[f, b] = rows[b][:, :128]
    if with_mass:
        shape = last_ref.shape[2:]
        for b in range(3):
            last_ref[4, b] = jnp.broadcast_to(mlast_ref[b], shape)
            first_ref[4, b] = jnp.broadcast_to(mfirst_ref[b], shape)


def first_rows(rows):
    return [
        weighted_sum([(SLOPES[a, k], rows[4 * k + j]) for k in range(4)])
        for a in range(4)
        for j in range(4)
    ]


def second_rows(rows):
    return [
        weighted_sum([(SLOPES[a, k], rows[4 * i + k]) for k in range(4)])
        for i in range(4)
        for a in range(4)
    ]


def adv_call(fields, g0, below, jac, rot, mass_canon, info, elements, mass_edges=None):
    levels = fields.shape[2]
    steps = levels // CHUNK
    with_mass = mass_edges is not None
    width = 5 if with_mass else 4
    small = pl.BlockSpec((16, 1, LANES), lambda i: (0, 0, 0))
    edge = pl.BlockSpec((width, 3, CHUNK, 128), lambda i: (0, 0, i, 0))
    edge_shape = jax.ShapeDtypeStruct((width, 3, levels, 128), jnp.float32)
    in_specs = [
        pl.BlockSpec((4, 16, CHUNK, LANES), lambda i: (0, 0, i, 0)),
        pl.BlockSpec((16, CHUNK, LANES), lambda i: (0, i, 0)),
        small,
        pl.BlockSpec((4, 16, 1, LANES), lambda i: (0, 0, 0, 0)),
        small,
        small,
        pl.BlockSpec((8, LANES), lambda i: (0, 0)),
    ]
    args = [fields, g0, below, jac, rot, mass_canon, info]
    if with_mass:
        in_specs += [pl.BlockSpec((4, 1, 128), lambda i: (0, 0, 0))] * 2
        args += list(mass_edges)
    return pl.pallas_call(
        functools.partial(adv_kernel, elements, with_mass),
        interpret=INTERPRET,
        grid=(steps,),
        in_specs=in_specs,
        out_specs=[pl.BlockSpec((4, 16, CHUNK, LANES), lambda i: (0, 0, i, 0)), edge, edge],
        out_shape=[jax.ShapeDtypeStruct(fields.shape, jnp.float32), edge_shape, edge_shape],
    )(*args)


def fin_kernel(rows_dev, elements, with_cells, with_mass, *refs):
    refs = list(refs)
    w_ref, hu_ref, hd_ref = refs[:3]
    if with_mass:
        mw_ref = refs[3]
        refs = refs[4:]
    else:
        mt_ref = refs[3]
        refs = refs[4:]
    info_ref = refs.pop(0)
    if with_cells:
        prev_ref, m_ref = refs[:2]
        refs = refs[2:]
    out_ref, cm_ref = refs[:2]
    if with_cells:
        cell_ref = refs[2]
    info = info_ref[...]
    rotation = info[0:1]
    col = info[1:2]
    row = info[2:3]
    if with_mass:
        mass_total = row_fold(
            [mw_ref[q] for q in range(16)],
            [hu_ref[4, b][0:1] for b in range(3)],
            [hd_ref[4, b][0:1] for b in range(3)],
            row,
            col,
            rows_dev,
            elements,
        )
        lane_ok = lax.broadcasted_iota(jnp.int32, (1, LANES), 1) < elements
        mass_total = [jnp.where(lane_ok, m, 1.0) for m in mass_total]
        for q in range(16):
            refs[-1][q] = mass_total[q]
    else:
        mass_total = [mt_ref[q] for q in range(16)]
    lane = lax.broadcasted_iota(jnp.int32, (1, LANES), 1)
    valid = lane < elements
    _, backward_order = rotation_tables()
    groups = [(0, 1, 4, 5), (2, 3, 6, 7), (8, 9, 12, 13), (10, 11, 14, 15)]
    for f in range(4):
        out = row_fold(
            [w_ref[f, q] for q in range(16)],
            [hu_ref[f, b] for b in range(3)],
            [hd_ref[f, b] for b in range(3)],
            row,
            col,
            rows_dev,
            elements,
        )
        out = [out[q] / mass_total[q] for q in range(16)]
        new = select_rows(out, rotation, backward_order)
        new = [jnp.where(valid, new[p], 0.0) for p in range(16)]
        for p in range(16):
            out_ref[f, p] = new[p]
        if f == 3:
            for p in range(16):
                part = jnp.sum(new[p], axis=0, keepdims=True)

                @pl.when(pl.program_id(0) == 0)
                def _():
                    cm_ref[p] = part

                @pl.when(pl.program_id(0) > 0)
                def _():
                    cm_ref[p] = cm_ref[p] + part
        if with_cells:
            average = [(prev_ref[f, p] + new[p]) / SUBSTEPS for p in range(16)]
            for c, group in enumerate(groups):
                m = [m_ref[p] for p in group]
                summed = (m[0] * average[group[0]] + m[1] * average[group[1]]) + (
                    m[2] * average[group[2]] + m[3] * average[group[3]]
                )
                area = (m[0] + m[1]) + (m[2] + m[3])
                cell_ref[c, f] = summed / area


def fin_call(w, halo_up, halo_down, mass_parts, info, rows_dev, elements, prev=None, mass=None):
    levels = w.shape[2]
    steps = levels // CHUNK
    block = pl.BlockSpec((4, 16, CHUNK, LANES), lambda i: (0, 0, i, 0))
    halo = pl.BlockSpec((halo_up.shape[0], 3, CHUNK, 128), lambda i: (0, 0, i, 0))
    small = pl.BlockSpec((16, 1, LANES), lambda i: (0, 0, 0))
    with_cells = prev is not None
    with_mass = halo_up.shape[0] == 5
    in_specs = [block, halo, halo, small]
    args = [w, halo_up, halo_down, mass_parts]
    in_specs.append(pl.BlockSpec((8, LANES), lambda i: (0, 0)))
    args.append(info)
    out_specs = [block, small]
    out_shape = [
        jax.ShapeDtypeStruct(w.shape, jnp.float32),
        jax.ShapeDtypeStruct((16, 1, LANES), jnp.float32),
    ]
    if with_cells:
        in_specs += [block, small]
        args += [prev, mass]
        out_specs.append(pl.BlockSpec((4, 4, CHUNK, LANES), lambda i: (0, 0, i, 0)))
        out_shape.append(jax.ShapeDtypeStruct((4, 4, levels, LANES), jnp.float32))
    if with_mass:
        out_specs.append(small)
        out_shape.append(jax.ShapeDtypeStruct((16, 1, LANES), jnp.float32))
    return pl.pallas_call(
        functools.partial(fin_kernel, rows_dev, elements, with_cells, with_mass),
        interpret=INTERPRET,
        grid=(steps,),
        in_specs=in_specs,
        out_specs=out_specs,
        out_shape=out_shape,
    )(*args)


def edge_exchange(last, first):
    seg_count = lax.axis_size("seg")
    up = [(i, (i + 1) % seg_count) for i in range(seg_count)]
    down = [(j, i) for i, j in up]
    return lax.ppermute(last, "seg", up), lax.ppermute(first, "seg", down)


def halo_exchange(w, elements):
    seg_count = lax.axis_size("seg")
    up = [(i, (i + 1) % seg_count) for i in range(seg_count)]
    down = [(j, i) for i, j in up]
    last = w[..., 12:16, :, elements - COLS : elements]
    first = w[..., 0:4, :, 0:COLS]
    prev_last = lax.ppermute(last, "seg", up)
    next_first = lax.ppermute(first, "seg", down)
    widths = [(0, 0)] * (w.ndim - 1)
    halo_up = jnp.pad(prev_last, widths + [(0, LANES - COLS)])
    halo_down = jnp.pad(next_first, widths + [(elements - COLS, LANES - elements)])
    return halo_up, halo_down


def mass_dss(mass_canon_rows, info, rows_dev, elements):
    col = info[1:2]
    row = info[2:3]
    rows = list(mass_canon_rows)
    for a in range(4):
        edge = rows[4 * a + 3]
        left = jnp.where(col == 0, jnp.roll(edge, -(COLS - 1), -1), jnp.roll(edge, 1, -1))
        total = rows[4 * a] + left
        rows[4 * a] = total
        rows[4 * a + 3] = jnp.where(
            col == COLS - 1, jnp.roll(total, COLS - 1, -1), jnp.roll(total, -1, -1)
        )
    w = jnp.stack(rows)
    halo_up, halo_down = halo_exchange(w, elements)
    out = list(rows)
    for b in range(4):
        from_up = jnp.where(row == 0, halo_up[b], jnp.roll(rows[12 + b], COLS, -1))
        out[b] = rows[b] + from_up
        from_down = jnp.where(row == rows_dev - 1, halo_down[b], jnp.roll(rows[b], -COLS, -1))
        out[12 + b] = rows[12 + b] + from_down
    total = jnp.stack(out)
    lane = jnp.arange(LANES)
    return jnp.where(lane < elements, total, 1.0)


def prep_kernel(elements, vel_ref, temp_ref, dp_ref, out_ref, cm_ref):
    chunk = out_ref.shape[2]
    zeros = jnp.zeros((chunk, 128), jnp.float32)
    blocks = [vel_ref[0], vel_ref[1], temp_ref[...], dp_ref[...]]
    for f, block in enumerate(blocks):
        grouped = block.reshape(chunk, 16, elements)
        for p in range(16):
            rows = grouped[:, p, :]
            out_ref[f, p, :, pl.ds(LANES - 128, 128)] = zeros
            out_ref[f, p, :, pl.ds(0, elements)] = rows
            if f == 3:
                part = jnp.sum(out_ref[f, p], axis=0, keepdims=True)

                @pl.when(pl.program_id(0) == 0)
                def _():
                    cm_ref[p] = part

                @pl.when(pl.program_id(0) > 0)
                def _():
                    cm_ref[p] = cm_ref[p] + part


def prep_call(velocity_pair, thermal_reading, layer_depth):
    levels, points, elements = thermal_reading.shape
    steps = levels // CHUNK
    rows = CHUNK * points
    vel = velocity_pair.reshape(2, levels * points, elements)
    temp = thermal_reading.reshape(levels * points, elements)
    dp = layer_depth.reshape(levels * points, elements)
    return pl.pallas_call(
        functools.partial(prep_kernel, elements),
        interpret=INTERPRET,
        grid=(steps,),
        in_specs=[
            pl.BlockSpec((2, rows, elements), lambda i: (0, i, 0)),
            pl.BlockSpec((rows, elements), lambda i: (i, 0)),
            pl.BlockSpec((rows, elements), lambda i: (i, 0)),
        ],
        out_specs=[
            pl.BlockSpec((4, 16, CHUNK, LANES), lambda i: (0, 0, i, 0)),
            pl.BlockSpec((16, 1, LANES), lambda i: (0, 0, 0)),
        ],
        out_shape=[
            jax.ShapeDtypeStruct((4, 16, levels, LANES), jnp.float32),
            jax.ShapeDtypeStruct((16, 1, LANES), jnp.float32),
        ],
    )(vel, temp, dp)


def local(
    velocity_pair,
    thermal_reading,
    layer_depth,
    jacobian_terms,
    rotation_frequency,
    integration_mass,
    shared_vertex_label,
    column_owner_slot,
):
    levels_dev = thermal_reading.shape[0]
    elements = thermal_reading.shape[2]
    seg_count = lax.axis_size("seg")
    lev_count = lax.axis_size("lev")
    rows_dev = elements // COLS
    node_cols = 3 * COLS
    first_row = 3 * rows_dev * lax.axis_index("seg")
    grid_rows = 3 * rows_dev * seg_count
    corner_ids = shared_vertex_label[0]
    element_pos = jnp.arange(elements)
    row_offset = (corner_ids // node_cols - first_row) % grid_rows - 3 * (element_pos // COLS)
    col_offset = (corner_ids % node_cols - 3 * (element_pos % COLS)) % node_cols
    rotation = jnp.where(
        row_offset == 0, jnp.where(col_offset == 0, 0, 1), jnp.where(col_offset == 3, 2, 3)
    )
    info = lane_info(rotation, elements)
    forward_order, _ = rotation_tables()

    fields, column_parts = prep_call(velocity_pair, thermal_reading, layer_depth)
    (
        mass_canon,
        mass_folded,
        mass_last,
        mass_first,
        mass,
        mass_one,
        jac,
        rot,
    ) = mass_call(integration_mass, jacobian_terms, rotation_frequency, info)
    mass_parts = mass_folded
    mass_edges = (mass_last, mass_first)
    column_mass = column_parts
    previous = None
    cells = None
    for substep in range(SUBSTEPS):
        above = carried_in(column_mass, "lev", False)
        g0, group_height = term_call(fields, above)
        below = carried_in(group_height, "lev", True)
        w, last, first = adv_call(
            fields, g0, below, jac, rot, mass_canon, info, elements, mass_edges
        )
        mass_edges = None
        halo_up, halo_down = edge_exchange(last, first)
        outs = fin_call(
            w,
            halo_up,
            halo_down,
            mass_parts,
            info,
            rows_dev,
            elements,
            previous if substep == SUBSTEPS - 1 else None,
            mass_one,
        )
        fields, column_parts = outs[:2]
        if substep == SUBSTEPS - 1:
            cells = outs[2]
        if substep == 0:
            mass_parts = outs[-1]
        previous = fields
        column_mass = column_parts
    channels = 4 * levels_dev
    cell_values = cells[..., :elements].reshape(4, channels, elements)
    payload = jnp.transpose(cell_values, (0, 2, 1)).reshape(4 * elements, channels)
    dev_count = seg_count * lev_count
    own_cols = 4 * elements * seg_count // dev_count
    per_pair = own_cols // seg_count
    capacity = per_pair + per_pair // 2
    targets = column_owner_slot.reshape(-1)
    owner_index = targets // own_cols
    slot_index = targets % own_cols
    cell_count = targets.shape[0]
    cell_pos = jnp.arange(cell_count)
    same_owner = owner_index[:, None] == owner_index[None, :]
    earlier = cell_pos[:, None] < cell_pos[None, :]
    rank = jnp.sum(jnp.logical_and(same_owner, earlier).astype(jnp.int32), axis=0)
    destination = owner_index * capacity + rank
    slots = jnp.arange(dev_count * capacity)
    code = cell_pos * (own_cols + 1) + slot_index + 1
    match = destination[:, None] == slots[None, :]
    found = jnp.sum(jnp.where(match, code[:, None], 0), axis=0)
    has = found > 0
    source_cell = jnp.maximum(found - 1, 0) // (own_cols + 1)
    source_pos = jnp.maximum(found - 1, 0) % (own_cols + 1)
    outgoing = payload[source_cell].reshape(dev_count, capacity, channels)
    ids = jnp.where(has, source_pos, -1).reshape(dev_count, capacity)
    received_ids = lax.all_to_all(ids, ("seg", "lev"), split_axis=0, concat_axis=0, tiled=True)
    flat = jnp.arange(dev_count * capacity).reshape(dev_count, capacity)
    source_lev = (jnp.arange(dev_count) % lev_count)[:, None]
    positions = jnp.arange(own_cols)
    picks = []
    for group in range(lev_count):
        hit = jnp.logical_and(
            received_ids[:, :, None] == positions[None, None, :], (source_lev == group)[:, :, None]
        )
        picks.append(jnp.sum(jnp.where(hit, flat[:, :, None], 0), axis=(0, 1)))
    received = lax.all_to_all(outgoing, ("seg", "lev"), split_axis=0, concat_axis=0, tiled=True)
    arrived = received.reshape(dev_count * capacity, channels)[jnp.stack(picks)]
    arrived = arrived.reshape(lev_count, own_cols, 4, levels_dev).transpose(2, 0, 3, 1)
    phys_state = arrived.reshape(4, lev_count * levels_dev, own_cols)
    mean_thickness = jnp.mean(phys_state[3], axis=0)
    dyn_state = jnp.transpose(fields[..., :elements], (0, 2, 1, 3))
    return (dyn_state, phys_state, mean_thickness)


def solution(mesh):
    in_specs = (
        P(None, "lev", None, "seg"),
        P("lev", None, "seg"),
        P("lev", None, "seg"),
        P(None, None, "seg"),
        P(None, "seg"),
        P(None, "seg"),
        P(None, "seg"),
        P(None, "seg"),
    )
    out_specs = (P(None, "lev", None, "seg"), P(None, None, ("seg", "lev")), P(("seg", "lev")))
    return jax.shard_map(local, mesh=mesh, in_specs=in_specs, out_specs=out_specs, check_vma=False)
```

```python
import functools

import jax
import jax.numpy as jnp
import numpy as np
from jax import lax
from jax.experimental import pallas as pl
from jax.experimental.pallas import tpu as pltpu
from jax.sharding import PartitionSpec as P

COLS = 120
SUBSTEPS = 2


top_pressure = 10.0
time_increment = 0.05


def gll_slopes():
    root_five = np.sqrt(5.0)
    gll_nodes = [-1.0, -1.0 / root_five, 1.0 / root_five, 1.0]
    legendre_values = [-1.0, 1.0 / root_five, -1.0 / root_five, 1.0]
    slopes = np.zeros((4, 4))
    for row_node in range(4):
        for column in range(4):
            if row_node != column:
                slopes[row_node, column] = (
                    legendre_values[row_node]
                    / legendre_values[column]
                    / (gll_nodes[row_node] - gll_nodes[column])
                )
    slopes[0, 0] = -3.0
    slopes[3, 3] = 3.0
    return slopes


SLOPES = gll_slopes().astype(np.float32)


def rotation_tables():
    forward = np.zeros((4, 16), np.int32)
    for first_pos in range(4):
        for second_pos in range(4):
            canonical = 4 * first_pos + second_pos
            forward[0, canonical] = 4 * first_pos + second_pos
            forward[1, canonical] = 4 * (3 - second_pos) + first_pos
            forward[2, canonical] = 4 * (3 - first_pos) + (3 - second_pos)
            forward[3, canonical] = 4 * second_pos + 3 - first_pos
    backward = np.argsort(forward, axis=1).astype(np.int32)
    return (forward, backward)


def weighted_sum(terms):
    acc = None
    for coef, value in terms:
        if coef == 0.0:
            continue
        part = jnp.float32(coef) * value
        acc = part if acc is None else acc + part
    return acc


def first_deriv(f):
    return jnp.stack(
        [
            weighted_sum([(SLOPES[a, k], f[4 * k + j]) for k in range(4)])
            for a in range(4)
            for j in range(4)
        ]
    )


def second_deriv(f):
    return jnp.stack(
        [
            weighted_sum([(SLOPES[a, k], f[4 * i + k]) for k in range(4)])
            for i in range(4)
            for a in range(4)
        ]
    )


def carried_in(part, axis, reverse):
    count = lax.axis_size(axis)
    place = lax.axis_index(axis)
    gathered = lax.all_gather(part, axis)
    index = jnp.arange(count).reshape((count,) + (1,) * part.ndim)
    chosen = index > place if reverse else index < place
    return jnp.sum(jnp.where(chosen, gathered, jnp.zeros_like(gathered)), axis=0)


def site_potential_energy(thermal_reading, layer_depth):
    column_mass = jnp.sum(layer_depth, axis=1)
    above_sum = carried_in(column_mass, "lev", False)
    layer_midpoint_load = (
        top_pressure + above_sum[:, None, :] + jnp.cumsum(layer_depth, axis=1) - 0.5 * layer_depth
    )
    surface_change_rate = thermal_reading * layer_depth / layer_midpoint_load
    group_height = jnp.sum(surface_change_rate, axis=1)
    below_sum = carried_in(group_height, "lev", True)
    return (
        below_sum[:, None, :]
        + lax.cumsum(surface_change_rate, axis=1, reverse=True)
        - 0.5 * surface_change_rate
    )


def tendency_step(u, v, temp, dp, geopotential, jac, rot):
    energy = geopotential + 0.5 * (u * u + v * v)
    energy_first = first_deriv(energy)
    energy_second = second_deriv(energy)
    zonal_slope = jac[0] * energy_first + jac[1] * energy_second
    meridional_slope = jac[2] * energy_first + jac[3] * energy_second
    initial_transport = jac[0] * u + jac[2] * v
    latter_transport = jac[1] * u + jac[3] * v
    advect_with_motion = initial_transport * first_deriv(temp) + latter_transport * second_deriv(
        temp
    )
    distribute_onto_vertices = first_deriv(dp * initial_transport) + second_deriv(
        dp * latter_transport
    )
    return (
        u + time_increment * (rot * v - zonal_slope),
        v - time_increment * (rot * u + meridional_slope),
        temp - time_increment * advect_with_motion,
        dp - time_increment * distribute_onto_vertices,
    )


def reorder(values, rotation, table):
    rows = []
    for q in range(16):
        pick = values[int(table[3, q])]
        for w in (2, 1, 0):
            pick = jnp.where(rotation == w, values[int(table[w, q])], pick)
        rows.append(pick)
    return jnp.stack(rows)


def node_sum(canon, col, row, rows_dev):
    elements = canon.shape[-1]

    def roll(y, shift):
        return jnp.roll(y, shift, axis=-1)

    rows = [canon[q] for q in range(16)]
    for a in range(4):
        left = jnp.where(col == 0, roll(rows[4 * a + 3], -(COLS - 1)), roll(rows[4 * a + 3], 1))
        total = rows[4 * a] + left
        rows[4 * a] = total
        rows[4 * a + 3] = jnp.where(col == COLS - 1, roll(total, COLS - 1), roll(total, -1))
    seg_count = lax.axis_size("seg")
    up = [(i, (i + 1) % seg_count) for i in range(seg_count)]
    down = [(j, i) for i, j in up]
    last = jnp.stack([rows[12 + b][:, elements - COLS :] for b in range(4)])
    first = jnp.stack([rows[b][:, :COLS] for b in range(4)])
    prev_last = lax.ppermute(last, "seg", up)
    next_first = lax.ppermute(first, "seg", down)
    pad = jnp.zeros(prev_last.shape[1:-1] + (elements - COLS,), canon.dtype)
    out = list(rows)
    for b in range(4):
        halo_up = jnp.concatenate([prev_last[b], pad], axis=-1)
        from_up = jnp.where(row == 0, halo_up, roll(rows[12 + b], COLS))
        out[b] = rows[b] + from_up
        halo_down = jnp.concatenate([pad, next_first[b]], axis=-1)
        from_down = jnp.where(row == rows_dev - 1, halo_down, roll(rows[b], -COLS))
        out[12 + b] = rows[12 + b] + from_down
    return jnp.stack(out)


LANES = 512
CHUNK = 16
INTERPRET = None


def lane_info(rotation, elements):
    element_pos = jnp.arange(elements)
    info = jnp.stack(
        [rotation, element_pos % COLS, element_pos // COLS]
        + [jnp.zeros_like(rotation)] * 5
    ).astype(jnp.int32)
    return jnp.pad(info, ((0, 0), (0, LANES - elements)), constant_values=-1)


def pad_lanes(x, value=0.0):
    widths = [(0, 0)] * (x.ndim - 1) + [(0, LANES - x.shape[-1])]
    return jnp.pad(x, widths, constant_values=value)


def select_rows(values, rotation, table):
    rows = []
    for q in range(16):
        pick = values[int(table[3, q])]
        for w in (2, 1, 0):
            pick = jnp.where(rotation == w, values[int(table[w, q])], pick)
        rows.append(pick)
    return rows


def term_kernel(levels, f_ref, above_ref, g_ref, gh_ref):
    level = lax.broadcasted_iota(jnp.int32, (levels, LANES), 0)
    for p in range(f_ref.shape[1]):
        temp = f_ref[0, p]
        dp = f_ref[1, p]
        cum = dp
        shift = 1
        while shift < levels:
            cum = cum + jnp.where(level >= shift, pltpu.roll(cum, shift, 0), 0.0)
            shift *= 2
        load = top_pressure + above_ref[p] + cum - 0.5 * dp
        term = temp * dp / load
        gh_ref[p] = jnp.sum(term, axis=0, keepdims=True)
        rcum = term
        shift = 1
        while shift < levels:
            rcum = rcum + jnp.where(
                level + shift < levels, pltpu.roll(rcum, levels - shift, 0), 0.0
            )
            shift *= 2
        g_ref[p] = rcum - 0.5 * term


def term_call(fields, above):
    levels = fields.shape[2]
    group = 16
    return pl.pallas_call(
        functools.partial(term_kernel, levels),
        interpret=INTERPRET,
        grid=(16 // group,),
        in_specs=[
            pl.BlockSpec((2, group, levels, LANES), lambda i: (1, i, 0, 0)),
            pl.BlockSpec((group, 1, LANES), lambda i: (i, 0, 0)),
        ],
        out_specs=[
            pl.BlockSpec((group, levels, LANES), lambda i: (i, 0, 0)),
            pl.BlockSpec((group, 1, LANES), lambda i: (i, 0, 0)),
        ],
        out_shape=[
            jax.ShapeDtypeStruct((16, levels, LANES), jnp.float32),
            jax.ShapeDtypeStruct((16, 1, LANES), jnp.float32),
        ],
    )(fields, above)


def lane_roll(y, shift):
    return pltpu.roll(y, shift % LANES, 1)


def column_fold(rows, col):
    rows = list(rows)
    for a in range(4):
        edge = rows[4 * a + 3]
        left = jnp.where(col == 0, lane_roll(edge, -(COLS - 1)), lane_roll(edge, 1))
        total = rows[4 * a] + left
        rows[4 * a] = total
        rows[4 * a + 3] = jnp.where(
            col == COLS - 1, lane_roll(total, COLS - 1), lane_roll(total, -1)
        )
    return rows


def shift_right(y, col):
    return jnp.where(col == COLS - 1, lane_roll(y, COLS - 1), lane_roll(y, -1))


def row_fold(rows, up_rows, down_rows, row, col, rows_dev, elements):
    fill = jnp.zeros((rows[0].shape[0], LANES - 128), jnp.float32)
    halo_up = [jnp.concatenate([up_rows[b], fill], axis=1) for b in range(3)]
    halo_down = [
        lane_roll(jnp.concatenate([down_rows[b], fill], axis=1), elements - COLS) for b in range(3)
    ]
    halo_up.append(shift_right(halo_up[0], col))
    halo_down.append(shift_right(halo_down[0], col))
    out = list(rows)
    for b in range(4):
        from_up = jnp.where(row == 0, halo_up[b], lane_roll(rows[12 + b], COLS))
        out[b] = rows[b] + from_up
        from_down = jnp.where(row == rows_dev - 1, halo_down[b], lane_roll(rows[b], -COLS))
        out[12 + b] = rows[12 + b] + from_down
    return out


def mass_kernel(elements, m_ref, j_ref, r_ref, info_ref, mc_ref, mw_ref, last_ref, first_ref, mp_ref, mo_ref, jp_ref, rp_ref):
    info = info_ref[...]
    forward_order, _ = rotation_tables()
    zero = jnp.zeros((1, 128), jnp.float32)
    one = jnp.ones((1, 128), jnp.float32)
    for p in range(16):
        row = m_ref[pl.ds(p, 1), :]
        mp_ref[p, :, pl.ds(LANES - 128, 128)] = zero
        mp_ref[p, :, pl.ds(0, elements)] = row
        mo_ref[p, :, pl.ds(LANES - 128, 128)] = one
        mo_ref[p, :, pl.ds(0, elements)] = row
        rp_ref[p, :, pl.ds(LANES - 128, 128)] = zero
        rp_ref[p, :, pl.ds(0, elements)] = r_ref[pl.ds(p, 1), :]
        for k in range(4):
            jp_ref[k, p, :, pl.ds(LANES - 128, 128)] = zero
            jp_ref[k, p, :, pl.ds(0, elements)] = j_ref[k, pl.ds(p, 1), :]
    canon = select_rows([mp_ref[p] for p in range(16)], info[0:1], forward_order)
    rows = column_fold(canon, info[1:2])
    for q in range(16):
        mc_ref[q] = canon[q]
        mw_ref[q] = rows[q]
    for b in range(4):
        last_ref[b] = lane_roll(rows[12 + b], COLS - elements)[:, :128]
        first_ref[b] = rows[b][:, :128]


def mass_call(mass, jac, rot, info):
    elements = mass.shape[-1]
    small = jax.ShapeDtypeStruct((16, 1, LANES), jnp.float32)
    edge = jax.ShapeDtypeStruct((4, 1, 128), jnp.float32)
    return pl.pallas_call(
        functools.partial(mass_kernel, elements),
        interpret=INTERPRET,
        out_shape=[
            small,
            small,
            edge,
            edge,
            small,
            small,
            jax.ShapeDtypeStruct((4, 16, 1, LANES), jnp.float32),
            small,
        ],
    )(mass, jac, rot, info)


def adv_kernel(elements, with_mass, *refs):
    f_ref, g_ref, below_ref, jac_ref, rot_ref, mc_ref, info_ref = refs[:7]
    if with_mass:
        mlast_ref, mfirst_ref = refs[7:9]
    out_ref, last_ref, first_ref = refs[-3:]
    info = info_ref[...]
    rotation = info[0:1]
    col = info[1:2]
    forward_order, _ = rotation_tables()
    u = [f_ref[0, p] for p in range(16)]
    v = [f_ref[1, p] for p in range(16)]
    temp = [f_ref[2, p] for p in range(16)]
    dp = [f_ref[3, p] for p in range(16)]
    jac = [[jac_ref[k, p] for p in range(16)] for k in range(4)]
    energy = [
        (below_ref[p] + g_ref[p]) + 0.5 * (u[p] * u[p] + v[p] * v[p]) for p in range(16)
    ]
    e1 = first_rows(energy)
    e2 = second_rows(energy)
    it = [jac[0][p] * u[p] + jac[2][p] * v[p] for p in range(16)]
    lt = [jac[1][p] * u[p] + jac[3][p] * v[p] for p in range(16)]
    t1 = first_rows(temp)
    t2 = second_rows(temp)
    d1 = first_rows([dp[p] * it[p] for p in range(16)])
    d2 = second_rows([dp[p] * lt[p] for p in range(16)])
    advanced = []
    for p in range(16):
        rot = rot_ref[p]
        zonal_slope = jac[0][p] * e1[p] + jac[1][p] * e2[p]
        meridional_slope = jac[2][p] * e1[p] + jac[3][p] * e2[p]
        advanced.append(
            (
                u[p] + time_increment * (rot * v[p] - zonal_slope),
                v[p] - time_increment * (rot * u[p] + meridional_slope),
                temp[p] - time_increment * (it[p] * t1[p] + lt[p] * t2[p]),
                dp[p] - time_increment * (d1[p] + d2[p]),
            )
        )
    for f in range(4):
        rows = select_rows([advanced[p][f] for p in range(16)], rotation, forward_order)
        rows = column_fold([rows[q] * mc_ref[q] for q in range(16)], col)
        for q in range(16):
            out_ref[f, q] = rows[q]
        for b in range(3):
            last_ref[f, b] = lane_roll(rows[12 + b], COLS - elements)[:, :128]
            first_ref[f, b] = rows[b][:, :128]
    if with_mass:
        shape = last_ref.shape[2:]
        for b in range(3):
            last_ref[4, b] = jnp.broadcast_to(mlast_ref[b], shape)
            first_ref[4, b] = jnp.broadcast_to(mfirst_ref[b], shape)


def first_rows(rows):
    return [
        weighted_sum([(SLOPES[a, k], rows[4 * k + j]) for k in range(4)])
        for a in range(4)
        for j in range(4)
    ]


def second_rows(rows):
    return [
        weighted_sum([(SLOPES[a, k], rows[4 * i + k]) for k in range(4)])
        for i in range(4)
        for a in range(4)
    ]


def adv_call(fields, g0, below, jac, rot, mass_canon, info, elements, mass_edges=None):
    levels = fields.shape[2]
    steps = levels // CHUNK
    with_mass = mass_edges is not None
    width = 5 if with_mass else 4
    small = pl.BlockSpec((16, 1, LANES), lambda i: (0, 0, 0))
    edge = pl.BlockSpec((width, 3, CHUNK, 128), lambda i: (0, 0, i, 0))
    edge_shape = jax.ShapeDtypeStruct((width, 3, levels, 128), jnp.float32)
    in_specs = [
        pl.BlockSpec((4, 16, CHUNK, LANES), lambda i: (0, 0, i, 0)),
        pl.BlockSpec((16, CHUNK, LANES), lambda i: (0, i, 0)),
        small,
        pl.BlockSpec((4, 16, 1, LANES), lambda i: (0, 0, 0, 0)),
        small,
        small,
        pl.BlockSpec((8, LANES), lambda i: (0, 0)),
    ]
    args = [fields, g0, below, jac, rot, mass_canon, info]
    if with_mass:
        in_specs += [pl.BlockSpec((4, 1, 128), lambda i: (0, 0, 0))] * 2
        args += list(mass_edges)
    return pl.pallas_call(
        functools.partial(adv_kernel, elements, with_mass),
        interpret=INTERPRET,
        grid=(steps,),
        in_specs=in_specs,
        out_specs=[pl.BlockSpec((4, 16, CHUNK, LANES), lambda i: (0, 0, i, 0)), edge, edge],
        out_shape=[jax.ShapeDtypeStruct(fields.shape, jnp.float32), edge_shape, edge_shape],
    )(*args)


def fin_kernel(rows_dev, elements, with_cells, with_mass, *refs):
    refs = list(refs)
    w_ref, hu_ref, hd_ref = refs[:3]
    if with_mass:
        mw_ref = refs[3]
        refs = refs[4:]
    else:
        mt_ref = refs[3]
        refs = refs[4:]
    info_ref = refs.pop(0)
    if with_cells:
        prev_ref, m_ref = refs[:2]
        refs = refs[2:]
    out_ref, cm_ref = refs[:2]
    if with_cells:
        cell_ref = refs[2]
    info = info_ref[...]
    rotation = info[0:1]
    col = info[1:2]
    row = info[2:3]
    if with_mass:
        mass_total = row_fold(
            [mw_ref[q] for q in range(16)],
            [hu_ref[4, b][0:1] for b in range(3)],
            [hd_ref[4, b][0:1] for b in range(3)],
            row,
            col,
            rows_dev,
            elements,
        )
        lane_ok = lax.broadcasted_iota(jnp.int32, (1, LANES), 1) < elements
        mass_total = [jnp.where(lane_ok, m, 1.0) for m in mass_total]
        for q in range(16):
            refs[-1][q] = mass_total[q]
    else:
        mass_total = [mt_ref[q] for q in range(16)]
    lane = lax.broadcasted_iota(jnp.int32, (1, LANES), 1)
    valid = lane < elements
    _, backward_order = rotation_tables()
    groups = [(0, 1, 4, 5), (2, 3, 6, 7), (8, 9, 12, 13), (10, 11, 14, 15)]
    for f in range(4):
        out = row_fold(
            [w_ref[f, q] for q in range(16)],
            [hu_ref[f, b] for b in range(3)],
            [hd_ref[f, b] for b in range(3)],
            row,
            col,
            rows_dev,
            elements,
        )
        out = [out[q] / mass_total[q] for q in range(16)]
        new = select_rows(out, rotation, backward_order)
        new = [jnp.where(valid, new[p], 0.0) for p in range(16)]
        for p in range(16):
            out_ref[f, p] = new[p]
        if f == 3:
            for p in range(16):
                part = jnp.sum(new[p], axis=0, keepdims=True)

                @pl.when(pl.program_id(0) == 0)
                def _():
                    cm_ref[p] = part

                @pl.when(pl.program_id(0) > 0)
                def _():
                    cm_ref[p] = cm_ref[p] + part
        if with_cells:
            average = [(prev_ref[f, p] + new[p]) / SUBSTEPS for p in range(16)]
            for c, group in enumerate(groups):
                m = [m_ref[p] for p in group]
                summed = (m[0] * average[group[0]] + m[1] * average[group[1]]) + (
                    m[2] * average[group[2]] + m[3] * average[group[3]]
                )
                area = (m[0] + m[1]) + (m[2] + m[3])
                cell_ref[c, f] = summed / area


def fin_call(w, halo_up, halo_down, mass_parts, info, rows_dev, elements, prev=None, mass=None):
    levels = w.shape[2]
    steps = levels // CHUNK
    block = pl.BlockSpec((4, 16, CHUNK, LANES), lambda i: (0, 0, i, 0))
    halo = pl.BlockSpec((halo_up.shape[0], 3, CHUNK, 128), lambda i: (0, 0, i, 0))
    small = pl.BlockSpec((16, 1, LANES), lambda i: (0, 0, 0))
    with_cells = prev is not None
    with_mass = halo_up.shape[0] == 5
    in_specs = [block, halo, halo, small]
    args = [w, halo_up, halo_down, mass_parts]
    in_specs.append(pl.BlockSpec((8, LANES), lambda i: (0, 0)))
    args.append(info)
    out_specs = [block, small]
    out_shape = [
        jax.ShapeDtypeStruct(w.shape, jnp.float32),
        jax.ShapeDtypeStruct((16, 1, LANES), jnp.float32),
    ]
    if with_cells:
        in_specs += [block, small]
        args += [prev, mass]
        out_specs.append(pl.BlockSpec((4, 4, CHUNK, LANES), lambda i: (0, 0, i, 0)))
        out_shape.append(jax.ShapeDtypeStruct((4, 4, levels, LANES), jnp.float32))
    if with_mass:
        out_specs.append(small)
        out_shape.append(jax.ShapeDtypeStruct((16, 1, LANES), jnp.float32))
    return pl.pallas_call(
        functools.partial(fin_kernel, rows_dev, elements, with_cells, with_mass),
        interpret=INTERPRET,
        grid=(steps,),
        in_specs=in_specs,
        out_specs=out_specs,
        out_shape=out_shape,
    )(*args)


def edge_exchange(last, first):
    seg_count = lax.axis_size("seg")
    up = [(i, (i + 1) % seg_count) for i in range(seg_count)]
    down = [(j, i) for i, j in up]
    return lax.ppermute(last, "seg", up), lax.ppermute(first, "seg", down)


def halo_exchange(w, elements):
    seg_count = lax.axis_size("seg")
    up = [(i, (i + 1) % seg_count) for i in range(seg_count)]
    down = [(j, i) for i, j in up]
    last = w[..., 12:16, :, elements - COLS : elements]
    first = w[..., 0:4, :, 0:COLS]
    prev_last = lax.ppermute(last, "seg", up)
    next_first = lax.ppermute(first, "seg", down)
    widths = [(0, 0)] * (w.ndim - 1)
    halo_up = jnp.pad(prev_last, widths + [(0, LANES - COLS)])
    halo_down = jnp.pad(next_first, widths + [(elements - COLS, LANES - elements)])
    return halo_up, halo_down


def mass_dss(mass_canon_rows, info, rows_dev, elements):
    col = info[1:2]
    row = info[2:3]
    rows = list(mass_canon_rows)
    for a in range(4):
        edge = rows[4 * a + 3]
        left = jnp.where(col == 0, jnp.roll(edge, -(COLS - 1), -1), jnp.roll(edge, 1, -1))
        total = rows[4 * a] + left
        rows[4 * a] = total
        rows[4 * a + 3] = jnp.where(
            col == COLS - 1, jnp.roll(total, COLS - 1, -1), jnp.roll(total, -1, -1)
        )
    w = jnp.stack(rows)
    halo_up, halo_down = halo_exchange(w, elements)
    out = list(rows)
    for b in range(4):
        from_up = jnp.where(row == 0, halo_up[b], jnp.roll(rows[12 + b], COLS, -1))
        out[b] = rows[b] + from_up
        from_down = jnp.where(row == rows_dev - 1, halo_down[b], jnp.roll(rows[b], -COLS, -1))
        out[12 + b] = rows[12 + b] + from_down
    total = jnp.stack(out)
    lane = jnp.arange(LANES)
    return jnp.where(lane < elements, total, 1.0)


def prep_kernel(elements, vel_ref, temp_ref, dp_ref, out_ref, cm_ref):
    chunk = out_ref.shape[2]
    zeros = jnp.zeros((chunk, 128), jnp.float32)
    blocks = [vel_ref[0], vel_ref[1], temp_ref[...], dp_ref[...]]
    for f, block in enumerate(blocks):
        grouped = block.reshape(chunk, 16, elements)
        for p in range(16):
            rows = grouped[:, p, :]
            out_ref[f, p, :, pl.ds(LANES - 128, 128)] = zeros
            out_ref[f, p, :, pl.ds(0, elements)] = rows
            if f == 3:
                part = jnp.sum(out_ref[f, p], axis=0, keepdims=True)

                @pl.when(pl.program_id(0) == 0)
                def _():
                    cm_ref[p] = part

                @pl.when(pl.program_id(0) > 0)
                def _():
                    cm_ref[p] = cm_ref[p] + part


def prep_call(velocity_pair, thermal_reading, layer_depth):
    levels, points, elements = thermal_reading.shape
    steps = levels // CHUNK
    rows = CHUNK * points
    vel = velocity_pair.reshape(2, levels * points, elements)
    temp = thermal_reading.reshape(levels * points, elements)
    dp = layer_depth.reshape(levels * points, elements)
    return pl.pallas_call(
        functools.partial(prep_kernel, elements),
        interpret=INTERPRET,
        grid=(steps,),
        in_specs=[
            pl.BlockSpec((2, rows, elements), lambda i: (0, i, 0)),
            pl.BlockSpec((rows, elements), lambda i: (i, 0)),
            pl.BlockSpec((rows, elements), lambda i: (i, 0)),
        ],
        out_specs=[
            pl.BlockSpec((4, 16, CHUNK, LANES), lambda i: (0, 0, i, 0)),
            pl.BlockSpec((16, 1, LANES), lambda i: (0, 0, 0)),
        ],
        out_shape=[
            jax.ShapeDtypeStruct((4, 16, levels, LANES), jnp.float32),
            jax.ShapeDtypeStruct((16, 1, LANES), jnp.float32),
        ],
    )(vel, temp, dp)


def local(
    velocity_pair,
    thermal_reading,
    layer_depth,
    jacobian_terms,
    rotation_frequency,
    integration_mass,
    shared_vertex_label,
    column_owner_slot,
):
    levels_dev = thermal_reading.shape[0]
    elements = thermal_reading.shape[2]
    seg_count = lax.axis_size("seg")
    lev_count = lax.axis_size("lev")
    rows_dev = elements // COLS
    node_cols = 3 * COLS
    first_row = 3 * rows_dev * lax.axis_index("seg")
    grid_rows = 3 * rows_dev * seg_count
    corner_ids = shared_vertex_label[0]
    element_pos = jnp.arange(elements)
    row_offset = (corner_ids // node_cols - first_row) % grid_rows - 3 * (element_pos // COLS)
    col_offset = (corner_ids % node_cols - 3 * (element_pos % COLS)) % node_cols
    rotation = jnp.where(
        row_offset == 0, jnp.where(col_offset == 0, 0, 1), jnp.where(col_offset == 3, 2, 3)
    )
    info = lane_info(rotation, elements)
    forward_order, _ = rotation_tables()

    fields, column_parts = prep_call(velocity_pair, thermal_reading, layer_depth)
    (
        mass_canon,
        mass_folded,
        mass_last,
        mass_first,
        mass,
        mass_one,
        jac,
        rot,
    ) = mass_call(integration_mass, jacobian_terms, rotation_frequency, info)
    mass_parts = mass_folded
    mass_edges = (mass_last, mass_first)
    column_mass = column_parts
    previous = None
    cells = None
    for substep in range(SUBSTEPS):
        above = carried_in(column_mass, "lev", False)
        g0, group_height = term_call(fields, above)
        below = carried_in(group_height, "lev", True)
        w, last, first = adv_call(
            fields, g0, below, jac, rot, mass_canon, info, elements, mass_edges
        )
        mass_edges = None
        halo_up, halo_down = edge_exchange(last, first)
        outs = fin_call(
            w,
            halo_up,
            halo_down,
            mass_parts,
            info,
            rows_dev,
            elements,
            previous if substep == SUBSTEPS - 1 else None,
            mass_one,
        )
        fields, column_parts = outs[:2]
        if substep == SUBSTEPS - 1:
            cells = outs[2]
        if substep == 0:
            mass_parts = outs[-1]
        previous = fields
        column_mass = column_parts
    channels = 4 * levels_dev
    cell_values = cells[..., :elements].reshape(4, channels, elements)
    payload = jnp.transpose(cell_values, (0, 2, 1)).reshape(4 * elements, channels)
    dev_count = seg_count * lev_count
    own_cols = 4 * elements * seg_count // dev_count
    per_pair = own_cols // seg_count
    capacity = per_pair + per_pair // 2
    targets = column_owner_slot.reshape(-1)
    owner_index = targets // own_cols
    slot_index = targets % own_cols
    cell_count = targets.shape[0]
    cell_pos = jnp.arange(cell_count)
    same_owner = owner_index[:, None] == owner_index[None, :]
    earlier = cell_pos[:, None] < cell_pos[None, :]
    rank = jnp.sum(jnp.logical_and(same_owner, earlier).astype(jnp.int32), axis=0)
    destination = owner_index * capacity + rank
    slots = jnp.arange(dev_count * capacity)
    code = cell_pos * (own_cols + 1) + slot_index + 1
    match = destination[:, None] == slots[None, :]
    found = jnp.sum(jnp.where(match, code[:, None], 0), axis=0)
    has = found > 0
    source_cell = jnp.maximum(found - 1, 0) // (own_cols + 1)
    source_pos = jnp.maximum(found - 1, 0) % (own_cols + 1)
    outgoing = payload[source_cell].reshape(dev_count, capacity, channels)
    ids = jnp.where(has, source_pos, -1).reshape(dev_count, capacity)
    received_ids = lax.all_to_all(ids, ("seg", "lev"), split_axis=0, concat_axis=0, tiled=True)
    flat = jnp.arange(dev_count * capacity).reshape(dev_count, capacity)
    source_lev = (jnp.arange(dev_count) % lev_count)[:, None]
    positions = jnp.arange(own_cols)
    picks = []
    for group in range(lev_count):
        hit = jnp.logical_and(
            received_ids[:, :, None] == positions[None, None, :], (source_lev == group)[:, :, None]
        )
        picks.append(jnp.sum(jnp.where(hit, flat[:, :, None], 0), axis=(0, 1)))
    received = lax.all_to_all(outgoing, ("seg", "lev"), split_axis=0, concat_axis=0, tiled=True)
    arrived = received.reshape(dev_count * capacity, channels)[jnp.stack(picks)]
    arrived = arrived.reshape(lev_count, own_cols, 4, levels_dev).transpose(2, 0, 3, 1)
    phys_state = arrived.reshape(4, lev_count * levels_dev, own_cols)
    mean_thickness = jnp.mean(phys_state[3], axis=0)
    dyn_state = jnp.transpose(fields[..., :elements], (0, 2, 1, 3))
    return (dyn_state, phys_state, mean_thickness)


def solution(mesh):
    in_specs = (
        P(None, "lev", None, "seg"),
        P("lev", None, "seg"),
        P("lev", None, "seg"),
        P(None, None, "seg"),
        P(None, "seg"),
        P(None, "seg"),
        P(None, "seg"),
        P(None, "seg"),
    )
    out_specs = (P(None, "lev", None, "seg"), P(None, None, ("seg", "lev")), P(("seg", "lev")))
    return jax.shard_map(local, mesh=mesh, in_specs=in_specs, out_specs=out_specs, check_vma=False)
```
